32 devices in a mesh: blk: 8 (over z, y), face: 4 (over x, core).
Axes of the slice: x: 2, y: 2, z: 4, core: 2. Of those that a mesh axis runs over, the one named last changes fastest.
Arguments:
- forcing: float32 [8, 4, 3, 64, 4096], P('blk', 'face'), may hold values from -6 to 6
- modulus: float32 [8, 4, 3], P('blk', 'face'), may hold values from 0.5 to 4
- orient_codes: int32 [8, 4], P('blk', 'face'), may hold values from 0 to 3
Outputs:
- displacement: float32 [8, 4, 3, 64, 4096], P('blk', 'face')
The draws below stay inside these ranges and needn't reach their ends.
All inputs are finite; a program needn't handle non-finite values.
Results may differ from the reference program's by a relative error of at most 0.0001.
Values sent between devices are 32-bit elements; how exact they have to be, the bound alone decides.
No kernel may reach another device: no remote copies, remote signals or barrier semaphores. Data moves between devices by JAX's collectives and lax.ppermute only.
A program may use at most 128 MiB of HBM per device.

```python
import math
import jax
import jax.numpy as jnp
from jax import lax

NODES = 64
ITERS = 2
NBX = 8
NBY = 4


def plant(entries, stream_key, low, high):
    index_at = [jax.random.randint(jax.random.fold_in(stream_key, axis), (), 0, length) for axis, length in enumerate(entries.shape)]
    longest = entries.shape.index(max(entries.shape))
    next_to = index_at[:longest] + [(index_at[longest] + 1) % entries.shape[longest]] + index_at[longest + 1:]
    return entries.at[tuple(index_at)].set(low).at[tuple(next_to)].set(high)


def shard_levels(rng, dims, split, least, high):
    loudness = 1.0
    for dim, parts in split:
        heights = jax.random.uniform(jax.random.fold_in(jax.random.fold_in(rng, 6), dim), (parts,), jnp.float32, least / len(split), high / len(split))
        loudness = loudness * jnp.repeat(jnp.exp(heights), dims[dim] // parts).reshape((-1,) + (1,) * (len(dims) - 1 - dim))
    return loudness


def bell_draw(key, shape, deviation, most, split=(), kind=jnp.bfloat16):
    gain = shard_levels(key, shape, split, -0.22, 0.18) if split else 1.0
    entries = jax.random.normal(key, shape, jnp.float32) * deviation * gain
    return jnp.minimum(jnp.maximum(entries, -most), most).astype(kind)


def setup_inputs(seed: int = 0) -> dict:
    key_of = jax.random.split(jax.random.key(seed), 4)
    return {
        "forcing": bell_draw(key_of[0], (NBX, NBY, 3, NODES, NODES * NODES), 1.0, 6.0, ((0, 8), (1, 4)), jnp.float32),
        "modulus": jnp.clip(jnp.exp(math.log(4.0) - 2.0794415 * jax.random.uniform(key_of[1], (NBX, NBY, 3), jnp.float32) ** shard_levels(key_of[1], (NBX, NBY, 3), ((0, 8), (1, 4)), -0.2, 0.2)), 0.5, 4.0),
        "orient_codes": plant(jax.random.randint(key_of[2], (NBX, NBY), 0, 4), jax.random.fold_in(key_of[2], 1), 0, 3).astype(jnp.int32),
    }


mass_shift = 0.02
inject_scale = 2.0
traction_mix = 0.5
penalty_mix = 0.25
lower_edge = 0.3
upper_edge = 1.5
highest = lax.Precision.HIGHEST

def tables(extent):
    node_index = jnp.arange(extent, dtype=jnp.float32) + 1.0
    basis = math.sqrt(2.0 / (extent + 1)) * jnp.sin(math.pi * node_index[:, None] * node_index[None, :] / (extent + 1))
    eigenvalues = 2.0 - 2.0 * jnp.cos(math.pi * node_index / (extent + 1))
    return (basis, eigenvalues)

def tangent_matrix(extent):
    node_index = jnp.arange(extent, dtype=jnp.int32)
    distance = jnp.abs(node_index[:, None] - node_index[None, :])
    end_rows = ((node_index == 0) | (node_index == extent - 1)).astype(jnp.float32)
    adjacent = (distance == 1).astype(jnp.float32)
    diagonal_part = (distance == 0).astype(jnp.float32) * (2.0 - end_rows[:, None])
    return adjacent - diagonal_part

def step_weights(step_count):
    midpoint = 0.5 * (upper_edge + lower_edge)
    radius = 0.5 * (upper_edge - lower_edge)
    return [1.0 / (midpoint + radius * math.cos(math.pi * (2 * turn_index + 1) / (2 * step_count))) for turn_index in range(step_count)]

def divisor(moduli, eigenvalues):
    extent = eigenvalues.shape[0]
    summed = eigenvalues[:, None, None] + eigenvalues[None, :, None] + eigenvalues[None, None, :]
    scaled = moduli[..., None, None, None] * summed + mass_shift
    return scaled.reshape(moduli.shape + (extent, extent * extent))

def transform(source_field, basis):
    extent = basis.shape[0]
    full_shape = source_field.shape
    cube_view = source_field.reshape(full_shape[:-1] + (extent, extent))
    cube_view = jnp.einsum('ix,...xyz->...iyz', basis, cube_view, precision=highest)
    cube_view = jnp.einsum('jy,...xyz->...xjz', basis, cube_view, precision=highest)
    cube_view = jnp.einsum('kz,...xyz->...xyk', basis, cube_view, precision=highest)
    return cube_view.reshape(full_shape)

def block_solve(right_side, moduli, basis, eigenvalues):
    return transform(transform(right_side, basis) / divisor(moduli, eigenvalues), basis)

def orient(face_field, code_table, extent):
    square = face_field.reshape(face_field.shape[:-1] + (extent, extent))
    flip_rows = (code_table % 2 == 1)[..., None, None, None]
    flip_cols = (code_table // 2 == 1)[..., None, None, None]
    square = jnp.where(flip_rows, jnp.flip(square, -2), square)
    square = jnp.where(flip_cols, jnp.flip(square, -1), square)
    return square.reshape(face_field.shape)

def face_data(solution, moduli):
    extent = solution.shape[-2]
    cube_view = solution.reshape(solution.shape[:-1] + (extent, extent))
    flat_shape = solution.shape[:-2] + (extent * extent,)

    def pack_side(planes):
        normal_slope = 11.0 / 6.0 * planes[0] - 3.0 * planes[1] + 1.5 * planes[2] - planes[3] / 3.0
        return (planes[0], moduli[..., None] * normal_slope)
    x_high = pack_side([solution[..., extent - 1 - plane_depth, :] for plane_depth in range(4)])
    x_low = pack_side([solution[..., plane_depth, :] for plane_depth in range(4)])
    y_high = pack_side([cube_view[..., extent - 1 - plane_depth, :].reshape(flat_shape) for plane_depth in range(4)])
    y_low = pack_side([cube_view[..., plane_depth, :].reshape(flat_shape) for plane_depth in range(4)])
    return (x_high, x_low, y_high, y_low)

def place_faces(source_field, moduli, x_low, x_high, y_low, y_high):
    extent = source_field.shape[-2]
    added = jnp.zeros_like(source_field)
    added = added.at[..., 0, :].add(x_low)
    added = added.at[..., extent - 1, :].add(x_high)
    cube_view = added.reshape(added.shape[:-1] + (extent, extent))
    low_square = y_low.reshape(y_low.shape[:-1] + (extent, extent))
    high_square = y_high.reshape(y_high.shape[:-1] + (extent, extent))
    cube_view = cube_view.at[..., 0, :].add(low_square)
    cube_view = cube_view.at[..., extent - 1, :].add(high_square)
    added = cube_view.reshape(source_field.shape)
    return source_field + inject_scale * moduli[..., None, None] * added

def trace_update(current, side_a, side_b, moduli_a, moduli_b, omega_step, tangent):
    extent = tangent.shape[0]
    weight_a = moduli_a[..., None]
    weight_b = moduli_b[..., None]
    residue = (weight_a * side_a[0] + weight_b * side_b[0] + traction_mix * (side_a[1] + side_b[1])) / (weight_a + weight_b) - current
    rows_view = residue.reshape(residue.shape[:-1] + (residue.shape[-1] // extent, extent))
    smoothed = rows_view + penalty_mix * jnp.einsum('...z,zk->...k', rows_view, tangent, precision=highest)
    return current + omega_step * smoothed.reshape(residue.shape)

def reference(forcing, modulus, orient_codes):
    slab_count = forcing.shape[0]
    extent = forcing.shape[3]
    basis, eigenvalues = tables(extent)
    tangent = tangent_matrix(extent)
    omegas = step_weights(ITERS)
    lam_x = jnp.zeros(forcing.shape[:3] + (extent * extent,), jnp.float32)
    lam_y = jnp.zeros(forcing.shape[:3] + (extent * extent,), jnp.float32)
    live_slab = (jnp.arange(slab_count) < slab_count - 1).astype(jnp.float32)[:, None, None, None]
    codes_below = jnp.concatenate([jnp.zeros_like(orient_codes[:1]), orient_codes[:-1]], 0)
    moduli_upper = jnp.concatenate([modulus[1:], jnp.zeros_like(modulus[:1])], 0)

    def solve_pair(block_pair):
        return block_solve(block_pair[0], block_pair[1], basis, eigenvalues)
    for sweep in range(ITERS + 1):
        x_low = orient(jnp.concatenate([jnp.zeros_like(lam_x[:1]), lam_x[:-1]], 0), codes_below, extent)
        y_low = jnp.roll(lam_y, 1, axis=1)
        right_side = place_faces(forcing, modulus, x_low, lam_x, y_low, lam_y)
        flat_rhs = right_side.reshape((-1,) + forcing.shape[2:])
        solution = lax.map(solve_pair, (flat_rhs, modulus.reshape(-1, 3))).reshape(forcing.shape)
        if sweep == ITERS:
            return solution
        x_high_side, x_low_side, y_high_side, y_low_side = face_data(solution, modulus)
        upper_value = orient(jnp.concatenate([x_low_side[0][1:], jnp.zeros_like(x_low_side[0][:1])], 0), orient_codes, extent)
        upper_slope = orient(jnp.concatenate([x_low_side[1][1:], jnp.zeros_like(x_low_side[1][:1])], 0), orient_codes, extent)
        lam_x = trace_update(lam_x, x_high_side, (upper_value, upper_slope), modulus, moduli_upper, omegas[sweep], tangent) * live_slab
        beside = (jnp.roll(y_low_side[0], -1, axis=1), jnp.roll(y_low_side[1], -1, axis=1))
        lam_y = trace_update(lam_y, y_high_side, beside, modulus, jnp.roll(modulus, -1, axis=1), omegas[sweep], tangent)
    return lam_x
```

```python
import math

import jax
import jax.numpy as jnp
from jax import lax
from jax.sharding import PartitionSpec as P
from jax.experimental import pallas as pl
from jax.experimental.pallas import tpu as pltpu
import numpy as np

ITERS = 2


mass_shift = 0.02
inject_scale = 2.0
traction_mix = 0.5
penalty_mix = 0.25
lower_edge = 0.3
upper_edge = 1.5
highest = lax.Precision.HIGHEST


def shifted(shard, axis, by):
    length = lax.axis_size(axis)
    pairs = [(i, i + by) for i in range(length) if 0 <= i + by < length]
    return lax.ppermute(shard, axis, pairs)


def shifted_2(shard, axis, by):
    length = lax.axis_size(axis)
    return lax.ppermute(shard, axis, [(i, (i + by) % length) for i in range(length)])


def tables(extent):
    node_index = jnp.arange(extent, dtype=jnp.float32) + 1.0
    basis = math.sqrt(2.0 / (extent + 1)) * jnp.sin(
        math.pi * node_index[:, None] * node_index[None, :] / (extent + 1)
    )
    eigenvalues = 2.0 - 2.0 * jnp.cos(math.pi * node_index / (extent + 1))
    return (basis, eigenvalues)


def tangent_matrix(extent):
    node_index = jnp.arange(extent, dtype=jnp.int32)
    distance = jnp.abs(node_index[:, None] - node_index[None, :])
    end_rows = ((node_index == 0) | (node_index == extent - 1)).astype(jnp.float32)
    adjacent = (distance == 1).astype(jnp.float32)
    diagonal_part = (distance == 0).astype(jnp.float32) * (2.0 - end_rows[:, None])
    return adjacent - diagonal_part


def step_weights(step_count):
    midpoint = 0.5 * (upper_edge + lower_edge)
    radius = 0.5 * (upper_edge - lower_edge)
    return [
        1.0 / (midpoint + radius * math.cos(math.pi * (2 * turn_index + 1) / (2 * step_count)))
        for turn_index in range(step_count)
    ]


def divisor(moduli, eigenvalues):
    extent = eigenvalues.shape[0]
    summed = eigenvalues[:, None, None] + eigenvalues[None, :, None] + eigenvalues[None, None, :]
    scaled = moduli[..., None, None, None] * summed + mass_shift
    return scaled.reshape(moduli.shape + (extent, extent * extent))


def body_transform(field_data, basis, paired_basis):
    extent = basis.shape[0]
    full_shape = field_data.shape
    pair_width = paired_basis.shape[0]
    sectioned = jnp.einsum("ix,bcxm->bcim", basis, field_data, precision=highest)
    sectioned = sectioned.reshape(full_shape[:-1] + (full_shape[-1] // pair_width, pair_width))
    sectioned = jnp.einsum("bcxpz,kz->bcxpk", sectioned, paired_basis, precision=highest)
    sectioned = sectioned.reshape(full_shape[:-1] + (extent, extent))
    sectioned = jnp.einsum("jy,bcxyz->bcxjz", basis, sectioned, precision=highest)
    return sectioned.reshape(full_shape)


def body_solve(right_side, scale_table, basis, paired_basis):
    return body_transform(
        body_transform(right_side, basis, paired_basis) / scale_table, basis, paired_basis
    )


HI = lax.Precision.HIGHEST
f32 = jnp.float32


def np_tables(n):
    g = np.float32
    idx = np.arange(n, dtype=g) + g(1.0)
    arg = (g(math.pi) * idx[:, None]) * idx[None, :] / g(n + 1)
    q = g(math.sqrt(2.0 / (n + 1))) * np.sin(arg)
    e = g(2.0) - g(2.0) * np.cos(g(math.pi) * idx / g(n + 1))
    return q.astype(g), e.astype(g)

def consts(n):
    q, e = np_tables(n)
    h = n // 2
    p = np.kron(np.eye(2, dtype=np.float32), q.T)
    qe = q[0::2]; qo = q[1::2]
    q00 = qe[:, 0::2]; q01 = qe[:, 1::2]; q10 = qo[:, 0::2]; q11 = qo[:, 1::2]
    mst = np.concatenate([np.concatenate([q00, q01], 1), np.concatenate([q11, q10], 1)], 0)
    lane = np.arange(2 * n) % n
    hh = np.arange(2 * n) // n
    ej = e[2 * np.arange(h)[:, None] + hh[None, :]]
    ek = np.ascontiguousarray(np.broadcast_to(e[lane][None, :], (h, 2 * n)))
    return q, p, mst, ej, ek, e

def solve_kernel(mod_ref, ex_ref, r_ref, q_ref, p_ref, mst_ref, ej_ref, ek_ref, o_ref, s_ref):
    n = q_ref.shape[0]
    h = n // 2
    nch = r_ref.shape[-1] // (2 * n)
    comp = pl.program_id(0)
    m = mod_ref[comp]
    q = q_ref[...]
    a = jnp.dot(q, r_ref[0], precision=HI, preferred_element_type=f32)
    for c in range(nch):
        s_ref[c * n:(c + 1) * n, :] = a[:, c * 2 * n:(c + 1) * 2 * n]
    s_ref[...] = jnp.dot(s_ref[...], p_ref[...], precision=HI, preferred_element_type=f32)
    mst = mst_ref[...]
    ej = ej_ref[...]
    ek = ek_ref[...]
    lane_lo = lax.broadcasted_iota(jnp.int32, (h, 2 * n), 1) < n
    G = 8

    def ycon(ys):
        zs = [jnp.concatenate([y, pltpu.roll(y, n, 1)], 0) for y in ys]
        w = jnp.dot(mst, jnp.concatenate(zs, 1), precision=HI, preferred_element_type=f32)
        out = []
        for t in range(len(ys)):
            wt = w[:, t * 2 * n:(t + 1) * 2 * n]
            out.append(jnp.where(lane_lo, wt[:h], wt[h:]))
        return out

    def body(g, carry):
        xs = [g * G + t for t in range(G)]
        ys = [s_ref[pl.ds(x, h, stride=n), :] for x in xs]
        ws = ycon(ys)
        ws = [w / (m * ((ex_ref[x] + ej) + ek) + 0.02) for w, x in zip(ws, xs)]
        ws = ycon(ws)
        for x, w in zip(xs, ws):
            s_ref[pl.ds(x, h, stride=n), :] = w
        return carry
    lax.fori_loop(0, n // G, body, 0)
    s_ref[...] = jnp.dot(s_ref[...], p_ref[...], precision=HI, preferred_element_type=f32)
    b = jnp.concatenate([s_ref[c * n:(c + 1) * n, :] for c in range(nch)], 1)
    o_ref[0] = jnp.dot(q, b, precision=HI, preferred_element_type=f32)

def kernel_solve(rhs, moduli, interpret=False):
    ncomp, n, nn = rhs.shape
    q, p, mst, ej, ek, e = consts(n)
    full = lambda shp: pl.BlockSpec(shp, lambda c: (0,) * len(shp))
    return pl.pallas_call(
        solve_kernel,
        grid=(ncomp,),
        in_specs=[pl.BlockSpec(memory_space=pltpu.SMEM), pl.BlockSpec(memory_space=pltpu.SMEM),
                  pl.BlockSpec((1, n, nn), lambda c: (c, 0, 0)),
                  full(q.shape), full(p.shape), full(mst.shape), full(ej.shape), full(ek.shape)],
        out_specs=pl.BlockSpec((1, n, nn), lambda c: (c, 0, 0)),
        out_shape=jax.ShapeDtypeStruct(rhs.shape, f32),
        scratch_shapes=[pltpu.VMEM((nn // 2, 2 * n), f32)],
        interpret=interpret,
    )(moduli, e, rhs, q, p, mst, ej, ek)


def orient(face_field, code_table, extent):
    square = face_field.reshape(face_field.shape[:-1] + (extent, extent))
    flip_rows = (code_table % 2 == 1)[..., None, None, None]
    flip_cols = (code_table // 2 == 1)[..., None, None, None]
    square = jnp.where(flip_rows, jnp.flip(square, -2), square)
    square = jnp.where(flip_cols, jnp.flip(square, -1), square)
    return square.reshape(face_field.shape)


def face_data(solution, moduli):
    extent = solution.shape[-2]
    cube_view = solution.reshape(solution.shape[:-1] + (extent, extent))
    flat_shape = solution.shape[:-2] + (extent * extent,)

    def pack_side(planes):
        normal_slope = 11.0 / 6.0 * planes[0] - 3.0 * planes[1] + 1.5 * planes[2] - planes[3] / 3.0
        return (planes[0], moduli[..., None] * normal_slope)

    x_high = pack_side([solution[..., extent - 1 - plane_depth, :] for plane_depth in range(4)])
    x_low = pack_side([solution[..., plane_depth, :] for plane_depth in range(4)])
    y_high = pack_side(
        [
            cube_view[..., extent - 1 - plane_depth, :].reshape(flat_shape)
            for plane_depth in range(4)
        ]
    )
    y_low = pack_side(
        [cube_view[..., plane_depth, :].reshape(flat_shape) for plane_depth in range(4)]
    )
    return (x_high, x_low, y_high, y_low)


def place_faces(source_field, moduli, x_low, x_high, y_low, y_high):
    extent = source_field.shape[-2]
    added = jnp.zeros_like(source_field)
    added = added.at[..., 0, :].add(x_low)
    added = added.at[..., extent - 1, :].add(x_high)
    cube_view = added.reshape(added.shape[:-1] + (extent, extent))
    low_square = y_low.reshape(y_low.shape[:-1] + (extent, extent))
    high_square = y_high.reshape(y_high.shape[:-1] + (extent, extent))
    cube_view = cube_view.at[..., 0, :].add(low_square)
    cube_view = cube_view.at[..., extent - 1, :].add(high_square)
    added = cube_view.reshape(source_field.shape)
    return source_field + inject_scale * moduli[..., None, None] * added


def trace_update(current, side_a, side_b, moduli_a, moduli_b, omega_step, tangent):
    extent = tangent.shape[0]
    weight_a = moduli_a[..., None]
    weight_b = moduli_b[..., None]
    residue = (
        weight_a * side_a[0] + weight_b * side_b[0] + traction_mix * (side_a[1] + side_b[1])
    ) / (weight_a + weight_b) - current
    rows_view = residue.reshape(residue.shape[:-1] + (residue.shape[-1] // extent, extent))
    smoothed = rows_view + penalty_mix * jnp.einsum(
        "...z,zk->...k", rows_view, tangent, precision=highest
    )
    return current + omega_step * smoothed.reshape(residue.shape)


def shards(forcing, modulus, orient_codes):
    extent = forcing.shape[3]
    blocks = forcing.shape[1]
    source_field = forcing[0]
    moduli = modulus[0]
    codes_here = orient_codes[0]
    basis, eigenvalues = tables(extent)
    paired_basis = jnp.kron(jnp.eye(2, dtype=jnp.float32), basis)
    scale_table = divisor(moduli, eigenvalues)
    tangent = tangent_matrix(extent)
    omegas = step_weights(ITERS)
    slab_count = lax.axis_size("blk")
    slab_index = lax.axis_index("blk")
    face_zeros = jnp.zeros((blocks, 3, extent * extent), jnp.float32)
    x_low = face_zeros
    x_high = face_zeros
    y_low = face_zeros
    y_high = face_zeros
    lam_x = face_zeros
    lam_y = face_zeros
    live_slab = (slab_index < slab_count - 1).astype(jnp.float32)
    solution = source_field
    for sweep in range(ITERS + 1):
        right_side = place_faces(source_field, moduli, x_low, x_high, y_low, y_high)
        solution = jnp.stack([kernel_solve(right_side[b], moduli[b]) for b in range(blocks)], 0)
        if sweep == ITERS:
            break
        x_high_side, x_low_side, y_high_side, y_low_side = face_data(solution, moduli)
        upper_value, upper_slope, upper_moduli = shifted(
            (x_low_side[0], x_low_side[1], moduli), "blk", -1
        )
        upper_value = orient(upper_value, codes_here, extent)
        upper_slope = orient(upper_slope, codes_here, extent)
        lam_x = (
            trace_update(
                lam_x,
                x_high_side,
                (upper_value, upper_slope),
                moduli,
                upper_moduli,
                omegas[sweep],
                tangent,
            )
            * live_slab
        )
        x_high = lam_x
        x_low = shifted(orient(lam_x, codes_here, extent), "blk", 1)
        next_value, next_slope, next_moduli = shifted_2(
            (y_low_side[0][0], y_low_side[1][0], moduli[0]), "face", -1
        )
        beside_value = jnp.concatenate([y_low_side[0][1:], next_value[None]], 0)
        beside_slope = jnp.concatenate([y_low_side[1][1:], next_slope[None]], 0)
        beside_moduli = jnp.concatenate([moduli[1:], next_moduli[None]], 0)
        lam_y = trace_update(
            lam_y,
            y_high_side,
            (beside_value, beside_slope),
            moduli,
            beside_moduli,
            omegas[sweep],
            tangent,
        )
        previous_trace = shifted_2(lam_y[blocks - 1], "face", 1)
        y_high = lam_y
        y_low = jnp.concatenate([previous_trace[None], lam_y[:-1]], 0)
    return solution[None]


def solution(mesh):
    placed = (P("blk", "face", None, None, None), P("blk", "face", None), P("blk", "face"))
    return jax.shard_map(
        shards,
        mesh=mesh,
        in_specs=placed,
        out_specs=P("blk", "face", None, None, None),
        check_vma=False,
    )
```

```python
import functools
import math

import jax
import jax.numpy as jnp
from jax import lax
from jax.sharding import PartitionSpec as P
from jax.experimental import pallas as pl
from jax.experimental.pallas import tpu as pltpu
import numpy as np

ITERS = 2


mass_shift = 0.02
inject_scale = 2.0
traction_mix = 0.5
penalty_mix = 0.25
lower_edge = 0.3
upper_edge = 1.5
highest = lax.Precision.HIGHEST


def shifted(shard, axis, by):
    length = lax.axis_size(axis)
    pairs = [(i, i + by) for i in range(length) if 0 <= i + by < length]
    return lax.ppermute(shard, axis, pairs)


def shifted_2(shard, axis, by):
    length = lax.axis_size(axis)
    return lax.ppermute(shard, axis, [(i, (i + by) % length) for i in range(length)])


def tables(extent):
    node_index = jnp.arange(extent, dtype=jnp.float32) + 1.0
    basis = math.sqrt(2.0 / (extent + 1)) * jnp.sin(
        math.pi * node_index[:, None] * node_index[None, :] / (extent + 1)
    )
    eigenvalues = 2.0 - 2.0 * jnp.cos(math.pi * node_index / (extent + 1))
    return (basis, eigenvalues)


def tangent_matrix(extent):
    node_index = jnp.arange(extent, dtype=jnp.int32)
    distance = jnp.abs(node_index[:, None] - node_index[None, :])
    end_rows = ((node_index == 0) | (node_index == extent - 1)).astype(jnp.float32)
    adjacent = (distance == 1).astype(jnp.float32)
    diagonal_part = (distance == 0).astype(jnp.float32) * (2.0 - end_rows[:, None])
    return adjacent - diagonal_part


def step_weights(step_count):
    midpoint = 0.5 * (upper_edge + lower_edge)
    radius = 0.5 * (upper_edge - lower_edge)
    return [
        1.0 / (midpoint + radius * math.cos(math.pi * (2 * turn_index + 1) / (2 * step_count)))
        for turn_index in range(step_count)
    ]


def divisor(moduli, eigenvalues):
    extent = eigenvalues.shape[0]
    summed = eigenvalues[:, None, None] + eigenvalues[None, :, None] + eigenvalues[None, None, :]
    scaled = moduli[..., None, None, None] * summed + mass_shift
    return scaled.reshape(moduli.shape + (extent, extent * extent))


def body_transform(field_data, basis, paired_basis):
    extent = basis.shape[0]
    full_shape = field_data.shape
    pair_width = paired_basis.shape[0]
    sectioned = jnp.einsum("ix,bcxm->bcim", basis, field_data, precision=highest)
    sectioned = sectioned.reshape(full_shape[:-1] + (full_shape[-1] // pair_width, pair_width))
    sectioned = jnp.einsum("bcxpz,kz->bcxpk", sectioned, paired_basis, precision=highest)
    sectioned = sectioned.reshape(full_shape[:-1] + (extent, extent))
    sectioned = jnp.einsum("jy,bcxyz->bcxjz", basis, sectioned, precision=highest)
    return sectioned.reshape(full_shape)


def body_solve(right_side, scale_table, basis, paired_basis):
    return body_transform(
        body_transform(right_side, basis, paired_basis) / scale_table, basis, paired_basis
    )


HI = lax.Precision.HIGHEST
f32 = jnp.float32


def np_tables(n):
    g = np.float32
    idx = np.arange(n, dtype=g) + g(1.0)
    arg = (g(math.pi) * idx[:, None]) * idx[None, :] / g(n + 1)
    q = g(math.sqrt(2.0 / (n + 1))) * np.sin(arg)
    e = g(2.0) - g(2.0) * np.cos(g(math.pi) * idx / g(n + 1))
    return q.astype(g), e.astype(g)

def consts(n):
    q, e = np_tables(n)
    h = n // 2
    p = np.kron(np.eye(2, dtype=np.float32), q.T)
    qe = q[0::2]; qo = q[1::2]
    q00 = qe[:, 0::2]; q01 = qe[:, 1::2]; q10 = qo[:, 0::2]; q11 = qo[:, 1::2]
    mst = np.concatenate([np.concatenate([q00, q01], 1), np.concatenate([q11, q10], 1)], 0)
    lane = np.arange(2 * n) % n
    hh = np.arange(2 * n) // n
    ej = e[2 * np.arange(h)[:, None] + hh[None, :]]
    ek = np.ascontiguousarray(np.broadcast_to(e[lane][None, :], (h, 2 * n)))
    return q, p, mst, ej, ek, e

def solve_kernel(*refs, with_faces, emit_u, emit_sides):
    it = iter(refs)
    mod_ref, ex_ref, f_ref = next(it), next(it), next(it)
    if with_faces:
        xlo_ref, xhi_ref, yadd_ref = next(it), next(it), next(it)
    q_ref, p_ref, mst_ref, ej_ref, ek_ref = next(it), next(it), next(it), next(it), next(it)
    o_ref = next(it) if emit_u else None
    if emit_sides:
        xf_ref, yf_ref = next(it), next(it)
    s_ref = next(it)
    n = q_ref.shape[0]
    h = n // 2
    w2 = 2 * n
    nn = f_ref.shape[-1]
    nch = nn // w2
    comp = pl.program_id(0)
    m = mod_ref[comp]
    q = q_ref[...]
    r = f_ref[0]
    if with_faces:
        rows = lax.broadcasted_iota(jnp.int32, (n, nn), 0)
        added = jnp.where(rows == 0, xlo_ref[0], 0.0) + jnp.where(rows == n - 1, xhi_ref[0], 0.0)
        lane = lax.broadcasted_iota(jnp.int32, (n, w2), 1)
        yadd = yadd_ref[0]
        first = added[:, :w2] + jnp.where(lane < n, yadd, 0.0)
        last = added[:, nn - w2:] + jnp.where(lane >= n, yadd, 0.0)
        added = jnp.concatenate([first, added[:, w2:nn - w2], last], 1)
        r = r + (2.0 * m) * added
    a = jnp.dot(q, r, precision=HI, preferred_element_type=f32)
    for c in range(nch):
        s_ref[c * n:(c + 1) * n, :] = a[:, c * w2:(c + 1) * w2]
    s_ref[...] = jnp.dot(s_ref[...], p_ref[...], precision=HI, preferred_element_type=f32)
    mst = mst_ref[...]
    ej = ej_ref[...]
    ek = ek_ref[...]
    lane_lo = lax.broadcasted_iota(jnp.int32, (h, w2), 1) < n
    G = 8

    def ycon(ys):
        zs = [jnp.concatenate([y, pltpu.roll(y, n, 1)], 0) for y in ys]
        w = jnp.dot(mst, jnp.concatenate(zs, 1), precision=HI, preferred_element_type=f32)
        out = []
        for t in range(len(ys)):
            wt = w[:, t * w2:(t + 1) * w2]
            out.append(jnp.where(lane_lo, wt[:h], wt[h:]))
        return out

    def body(g, carry):
        xs = [g * G + t for t in range(G)]
        ys = [s_ref[pl.ds(x, h, stride=n), :] for x in xs]
        ws = ycon(ys)
        ws = [w / (m * ((ex_ref[x] + ej) + ek) + 0.02) for w, x in zip(ws, xs)]
        ws = ycon(ws)
        for x, w in zip(xs, ws):
            s_ref[pl.ds(x, h, stride=n), :] = w
        return carry
    lax.fori_loop(0, n // G, body, 0)
    s_ref[...] = jnp.dot(s_ref[...], p_ref[...], precision=HI, preferred_element_type=f32)
    b = jnp.concatenate([s_ref[c * n:(c + 1) * n, :] for c in range(nch)], 1)
    u = jnp.dot(q, b, precision=HI, preferred_element_type=f32)
    if emit_u:
        o_ref[0] = u

    def slope(p0, p1, p2, p3):
        return m * (11.0 / 6.0 * p0 - 3.0 * p1 + 1.5 * p2 - p3 / 3.0)
    if emit_sides:
        xf_ref[0, 0:1, :] = u[n - 1:n]
        xf_ref[0, 1:2, :] = slope(u[n - 1:n], u[n - 2:n - 1], u[n - 3:n - 2], u[n - 4:n - 3])
        xf_ref[0, 2:3, :] = u[0:1]
        xf_ref[0, 3:4, :] = slope(u[0:1], u[1:2], u[2:3], u[3:4])
        c_hi = u[:, nn - w2:]
        c_hi2 = u[:, nn - 2 * w2:nn - w2]
        yf_ref[0, 0] = c_hi
        yf_ref[0, 1] = slope(c_hi, pltpu.roll(c_hi, n, 1), c_hi2, pltpu.roll(c_hi2, n, 1))
        c_lo = u[:, :w2]
        c_lo2 = u[:, w2:2 * w2]
        yf_ref[0, 2] = c_lo
        yf_ref[0, 3] = slope(c_lo, pltpu.roll(c_lo, n, 1), c_lo2, pltpu.roll(c_lo2, n, 1))


def kernel_sweep(rhs, moduli, faces=None, emit_u=True, emit_sides=False):
    ncomp, n, nn = rhs.shape
    q, p, mst, ej, ek, e = consts(n)
    full = lambda shp: pl.BlockSpec(shp, lambda c: (0,) * len(shp))
    comp3 = lambda shp: pl.BlockSpec((1,) + shp, lambda c: (c,) + (0,) * len(shp))
    smem = pl.BlockSpec(memory_space=pltpu.SMEM)
    in_specs = [smem, smem, comp3((n, nn))]
    args = [moduli, e, rhs]
    if faces is not None:
        xlo, xhi, yadd = faces
        in_specs += [comp3((1, nn)), comp3((1, nn)), comp3((n, 2 * n))]
        args += [xlo.reshape(ncomp, 1, nn), xhi.reshape(ncomp, 1, nn), yadd]
    in_specs += [full(q.shape), full(p.shape), full(mst.shape), full(ej.shape), full(ek.shape)]
    args += [q, p, mst, ej, ek]
    out_specs, out_shape = [], []
    if emit_u:
        out_specs.append(comp3((n, nn)))
        out_shape.append(jax.ShapeDtypeStruct(rhs.shape, f32))
    if emit_sides:
        out_specs += [comp3((4, nn)), comp3((4, n, 2 * n))]
        out_shape += [jax.ShapeDtypeStruct((ncomp, 4, nn), f32), jax.ShapeDtypeStruct((ncomp, 4, n, 2 * n), f32)]
    kernel = functools.partial(solve_kernel, with_faces=faces is not None, emit_u=emit_u, emit_sides=emit_sides)
    return pl.pallas_call(
        kernel,
        grid=(ncomp,),
        in_specs=in_specs,
        out_specs=out_specs,
        out_shape=out_shape,
        scratch_shapes=[pltpu.VMEM((nn // 2, 2 * n), f32)],
    )(*args)


def orient(face_field, code_table, extent):
    square = face_field.reshape(face_field.shape[:-1] + (extent, extent))
    flip_rows = (code_table % 2 == 1)[..., None, None, None]
    flip_cols = (code_table // 2 == 1)[..., None, None, None]
    square = jnp.where(flip_rows, jnp.flip(square, -2), square)
    square = jnp.where(flip_cols, jnp.flip(square, -1), square)
    return square.reshape(face_field.shape)


def face_data(solution, moduli):
    extent = solution.shape[-2]
    cube_view = solution.reshape(solution.shape[:-1] + (extent, extent))
    flat_shape = solution.shape[:-2] + (extent * extent,)

    def pack_side(planes):
        normal_slope = 11.0 / 6.0 * planes[0] - 3.0 * planes[1] + 1.5 * planes[2] - planes[3] / 3.0
        return (planes[0], moduli[..., None] * normal_slope)

    x_high = pack_side([solution[..., extent - 1 - plane_depth, :] for plane_depth in range(4)])
    x_low = pack_side([solution[..., plane_depth, :] for plane_depth in range(4)])
    y_high = pack_side(
        [
            cube_view[..., extent - 1 - plane_depth, :].reshape(flat_shape)
            for plane_depth in range(4)
        ]
    )
    y_low = pack_side(
        [cube_view[..., plane_depth, :].reshape(flat_shape) for plane_depth in range(4)]
    )
    return (x_high, x_low, y_high, y_low)


def place_faces(source_field, moduli, x_low, x_high, y_low, y_high):
    extent = source_field.shape[-2]
    added = jnp.zeros_like(source_field)
    added = added.at[..., 0, :].add(x_low)
    added = added.at[..., extent - 1, :].add(x_high)
    cube_view = added.reshape(added.shape[:-1] + (extent, extent))
    low_square = y_low.reshape(y_low.shape[:-1] + (extent, extent))
    high_square = y_high.reshape(y_high.shape[:-1] + (extent, extent))
    cube_view = cube_view.at[..., 0, :].add(low_square)
    cube_view = cube_view.at[..., extent - 1, :].add(high_square)
    added = cube_view.reshape(source_field.shape)
    return source_field + inject_scale * moduli[..., None, None] * added


def trace_update(current, side_a, side_b, moduli_a, moduli_b, omega_step, tangent):
    extent = tangent.shape[0]
    weight_a = moduli_a[..., None]
    weight_b = moduli_b[..., None]
    residue = (
        weight_a * side_a[0] + weight_b * side_b[0] + traction_mix * (side_a[1] + side_b[1])
    ) / (weight_a + weight_b) - current
    rows_view = residue.reshape(residue.shape[:-1] + (residue.shape[-1] // extent, extent))
    smoothed = rows_view + penalty_mix * jnp.einsum(
        "...z,zk->...k", rows_view, tangent, precision=highest
    )
    return current + omega_step * smoothed.reshape(residue.shape)


def shards(forcing, modulus, orient_codes):
    extent = forcing.shape[3]
    blocks = forcing.shape[1]
    flat = extent * extent
    source_field = forcing[0]
    moduli = modulus[0]
    codes_here = orient_codes[0]
    tangent = tangent_matrix(extent)
    omegas = step_weights(ITERS)
    slab_count = lax.axis_size("blk")
    slab_index = lax.axis_index("blk")
    face_zeros = jnp.zeros((blocks, 3, flat), jnp.float32)
    lam_x = face_zeros
    lam_y = face_zeros
    live_slab = (slab_index < slab_count - 1).astype(jnp.float32)
    faces = [None] * blocks
    for sweep in range(ITERS + 1):
        last = sweep == ITERS
        outs = [
            kernel_sweep(source_field[b], moduli[b], faces[b], emit_u=last, emit_sides=not last)
            for b in range(blocks)
        ]
        if last:
            return jnp.stack([o[0] for o in outs], 0)[None]
        xf = jnp.stack([o[0] for o in outs], 0)
        yf = jnp.stack([o[1] for o in outs], 0)
        x_high_side = (xf[:, :, 0], xf[:, :, 1])
        x_low_side = (xf[:, :, 2], xf[:, :, 3])
        y_high_side = tuple(yf[:, :, k, :, extent:].reshape(blocks, 3, flat) for k in (0, 1))
        y_low_side = tuple(yf[:, :, k, :, :extent].reshape(blocks, 3, flat) for k in (2, 3))
        upper_value, upper_slope, upper_moduli = shifted(
            (x_low_side[0], x_low_side[1], moduli), "blk", -1
        )
        upper_value = orient(upper_value, codes_here, extent)
        upper_slope = orient(upper_slope, codes_here, extent)
        lam_x = (
            trace_update(
                lam_x,
                x_high_side,
                (upper_value, upper_slope),
                moduli,
                upper_moduli,
                omegas[sweep],
                tangent,
            )
            * live_slab
        )
        x_high = lam_x
        x_low = shifted(orient(lam_x, codes_here, extent), "blk", 1)
        next_value, next_slope, next_moduli = shifted_2(
            (y_low_side[0][0], y_low_side[1][0], moduli[0]), "face", -1
        )
        beside_value = jnp.concatenate([y_low_side[0][1:], next_value[None]], 0)
        beside_slope = jnp.concatenate([y_low_side[1][1:], next_slope[None]], 0)
        beside_moduli = jnp.concatenate([moduli[1:], next_moduli[None]], 0)
        lam_y = trace_update(
            lam_y,
            y_high_side,
            (beside_value, beside_slope),
            moduli,
            beside_moduli,
            omegas[sweep],
            tangent,
        )
        previous_trace = shifted_2(lam_y[blocks - 1], "face", 1)
        y_high = lam_y
        y_low = jnp.concatenate([previous_trace[None], lam_y[:-1]], 0)
        yadd = jnp.concatenate(
            [y_low.reshape(blocks, 3, extent, extent), y_high.reshape(blocks, 3, extent, extent)], -1
        )
        faces = [(x_low[b], x_high[b], yadd[b]) for b in range(blocks)]


def solution(mesh):
    placed = (P("blk", "face", None, None, None), P("blk", "face", None), P("blk", "face"))
    return jax.shard_map(
        shards,
        mesh=mesh,
        in_specs=placed,
        out_specs=P("blk", "face", None, None, None),
        check_vma=False,
    )
```

```python
import functools
import math

import jax
import jax.numpy as jnp
from jax import lax
from jax.sharding import PartitionSpec as P
from jax.experimental import pallas as pl
from jax.experimental.pallas import tpu as pltpu
import numpy as np
import ml_dtypes

ITERS = 2


mass_shift = 0.02
inject_scale = 2.0
traction_mix = 0.5
penalty_mix = 0.25
lower_edge = 0.3
upper_edge = 1.5
highest = lax.Precision.HIGHEST


def shifted(shard, axis, by):
    length = lax.axis_size(axis)
    pairs = [(i, i + by) for i in range(length) if 0 <= i + by < length]
    return lax.ppermute(shard, axis, pairs)


def shifted_2(shard, axis, by):
    length = lax.axis_size(axis)
    return lax.ppermute(shard, axis, [(i, (i + by) % length) for i in range(length)])


def tables(extent):
    node_index = jnp.arange(extent, dtype=jnp.float32) + 1.0
    basis = math.sqrt(2.0 / (extent + 1)) * jnp.sin(
        math.pi * node_index[:, None] * node_index[None, :] / (extent + 1)
    )
    eigenvalues = 2.0 - 2.0 * jnp.cos(math.pi * node_index / (extent + 1))
    return (basis, eigenvalues)


def tangent_matrix(extent):
    node_index = jnp.arange(extent, dtype=jnp.int32)
    distance = jnp.abs(node_index[:, None] - node_index[None, :])
    end_rows = ((node_index == 0) | (node_index == extent - 1)).astype(jnp.float32)
    adjacent = (distance == 1).astype(jnp.float32)
    diagonal_part = (distance == 0).astype(jnp.float32) * (2.0 - end_rows[:, None])
    return adjacent - diagonal_part


def step_weights(step_count):
    midpoint = 0.5 * (upper_edge + lower_edge)
    radius = 0.5 * (upper_edge - lower_edge)
    return [
        1.0 / (midpoint + radius * math.cos(math.pi * (2 * turn_index + 1) / (2 * step_count)))
        for turn_index in range(step_count)
    ]


def divisor(moduli, eigenvalues):
    extent = eigenvalues.shape[0]
    summed = eigenvalues[:, None, None] + eigenvalues[None, :, None] + eigenvalues[None, None, :]
    scaled = moduli[..., None, None, None] * summed + mass_shift
    return scaled.reshape(moduli.shape + (extent, extent * extent))


def body_transform(field_data, basis, paired_basis):
    extent = basis.shape[0]
    full_shape = field_data.shape
    pair_width = paired_basis.shape[0]
    sectioned = jnp.einsum("ix,bcxm->bcim", basis, field_data, precision=highest)
    sectioned = sectioned.reshape(full_shape[:-1] + (full_shape[-1] // pair_width, pair_width))
    sectioned = jnp.einsum("bcxpz,kz->bcxpk", sectioned, paired_basis, precision=highest)
    sectioned = sectioned.reshape(full_shape[:-1] + (extent, extent))
    sectioned = jnp.einsum("jy,bcxyz->bcxjz", basis, sectioned, precision=highest)
    return sectioned.reshape(full_shape)


def body_solve(right_side, scale_table, basis, paired_basis):
    return body_transform(
        body_transform(right_side, basis, paired_basis) / scale_table, basis, paired_basis
    )


f32 = jnp.float32


def np_tables(n):
    g = np.float32
    idx = np.arange(n, dtype=g) + g(1.0)
    arg = (g(math.pi) * idx[:, None]) * idx[None, :] / g(n + 1)
    q = g(math.sqrt(2.0 / (n + 1))) * np.sin(arg)
    e = g(2.0) - g(2.0) * np.cos(g(math.pi) * idx / g(n + 1))
    return q.astype(g), e.astype(g)


def consts(n):
    q, e = np_tables(n)
    h = n // 2
    p4 = np.kron(np.eye(4, dtype=np.float32), q.T)
    w = np.zeros((2, 4, h, 2, 4, h), np.float32)
    qq = q.reshape(h, 2, h, 2)
    for xl in range(4):
        w[:, xl, :, :, xl, :] = np.transpose(qq, (3, 2, 1, 0))
    wy = w.reshape(8 * h, 8 * h)
    ng = n // 4
    lane_h = np.arange(8 * h) // (4 * h)
    lane_xl = (np.arange(8 * h) // h) % 4
    lane_c = np.arange(8 * h) % h
    exy = (e[4 * np.arange(ng)[:, None] + lane_xl[None, :]] + e[2 * lane_c + lane_h][None, :]).astype(np.float32)
    ez = np.ascontiguousarray(np.broadcast_to(e[:, None], (n, 8 * h))).astype(np.float32)
    return stack_left(q), stack_right(p4), stack_right(wy), exy, ez


BF = jnp.bfloat16

def np_split3(w):
    b = ml_dtypes.bfloat16
    w1 = w.astype(b)
    r1 = w - w1.astype(np.float32)
    w2 = r1.astype(b)
    w3 = (r1 - w2.astype(np.float32)).astype(b)
    return w1, w2, w3


def stack_right(w):
    w1, w2, w3 = np_split3(w)
    return np.concatenate([w1, w2, w3, w1, w2, w1], 0)


def stack_left(w):
    w1, w2, w3 = np_split3(w)
    return np.concatenate([w1, w2, w3, w1, w2, w1], 1)


def split3(d):
    d1 = d.astype(BF)
    r1 = d - d1.astype(f32)
    d2 = r1.astype(BF)
    d3 = (r1 - d2.astype(f32)).astype(BF)
    return d1, d2, d3


def sdot(d, w6):
    d1, d2, d3 = split3(d)
    return jnp.dot(jnp.concatenate([d1, d1, d1, d2, d2, d3], 1), w6, preferred_element_type=f32)


def sdot_left(w6, d):
    d1, d2, d3 = split3(d)
    return jnp.dot(w6, jnp.concatenate([d1, d1, d1, d2, d2, d3], 0), preferred_element_type=f32)


def solve_kernel(*refs, with_faces, emit_u, emit_sides):
    it = iter(refs)
    mod_ref, f_ref = next(it), next(it)
    if with_faces:
        xlo_ref, xhi_ref, yadd_ref = next(it), next(it), next(it)
    q_ref, p_ref, wy_ref, exy_ref, ez_ref = next(it), next(it), next(it), next(it), next(it)
    o_ref = next(it) if emit_u else None
    if emit_sides:
        xf_ref, yf_ref = next(it), next(it)
    s_ref, z_ref = next(it), next(it)
    n = q_ref.shape[0]
    h = n // 2
    w2 = 2 * n
    w4 = 4 * n
    nn = f_ref.shape[-1]
    nch = nn // w2
    npair = nn // w4
    comp = pl.program_id(0)
    m = mod_ref[comp]
    q = q_ref[...]
    r = f_ref[0]
    if with_faces:
        rows = lax.broadcasted_iota(jnp.int32, (n, nn), 0)
        added = jnp.where(rows == 0, xlo_ref[0], 0.0) + jnp.where(rows == n - 1, xhi_ref[0], 0.0)
        lane = lax.broadcasted_iota(jnp.int32, (n, w2), 1)
        yadd = yadd_ref[0]
        first = added[:, :w2] + jnp.where(lane < n, yadd, 0.0)
        last = added[:, nn - w2:] + jnp.where(lane >= n, yadd, 0.0)
        added = jnp.concatenate([first, added[:, w2:nn - w2], last], 1)
        r = r + (2.0 * m) * added
    a = sdot_left(q, r)
    for cp in range(npair):
        z_ref[cp * n:(cp + 1) * n, :] = a[:, cp * w4:(cp + 1) * w4]
    zo = sdot(z_ref[...], p_ref[...])
    for cp in range(npair):
        for cb in range(2):
            s_ref[(2 * cp + cb) * n:(2 * cp + cb + 1) * n, :] = zo[cp * n:(cp + 1) * n, cb * w2:(cb + 1) * w2]
    wy = wy_ref[...]
    ez = ez_ref[...]
    XG = 4
    GPI = 4

    def body(it_, carry):
        lhs = []
        for gi in range(GPI):
            g = it_ * GPI + gi
            blk = jnp.concatenate([s_ref[pl.ds(g * XG + xl, h, stride=n), :] for xl in range(XG)], 0)
            tb = blk.T
            lhs.append(jnp.concatenate([tb[:n], tb[n:]], 1))
        v = sdot(jnp.concatenate(lhs, 0), wy)
        div = jnp.concatenate([m * (exy_ref[pl.ds(it_ * GPI + gi, 1), :] + ez) + 0.02 for gi in range(GPI)], 0)
        v = v / div
        v = sdot(v, wy)
        for gi in range(GPI):
            g = it_ * GPI + gi
            vg = v[gi * n:(gi + 1) * n]
            tb = jnp.concatenate([vg[:, :w2], vg[:, w2:]], 0).T
            for xl in range(XG):
                s_ref[pl.ds(g * XG + xl, h, stride=n), :] = tb[xl * h:(xl + 1) * h]
        return carry
    lax.fori_loop(0, n // (XG * GPI), body, 0)
    for cp in range(npair):
        z_ref[cp * n:(cp + 1) * n, :] = jnp.concatenate(
            [s_ref[(2 * cp) * n:(2 * cp + 1) * n, :], s_ref[(2 * cp + 1) * n:(2 * cp + 2) * n, :]], 1)
    zo = sdot(z_ref[...], p_ref[...])
    b = jnp.concatenate([zo[cp * n:(cp + 1) * n, :] for cp in range(npair)], 1)
    u = sdot_left(q, b)
    if emit_u:
        o_ref[0] = u

    def slope(p0, p1, p2, p3):
        return m * (11.0 / 6.0 * p0 - 3.0 * p1 + 1.5 * p2 - p3 / 3.0)
    if emit_sides:
        xf_ref[0, 0:1, :] = u[n - 1:n]
        xf_ref[0, 1:2, :] = slope(u[n - 1:n], u[n - 2:n - 1], u[n - 3:n - 2], u[n - 4:n - 3])
        xf_ref[0, 2:3, :] = u[0:1]
        xf_ref[0, 3:4, :] = slope(u[0:1], u[1:2], u[2:3], u[3:4])
        c_hi = u[:, nn - w2:]
        c_hi2 = u[:, nn - 2 * w2:nn - w2]
        yf_ref[0, 0] = c_hi
        yf_ref[0, 1] = slope(c_hi, pltpu.roll(c_hi, n, 1), c_hi2, pltpu.roll(c_hi2, n, 1))
        c_lo = u[:, :w2]
        c_lo2 = u[:, w2:2 * w2]
        yf_ref[0, 2] = c_lo
        yf_ref[0, 3] = slope(c_lo, pltpu.roll(c_lo, n, 1), c_lo2, pltpu.roll(c_lo2, n, 1))


def kernel_sweep(rhs, moduli, faces=None, emit_u=True, emit_sides=False, interpret=False):
    ncomp, n, nn = rhs.shape
    q, p4, wy, exy, ez = consts(n)
    full = lambda shp: pl.BlockSpec(shp, lambda c: (0,) * len(shp))
    comp3 = lambda shp: pl.BlockSpec((1,) + shp, lambda c: (c,) + (0,) * len(shp))
    smem = pl.BlockSpec(memory_space=pltpu.SMEM)
    in_specs = [smem, comp3((n, nn))]
    args = [moduli, rhs]
    if faces is not None:
        xlo, xhi, yadd = faces
        in_specs += [comp3((1, nn)), comp3((1, nn)), comp3((n, 2 * n))]
        args += [xlo.reshape(ncomp, 1, nn), xhi.reshape(ncomp, 1, nn), yadd]
    in_specs += [full(q.shape), full(p4.shape), full(wy.shape), full(exy.shape), full(ez.shape)]
    args += [q, p4, wy, exy, ez]
    out_specs, out_shape = [], []
    if emit_u:
        out_specs.append(comp3((n, nn)))
        out_shape.append(jax.ShapeDtypeStruct(rhs.shape, f32))
    if emit_sides:
        out_specs += [comp3((4, nn)), comp3((4, n, 2 * n))]
        out_shape += [jax.ShapeDtypeStruct((ncomp, 4, nn), f32), jax.ShapeDtypeStruct((ncomp, 4, n, 2 * n), f32)]
    kernel = functools.partial(solve_kernel, with_faces=faces is not None, emit_u=emit_u, emit_sides=emit_sides)
    return pl.pallas_call(
        kernel,
        grid=(ncomp,),
        in_specs=in_specs,
        out_specs=out_specs,
        out_shape=out_shape,
        scratch_shapes=[pltpu.VMEM((nn // 2, 2 * n), f32), pltpu.VMEM((nn // 4, 4 * n), f32)],
        interpret=interpret,
    )(*args)


def orient(face_field, code_table, extent):
    square = face_field.reshape(face_field.shape[:-1] + (extent, extent))
    flip_rows = (code_table % 2 == 1)[..., None, None, None]
    flip_cols = (code_table // 2 == 1)[..., None, None, None]
    square = jnp.where(flip_rows, jnp.flip(square, -2), square)
    square = jnp.where(flip_cols, jnp.flip(square, -1), square)
    return square.reshape(face_field.shape)


def face_data(solution, moduli):
    extent = solution.shape[-2]
    cube_view = solution.reshape(solution.shape[:-1] + (extent, extent))
    flat_shape = solution.shape[:-2] + (extent * extent,)

    def pack_side(planes):
        normal_slope = 11.0 / 6.0 * planes[0] - 3.0 * planes[1] + 1.5 * planes[2] - planes[3] / 3.0
        return (planes[0], moduli[..., None] * normal_slope)

    x_high = pack_side([solution[..., extent - 1 - plane_depth, :] for plane_depth in range(4)])
    x_low = pack_side([solution[..., plane_depth, :] for plane_depth in range(4)])
    y_high = pack_side(
        [
            cube_view[..., extent - 1 - plane_depth, :].reshape(flat_shape)
            for plane_depth in range(4)
        ]
    )
    y_low = pack_side(
        [cube_view[..., plane_depth, :].reshape(flat_shape) for plane_depth in range(4)]
    )
    return (x_high, x_low, y_high, y_low)


def place_faces(source_field, moduli, x_low, x_high, y_low, y_high):
    extent = source_field.shape[-2]
    added = jnp.zeros_like(source_field)
    added = added.at[..., 0, :].add(x_low)
    added = added.at[..., extent - 1, :].add(x_high)
    cube_view = added.reshape(added.shape[:-1] + (extent, extent))
    low_square = y_low.reshape(y_low.shape[:-1] + (extent, extent))
    high_square = y_high.reshape(y_high.shape[:-1] + (extent, extent))
    cube_view = cube_view.at[..., 0, :].add(low_square)
    cube_view = cube_view.at[..., extent - 1, :].add(high_square)
    added = cube_view.reshape(source_field.shape)
    return source_field + inject_scale * moduli[..., None, None] * added


def trace_update(current, side_a, side_b, moduli_a, moduli_b, omega_step, tangent):
    extent = tangent.shape[0]
    weight_a = moduli_a[..., None]
    weight_b = moduli_b[..., None]
    residue = (
        weight_a * side_a[0] + weight_b * side_b[0] + traction_mix * (side_a[1] + side_b[1])
    ) / (weight_a + weight_b) - current
    rows_view = residue.reshape(residue.shape[:-1] + (residue.shape[-1] // extent, extent))
    smoothed = rows_view + penalty_mix * jnp.einsum(
        "...z,zk->...k", rows_view, tangent, precision=highest
    )
    return current + omega_step * smoothed.reshape(residue.shape)


def shards(forcing, modulus, orient_codes):
    extent = forcing.shape[3]
    blocks = forcing.shape[1]
    flat = extent * extent
    source_field = forcing[0]
    moduli = modulus[0]
    codes_here = orient_codes[0]
    tangent = tangent_matrix(extent)
    omegas = step_weights(ITERS)
    slab_count = lax.axis_size("blk")
    slab_index = lax.axis_index("blk")
    face_zeros = jnp.zeros((blocks, 3, flat), jnp.float32)
    lam_x = face_zeros
    lam_y = face_zeros
    live_slab = (slab_index < slab_count - 1).astype(jnp.float32)
    faces = [None] * blocks
    for sweep in range(ITERS + 1):
        last = sweep == ITERS
        outs = [
            kernel_sweep(source_field[b], moduli[b], faces[b], emit_u=last, emit_sides=not last)
            for b in range(blocks)
        ]
        if last:
            return jnp.stack([o[0] for o in outs], 0)[None]
        xf = jnp.stack([o[0] for o in outs], 0)
        yf = jnp.stack([o[1] for o in outs], 0)
        x_high_side = (xf[:, :, 0], xf[:, :, 1])
        x_low_side = (xf[:, :, 2], xf[:, :, 3])
        y_high_side = tuple(yf[:, :, k, :, extent:].reshape(blocks, 3, flat) for k in (0, 1))
        y_low_side = tuple(yf[:, :, k, :, :extent].reshape(blocks, 3, flat) for k in (2, 3))
        upper_value, upper_slope, upper_moduli = shifted(
            (x_low_side[0], x_low_side[1], moduli), "blk", -1
        )
        upper_value = orient(upper_value, codes_here, extent)
        upper_slope = orient(upper_slope, codes_here, extent)
        lam_x = (
            trace_update(
                lam_x,
                x_high_side,
                (upper_value, upper_slope),
                moduli,
                upper_moduli,
                omegas[sweep],
                tangent,
            )
            * live_slab
        )
        x_high = lam_x
        x_low = shifted(orient(lam_x, codes_here, extent), "blk", 1)
        next_value, next_slope, next_moduli = shifted_2(
            (y_low_side[0][0], y_low_side[1][0], moduli[0]), "face", -1
        )
        beside_value = jnp.concatenate([y_low_side[0][1:], next_value[None]], 0)
        beside_slope = jnp.concatenate([y_low_side[1][1:], next_slope[None]], 0)
        beside_moduli = jnp.concatenate([moduli[1:], next_moduli[None]], 0)
        lam_y = trace_update(
            lam_y,
            y_high_side,
            (beside_value, beside_slope),
            moduli,
            beside_moduli,
            omegas[sweep],
            tangent,
        )
        previous_trace = shifted_2(lam_y[blocks - 1], "face", 1)
        y_high = lam_y
        y_low = jnp.concatenate([previous_trace[None], lam_y[:-1]], 0)
        yadd = jnp.concatenate(
            [y_low.reshape(blocks, 3, extent, extent), y_high.reshape(blocks, 3, extent, extent)], -1
        )
        faces = [(x_low[b], x_high[b], yadd[b]) for b in range(blocks)]


def solution(mesh):
    placed = (P("blk", "face", None, None, None), P("blk", "face", None), P("blk", "face"))
    return jax.shard_map(
        shards,
        mesh=mesh,
        in_specs=placed,
        out_specs=P("blk", "face", None, None, None),
        check_vma=False,
    )
```

```python
import functools
import math

import jax
import jax.numpy as jnp
from jax import lax
from jax.sharding import PartitionSpec as P
from jax.experimental import pallas as pl
from jax.experimental.pallas import tpu as pltpu
import numpy as np
import ml_dtypes

ITERS = 2


mass_shift = 0.02
inject_scale = 2.0
traction_mix = 0.5
penalty_mix = 0.25
lower_edge = 0.3
upper_edge = 1.5
highest = lax.Precision.HIGHEST


def shifted(shard, axis, by):
    length = lax.axis_size(axis)
    pairs = [(i, i + by) for i in range(length) if 0 <= i + by < length]
    return lax.ppermute(shard, axis, pairs)


def shifted_2(shard, axis, by):
    length = lax.axis_size(axis)
    return lax.ppermute(shard, axis, [(i, (i + by) % length) for i in range(length)])


def tables(extent):
    node_index = jnp.arange(extent, dtype=jnp.float32) + 1.0
    basis = math.sqrt(2.0 / (extent + 1)) * jnp.sin(
        math.pi * node_index[:, None] * node_index[None, :] / (extent + 1)
    )
    eigenvalues = 2.0 - 2.0 * jnp.cos(math.pi * node_index / (extent + 1))
    return (basis, eigenvalues)


def tangent_matrix(extent):
    node_index = jnp.arange(extent, dtype=jnp.int32)
    distance = jnp.abs(node_index[:, None] - node_index[None, :])
    end_rows = ((node_index == 0) | (node_index == extent - 1)).astype(jnp.float32)
    adjacent = (distance == 1).astype(jnp.float32)
    diagonal_part = (distance == 0).astype(jnp.float32) * (2.0 - end_rows[:, None])
    return adjacent - diagonal_part


def step_weights(step_count):
    midpoint = 0.5 * (upper_edge + lower_edge)
    radius = 0.5 * (upper_edge - lower_edge)
    return [
        1.0 / (midpoint + radius * math.cos(math.pi * (2 * turn_index + 1) / (2 * step_count)))
        for turn_index in range(step_count)
    ]


def divisor(moduli, eigenvalues):
    extent = eigenvalues.shape[0]
    summed = eigenvalues[:, None, None] + eigenvalues[None, :, None] + eigenvalues[None, None, :]
    scaled = moduli[..., None, None, None] * summed + mass_shift
    return scaled.reshape(moduli.shape + (extent, extent * extent))


def body_transform(field_data, basis, paired_basis):
    extent = basis.shape[0]
    full_shape = field_data.shape
    pair_width = paired_basis.shape[0]
    sectioned = jnp.einsum("ix,bcxm->bcim", basis, field_data, precision=highest)
    sectioned = sectioned.reshape(full_shape[:-1] + (full_shape[-1] // pair_width, pair_width))
    sectioned = jnp.einsum("bcxpz,kz->bcxpk", sectioned, paired_basis, precision=highest)
    sectioned = sectioned.reshape(full_shape[:-1] + (extent, extent))
    sectioned = jnp.einsum("jy,bcxyz->bcxjz", basis, sectioned, precision=highest)
    return sectioned.reshape(full_shape)


def body_solve(right_side, scale_table, basis, paired_basis):
    return body_transform(
        body_transform(right_side, basis, paired_basis) / scale_table, basis, paired_basis
    )


f32 = jnp.float32


def np_tables(n):
    g = np.float32
    idx = np.arange(n, dtype=g) + g(1.0)
    arg = (g(math.pi) * idx[:, None]) * idx[None, :] / g(n + 1)
    q = g(math.sqrt(2.0 / (n + 1))) * np.sin(arg)
    e = g(2.0) - g(2.0) * np.cos(g(math.pi) * idx / g(n + 1))
    return q.astype(g), e.astype(g)


def consts(n):
    q, e = np_tables(n)
    h = n // 2
    p4 = np.kron(np.eye(4, dtype=np.float32), q.T)
    w = np.zeros((2, 4, h, 2, 4, h), np.float32)
    qq = q.reshape(h, 2, h, 2)
    for xl in range(4):
        w[:, xl, :, :, xl, :] = np.transpose(qq, (3, 2, 1, 0))
    wy = w.reshape(8 * h, 8 * h)
    ng = n // 4
    lane_h = np.arange(8 * h) // (4 * h)
    lane_xl = (np.arange(8 * h) // h) % 4
    lane_c = np.arange(8 * h) % h
    exy = (e[4 * np.arange(ng)[:, None] + lane_xl[None, :]] + e[2 * lane_c + lane_h][None, :]).astype(np.float32)
    ez = np.ascontiguousarray(np.broadcast_to(e[:, None], (n, 8 * h))).astype(np.float32)
    return stack_left(q), stack_right(p4), stack_right(wy), exy, ez


BF = jnp.bfloat16

def np_split3(w):
    b = ml_dtypes.bfloat16
    w1 = w.astype(b)
    r1 = w - w1.astype(np.float32)
    w2 = r1.astype(b)
    w3 = (r1 - w2.astype(np.float32)).astype(b)
    return w1, w2, w3


def stack_right(w):
    w1, w2, w3 = np_split3(w)
    return np.concatenate([w1, w2, w3, w1, w2, w1], 0)


def stack_left(w):
    w1, w2, w3 = np_split3(w)
    return np.concatenate([w1, w2, w3, w1, w2, w1], 1)


def split3(d):
    d1 = d.astype(BF)
    r1 = d - d1.astype(f32)
    d2 = r1.astype(BF)
    d3 = (r1 - d2.astype(f32)).astype(BF)
    return d1, d2, d3


def sdot(d, w6):
    d1, d2, d3 = split3(d)
    return jnp.dot(jnp.concatenate([d1, d1, d1, d2, d2, d3], 1), w6, preferred_element_type=f32)


def sdot_left(w6, d):
    d1, d2, d3 = split3(d)
    return jnp.dot(w6, jnp.concatenate([d1, d1, d1, d2, d2, d3], 0), preferred_element_type=f32)


def solve_kernel(*refs, with_faces, emit_u, emit_sides):
    it = iter(refs)
    mod_ref, f_ref = next(it), next(it)
    if with_faces:
        xlo_ref, xhi_ref, yadd_ref = next(it), next(it), next(it)
    q_ref, p_ref, wy_ref, exy_ref, ez_ref = next(it), next(it), next(it), next(it), next(it)
    o_ref = next(it) if emit_u else None
    if emit_sides:
        xf_ref, yf_ref = next(it), next(it)
    s_ref, z_ref = next(it), next(it)
    n = q_ref.shape[0]
    h = n // 2
    w2 = 2 * n
    w4 = 4 * n
    nn = f_ref.shape[-1]
    nch = nn // w2
    npair = nn // w4
    comp = pl.program_id(0)
    m = mod_ref[comp]
    q = q_ref[...]
    r = f_ref[0]
    if with_faces:
        rows = lax.broadcasted_iota(jnp.int32, (n, nn), 0)
        added = jnp.where(rows == 0, xlo_ref[0], 0.0) + jnp.where(rows == n - 1, xhi_ref[0], 0.0)
        lane = lax.broadcasted_iota(jnp.int32, (n, w2), 1)
        yadd = yadd_ref[0]
        first = added[:, :w2] + jnp.where(lane < n, yadd, 0.0)
        last = added[:, nn - w2:] + jnp.where(lane >= n, yadd, 0.0)
        added = jnp.concatenate([first, added[:, w2:nn - w2], last], 1)
        r = r + (2.0 * m) * added
    a = sdot_left(q, r)
    for cp in range(npair):
        z_ref[cp * n:(cp + 1) * n, :] = a[:, cp * w4:(cp + 1) * w4]
    zo = sdot(z_ref[...], p_ref[...])
    for cp in range(npair):
        for cb in range(2):
            s_ref[(2 * cp + cb) * n:(2 * cp + cb + 1) * n, :] = zo[cp * n:(cp + 1) * n, cb * w2:(cb + 1) * w2]
    wy = wy_ref[...]
    ez = ez_ref[...]
    XG = 4
    GPI = 4

    def body(it_, carry):
        lhs = []
        for gi in range(GPI):
            g = it_ * GPI + gi
            blk = jnp.concatenate([s_ref[pl.ds(g * XG + xl, h, stride=n), :] for xl in range(XG)], 0)
            tb = blk.T
            lhs.append(jnp.concatenate([tb[:n], tb[n:]], 1))
        v = sdot(jnp.concatenate(lhs, 0), wy)
        div = jnp.concatenate([m * (exy_ref[pl.ds(it_ * GPI + gi, 1), :] + ez) + 0.02 for gi in range(GPI)], 0)
        v = v / div
        v = sdot(v, wy)
        for gi in range(GPI):
            g = it_ * GPI + gi
            vg = v[gi * n:(gi + 1) * n]
            tb = jnp.concatenate([vg[:, :w2], vg[:, w2:]], 0).T
            for xl in range(XG):
                s_ref[pl.ds(g * XG + xl, h, stride=n), :] = tb[xl * h:(xl + 1) * h]
        return carry
    lax.fori_loop(0, n // (XG * GPI), body, 0)
    for cp in range(npair):
        z_ref[cp * n:(cp + 1) * n, :] = jnp.concatenate(
            [s_ref[(2 * cp) * n:(2 * cp + 1) * n, :], s_ref[(2 * cp + 1) * n:(2 * cp + 2) * n, :]], 1)
    zo = sdot(z_ref[...], p_ref[...])
    b = jnp.concatenate([zo[cp * n:(cp + 1) * n, :] for cp in range(npair)], 1)
    u = sdot_left(q, b)
    if emit_u:
        o_ref[0] = u

    def slope(p0, p1, p2, p3):
        return m * (11.0 / 6.0 * p0 - 3.0 * p1 + 1.5 * p2 - p3 / 3.0)
    if emit_sides:
        xf_ref[0, 0:1, :] = u[n - 1:n]
        xf_ref[0, 1:2, :] = slope(u[n - 1:n], u[n - 2:n - 1], u[n - 3:n - 2], u[n - 4:n - 3])
        xf_ref[0, 2:3, :] = u[0:1]
        xf_ref[0, 3:4, :] = slope(u[0:1], u[1:2], u[2:3], u[3:4])
        c_hi = u[:, nn - w2:]
        c_hi2 = u[:, nn - 2 * w2:nn - w2]
        yf_ref[0, 0] = c_hi
        yf_ref[0, 1] = slope(c_hi, pltpu.roll(c_hi, n, 1), c_hi2, pltpu.roll(c_hi2, n, 1))
        c_lo = u[:, :w2]
        c_lo2 = u[:, w2:2 * w2]
        yf_ref[0, 2] = c_lo
        yf_ref[0, 3] = slope(c_lo, pltpu.roll(c_lo, n, 1), c_lo2, pltpu.roll(c_lo2, n, 1))


def kernel_sweep(rhs, moduli, faces=None, emit_u=True, emit_sides=False, interpret=False):
    ncomp, n, nn = rhs.shape
    q, p4, wy, exy, ez = consts(n)
    full = lambda shp: pl.BlockSpec(shp, lambda c: (0,) * len(shp))
    comp3 = lambda shp: pl.BlockSpec((1,) + shp, lambda c: (c,) + (0,) * len(shp))
    smem = pl.BlockSpec(memory_space=pltpu.SMEM)
    in_specs = [smem, comp3((n, nn))]
    args = [moduli, rhs]
    if faces is not None:
        xlo, xhi, yadd = faces
        in_specs += [comp3((1, nn)), comp3((1, nn)), comp3((n, 2 * n))]
        args += [xlo.reshape(ncomp, 1, nn), xhi.reshape(ncomp, 1, nn), yadd]
    in_specs += [full(q.shape), full(p4.shape), full(wy.shape), full(exy.shape), full(ez.shape)]
    args += [q, p4, wy, exy, ez]
    out_specs, out_shape = [], []
    if emit_u:
        out_specs.append(comp3((n, nn)))
        out_shape.append(jax.ShapeDtypeStruct(rhs.shape, f32))
    if emit_sides:
        out_specs += [comp3((4, nn)), comp3((4, n, 2 * n))]
        out_shape += [jax.ShapeDtypeStruct((ncomp, 4, nn), f32), jax.ShapeDtypeStruct((ncomp, 4, n, 2 * n), f32)]
    kernel = functools.partial(solve_kernel, with_faces=faces is not None, emit_u=emit_u, emit_sides=emit_sides)
    return pl.pallas_call(
        kernel,
        grid=(ncomp,),
        in_specs=in_specs,
        out_specs=out_specs,
        out_shape=out_shape,
        scratch_shapes=[pltpu.VMEM((nn // 2, 2 * n), f32), pltpu.VMEM((nn // 4, 4 * n), f32)],
        interpret=interpret,
    )(*args)


def orient(face_field, code_table, extent):
    square = face_field.reshape(face_field.shape[:-1] + (extent, extent))
    flip_rows = (code_table % 2 == 1)[..., None, None, None]
    flip_cols = (code_table // 2 == 1)[..., None, None, None]
    square = jnp.where(flip_rows, jnp.flip(square, -2), square)
    square = jnp.where(flip_cols, jnp.flip(square, -1), square)
    return square.reshape(face_field.shape)


def face_data(solution, moduli):
    extent = solution.shape[-2]
    cube_view = solution.reshape(solution.shape[:-1] + (extent, extent))
    flat_shape = solution.shape[:-2] + (extent * extent,)

    def pack_side(planes):
        normal_slope = 11.0 / 6.0 * planes[0] - 3.0 * planes[1] + 1.5 * planes[2] - planes[3] / 3.0
        return (planes[0], moduli[..., None] * normal_slope)

    x_high = pack_side([solution[..., extent - 1 - plane_depth, :] for plane_depth in range(4)])
    x_low = pack_side([solution[..., plane_depth, :] for plane_depth in range(4)])
    y_high = pack_side(
        [
            cube_view[..., extent - 1 - plane_depth, :].reshape(flat_shape)
            for plane_depth in range(4)
        ]
    )
    y_low = pack_side(
        [cube_view[..., plane_depth, :].reshape(flat_shape) for plane_depth in range(4)]
    )
    return (x_high, x_low, y_high, y_low)


def place_faces(source_field, moduli, x_low, x_high, y_low, y_high):
    extent = source_field.shape[-2]
    added = jnp.zeros_like(source_field)
    added = added.at[..., 0, :].add(x_low)
    added = added.at[..., extent - 1, :].add(x_high)
    cube_view = added.reshape(added.shape[:-1] + (extent, extent))
    low_square = y_low.reshape(y_low.shape[:-1] + (extent, extent))
    high_square = y_high.reshape(y_high.shape[:-1] + (extent, extent))
    cube_view = cube_view.at[..., 0, :].add(low_square)
    cube_view = cube_view.at[..., extent - 1, :].add(high_square)
    added = cube_view.reshape(source_field.shape)
    return source_field + inject_scale * moduli[..., None, None] * added


def trace_update(current, side_a, side_b, moduli_a, moduli_b, omega_step, tangent):
    extent = tangent.shape[0]
    weight_a = moduli_a[..., None]
    weight_b = moduli_b[..., None]
    residue = (
        weight_a * side_a[0] + weight_b * side_b[0] + traction_mix * (side_a[1] + side_b[1])
    ) / (weight_a + weight_b) - current
    rows_view = residue.reshape(residue.shape[:-1] + (residue.shape[-1] // extent, extent))
    smoothed = rows_view + penalty_mix * jnp.einsum(
        "...z,zk->...k", rows_view, tangent, precision=highest
    )
    return current + omega_step * smoothed.reshape(residue.shape)


def pack_side(side):
    return jnp.stack(side, 1)


def unpack_side(packed):
    return (packed[:, 0], packed[:, 1])


def oriented(side, codes, extent):
    return (orient(side[0], codes, extent), orient(side[1], codes, extent))


def shards(forcing, modulus, orient_codes):
    extent = forcing.shape[3]
    blocks = forcing.shape[1]
    flat = extent * extent
    source_field = forcing[0]
    moduli = modulus[0]
    codes_here = orient_codes[0]
    tangent = tangent_matrix(extent)
    omegas = step_weights(ITERS)
    slab_count = lax.axis_size("blk")
    slab_index = lax.axis_index("blk")
    has_up = (slab_index < slab_count - 1).astype(jnp.float32)
    has_down = (slab_index > 0).astype(jnp.float32)
    moduli_up = shifted(moduli, "blk", -1)
    moduli_down, codes_down = shifted((moduli, codes_here), "blk", 1)
    moduli_next = jnp.concatenate([moduli[1:], shifted_2(moduli[:1], "face", -1)], 0)
    moduli_prev = jnp.concatenate([shifted_2(moduli[-1:], "face", 1), moduli[:-1]], 0)
    face_zeros = jnp.zeros((blocks, 3, flat), jnp.float32)
    lam_x_up = face_zeros
    lam_x_down = face_zeros
    lam_y_next = face_zeros
    lam_y_prev = face_zeros
    faces = [None] * blocks
    for sweep in range(ITERS + 1):
        last = sweep == ITERS
        outs = [
            kernel_sweep(source_field[b], moduli[b], faces[b], emit_u=last, emit_sides=not last)
            for b in range(blocks)
        ]
        if last:
            return jnp.stack([o[0] for o in outs], 0)[None]
        xf = jnp.stack([o[0] for o in outs], 0)
        yf = jnp.stack([o[1] for o in outs], 0)
        x_high_side = xf[:, :, 0:2].transpose(0, 2, 1, 3)
        x_low_side = xf[:, :, 2:4].transpose(0, 2, 1, 3)
        y_high_side = yf[:, :, 0:2, :, extent:].transpose(0, 2, 1, 3, 4).reshape(blocks, 2, 3, flat)
        y_low_side = yf[:, :, 2:4, :, :extent].transpose(0, 2, 1, 3, 4).reshape(blocks, 2, 3, flat)
        upper_side = shifted(x_low_side, "blk", -1)
        lower_side = shifted(x_high_side, "blk", 1)
        next_side = jnp.concatenate([y_low_side[1:], shifted_2(y_low_side[:1], "face", -1)], 0)
        prev_side = jnp.concatenate([shifted_2(y_high_side[-1:], "face", 1), y_high_side[:-1]], 0)
        lam_x_up = (
            trace_update(
                lam_x_up,
                unpack_side(x_high_side),
                oriented(unpack_side(upper_side), codes_here, extent),
                moduli,
                moduli_up,
                omegas[sweep],
                tangent,
            )
            * has_up
        )
        lam_x_down = (
            trace_update(
                lam_x_down,
                unpack_side(lower_side),
                oriented(unpack_side(x_low_side), codes_down, extent),
                moduli_down,
                moduli,
                omegas[sweep],
                tangent,
            )
            * has_down
        )
        lam_y_next = trace_update(
            lam_y_next, unpack_side(y_high_side), unpack_side(next_side), moduli, moduli_next,
            omegas[sweep], tangent,
        )
        lam_y_prev = trace_update(
            lam_y_prev, unpack_side(prev_side), unpack_side(y_low_side), moduli_prev, moduli,
            omegas[sweep], tangent,
        )
        x_low = orient(lam_x_down, codes_down, extent)
        yadd = jnp.concatenate(
            [lam_y_prev.reshape(blocks, 3, extent, extent), lam_y_next.reshape(blocks, 3, extent, extent)], -1
        )
        faces = [(x_low[b], lam_x_up[b], yadd[b]) for b in range(blocks)]


def solution(mesh):
    placed = (P("blk", "face", None, None, None), P("blk", "face", None), P("blk", "face"))
    return jax.shard_map(
        shards,
        mesh=mesh,
        in_specs=placed,
        out_specs=P("blk", "face", None, None, None),
        check_vma=False,
    )
```

```python
import functools
import math

import jax
import jax.numpy as jnp
from jax import lax
from jax.sharding import PartitionSpec as P
from jax.experimental import pallas as pl
from jax.experimental.pallas import tpu as pltpu
import numpy as np
import ml_dtypes

ITERS = 2


mass_shift = 0.02
inject_scale = 2.0
traction_mix = 0.5
penalty_mix = 0.25
lower_edge = 0.3
upper_edge = 1.5
highest = lax.Precision.HIGHEST


def shifted(shard, axis, by):
    length = lax.axis_size(axis)
    pairs = [(i, i + by) for i in range(length) if 0 <= i + by < length]
    return lax.ppermute(shard, axis, pairs)


def shifted_2(shard, axis, by):
    length = lax.axis_size(axis)
    return lax.ppermute(shard, axis, [(i, (i + by) % length) for i in range(length)])


def tables(extent):
    node_index = jnp.arange(extent, dtype=jnp.float32) + 1.0
    basis = math.sqrt(2.0 / (extent + 1)) * jnp.sin(
        math.pi * node_index[:, None] * node_index[None, :] / (extent + 1)
    )
    eigenvalues = 2.0 - 2.0 * jnp.cos(math.pi * node_index / (extent + 1))
    return (basis, eigenvalues)


def tangent_matrix(extent):
    node_index = jnp.arange(extent, dtype=jnp.int32)
    distance = jnp.abs(node_index[:, None] - node_index[None, :])
    end_rows = ((node_index == 0) | (node_index == extent - 1)).astype(jnp.float32)
    adjacent = (distance == 1).astype(jnp.float32)
    diagonal_part = (distance == 0).astype(jnp.float32) * (2.0 - end_rows[:, None])
    return adjacent - diagonal_part


def step_weights(step_count):
    midpoint = 0.5 * (upper_edge + lower_edge)
    radius = 0.5 * (upper_edge - lower_edge)
    return [
        1.0 / (midpoint + radius * math.cos(math.pi * (2 * turn_index + 1) / (2 * step_count)))
        for turn_index in range(step_count)
    ]


def divisor(moduli, eigenvalues):
    extent = eigenvalues.shape[0]
    summed = eigenvalues[:, None, None] + eigenvalues[None, :, None] + eigenvalues[None, None, :]
    scaled = moduli[..., None, None, None] * summed + mass_shift
    return scaled.reshape(moduli.shape + (extent, extent * extent))


def body_transform(field_data, basis, paired_basis):
    extent = basis.shape[0]
    full_shape = field_data.shape
    pair_width = paired_basis.shape[0]
    sectioned = jnp.einsum("ix,bcxm->bcim", basis, field_data, precision=highest)
    sectioned = sectioned.reshape(full_shape[:-1] + (full_shape[-1] // pair_width, pair_width))
    sectioned = jnp.einsum("bcxpz,kz->bcxpk", sectioned, paired_basis, precision=highest)
    sectioned = sectioned.reshape(full_shape[:-1] + (extent, extent))
    sectioned = jnp.einsum("jy,bcxyz->bcxjz", basis, sectioned, precision=highest)
    return sectioned.reshape(full_shape)


def body_solve(right_side, scale_table, basis, paired_basis):
    return body_transform(
        body_transform(right_side, basis, paired_basis) / scale_table, basis, paired_basis
    )


f32 = jnp.float32


def np_tables(n):
    g = np.float32
    idx = np.arange(n, dtype=g) + g(1.0)
    arg = (g(math.pi) * idx[:, None]) * idx[None, :] / g(n + 1)
    q = g(math.sqrt(2.0 / (n + 1))) * np.sin(arg)
    e = g(2.0) - g(2.0) * np.cos(g(math.pi) * idx / g(n + 1))
    return q.astype(g), e.astype(g)


def consts(n):
    q, e = np_tables(n)
    h = n // 2
    p4 = np.kron(np.eye(4, dtype=np.float32), q.T)
    w = np.zeros((2, 4, h, 2, 4, h), np.float32)
    qq = q.reshape(h, 2, h, 2)
    for xl in range(4):
        w[:, xl, :, :, xl, :] = np.transpose(qq, (3, 2, 1, 0))
    wy = w.reshape(8 * h, 8 * h)
    ng = n // 4
    lane_h = np.arange(8 * h) // (4 * h)
    lane_xl = (np.arange(8 * h) // h) % 4
    lane_c = np.arange(8 * h) % h
    exy = (e[4 * np.arange(ng)[:, None] + lane_xl[None, :]] + e[2 * lane_c + lane_h][None, :]).astype(np.float32)
    ez = np.ascontiguousarray(np.broadcast_to(e[:, None], (n, 8 * h))).astype(np.float32)
    return stack_left(q), stack_right(p4), stack_right(wy), exy, ez


BF = jnp.bfloat16

def np_split3(w):
    b = ml_dtypes.bfloat16
    w1 = w.astype(b)
    r1 = w - w1.astype(np.float32)
    w2 = r1.astype(b)
    w3 = (r1 - w2.astype(np.float32)).astype(b)
    return w1, w2, w3


def stack_right(w):
    w1, w2, w3 = np_split3(w)
    return np.concatenate([w1, w2, w3, w1, w2, w1], 0)


def stack_left(w):
    w1, w2, w3 = np_split3(w)
    return np.concatenate([w1, w2, w3, w1, w2, w1], 1)


def split3(d):
    d1 = d.astype(BF)
    r1 = d - d1.astype(f32)
    d2 = r1.astype(BF)
    d3 = (r1 - d2.astype(f32)).astype(BF)
    return d1, d2, d3


def sdot(d, w6):
    d1, d2, d3 = split3(d)
    return jnp.dot(jnp.concatenate([d1, d1, d1, d2, d2, d3], 1), w6, preferred_element_type=f32)


def sdot_left(w6, d):
    d1, d2, d3 = split3(d)
    return jnp.dot(w6, jnp.concatenate([d1, d1, d1, d2, d2, d3], 0), preferred_element_type=f32)


def solve_kernel(mod_ref, f_ref, xlo_ref, xhi_ref, yadd_ref, q_ref, p_ref, wy_ref, exy_ref, ez_ref,
                 o_ref, xf_ref, yf_ref, s_ref):
    n = q_ref.shape[0]
    h = n // 2
    w2 = 2 * n
    w4 = 4 * n
    nn = f_ref.shape[-1]
    npair = nn // w4
    comp = pl.program_id(0)
    m = mod_ref[comp]
    two_m = 2.0 * m
    q = q_ref[...]
    p = p_ref[...]
    rows = lax.broadcasted_iota(jnp.int32, (n, w4), 0)
    lane4 = lax.broadcasted_iota(jnp.int32, (n, w4), 1)
    yadd = yadd_ref[0]
    yadd2 = jnp.concatenate([yadd, yadd], 1)
    y_first = jnp.where(lane4 < n, yadd2, 0.0)
    y_last = jnp.where(lane4 >= w4 - n, yadd2, 0.0)

    def stage_in(cp, carry):
        off = pl.multiple_of(cp * w4, w4)
        r = f_ref[0, :, pl.ds(off, w4)]
        added = jnp.where(rows == 0, xlo_ref[0, :, pl.ds(off, w4)], 0.0) + jnp.where(
            rows == n - 1, xhi_ref[0, :, pl.ds(off, w4)], 0.0)
        added = added + jnp.where(cp == 0, y_first, 0.0) + jnp.where(cp == npair - 1, y_last, 0.0)
        r = r + two_m * added
        zc = sdot(sdot_left(q, r), p)
        s_ref[pl.ds(2 * cp * n, n), :] = zc[:, :w2]
        s_ref[pl.ds((2 * cp + 1) * n, n), :] = zc[:, w2:]
        return carry
    lax.fori_loop(0, npair, stage_in, 0)
    wy = wy_ref[...]
    ez = ez_ref[...]
    XG = 4
    GPI = 4

    def body(it_, carry):
        lhs = []
        for gi in range(GPI):
            g = it_ * GPI + gi
            blk = jnp.concatenate([s_ref[pl.ds(g * XG + xl, h, stride=n), :] for xl in range(XG)], 0)
            tb = blk.T
            lhs.append(jnp.concatenate([tb[:n], tb[n:]], 1))
        v = sdot(jnp.concatenate(lhs, 0), wy)
        div = jnp.concatenate([m * (exy_ref[pl.ds(it_ * GPI + gi, 1), :] + ez) + 0.02 for gi in range(GPI)], 0)
        v = v / div
        v = sdot(v, wy)
        for gi in range(GPI):
            g = it_ * GPI + gi
            vg = v[gi * n:(gi + 1) * n]
            tb = jnp.concatenate([vg[:, :w2], vg[:, w2:]], 0).T
            for xl in range(XG):
                s_ref[pl.ds(g * XG + xl, h, stride=n), :] = tb[xl * h:(xl + 1) * h]
        return carry
    lax.fori_loop(0, n // (XG * GPI), body, 0)

    def slope(p0, p1, p2, p3):
        return m * (11.0 / 6.0 * p0 - 3.0 * p1 + 1.5 * p2 - p3 / 3.0)

    def stage_out(cp, carry):
        off = pl.multiple_of(cp * w4, w4)
        zin = jnp.concatenate([s_ref[pl.ds(2 * cp * n, n), :], s_ref[pl.ds((2 * cp + 1) * n, n), :]], 1)
        u = sdot_left(q, sdot(zin, p))
        o_ref[0, :, pl.ds(off, w4)] = u
        xf_ref[0, 0:1, pl.ds(off, w4)] = u[n - 1:n]
        xf_ref[0, 1:2, pl.ds(off, w4)] = slope(u[n - 1:n], u[n - 2:n - 1], u[n - 3:n - 2], u[n - 4:n - 3])
        xf_ref[0, 2:3, pl.ds(off, w4)] = u[0:1]
        xf_ref[0, 3:4, pl.ds(off, w4)] = slope(u[0:1], u[1:2], u[2:3], u[3:4])
        return carry
    lax.fori_loop(0, npair, stage_out, 0)
    c_hi = o_ref[0, :, nn - w2:]
    c_hi2 = o_ref[0, :, nn - 2 * w2:nn - w2]
    yf_ref[0, 0] = c_hi
    yf_ref[0, 1] = slope(c_hi, pltpu.roll(c_hi, n, 1), c_hi2, pltpu.roll(c_hi2, n, 1))
    c_lo = o_ref[0, :, :w2]
    c_lo2 = o_ref[0, :, w2:2 * w2]
    yf_ref[0, 2] = c_lo
    yf_ref[0, 3] = slope(c_lo, pltpu.roll(c_lo, n, 1), c_lo2, pltpu.roll(c_lo2, n, 1))


def kernel_sweep(rhs, moduli, faces):
    ncomp, n, nn = rhs.shape
    q, p4, wy, exy, ez = consts(n)
    full = lambda shp: pl.BlockSpec(shp, lambda c: (0,) * len(shp))
    comp3 = lambda shp: pl.BlockSpec((1,) + shp, lambda c: (c,) + (0,) * len(shp))
    smem = pl.BlockSpec(memory_space=pltpu.SMEM)
    xlo, xhi, yadd = faces
    in_specs = [smem, comp3((n, nn)), comp3((1, nn)), comp3((1, nn)), comp3((n, 2 * n)),
                full(q.shape), full(p4.shape), full(wy.shape), full(exy.shape), full(ez.shape)]
    args = [moduli, rhs, xlo.reshape(ncomp, 1, nn), xhi.reshape(ncomp, 1, nn), yadd, q, p4, wy, exy, ez]
    out_specs = [comp3((n, nn)), comp3((4, nn)), comp3((4, n, 2 * n))]
    out_shape = [jax.ShapeDtypeStruct(rhs.shape, f32), jax.ShapeDtypeStruct((ncomp, 4, nn), f32),
                 jax.ShapeDtypeStruct((ncomp, 4, n, 2 * n), f32)]
    return pl.pallas_call(
        solve_kernel,
        grid=(ncomp,),
        in_specs=in_specs,
        out_specs=out_specs,
        out_shape=out_shape,
        scratch_shapes=[pltpu.VMEM((nn // 2, 2 * n), f32)],
    )(*args)


def orient(face_field, code_table, extent):
    square = face_field.reshape(face_field.shape[:-1] + (extent, extent))
    flip_rows = (code_table % 2 == 1)[..., None, None, None]
    flip_cols = (code_table // 2 == 1)[..., None, None, None]
    square = jnp.where(flip_rows, jnp.flip(square, -2), square)
    square = jnp.where(flip_cols, jnp.flip(square, -1), square)
    return square.reshape(face_field.shape)


def face_data(solution, moduli):
    extent = solution.shape[-2]
    cube_view = solution.reshape(solution.shape[:-1] + (extent, extent))
    flat_shape = solution.shape[:-2] + (extent * extent,)

    def pack_side(planes):
        normal_slope = 11.0 / 6.0 * planes[0] - 3.0 * planes[1] + 1.5 * planes[2] - planes[3] / 3.0
        return (planes[0], moduli[..., None] * normal_slope)

    x_high = pack_side([solution[..., extent - 1 - plane_depth, :] for plane_depth in range(4)])
    x_low = pack_side([solution[..., plane_depth, :] for plane_depth in range(4)])
    y_high = pack_side(
        [
            cube_view[..., extent - 1 - plane_depth, :].reshape(flat_shape)
            for plane_depth in range(4)
        ]
    )
    y_low = pack_side(
        [cube_view[..., plane_depth, :].reshape(flat_shape) for plane_depth in range(4)]
    )
    return (x_high, x_low, y_high, y_low)


def place_faces(source_field, moduli, x_low, x_high, y_low, y_high):
    extent = source_field.shape[-2]
    added = jnp.zeros_like(source_field)
    added = added.at[..., 0, :].add(x_low)
    added = added.at[..., extent - 1, :].add(x_high)
    cube_view = added.reshape(added.shape[:-1] + (extent, extent))
    low_square = y_low.reshape(y_low.shape[:-1] + (extent, extent))
    high_square = y_high.reshape(y_high.shape[:-1] + (extent, extent))
    cube_view = cube_view.at[..., 0, :].add(low_square)
    cube_view = cube_view.at[..., extent - 1, :].add(high_square)
    added = cube_view.reshape(source_field.shape)
    return source_field + inject_scale * moduli[..., None, None] * added


def trace_update(current, side_a, side_b, moduli_a, moduli_b, omega_step, tangent):
    extent = tangent.shape[0]
    weight_a = moduli_a[..., None]
    weight_b = moduli_b[..., None]
    residue = (
        weight_a * side_a[0] + weight_b * side_b[0] + traction_mix * (side_a[1] + side_b[1])
    ) / (weight_a + weight_b) - current
    rows_view = residue.reshape(residue.shape[:-1] + (residue.shape[-1] // extent, extent))
    smoothed = rows_view + penalty_mix * jnp.einsum(
        "...z,zk->...k", rows_view, tangent, precision=highest
    )
    return current + omega_step * smoothed.reshape(residue.shape)


def pack_side(side):
    return jnp.stack(side, 1)


def unpack_side(packed):
    return (packed[:, 0], packed[:, 1])


def oriented(side, codes, extent):
    return (orient(side[0], codes, extent), orient(side[1], codes, extent))


def shards(forcing, modulus, orient_codes):
    extent = forcing.shape[3]
    blocks = forcing.shape[1]
    flat = extent * extent
    source_field = forcing[0]
    moduli = modulus[0]
    codes_here = orient_codes[0]
    tangent = tangent_matrix(extent)
    omegas = step_weights(ITERS)
    slab_count = lax.axis_size("blk")
    slab_index = lax.axis_index("blk")
    has_up = (slab_index < slab_count - 1).astype(jnp.float32)
    has_down = (slab_index > 0).astype(jnp.float32)
    moduli_up = shifted(moduli, "blk", -1)
    moduli_down, codes_down = shifted((moduli, codes_here), "blk", 1)
    moduli_next = jnp.concatenate([moduli[1:], shifted_2(moduli[:1], "face", -1)], 0)
    moduli_prev = jnp.concatenate([shifted_2(moduli[-1:], "face", 1), moduli[:-1]], 0)
    face_zeros = jnp.zeros((blocks, 3, flat), jnp.float32)
    lam_x_up = face_zeros
    lam_x_down = face_zeros
    lam_y_next = face_zeros
    lam_y_prev = face_zeros
    faces = [(face_zeros[b], face_zeros[b], jnp.zeros((3, extent, 2 * extent), jnp.float32)) for b in range(blocks)]
    for sweep in range(ITERS + 1):
        last = sweep == ITERS
        outs = [kernel_sweep(source_field[b], moduli[b], faces[b]) for b in range(blocks)]
        if last:
            return jnp.stack([o[0] for o in outs], 0)[None]
        xf = jnp.stack([o[1] for o in outs], 0)
        yf = jnp.stack([o[2] for o in outs], 0)
        x_high_side = xf[:, :, 0:2].transpose(0, 2, 1, 3)
        x_low_side = xf[:, :, 2:4].transpose(0, 2, 1, 3)
        y_high_side = yf[:, :, 0:2, :, extent:].transpose(0, 2, 1, 3, 4).reshape(blocks, 2, 3, flat)
        y_low_side = yf[:, :, 2:4, :, :extent].transpose(0, 2, 1, 3, 4).reshape(blocks, 2, 3, flat)
        upper_side = shifted(x_low_side, "blk", -1)
        lower_side = shifted(x_high_side, "blk", 1)
        next_side = jnp.concatenate([y_low_side[1:], shifted_2(y_low_side[:1], "face", -1)], 0)
        prev_side = jnp.concatenate([shifted_2(y_high_side[-1:], "face", 1), y_high_side[:-1]], 0)
        lam_x_up = (
            trace_update(
                lam_x_up,
                unpack_side(x_high_side),
                oriented(unpack_side(upper_side), codes_here, extent),
                moduli,
                moduli_up,
                omegas[sweep],
                tangent,
            )
            * has_up
        )
        lam_x_down = (
            trace_update(
                lam_x_down,
                unpack_side(lower_side),
                oriented(unpack_side(x_low_side), codes_down, extent),
                moduli_down,
                moduli,
                omegas[sweep],
                tangent,
            )
            * has_down
        )
        lam_y_next = trace_update(
            lam_y_next, unpack_side(y_high_side), unpack_side(next_side), moduli, moduli_next,
            omegas[sweep], tangent,
        )
        lam_y_prev = trace_update(
            lam_y_prev, unpack_side(prev_side), unpack_side(y_low_side), moduli_prev, moduli,
            omegas[sweep], tangent,
        )
        x_low = orient(lam_x_down, codes_down, extent)
        yadd = jnp.concatenate(
            [lam_y_prev.reshape(blocks, 3, extent, extent), lam_y_next.reshape(blocks, 3, extent, extent)], -1
        )
        faces = [(x_low[b], lam_x_up[b], yadd[b]) for b in range(blocks)]


def solution(mesh):
    placed = (P("blk", "face", None, None, None), P("blk", "face", None), P("blk", "face"))
    return jax.shard_map(
        shards,
        mesh=mesh,
        in_specs=placed,
        out_specs=P("blk", "face", None, None, None),
        check_vma=False,
    )
```

```python
import functools
import math

import jax
import jax.numpy as jnp
from jax import lax
from jax.sharding import PartitionSpec as P
from jax.experimental import pallas as pl
from jax.experimental.pallas import tpu as pltpu
import numpy as np
import ml_dtypes

ITERS = 2


mass_shift = 0.02
inject_scale = 2.0
traction_mix = 0.5
penalty_mix = 0.25
lower_edge = 0.3
upper_edge = 1.5
highest = lax.Precision.HIGHEST


def shifted(shard, axis, by):
    length = lax.axis_size(axis)
    pairs = [(i, i + by) for i in range(length) if 0 <= i + by < length]
    return lax.ppermute(shard, axis, pairs)


def shifted_2(shard, axis, by):
    length = lax.axis_size(axis)
    return lax.ppermute(shard, axis, [(i, (i + by) % length) for i in range(length)])


def tables(extent):
    node_index = jnp.arange(extent, dtype=jnp.float32) + 1.0
    basis = math.sqrt(2.0 / (extent + 1)) * jnp.sin(
        math.pi * node_index[:, None] * node_index[None, :] / (extent + 1)
    )
    eigenvalues = 2.0 - 2.0 * jnp.cos(math.pi * node_index / (extent + 1))
    return (basis, eigenvalues)


def tangent_matrix(extent):
    node_index = jnp.arange(extent, dtype=jnp.int32)
    distance = jnp.abs(node_index[:, None] - node_index[None, :])
    end_rows = ((node_index == 0) | (node_index == extent - 1)).astype(jnp.float32)
    adjacent = (distance == 1).astype(jnp.float32)
    diagonal_part = (distance == 0).astype(jnp.float32) * (2.0 - end_rows[:, None])
    return adjacent - diagonal_part


def step_weights(step_count):
    midpoint = 0.5 * (upper_edge + lower_edge)
    radius = 0.5 * (upper_edge - lower_edge)
    return [
        1.0 / (midpoint + radius * math.cos(math.pi * (2 * turn_index + 1) / (2 * step_count)))
        for turn_index in range(step_count)
    ]


def divisor(moduli, eigenvalues):
    extent = eigenvalues.shape[0]
    summed = eigenvalues[:, None, None] + eigenvalues[None, :, None] + eigenvalues[None, None, :]
    scaled = moduli[..., None, None, None] * summed + mass_shift
    return scaled.reshape(moduli.shape + (extent, extent * extent))


def body_transform(field_data, basis, paired_basis):
    extent = basis.shape[0]
    full_shape = field_data.shape
    pair_width = paired_basis.shape[0]
    sectioned = jnp.einsum("ix,bcxm->bcim", basis, field_data, precision=highest)
    sectioned = sectioned.reshape(full_shape[:-1] + (full_shape[-1] // pair_width, pair_width))
    sectioned = jnp.einsum("bcxpz,kz->bcxpk", sectioned, paired_basis, precision=highest)
    sectioned = sectioned.reshape(full_shape[:-1] + (extent, extent))
    sectioned = jnp.einsum("jy,bcxyz->bcxjz", basis, sectioned, precision=highest)
    return sectioned.reshape(full_shape)


def body_solve(right_side, scale_table, basis, paired_basis):
    return body_transform(
        body_transform(right_side, basis, paired_basis) / scale_table, basis, paired_basis
    )


f32 = jnp.float32


def np_tables(n):
    g = np.float32
    idx = np.arange(n, dtype=g) + g(1.0)
    arg = (g(math.pi) * idx[:, None]) * idx[None, :] / g(n + 1)
    q = g(math.sqrt(2.0 / (n + 1))) * np.sin(arg)
    e = g(2.0) - g(2.0) * np.cos(g(math.pi) * idx / g(n + 1))
    return q.astype(g), e.astype(g)


def consts(n):
    q, e = np_tables(n)
    h = n // 2
    p4 = np.kron(np.eye(4, dtype=np.float32), q.T)
    w = np.zeros((2, 4, h, 2, 4, h), np.float32)
    qq = q.reshape(h, 2, h, 2)
    for xl in range(4):
        w[:, xl, :, :, xl, :] = np.transpose(qq, (3, 2, 1, 0))
    wy = w.reshape(8 * h, 8 * h)
    ng = n // 4
    lane_h = np.arange(8 * h) // (4 * h)
    lane_xl = (np.arange(8 * h) // h) % 4
    lane_c = np.arange(8 * h) % h
    exy = (e[4 * np.arange(ng)[:, None] + lane_xl[None, :]] + e[2 * lane_c + lane_h][None, :]).astype(np.float32)
    ez = np.ascontiguousarray(np.broadcast_to(e[:, None], (n, 8 * h))).astype(np.float32)
    return stack_left(q), stack_right(p4), stack_right(wy), exy, ez


BF = jnp.bfloat16

def np_split3(w):
    b = ml_dtypes.bfloat16
    w1 = w.astype(b)
    r1 = w - w1.astype(np.float32)
    w2 = r1.astype(b)
    w3 = (r1 - w2.astype(np.float32)).astype(b)
    return w1, w2, w3


def stack_right(w):
    w1, w2, w3 = np_split3(w)
    return np.concatenate([w1, w2, w1, w1], 0)


def stack_left(w):
    w1, w2, w3 = np_split3(w)
    return np.concatenate([w1, w2, w1, w1], 1)


def split3(d):
    d1 = d.astype(BF)
    r1 = d - d1.astype(f32)
    d2 = r1.astype(BF)
    d3 = (r1 - d2.astype(f32)).astype(BF)
    return d1, d2, d3


def sdot(d, w6):
    d1, d2, d3 = split3(d)
    return jnp.dot(jnp.concatenate([d1, d1, d2, d3], 1), w6, preferred_element_type=f32)


def sdot_left(w6, d):
    d1, d2, d3 = split3(d)
    return jnp.dot(w6, jnp.concatenate([d1, d1, d2, d3], 0), preferred_element_type=f32)


def solve_kernel(*refs, with_faces, emit_u, emit_sides):
    it = iter(refs)
    mod_ref, f_ref = next(it), next(it)
    if with_faces:
        xlo_ref, xhi_ref, yadd_ref = next(it), next(it), next(it)
    q_ref, p_ref, wy_ref, exy_ref, ez_ref = next(it), next(it), next(it), next(it), next(it)
    o_ref = next(it) if emit_u else None
    if emit_sides:
        xf_ref, yf_ref = next(it), next(it)
    s_ref, z_ref = next(it), next(it)
    n = q_ref.shape[0]
    h = n // 2
    w2 = 2 * n
    w4 = 4 * n
    nn = f_ref.shape[-1]
    nch = nn // w2
    npair = nn // w4
    comp = pl.program_id(0)
    m = mod_ref[comp]
    q = q_ref[...]
    r = f_ref[0]
    if with_faces:
        rows = lax.broadcasted_iota(jnp.int32, (n, nn), 0)
        added = jnp.where(rows == 0, xlo_ref[0], 0.0) + jnp.where(rows == n - 1, xhi_ref[0], 0.0)
        lane = lax.broadcasted_iota(jnp.int32, (n, w2), 1)
        yadd = yadd_ref[0]
        first = added[:, :w2] + jnp.where(lane < n, yadd, 0.0)
        last = added[:, nn - w2:] + jnp.where(lane >= n, yadd, 0.0)
        added = jnp.concatenate([first, added[:, w2:nn - w2], last], 1)
        r = r + (2.0 * m) * added
    a = sdot_left(q, r)
    for cp in range(npair):
        z_ref[cp * n:(cp + 1) * n, :] = a[:, cp * w4:(cp + 1) * w4]
    zo = sdot(z_ref[...], p_ref[...])
    for cp in range(npair):
        for cb in range(2):
            s_ref[(2 * cp + cb) * n:(2 * cp + cb + 1) * n, :] = zo[cp * n:(cp + 1) * n, cb * w2:(cb + 1) * w2]
    wy = wy_ref[...]
    ez = ez_ref[...]
    XG = 4
    GPI = 4

    def body(it_, carry):
        lhs = []
        for gi in range(GPI):
            g = it_ * GPI + gi
            blk = jnp.concatenate([s_ref[pl.ds(g * XG + xl, h, stride=n), :] for xl in range(XG)], 0)
            tb = blk.T
            lhs.append(jnp.concatenate([tb[:n], tb[n:]], 1))
        v = sdot(jnp.concatenate(lhs, 0), wy)
        div = jnp.concatenate([m * (exy_ref[pl.ds(it_ * GPI + gi, 1), :] + ez) + 0.02 for gi in range(GPI)], 0)
        v = v / div
        v = sdot(v, wy)
        for gi in range(GPI):
            g = it_ * GPI + gi
            vg = v[gi * n:(gi + 1) * n]
            tb = jnp.concatenate([vg[:, :w2], vg[:, w2:]], 0).T
            for xl in range(XG):
                s_ref[pl.ds(g * XG + xl, h, stride=n), :] = tb[xl * h:(xl + 1) * h]
        return carry
    lax.fori_loop(0, n // (XG * GPI), body, 0)
    for cp in range(npair):
        z_ref[cp * n:(cp + 1) * n, :] = jnp.concatenate(
            [s_ref[(2 * cp) * n:(2 * cp + 1) * n, :], s_ref[(2 * cp + 1) * n:(2 * cp + 2) * n, :]], 1)
    zo = sdot(z_ref[...], p_ref[...])
    b = jnp.concatenate([zo[cp * n:(cp + 1) * n, :] for cp in range(npair)], 1)
    u = sdot_left(q, b)
    if emit_u:
        o_ref[0] = u

    def slope(p0, p1, p2, p3):
        return m * (11.0 / 6.0 * p0 - 3.0 * p1 + 1.5 * p2 - p3 / 3.0)
    if emit_sides:
        xf_ref[0, 0:1, :] = u[n - 1:n]
        xf_ref[0, 1:2, :] = slope(u[n - 1:n], u[n - 2:n - 1], u[n - 3:n - 2], u[n - 4:n - 3])
        xf_ref[0, 2:3, :] = u[0:1]
        xf_ref[0, 3:4, :] = slope(u[0:1], u[1:2], u[2:3], u[3:4])
        c_hi = u[:, nn - w2:]
        c_hi2 = u[:, nn - 2 * w2:nn - w2]
        yf_ref[0, 0] = c_hi
        yf_ref[0, 1] = slope(c_hi, pltpu.roll(c_hi, n, 1), c_hi2, pltpu.roll(c_hi2, n, 1))
        c_lo = u[:, :w2]
        c_lo2 = u[:, w2:2 * w2]
        yf_ref[0, 2] = c_lo
        yf_ref[0, 3] = slope(c_lo, pltpu.roll(c_lo, n, 1), c_lo2, pltpu.roll(c_lo2, n, 1))


def kernel_sweep(rhs, moduli, faces=None, emit_u=True, emit_sides=False, interpret=False):
    ncomp, n, nn = rhs.shape
    q, p4, wy, exy, ez = consts(n)
    full = lambda shp: pl.BlockSpec(shp, lambda c: (0,) * len(shp))
    comp3 = lambda shp: pl.BlockSpec((1,) + shp, lambda c: (c,) + (0,) * len(shp))
    smem = pl.BlockSpec(memory_space=pltpu.SMEM)
    in_specs = [smem, comp3((n, nn))]
    args = [moduli, rhs]
    if faces is not None:
        xlo, xhi, yadd = faces
        in_specs += [comp3((1, nn)), comp3((1, nn)), comp3((n, 2 * n))]
        args += [xlo.reshape(ncomp, 1, nn), xhi.reshape(ncomp, 1, nn), yadd]
    in_specs += [full(q.shape), full(p4.shape), full(wy.shape), full(exy.shape), full(ez.shape)]
    args += [q, p4, wy, exy, ez]
    out_specs, out_shape = [], []
    if emit_u:
        out_specs.append(comp3((n, nn)))
        out_shape.append(jax.ShapeDtypeStruct(rhs.shape, f32))
    if emit_sides:
        out_specs += [comp3((4, nn)), comp3((4, n, 2 * n))]
        out_shape += [jax.ShapeDtypeStruct((ncomp, 4, nn), f32), jax.ShapeDtypeStruct((ncomp, 4, n, 2 * n), f32)]
    kernel = functools.partial(solve_kernel, with_faces=faces is not None, emit_u=emit_u, emit_sides=emit_sides)
    return pl.pallas_call(
        kernel,
        grid=(ncomp,),
        in_specs=in_specs,
        out_specs=out_specs,
        out_shape=out_shape,
        scratch_shapes=[pltpu.VMEM((nn // 2, 2 * n), f32), pltpu.VMEM((nn // 4, 4 * n), f32)],
        interpret=interpret,
    )(*args)


def orient(face_field, code_table, extent):
    square = face_field.reshape(face_field.shape[:-1] + (extent, extent))
    flip_rows = (code_table % 2 == 1)[..., None, None, None]
    flip_cols = (code_table // 2 == 1)[..., None, None, None]
    square = jnp.where(flip_rows, jnp.flip(square, -2), square)
    square = jnp.where(flip_cols, jnp.flip(square, -1), square)
    return square.reshape(face_field.shape)


def face_data(solution, moduli):
    extent = solution.shape[-2]
    cube_view = solution.reshape(solution.shape[:-1] + (extent, extent))
    flat_shape = solution.shape[:-2] + (extent * extent,)

    def pack_side(planes):
        normal_slope = 11.0 / 6.0 * planes[0] - 3.0 * planes[1] + 1.5 * planes[2] - planes[3] / 3.0
        return (planes[0], moduli[..., None] * normal_slope)

    x_high = pack_side([solution[..., extent - 1 - plane_depth, :] for plane_depth in range(4)])
    x_low = pack_side([solution[..., plane_depth, :] for plane_depth in range(4)])
    y_high = pack_side(
        [
            cube_view[..., extent - 1 - plane_depth, :].reshape(flat_shape)
            for plane_depth in range(4)
        ]
    )
    y_low = pack_side(
        [cube_view[..., plane_depth, :].reshape(flat_shape) for plane_depth in range(4)]
    )
    return (x_high, x_low, y_high, y_low)


def place_faces(source_field, moduli, x_low, x_high, y_low, y_high):
    extent = source_field.shape[-2]
    added = jnp.zeros_like(source_field)
    added = added.at[..., 0, :].add(x_low)
    added = added.at[..., extent - 1, :].add(x_high)
    cube_view = added.reshape(added.shape[:-1] + (extent, extent))
    low_square = y_low.reshape(y_low.shape[:-1] + (extent, extent))
    high_square = y_high.reshape(y_high.shape[:-1] + (extent, extent))
    cube_view = cube_view.at[..., 0, :].add(low_square)
    cube_view = cube_view.at[..., extent - 1, :].add(high_square)
    added = cube_view.reshape(source_field.shape)
    return source_field + inject_scale * moduli[..., None, None] * added


def trace_update(current, side_a, side_b, moduli_a, moduli_b, omega_step, tangent):
    extent = tangent.shape[0]
    weight_a = moduli_a[..., None]
    weight_b = moduli_b[..., None]
    residue = (
        weight_a * side_a[0] + weight_b * side_b[0] + traction_mix * (side_a[1] + side_b[1])
    ) / (weight_a + weight_b) - current
    rows_view = residue.reshape(residue.shape[:-1] + (residue.shape[-1] // extent, extent))
    smoothed = rows_view + penalty_mix * jnp.einsum(
        "...z,zk->...k", rows_view, tangent, precision=highest
    )
    return current + omega_step * smoothed.reshape(residue.shape)


def shards(forcing, modulus, orient_codes):
    extent = forcing.shape[3]
    blocks = forcing.shape[1]
    flat = extent * extent
    source_field = forcing[0]
    moduli = modulus[0]
    codes_here = orient_codes[0]
    tangent = tangent_matrix(extent)
    omegas = step_weights(ITERS)
    slab_count = lax.axis_size("blk")
    slab_index = lax.axis_index("blk")
    face_zeros = jnp.zeros((blocks, 3, flat), jnp.float32)
    lam_x = face_zeros
    lam_y = face_zeros
    live_slab = (slab_index < slab_count - 1).astype(jnp.float32)
    faces = [None] * blocks
    for sweep in range(ITERS + 1):
        last = sweep == ITERS
        outs = [
            kernel_sweep(source_field[b], moduli[b], faces[b], emit_u=last, emit_sides=not last)
            for b in range(blocks)
        ]
        if last:
            return jnp.stack([o[0] for o in outs], 0)[None]
        xf = jnp.stack([o[0] for o in outs], 0)
        yf = jnp.stack([o[1] for o in outs], 0)
        x_high_side = (xf[:, :, 0], xf[:, :, 1])
        x_low_side = (xf[:, :, 2], xf[:, :, 3])
        y_high_side = tuple(yf[:, :, k, :, extent:].reshape(blocks, 3, flat) for k in (0, 1))
        y_low_side = tuple(yf[:, :, k, :, :extent].reshape(blocks, 3, flat) for k in (2, 3))
        upper_value, upper_slope, upper_moduli = shifted(
            (x_low_side[0], x_low_side[1], moduli), "blk", -1
        )
        upper_value = orient(upper_value, codes_here, extent)
        upper_slope = orient(upper_slope, codes_here, extent)
        lam_x = (
            trace_update(
                lam_x,
                x_high_side,
                (upper_value, upper_slope),
                moduli,
                upper_moduli,
                omegas[sweep],
                tangent,
            )
            * live_slab
        )
        x_high = lam_x
        x_low = shifted(orient(lam_x, codes_here, extent), "blk", 1)
        next_value, next_slope, next_moduli = shifted_2(
            (y_low_side[0][0], y_low_side[1][0], moduli[0]), "face", -1
        )
        beside_value = jnp.concatenate([y_low_side[0][1:], next_value[None]], 0)
        beside_slope = jnp.concatenate([y_low_side[1][1:], next_slope[None]], 0)
        beside_moduli = jnp.concatenate([moduli[1:], next_moduli[None]], 0)
        lam_y = trace_update(
            lam_y,
            y_high_side,
            (beside_value, beside_slope),
            moduli,
            beside_moduli,
            omegas[sweep],
            tangent,
        )
        previous_trace = shifted_2(lam_y[blocks - 1], "face", 1)
        y_high = lam_y
        y_low = jnp.concatenate([previous_trace[None], lam_y[:-1]], 0)
        yadd = jnp.concatenate(
            [y_low.reshape(blocks, 3, extent, extent), y_high.reshape(blocks, 3, extent, extent)], -1
        )
        faces = [(x_low[b], x_high[b], yadd[b]) for b in range(blocks)]


def solution(mesh):
    placed = (P("blk", "face", None, None, None), P("blk", "face", None), P("blk", "face"))
    return jax.shard_map(
        shards,
        mesh=mesh,
        in_specs=placed,
        out_specs=P("blk", "face", None, None, None),
        check_vma=False,
    )
```

```python
import functools
import math

import jax
import jax.numpy as jnp
from jax import lax
from jax.sharding import PartitionSpec as P
from jax.experimental import pallas as pl
from jax.experimental.pallas import tpu as pltpu
import numpy as np
import ml_dtypes

ITERS = 2


mass_shift = 0.02
inject_scale = 2.0
traction_mix = 0.5
penalty_mix = 0.25
lower_edge = 0.3
upper_edge = 1.5
highest = lax.Precision.HIGHEST


def shifted(shard, axis, by):
    length = lax.axis_size(axis)
    pairs = [(i, i + by) for i in range(length) if 0 <= i + by < length]
    return lax.ppermute(shard, axis, pairs)


def shifted_2(shard, axis, by):
    length = lax.axis_size(axis)
    return lax.ppermute(shard, axis, [(i, (i + by) % length) for i in range(length)])


def tables(extent):
    node_index = jnp.arange(extent, dtype=jnp.float32) + 1.0
    basis = math.sqrt(2.0 / (extent + 1)) * jnp.sin(
        math.pi * node_index[:, None] * node_index[None, :] / (extent + 1)
    )
    eigenvalues = 2.0 - 2.0 * jnp.cos(math.pi * node_index / (extent + 1))
    return (basis, eigenvalues)


def tangent_matrix(extent):
    node_index = jnp.arange(extent, dtype=jnp.int32)
    distance = jnp.abs(node_index[:, None] - node_index[None, :])
    end_rows = ((node_index == 0) | (node_index == extent - 1)).astype(jnp.float32)
    adjacent = (distance == 1).astype(jnp.float32)
    diagonal_part = (distance == 0).astype(jnp.float32) * (2.0 - end_rows[:, None])
    return adjacent - diagonal_part


def step_weights(step_count):
    midpoint = 0.5 * (upper_edge + lower_edge)
    radius = 0.5 * (upper_edge - lower_edge)
    return [
        1.0 / (midpoint + radius * math.cos(math.pi * (2 * turn_index + 1) / (2 * step_count)))
        for turn_index in range(step_count)
    ]


def divisor(moduli, eigenvalues):
    extent = eigenvalues.shape[0]
    summed = eigenvalues[:, None, None] + eigenvalues[None, :, None] + eigenvalues[None, None, :]
    scaled = moduli[..., None, None, None] * summed + mass_shift
    return scaled.reshape(moduli.shape + (extent, extent * extent))


def body_transform(field_data, basis, paired_basis):
    extent = basis.shape[0]
    full_shape = field_data.shape
    pair_width = paired_basis.shape[0]
    sectioned = jnp.einsum("ix,bcxm->bcim", basis, field_data, precision=highest)
    sectioned = sectioned.reshape(full_shape[:-1] + (full_shape[-1] // pair_width, pair_width))
    sectioned = jnp.einsum("bcxpz,kz->bcxpk", sectioned, paired_basis, precision=highest)
    sectioned = sectioned.reshape(full_shape[:-1] + (extent, extent))
    sectioned = jnp.einsum("jy,bcxyz->bcxjz", basis, sectioned, precision=highest)
    return sectioned.reshape(full_shape)


def body_solve(right_side, scale_table, basis, paired_basis):
    return body_transform(
        body_transform(right_side, basis, paired_basis) / scale_table, basis, paired_basis
    )


f32 = jnp.float32


def np_tables(n):
    g = np.float32
    idx = np.arange(n, dtype=g) + g(1.0)
    arg = (g(math.pi) * idx[:, None]) * idx[None, :] / g(n + 1)
    q = g(math.sqrt(2.0 / (n + 1))) * np.sin(arg)
    e = g(2.0) - g(2.0) * np.cos(g(math.pi) * idx / g(n + 1))
    return q.astype(g), e.astype(g)


def consts(n):
    q, e = np_tables(n)
    h = n // 2
    p4 = np.kron(np.eye(4, dtype=np.float32), q.T)
    w = np.zeros((2, 4, h, 2, 4, h), np.float32)
    qq = q.reshape(h, 2, h, 2)
    for xl in range(4):
        w[:, xl, :, :, xl, :] = np.transpose(qq, (3, 2, 1, 0))
    wy = w.reshape(8 * h, 8 * h)
    ng = n // 4
    lane_h = np.arange(8 * h) // (4 * h)
    lane_xl = (np.arange(8 * h) // h) % 4
    lane_c = np.arange(8 * h) % h
    exy = (e[4 * np.arange(ng)[:, None] + lane_xl[None, :]] + e[2 * lane_c + lane_h][None, :]).astype(np.float32)
    ez = np.ascontiguousarray(np.broadcast_to(e[:, None], (n, 8 * h))).astype(np.float32)
    return stack_left(q), stack_right(p4), stack_right(wy), exy, ez


BF = jnp.bfloat16

def np_split3(w):
    b = ml_dtypes.bfloat16
    w1 = w.astype(b)
    r1 = w - w1.astype(np.float32)
    w2 = r1.astype(b)
    w3 = (r1 - w2.astype(np.float32)).astype(b)
    return w1, w2, w3


def stack_right(w):
    w1, w2, w3 = np_split3(w)
    return np.concatenate([w1, w2, w1, w1], 0)


def stack_left(w):
    w1, w2, w3 = np_split3(w)
    return np.concatenate([w1, w2, w1, w1], 1)


def split3(d):
    d1 = d.astype(BF)
    r1 = d - d1.astype(f32)
    d2 = r1.astype(BF)
    d3 = (r1 - d2.astype(f32)).astype(BF)
    return d1, d2, d3


def sdot(d, w6):
    d1, d2, d3 = split3(d)
    return jnp.dot(jnp.concatenate([d1, d1, d2, d3], 1), w6, preferred_element_type=f32)


def sdot_left(w6, d):
    d1, d2, d3 = split3(d)
    return jnp.dot(w6, jnp.concatenate([d1, d1, d2, d3], 0), preferred_element_type=f32)


def solve_kernel(*refs, with_faces, emit_u, emit_sides):
    it = iter(refs)
    mod_ref, f_ref = next(it), next(it)
    if with_faces:
        xlo_ref, xhi_ref, yadd_ref = next(it), next(it), next(it)
    q_ref, p_ref, wy_ref, exy_ref, ez_ref = next(it), next(it), next(it), next(it), next(it)
    o_ref = next(it) if emit_u else None
    if emit_sides:
        xf_ref, yf_ref = next(it), next(it)
    s_ref, z_ref = next(it), next(it)
    n = q_ref.shape[0]
    h = n // 2
    w2 = 2 * n
    w4 = 4 * n
    nn = f_ref.shape[-1]
    nch = nn // w2
    npair = nn // w4
    comp = pl.program_id(0)
    m = mod_ref[comp]
    q = q_ref[...]
    r = f_ref[0]
    if with_faces:
        rows = lax.broadcasted_iota(jnp.int32, (n, nn), 0)
        added = jnp.where(rows == 0, xlo_ref[0], 0.0) + jnp.where(rows == n - 1, xhi_ref[0], 0.0)
        lane = lax.broadcasted_iota(jnp.int32, (n, w2), 1)
        yadd = yadd_ref[0]
        first = added[:, :w2] + jnp.where(lane < n, yadd, 0.0)
        last = added[:, nn - w2:] + jnp.where(lane >= n, yadd, 0.0)
        added = jnp.concatenate([first, added[:, w2:nn - w2], last], 1)
        r = r + (2.0 * m) * added
    a = sdot_left(q, r)
    for cp in range(npair):
        z_ref[cp * n:(cp + 1) * n, :] = a[:, cp * w4:(cp + 1) * w4]
    zo = sdot(z_ref[...], p_ref[...])
    for cp in range(npair):
        for cb in range(2):
            s_ref[(2 * cp + cb) * n:(2 * cp + cb + 1) * n, :] = zo[cp * n:(cp + 1) * n, cb * w2:(cb + 1) * w2]
    wy = wy_ref[...]
    ez = ez_ref[...]
    XG = 4
    GPI = 4

    def body(it_, carry):
        lhs = []
        for gi in range(GPI):
            g = it_ * GPI + gi
            blk = jnp.concatenate([s_ref[pl.ds(g * XG + xl, h, stride=n), :] for xl in range(XG)], 0)
            tb = blk.T
            lhs.append(jnp.concatenate([tb[:n], tb[n:]], 1))
        v = sdot(jnp.concatenate(lhs, 0), wy)
        div = jnp.concatenate([m * (exy_ref[pl.ds(it_ * GPI + gi, 1), :] + ez) + 0.02 for gi in range(GPI)], 0)
        v = v / div
        v = sdot(v, wy)
        for gi in range(GPI):
            g = it_ * GPI + gi
            vg = v[gi * n:(gi + 1) * n]
            tb = jnp.concatenate([vg[:, :w2], vg[:, w2:]], 0).T
            for xl in range(XG):
                s_ref[pl.ds(g * XG + xl, h, stride=n), :] = tb[xl * h:(xl + 1) * h]
        return carry
    lax.fori_loop(0, n // (XG * GPI), body, 0)
    for cp in range(npair):
        z_ref[cp * n:(cp + 1) * n, :] = jnp.concatenate(
            [s_ref[(2 * cp) * n:(2 * cp + 1) * n, :], s_ref[(2 * cp + 1) * n:(2 * cp + 2) * n, :]], 1)
    zo = sdot(z_ref[...], p_ref[...])
    b = jnp.concatenate([zo[cp * n:(cp + 1) * n, :] for cp in range(npair)], 1)
    u = sdot_left(q, b)
    if emit_u:
        o_ref[0] = u

    def slope(p0, p1, p2, p3):
        return m * (11.0 / 6.0 * p0 - 3.0 * p1 + 1.5 * p2 - p3 / 3.0)
    if emit_sides:
        xf_ref[0, 0:1, :] = u[n - 1:n]
        xf_ref[0, 1:2, :] = slope(u[n - 1:n], u[n - 2:n - 1], u[n - 3:n - 2], u[n - 4:n - 3])
        xf_ref[0, 2:3, :] = u[0:1]
        xf_ref[0, 3:4, :] = slope(u[0:1], u[1:2], u[2:3], u[3:4])
        c_hi = u[:, nn - w2:]
        c_hi2 = u[:, nn - 2 * w2:nn - w2]
        yf_ref[0, 0] = c_hi
        yf_ref[0, 1] = slope(c_hi, pltpu.roll(c_hi, n, 1), c_hi2, pltpu.roll(c_hi2, n, 1))
        c_lo = u[:, :w2]
        c_lo2 = u[:, w2:2 * w2]
        yf_ref[0, 2] = c_lo
        yf_ref[0, 3] = slope(c_lo, pltpu.roll(c_lo, n, 1), c_lo2, pltpu.roll(c_lo2, n, 1))


def kernel_sweep(rhs, moduli, faces=None, emit_u=True, emit_sides=False, interpret=False):
    ncomp, n, nn = rhs.shape
    q, p4, wy, exy, ez = consts(n)
    full = lambda shp: pl.BlockSpec(shp, lambda c: (0,) * len(shp))
    comp3 = lambda shp: pl.BlockSpec((1,) + shp, lambda c: (c,) + (0,) * len(shp))
    smem = pl.BlockSpec(memory_space=pltpu.SMEM)
    in_specs = [smem, comp3((n, nn))]
    args = [moduli, rhs]
    if faces is not None:
        xlo, xhi, yadd = faces
        in_specs += [comp3((1, nn)), comp3((1, nn)), comp3((n, 2 * n))]
        args += [xlo.reshape(ncomp, 1, nn), xhi.reshape(ncomp, 1, nn), yadd]
    in_specs += [full(q.shape), full(p4.shape), full(wy.shape), full(exy.shape), full(ez.shape)]
    args += [q, p4, wy, exy, ez]
    out_specs, out_shape = [], []
    if emit_u:
        out_specs.append(comp3((n, nn)))
        out_shape.append(jax.ShapeDtypeStruct(rhs.shape, f32))
    if emit_sides:
        out_specs += [comp3((4, nn)), comp3((4, n, 2 * n))]
        out_shape += [jax.ShapeDtypeStruct((ncomp, 4, nn), f32), jax.ShapeDtypeStruct((ncomp, 4, n, 2 * n), f32)]
    kernel = functools.partial(solve_kernel, with_faces=faces is not None, emit_u=emit_u, emit_sides=emit_sides)
    return pl.pallas_call(
        kernel,
        grid=(ncomp,),
        in_specs=in_specs,
        out_specs=out_specs,
        out_shape=out_shape,
        scratch_shapes=[pltpu.VMEM((nn // 2, 2 * n), f32), pltpu.VMEM((nn // 4, 4 * n), f32)],
        interpret=interpret,
    )(*args)


def orient(face_field, code_table, extent):
    square = face_field.reshape(face_field.shape[:-1] + (extent, extent))
    flip_rows = (code_table % 2 == 1)[..., None, None, None]
    flip_cols = (code_table // 2 == 1)[..., None, None, None]
    square = jnp.where(flip_rows, jnp.flip(square, -2), square)
    square = jnp.where(flip_cols, jnp.flip(square, -1), square)
    return square.reshape(face_field.shape)


def face_data(solution, moduli):
    extent = solution.shape[-2]
    cube_view = solution.reshape(solution.shape[:-1] + (extent, extent))
    flat_shape = solution.shape[:-2] + (extent * extent,)

    def pack_side(planes):
        normal_slope = 11.0 / 6.0 * planes[0] - 3.0 * planes[1] + 1.5 * planes[2] - planes[3] / 3.0
        return (planes[0], moduli[..., None] * normal_slope)

    x_high = pack_side([solution[..., extent - 1 - plane_depth, :] for plane_depth in range(4)])
    x_low = pack_side([solution[..., plane_depth, :] for plane_depth in range(4)])
    y_high = pack_side(
        [
            cube_view[..., extent - 1 - plane_depth, :].reshape(flat_shape)
            for plane_depth in range(4)
        ]
    )
    y_low = pack_side(
        [cube_view[..., plane_depth, :].reshape(flat_shape) for plane_depth in range(4)]
    )
    return (x_high, x_low, y_high, y_low)


def place_faces(source_field, moduli, x_low, x_high, y_low, y_high):
    extent = source_field.shape[-2]
    added = jnp.zeros_like(source_field)
    added = added.at[..., 0, :].add(x_low)
    added = added.at[..., extent - 1, :].add(x_high)
    cube_view = added.reshape(added.shape[:-1] + (extent, extent))
    low_square = y_low.reshape(y_low.shape[:-1] + (extent, extent))
    high_square = y_high.reshape(y_high.shape[:-1] + (extent, extent))
    cube_view = cube_view.at[..., 0, :].add(low_square)
    cube_view = cube_view.at[..., extent - 1, :].add(high_square)
    added = cube_view.reshape(source_field.shape)
    return source_field + inject_scale * moduli[..., None, None] * added


def trace_update(current, side_a, side_b, moduli_a, moduli_b, omega_step, tangent):
    extent = tangent.shape[0]
    weight_a = moduli_a[..., None]
    weight_b = moduli_b[..., None]
    residue = (
        weight_a * side_a[0] + weight_b * side_b[0] + traction_mix * (side_a[1] + side_b[1])
    ) / (weight_a + weight_b) - current
    rows_view = residue.reshape(residue.shape[:-1] + (residue.shape[-1] // extent, extent))
    smoothed = rows_view + penalty_mix * jnp.einsum(
        "...z,zk->...k", rows_view, tangent, precision=highest
    )
    return current + omega_step * smoothed.reshape(residue.shape)


def pack_side(side):
    return jnp.stack(side, 1)


def unpack_side(packed):
    return (packed[:, 0], packed[:, 1])


def oriented(side, codes, extent):
    return (orient(side[0], codes, extent), orient(side[1], codes, extent))


def shards(forcing, modulus, orient_codes):
    extent = forcing.shape[3]
    blocks = forcing.shape[1]
    flat = extent * extent
    source_field = forcing[0]
    moduli = modulus[0]
    codes_here = orient_codes[0]
    tangent = tangent_matrix(extent)
    omegas = step_weights(ITERS)
    slab_count = lax.axis_size("blk")
    slab_index = lax.axis_index("blk")
    has_up = (slab_index < slab_count - 1).astype(jnp.float32)
    has_down = (slab_index > 0).astype(jnp.float32)
    moduli_rows = jnp.broadcast_to(moduli[:, None, :, None], (blocks, 1, 3, flat))
    codes_rows = jnp.broadcast_to(codes_here.astype(jnp.float32)[:, None, None, None], (blocks, 1, 3, flat))
    face_zeros = jnp.zeros((blocks, 3, flat), jnp.float32)
    lam_x_up = face_zeros
    lam_x_down = face_zeros
    lam_y_next = face_zeros
    lam_y_prev = face_zeros
    faces = [None] * blocks
    for sweep in range(ITERS + 1):
        last = sweep == ITERS
        outs = [
            kernel_sweep(source_field[b], moduli[b], faces[b], emit_u=last, emit_sides=not last)
            for b in range(blocks)
        ]
        if last:
            return jnp.stack([o[0] for o in outs], 0)[None]
        xf = jnp.stack([o[0] for o in outs], 0)
        yf = jnp.stack([o[1] for o in outs], 0)
        x_high_side = xf[:, :, 0:2].transpose(0, 2, 1, 3)
        x_low_side = xf[:, :, 2:4].transpose(0, 2, 1, 3)
        y_high_side = yf[:, :, 0:2, :, extent:].transpose(0, 2, 1, 3, 4).reshape(blocks, 2, 3, flat)
        y_low_side = yf[:, :, 2:4, :, :extent].transpose(0, 2, 1, 3, 4).reshape(blocks, 2, 3, flat)
        first = sweep == 0
        if first:
            x_low_side = jnp.concatenate([x_low_side, moduli_rows], 1)
            x_high_side = jnp.concatenate([x_high_side, moduli_rows, codes_rows], 1)
            y_low_side = jnp.concatenate([y_low_side, moduli_rows], 1)
            y_high_side = jnp.concatenate([y_high_side, moduli_rows], 1)
        upper_side = shifted(x_low_side, "blk", -1)
        lower_side = shifted(x_high_side, "blk", 1)
        next_side = jnp.concatenate([y_low_side[1:], shifted_2(y_low_side[:1], "face", -1)], 0)
        prev_side = jnp.concatenate([shifted_2(y_high_side[-1:], "face", 1), y_high_side[:-1]], 0)
        if first:
            moduli_up = upper_side[:, 2, :, 0]
            moduli_down = lower_side[:, 2, :, 0]
            codes_down = lower_side[:, 3, 0, 0].astype(jnp.int32)
            moduli_next = next_side[:, 2, :, 0]
            moduli_prev = prev_side[:, 2, :, 0]
        lam_x_up = (
            trace_update(
                lam_x_up,
                unpack_side(x_high_side),
                oriented(unpack_side(upper_side), codes_here, extent),
                moduli,
                moduli_up,
                omegas[sweep],
                tangent,
            )
            * has_up
        )
        lam_x_down = (
            trace_update(
                lam_x_down,
                unpack_side(lower_side),
                oriented(unpack_side(x_low_side), codes_down, extent),
                moduli_down,
                moduli,
                omegas[sweep],
                tangent,
            )
            * has_down
        )
        lam_y_next = trace_update(
            lam_y_next, unpack_side(y_high_side), unpack_side(next_side), moduli, moduli_next,
            omegas[sweep], tangent,
        )
        lam_y_prev = trace_update(
            lam_y_prev, unpack_side(prev_side), unpack_side(y_low_side), moduli_prev, moduli,
            omegas[sweep], tangent,
        )
        x_low = orient(lam_x_down, codes_down, extent)
        yadd = jnp.concatenate(
            [lam_y_prev.reshape(blocks, 3, extent, extent), lam_y_next.reshape(blocks, 3, extent, extent)], -1
        )
        faces = [(x_low[b], lam_x_up[b], yadd[b]) for b in range(blocks)]


def solution(mesh):
    placed = (P("blk", "face", None, None, None), P("blk", "face", None), P("blk", "face"))
    return jax.shard_map(
        shards,
        mesh=mesh,
        in_specs=placed,
        out_specs=P("blk", "face", None, None, None),
        check_vma=False,
    )
```

```python
import functools
import math

import jax
import jax.numpy as jnp
from jax import lax
from jax.sharding import PartitionSpec as P
from jax.experimental import pallas as pl
from jax.experimental.pallas import tpu as pltpu
import numpy as np
import ml_dtypes

ITERS = 2


mass_shift = 0.02
inject_scale = 2.0
traction_mix = 0.5
penalty_mix = 0.25
lower_edge = 0.3
upper_edge = 1.5
highest = lax.Precision.HIGHEST


def shifted(shard, axis, by):
    length = lax.axis_size(axis)
    pairs = [(i, i + by) for i in range(length) if 0 <= i + by < length]
    return lax.ppermute(shard, axis, pairs)


def shifted_2(shard, axis, by):
    length = lax.axis_size(axis)
    return lax.ppermute(shard, axis, [(i, (i + by) % length) for i in range(length)])


def tables(extent):
    node_index = jnp.arange(extent, dtype=jnp.float32) + 1.0
    basis = math.sqrt(2.0 / (extent + 1)) * jnp.sin(
        math.pi * node_index[:, None] * node_index[None, :] / (extent + 1)
    )
    eigenvalues = 2.0 - 2.0 * jnp.cos(math.pi * node_index / (extent + 1))
    return (basis, eigenvalues)


def tangent_matrix(extent):
    node_index = jnp.arange(extent, dtype=jnp.int32)
    distance = jnp.abs(node_index[:, None] - node_index[None, :])
    end_rows = ((node_index == 0) | (node_index == extent - 1)).astype(jnp.float32)
    adjacent = (distance == 1).astype(jnp.float32)
    diagonal_part = (distance == 0).astype(jnp.float32) * (2.0 - end_rows[:, None])
    return adjacent - diagonal_part


def step_weights(step_count):
    midpoint = 0.5 * (upper_edge + lower_edge)
    radius = 0.5 * (upper_edge - lower_edge)
    return [
        1.0 / (midpoint + radius * math.cos(math.pi * (2 * turn_index + 1) / (2 * step_count)))
        for turn_index in range(step_count)
    ]


def divisor(moduli, eigenvalues):
    extent = eigenvalues.shape[0]
    summed = eigenvalues[:, None, None] + eigenvalues[None, :, None] + eigenvalues[None, None, :]
    scaled = moduli[..., None, None, None] * summed + mass_shift
    return scaled.reshape(moduli.shape + (extent, extent * extent))


def body_transform(field_data, basis, paired_basis):
    extent = basis.shape[0]
    full_shape = field_data.shape
    pair_width = paired_basis.shape[0]
    sectioned = jnp.einsum("ix,bcxm->bcim", basis, field_data, precision=highest)
    sectioned = sectioned.reshape(full_shape[:-1] + (full_shape[-1] // pair_width, pair_width))
    sectioned = jnp.einsum("bcxpz,kz->bcxpk", sectioned, paired_basis, precision=highest)
    sectioned = sectioned.reshape(full_shape[:-1] + (extent, extent))
    sectioned = jnp.einsum("jy,bcxyz->bcxjz", basis, sectioned, precision=highest)
    return sectioned.reshape(full_shape)


def body_solve(right_side, scale_table, basis, paired_basis):
    return body_transform(
        body_transform(right_side, basis, paired_basis) / scale_table, basis, paired_basis
    )


f32 = jnp.float32


def np_tables(n):
    g = np.float32
    idx = np.arange(n, dtype=g) + g(1.0)
    arg = (g(math.pi) * idx[:, None]) * idx[None, :] / g(n + 1)
    q = g(math.sqrt(2.0 / (n + 1))) * np.sin(arg)
    e = g(2.0) - g(2.0) * np.cos(g(math.pi) * idx / g(n + 1))
    return q.astype(g), e.astype(g)


def consts(n):
    q, e = np_tables(n)
    h = n // 2
    p4 = np.kron(np.eye(4, dtype=np.float32), q.T)
    w = np.zeros((2, 4, h, 2, 4, h), np.float32)
    qq = q.reshape(h, 2, h, 2)
    for xl in range(4):
        w[:, xl, :, :, xl, :] = np.transpose(qq, (3, 2, 1, 0))
    wy = w.reshape(8 * h, 8 * h)
    ng = n // 4
    lane_h = np.arange(8 * h) // (4 * h)
    lane_xl = (np.arange(8 * h) // h) % 4
    lane_c = np.arange(8 * h) % h
    exy = (e[4 * np.arange(ng)[:, None] + lane_xl[None, :]] + e[2 * lane_c + lane_h][None, :]).astype(np.float32)
    ez = np.ascontiguousarray(np.broadcast_to(e[:, None], (n, 8 * h))).astype(np.float32)
    return stack_left(q), stack_right(p4), stack_right(wy), exy, ez


BF = jnp.bfloat16

def np_split3(w):
    b = ml_dtypes.bfloat16
    w1 = w.astype(b)
    r1 = w - w1.astype(np.float32)
    w2 = r1.astype(b)
    w3 = (r1 - w2.astype(np.float32)).astype(b)
    return w1, w2, w3


def stack_right(w):
    w1, w2, w3 = np_split3(w)
    return np.concatenate([w1, w2, w1, w1], 0)


def stack_left(w):
    w1, w2, w3 = np_split3(w)
    return np.concatenate([w1, w2, w1, w1], 1)


def split3(d):
    d1 = d.astype(BF)
    r1 = d - d1.astype(f32)
    d2 = r1.astype(BF)
    d3 = (r1 - d2.astype(f32)).astype(BF)
    return d1, d2, d3


def sdot(d, w6):
    d1, d2, d3 = split3(d)
    return jnp.dot(jnp.concatenate([d1, d1, d2, d3], 1), w6, preferred_element_type=f32)


def sdot_left(w6, d):
    d1, d2, d3 = split3(d)
    return jnp.dot(w6, jnp.concatenate([d1, d1, d2, d3], 0), preferred_element_type=f32)


def solve_kernel(*refs, with_faces, emit_u, emit_sides):
    it = iter(refs)
    mod_ref, f_ref = next(it), next(it)
    if with_faces:
        xlo_ref, xhi_ref, yadd_ref = next(it), next(it), next(it)
    q_ref, p_ref, wy_ref, exy_ref, ez_ref = next(it), next(it), next(it), next(it), next(it)
    code_ref = next(it)
    o_ref = next(it) if emit_u else None
    if emit_sides:
        xh_ref, xl_ref, yh_ref, yl_ref = next(it), next(it), next(it), next(it)
    s_ref, z_ref = next(it), next(it)
    n = q_ref.shape[0]
    h = n // 2
    w2 = 2 * n
    w4 = 4 * n
    nn = f_ref.shape[-1]
    nch = nn // w2
    npair = nn // w4
    comp = pl.program_id(0)
    m = mod_ref[comp]
    q = q_ref[...]
    r = f_ref[0]
    if with_faces:
        rows = lax.broadcasted_iota(jnp.int32, (n, nn), 0)
        added = jnp.where(rows == 0, xlo_ref[0], 0.0) + jnp.where(rows == n - 1, xhi_ref[0], 0.0)
        lane = lax.broadcasted_iota(jnp.int32, (n, w2), 1)
        yadd = yadd_ref[0]
        first = added[:, :w2] + jnp.where(lane < n, yadd, 0.0)
        last = added[:, nn - w2:] + jnp.where(lane >= n, yadd, 0.0)
        added = jnp.concatenate([first, added[:, w2:nn - w2], last], 1)
        r = r + (2.0 * m) * added
    a = sdot_left(q, r)
    for cp in range(npair):
        z_ref[cp * n:(cp + 1) * n, :] = a[:, cp * w4:(cp + 1) * w4]
    zo = sdot(z_ref[...], p_ref[...])
    for cp in range(npair):
        for cb in range(2):
            s_ref[(2 * cp + cb) * n:(2 * cp + cb + 1) * n, :] = zo[cp * n:(cp + 1) * n, cb * w2:(cb + 1) * w2]
    wy = wy_ref[...]
    ez = ez_ref[...]
    XG = 4
    GPI = 4

    def body(it_, carry):
        lhs = []
        for gi in range(GPI):
            g = it_ * GPI + gi
            blk = jnp.concatenate([s_ref[pl.ds(g * XG + xl, h, stride=n), :] for xl in range(XG)], 0)
            tb = blk.T
            lhs.append(jnp.concatenate([tb[:n], tb[n:]], 1))
        v = sdot(jnp.concatenate(lhs, 0), wy)
        div = jnp.concatenate([m * (exy_ref[pl.ds(it_ * GPI + gi, 1), :] + ez) + 0.02 for gi in range(GPI)], 0)
        v = v / div
        v = sdot(v, wy)
        for gi in range(GPI):
            g = it_ * GPI + gi
            vg = v[gi * n:(gi + 1) * n]
            tb = jnp.concatenate([vg[:, :w2], vg[:, w2:]], 0).T
            for xl in range(XG):
                s_ref[pl.ds(g * XG + xl, h, stride=n), :] = tb[xl * h:(xl + 1) * h]
        return carry
    lax.fori_loop(0, n // (XG * GPI), body, 0)
    for cp in range(npair):
        z_ref[cp * n:(cp + 1) * n, :] = jnp.concatenate(
            [s_ref[(2 * cp) * n:(2 * cp + 1) * n, :], s_ref[(2 * cp + 1) * n:(2 * cp + 2) * n, :]], 1)
    zo = sdot(z_ref[...], p_ref[...])
    b = jnp.concatenate([zo[cp * n:(cp + 1) * n, :] for cp in range(npair)], 1)
    u = sdot_left(q, b)
    if emit_u:
        o_ref[0] = u

    def slope(p0, p1, p2, p3):
        return m * (11.0 / 6.0 * p0 - 3.0 * p1 + 1.5 * p2 - p3 / 3.0)
    if emit_sides:
        m_row = jnp.full((1, nn), m, f32)
        xh_ref[0, 0:1, :] = u[n - 1:n]
        xh_ref[0, 1:2, :] = slope(u[n - 1:n], u[n - 2:n - 1], u[n - 3:n - 2], u[n - 4:n - 3])
        xh_ref[0, 2:3, :] = m_row
        xh_ref[0, 3:4, :] = jnp.full((1, nn), code_ref[0], f32)
        xl_ref[0, 0:1, :] = u[0:1]
        xl_ref[0, 1:2, :] = slope(u[0:1], u[1:2], u[2:3], u[3:4])
        xl_ref[0, 2:3, :] = m_row
        m_sq = jnp.full((n, w2), m, f32)
        c_hi = u[:, nn - w2:]
        c_hi2 = u[:, nn - 2 * w2:nn - w2]
        yh_ref[0, 0] = c_hi
        yh_ref[0, 1] = slope(c_hi, pltpu.roll(c_hi, n, 1), c_hi2, pltpu.roll(c_hi2, n, 1))
        yh_ref[0, 2] = m_sq
        c_lo = u[:, :w2]
        c_lo2 = u[:, w2:2 * w2]
        yl_ref[0, 0] = c_lo
        yl_ref[0, 1] = slope(c_lo, pltpu.roll(c_lo, n, 1), c_lo2, pltpu.roll(c_lo2, n, 1))
        yl_ref[0, 2] = m_sq


def kernel_sweep(rhs, moduli, code, faces=None, emit_u=True, emit_sides=False, interpret=False):
    ncomp, n, nn = rhs.shape
    q, p4, wy, exy, ez = consts(n)
    full = lambda shp: pl.BlockSpec(shp, lambda c: (0,) * len(shp))
    comp3 = lambda shp: pl.BlockSpec((1,) + shp, lambda c: (c,) + (0,) * len(shp))
    smem = pl.BlockSpec(memory_space=pltpu.SMEM)
    in_specs = [smem, comp3((n, nn))]
    args = [moduli, rhs]
    if faces is not None:
        xlo, xhi, yadd = faces
        in_specs += [comp3((1, nn)), comp3((1, nn)), comp3((n, 2 * n))]
        args += [xlo.reshape(ncomp, 1, nn), xhi.reshape(ncomp, 1, nn), yadd]
    in_specs += [full(q.shape), full(p4.shape), full(wy.shape), full(exy.shape), full(ez.shape), smem]
    args += [q, p4, wy, exy, ez, code]
    out_specs, out_shape = [], []
    if emit_u:
        out_specs.append(comp3((n, nn)))
        out_shape.append(jax.ShapeDtypeStruct(rhs.shape, f32))
    if emit_sides:
        out_specs += [comp3((4, nn)), comp3((3, nn)), comp3((3, n, 2 * n)), comp3((3, n, 2 * n))]
        out_shape += [jax.ShapeDtypeStruct((ncomp, 4, nn), f32), jax.ShapeDtypeStruct((ncomp, 3, nn), f32),
                      jax.ShapeDtypeStruct((ncomp, 3, n, 2 * n), f32), jax.ShapeDtypeStruct((ncomp, 3, n, 2 * n), f32)]
    kernel = functools.partial(solve_kernel, with_faces=faces is not None, emit_u=emit_u, emit_sides=emit_sides)
    return pl.pallas_call(
        kernel,
        grid=(ncomp,),
        in_specs=in_specs,
        out_specs=out_specs,
        out_shape=out_shape,
        scratch_shapes=[pltpu.VMEM((nn // 2, 2 * n), f32), pltpu.VMEM((nn // 4, 4 * n), f32)],
        interpret=interpret,
    )(*args)


def orient(face_field, code_table, extent):
    square = face_field.reshape(face_field.shape[:-1] + (extent, extent))
    flip_rows = (code_table % 2 == 1)[..., None, None, None]
    flip_cols = (code_table // 2 == 1)[..., None, None, None]
    square = jnp.where(flip_rows, jnp.flip(square, -2), square)
    square = jnp.where(flip_cols, jnp.flip(square, -1), square)
    return square.reshape(face_field.shape)


def face_data(solution, moduli):
    extent = solution.shape[-2]
    cube_view = solution.reshape(solution.shape[:-1] + (extent, extent))
    flat_shape = solution.shape[:-2] + (extent * extent,)

    def pack_side(planes):
        normal_slope = 11.0 / 6.0 * planes[0] - 3.0 * planes[1] + 1.5 * planes[2] - planes[3] / 3.0
        return (planes[0], moduli[..., None] * normal_slope)

    x_high = pack_side([solution[..., extent - 1 - plane_depth, :] for plane_depth in range(4)])
    x_low = pack_side([solution[..., plane_depth, :] for plane_depth in range(4)])
    y_high = pack_side(
        [
            cube_view[..., extent - 1 - plane_depth, :].reshape(flat_shape)
            for plane_depth in range(4)
        ]
    )
    y_low = pack_side(
        [cube_view[..., plane_depth, :].reshape(flat_shape) for plane_depth in range(4)]
    )
    return (x_high, x_low, y_high, y_low)


def place_faces(source_field, moduli, x_low, x_high, y_low, y_high):
    extent = source_field.shape[-2]
    added = jnp.zeros_like(source_field)
    added = added.at[..., 0, :].add(x_low)
    added = added.at[..., extent - 1, :].add(x_high)
    cube_view = added.reshape(added.shape[:-1] + (extent, extent))
    low_square = y_low.reshape(y_low.shape[:-1] + (extent, extent))
    high_square = y_high.reshape(y_high.shape[:-1] + (extent, extent))
    cube_view = cube_view.at[..., 0, :].add(low_square)
    cube_view = cube_view.at[..., extent - 1, :].add(high_square)
    added = cube_view.reshape(source_field.shape)
    return source_field + inject_scale * moduli[..., None, None] * added


def trace_update(current, side_a, side_b, moduli_a, moduli_b, omega_step, tangent):
    extent = tangent.shape[0]
    weight_a = moduli_a[..., None]
    weight_b = moduli_b[..., None]
    residue = (
        weight_a * side_a[0] + weight_b * side_b[0] + traction_mix * (side_a[1] + side_b[1])
    ) / (weight_a + weight_b) - current
    rows_view = residue.reshape(residue.shape[:-1] + (residue.shape[-1] // extent, extent))
    smoothed = rows_view + penalty_mix * jnp.einsum(
        "...z,zk->...k", rows_view, tangent, precision=highest
    )
    return current + omega_step * smoothed.reshape(residue.shape)


def x_side(packet):
    return (packet[:, :, 0], packet[:, :, 1])


def y_side(packet, low):
    extent = packet.shape[-2]
    part = packet[..., :extent] if low else packet[..., extent:]
    return (part[:, :, 0], part[:, :, 1])


def oriented(side, codes, extent):
    return (orient(side[0], codes, extent), orient(side[1], codes, extent))


def square_update(current, side_a, side_b, moduli_a, moduli_b, omega_step, tangent):
    weight_a = moduli_a[..., None, None]
    weight_b = moduli_b[..., None, None]
    residue = (
        weight_a * side_a[0] + weight_b * side_b[0] + traction_mix * (side_a[1] + side_b[1])
    ) / (weight_a + weight_b) - current
    smoothed = residue + penalty_mix * jnp.einsum("...z,zk->...k", residue, tangent, precision=highest)
    return current + omega_step * smoothed


def shards(forcing, modulus, orient_codes):
    extent = forcing.shape[3]
    blocks = forcing.shape[1]
    flat = extent * extent
    source_field = forcing[0]
    moduli = modulus[0]
    codes_here = orient_codes[0]
    code_values = codes_here.astype(jnp.float32)
    tangent = tangent_matrix(extent)
    omegas = step_weights(ITERS)
    slab_count = lax.axis_size("blk")
    slab_index = lax.axis_index("blk")
    has_up = (slab_index < slab_count - 1).astype(jnp.float32)
    has_down = (slab_index > 0).astype(jnp.float32)
    lam_x_up = jnp.zeros((blocks, 3, flat), jnp.float32)
    lam_x_down = lam_x_up
    lam_y_next = jnp.zeros((blocks, 3, extent, extent), jnp.float32)
    lam_y_prev = lam_y_next
    faces = [None] * blocks
    for sweep in range(ITERS + 1):
        last = sweep == ITERS
        outs = [
            kernel_sweep(source_field[b], moduli[b], code_values[b:b + 1], faces[b], emit_u=last, emit_sides=not last)
            for b in range(blocks)
        ]
        if last:
            return jnp.stack([o[0] for o in outs], 0)[None]
        xh, xl, yh, yl = (jnp.stack([o[k] for o in outs], 0) for k in range(4))
        upper = shifted(xl, "blk", -1)
        lower = shifted(xh, "blk", 1)
        nxt = jnp.concatenate([yl[1:], shifted_2(yl[:1], "face", -1)], 0)
        prv = jnp.concatenate([shifted_2(yh[-1:], "face", 1), yh[:-1]], 0)
        if sweep == 0:
            moduli_up = upper[:, :, 2, 0]
            moduli_down = lower[:, :, 2, 0]
            codes_down = lower[:, 0, 3, 0].astype(jnp.int32)
            moduli_next = nxt[:, :, 2, 0, 0]
            moduli_prev = prv[:, :, 2, 0, 0]
        lam_x_up = (
            trace_update(
                lam_x_up, x_side(xh), oriented(x_side(upper), codes_here, extent),
                moduli, moduli_up, omegas[sweep], tangent,
            )
            * has_up
        )
        lam_x_down = (
            trace_update(
                lam_x_down, x_side(lower), oriented(x_side(xl), codes_down, extent),
                moduli_down, moduli, omegas[sweep], tangent,
            )
            * has_down
        )
        lam_y_next = square_update(
            lam_y_next, y_side(yh, False), y_side(nxt, True), moduli, moduli_next, omegas[sweep], tangent
        )
        lam_y_prev = square_update(
            lam_y_prev, y_side(prv, False), y_side(yl, True), moduli_prev, moduli, omegas[sweep], tangent
        )
        x_low = orient(lam_x_down, codes_down, extent)
        yadd = jnp.concatenate([lam_y_prev, lam_y_next], -1)
        faces = [(x_low[b], lam_x_up[b], yadd[b]) for b in range(blocks)]


def solution(mesh):
    placed = (P("blk", "face", None, None, None), P("blk", "face", None), P("blk", "face"))
    return jax.shard_map(
        shards,
        mesh=mesh,
        in_specs=placed,
        out_specs=P("blk", "face", None, None, None),
        check_vma=False,
    )
```

```python
import functools
import math

import jax
import jax.numpy as jnp
from jax import lax
from jax.sharding import PartitionSpec as P
from jax.experimental import pallas as pl
from jax.experimental.pallas import tpu as pltpu
import numpy as np
import ml_dtypes

ITERS = 2


mass_shift = 0.02
inject_scale = 2.0
traction_mix = 0.5
penalty_mix = 0.25
lower_edge = 0.3
upper_edge = 1.5
highest = lax.Precision.HIGHEST


def shifted(shard, axis, by):
    length = lax.axis_size(axis)
    pairs = [(i, i + by) for i in range(length) if 0 <= i + by < length]
    return lax.ppermute(shard, axis, pairs)


def shifted_2(shard, axis, by):
    length = lax.axis_size(axis)
    return lax.ppermute(shard, axis, [(i, (i + by) % length) for i in range(length)])


def tables(extent):
    node_index = jnp.arange(extent, dtype=jnp.float32) + 1.0
    basis = math.sqrt(2.0 / (extent + 1)) * jnp.sin(
        math.pi * node_index[:, None] * node_index[None, :] / (extent + 1)
    )
    eigenvalues = 2.0 - 2.0 * jnp.cos(math.pi * node_index / (extent + 1))
    return (basis, eigenvalues)


def tangent_matrix(extent):
    node_index = jnp.arange(extent, dtype=jnp.int32)
    distance = jnp.abs(node_index[:, None] - node_index[None, :])
    end_rows = ((node_index == 0) | (node_index == extent - 1)).astype(jnp.float32)
    adjacent = (distance == 1).astype(jnp.float32)
    diagonal_part = (distance == 0).astype(jnp.float32) * (2.0 - end_rows[:, None])
    return adjacent - diagonal_part


def step_weights(step_count):
    midpoint = 0.5 * (upper_edge + lower_edge)
    radius = 0.5 * (upper_edge - lower_edge)
    return [
        1.0 / (midpoint + radius * math.cos(math.pi * (2 * turn_index + 1) / (2 * step_count)))
        for turn_index in range(step_count)
    ]


def divisor(moduli, eigenvalues):
    extent = eigenvalues.shape[0]
    summed = eigenvalues[:, None, None] + eigenvalues[None, :, None] + eigenvalues[None, None, :]
    scaled = moduli[..., None, None, None] * summed + mass_shift
    return scaled.reshape(moduli.shape + (extent, extent * extent))


def body_transform(field_data, basis, paired_basis):
    extent = basis.shape[0]
    full_shape = field_data.shape
    pair_width = paired_basis.shape[0]
    sectioned = jnp.einsum("ix,bcxm->bcim", basis, field_data, precision=highest)
    sectioned = sectioned.reshape(full_shape[:-1] + (full_shape[-1] // pair_width, pair_width))
    sectioned = jnp.einsum("bcxpz,kz->bcxpk", sectioned, paired_basis, precision=highest)
    sectioned = sectioned.reshape(full_shape[:-1] + (extent, extent))
    sectioned = jnp.einsum("jy,bcxyz->bcxjz", basis, sectioned, precision=highest)
    return sectioned.reshape(full_shape)


def body_solve(right_side, scale_table, basis, paired_basis):
    return body_transform(
        body_transform(right_side, basis, paired_basis) / scale_table, basis, paired_basis
    )


f32 = jnp.float32


def np_tables(n):
    g = np.float32
    idx = np.arange(n, dtype=g) + g(1.0)
    arg = (g(math.pi) * idx[:, None]) * idx[None, :] / g(n + 1)
    q = g(math.sqrt(2.0 / (n + 1))) * np.sin(arg)
    e = g(2.0) - g(2.0) * np.cos(g(math.pi) * idx / g(n + 1))
    return q.astype(g), e.astype(g)


def consts(n):
    q, e = np_tables(n)
    h = n // 2
    p4 = np.kron(np.eye(4, dtype=np.float32), q.T)
    w = np.zeros((2, 4, h, 2, 4, h), np.float32)
    qq = q.reshape(h, 2, h, 2)
    for xl in range(4):
        w[:, xl, :, :, xl, :] = np.transpose(qq, (3, 2, 1, 0))
    wy = w.reshape(8 * h, 8 * h)
    ng = n // 4
    lane_h = np.arange(8 * h) // (4 * h)
    lane_xl = (np.arange(8 * h) // h) % 4
    lane_c = np.arange(8 * h) % h
    exy = (e[4 * np.arange(ng)[:, None] + lane_xl[None, :]] + e[2 * lane_c + lane_h][None, :]).astype(np.float32)
    ez = np.ascontiguousarray(np.broadcast_to(e[:, None], (n, 8 * h))).astype(np.float32)
    return stack_left(q), stack_right(p4), stack_right(wy), exy, ez


BF = jnp.bfloat16

def np_split3(w):
    b = ml_dtypes.bfloat16
    w1 = w.astype(b)
    r1 = w - w1.astype(np.float32)
    w2 = r1.astype(b)
    w3 = (r1 - w2.astype(np.float32)).astype(b)
    return w1, w2, w3


def stack_right(w):
    w1, w2, w3 = np_split3(w)
    return np.concatenate([w1, w2, w1, w1], 0)


def stack_left(w):
    w1, w2, w3 = np_split3(w)
    return np.concatenate([w1, w2, w1, w1], 1)


def split3(d):
    d1 = d.astype(BF)
    r1 = d - d1.astype(f32)
    d2 = r1.astype(BF)
    d3 = (r1 - d2.astype(f32)).astype(BF)
    return d1, d2, d3


def sdot(d, w6):
    d1, d2, d3 = split3(d)
    return jnp.dot(jnp.concatenate([d1, d1, d2, d3], 1), w6, preferred_element_type=f32)


def sdot_left(w6, d):
    d1, d2, d3 = split3(d)
    return jnp.dot(w6, jnp.concatenate([d1, d1, d2, d3], 0), preferred_element_type=f32)


def solve_kernel(*refs, with_faces, emit_u, emit_sides):
    it = iter(refs)
    mod_ref, f_ref = next(it), next(it)
    if with_faces:
        xlo_ref, xhi_ref, yadd_ref = next(it), next(it), next(it)
    q_ref, p_ref, wy_ref, exy_ref, ez_ref = next(it), next(it), next(it), next(it), next(it)
    code_ref = next(it)
    o_ref = next(it) if emit_u else None
    if emit_sides:
        xh_ref, xl_ref, yh_ref, yl_ref = next(it), next(it), next(it), next(it)
    s_ref, z_ref = next(it), next(it)
    n = q_ref.shape[0]
    h = n // 2
    w2 = 2 * n
    w4 = 4 * n
    nn = f_ref.shape[-1]
    nch = nn // w2
    npair = nn // w4
    comp = pl.program_id(0)
    m = mod_ref[comp]
    q = q_ref[...]
    r = f_ref[0]
    if with_faces:
        rows = lax.broadcasted_iota(jnp.int32, (n, nn), 0)
        added = jnp.where(rows == 0, xlo_ref[0], 0.0) + jnp.where(rows == n - 1, xhi_ref[0], 0.0)
        lane = lax.broadcasted_iota(jnp.int32, (n, w2), 1)
        yadd = yadd_ref[0]
        first = added[:, :w2] + jnp.where(lane < n, yadd, 0.0)
        last = added[:, nn - w2:] + jnp.where(lane >= n, yadd, 0.0)
        added = jnp.concatenate([first, added[:, w2:nn - w2], last], 1)
        r = r + (2.0 * m) * added
    a = sdot_left(q, r)
    for cp in range(npair):
        z_ref[cp * n:(cp + 1) * n, :] = a[:, cp * w4:(cp + 1) * w4]
    zo = sdot(z_ref[...], p_ref[...])
    for cp in range(npair):
        for cb in range(2):
            s_ref[(2 * cp + cb) * n:(2 * cp + cb + 1) * n, :] = zo[cp * n:(cp + 1) * n, cb * w2:(cb + 1) * w2]
    wy = wy_ref[...]
    ez = ez_ref[...]
    XG = 4
    GPI = 4

    def body(it_, carry):
        lhs = []
        for gi in range(GPI):
            g = it_ * GPI + gi
            blk = jnp.concatenate([s_ref[pl.ds(g * XG + xl, h, stride=n), :] for xl in range(XG)], 0)
            tb = blk.T
            lhs.append(jnp.concatenate([tb[:n], tb[n:]], 1))
        v = sdot(jnp.concatenate(lhs, 0), wy)
        div = jnp.concatenate([m * (exy_ref[pl.ds(it_ * GPI + gi, 1), :] + ez) + 0.02 for gi in range(GPI)], 0)
        v = v / div
        v = sdot(v, wy)
        for gi in range(GPI):
            g = it_ * GPI + gi
            vg = v[gi * n:(gi + 1) * n]
            tb = jnp.concatenate([vg[:, :w2], vg[:, w2:]], 0).T
            for xl in range(XG):
                s_ref[pl.ds(g * XG + xl, h, stride=n), :] = tb[xl * h:(xl + 1) * h]
        return carry
    lax.fori_loop(0, n // (XG * GPI), body, 0)
    for cp in range(npair):
        z_ref[cp * n:(cp + 1) * n, :] = jnp.concatenate(
            [s_ref[(2 * cp) * n:(2 * cp + 1) * n, :], s_ref[(2 * cp + 1) * n:(2 * cp + 2) * n, :]], 1)
    zo = sdot(z_ref[...], p_ref[...])
    b = jnp.concatenate([zo[cp * n:(cp + 1) * n, :] for cp in range(npair)], 1)
    u = sdot_left(q, b)
    if emit_u:
        o_ref[0] = u

    def slope(p0, p1, p2, p3):
        return m * (11.0 / 6.0 * p0 - 3.0 * p1 + 1.5 * p2 - p3 / 3.0)
    if emit_sides:
        m_row = jnp.full((1, nn), m, f32)
        xh_ref[0, 0:1, :] = m * u[n - 1:n] + 0.5 * slope(u[n - 1:n], u[n - 2:n - 1], u[n - 3:n - 2], u[n - 4:n - 3])
        xh_ref[0, 1:2, :] = m_row
        xh_ref[0, 2:3, :] = jnp.full((1, nn), code_ref[0], f32)
        xl_ref[0, 0:1, :] = m * u[0:1] + 0.5 * slope(u[0:1], u[1:2], u[2:3], u[3:4])
        xl_ref[0, 1:2, :] = m_row
        m_sq = jnp.full((n, n), m, f32)
        c_hi = u[:, nn - w2:]
        c_hi2 = u[:, nn - 2 * w2:nn - w2]
        s_hi = m * c_hi + 0.5 * slope(c_hi, pltpu.roll(c_hi, n, 1), c_hi2, pltpu.roll(c_hi2, n, 1))
        yh_ref[0, 0] = pltpu.roll(s_hi, n, 1)[:, :n]
        yh_ref[0, 1] = m_sq
        c_lo = u[:, :w2]
        c_lo2 = u[:, w2:2 * w2]
        s_lo = m * c_lo + 0.5 * slope(c_lo, pltpu.roll(c_lo, n, 1), c_lo2, pltpu.roll(c_lo2, n, 1))
        yl_ref[0, 0] = s_lo[:, :n]
        yl_ref[0, 1] = m_sq


def kernel_sweep(rhs, moduli, code, faces=None, emit_u=True, emit_sides=False, interpret=False):
    ncomp, n, nn = rhs.shape
    q, p4, wy, exy, ez = consts(n)
    full = lambda shp: pl.BlockSpec(shp, lambda c: (0,) * len(shp))
    comp3 = lambda shp: pl.BlockSpec((1,) + shp, lambda c: (c,) + (0,) * len(shp))
    smem = pl.BlockSpec(memory_space=pltpu.SMEM)
    in_specs = [smem, comp3((n, nn))]
    args = [moduli, rhs]
    if faces is not None:
        xlo, xhi, yadd = faces
        in_specs += [comp3((1, nn)), comp3((1, nn)), comp3((n, 2 * n))]
        args += [xlo.reshape(ncomp, 1, nn), xhi.reshape(ncomp, 1, nn), yadd]
    in_specs += [full(q.shape), full(p4.shape), full(wy.shape), full(exy.shape), full(ez.shape), smem]
    args += [q, p4, wy, exy, ez, code]
    out_specs, out_shape = [], []
    if emit_u:
        out_specs.append(comp3((n, nn)))
        out_shape.append(jax.ShapeDtypeStruct(rhs.shape, f32))
    if emit_sides:
        out_specs += [comp3((3, nn)), comp3((2, nn)), comp3((2, n, n)), comp3((2, n, n))]
        out_shape += [jax.ShapeDtypeStruct((ncomp, 3, nn), f32), jax.ShapeDtypeStruct((ncomp, 2, nn), f32),
                      jax.ShapeDtypeStruct((ncomp, 2, n, n), f32), jax.ShapeDtypeStruct((ncomp, 2, n, n), f32)]
    kernel = functools.partial(solve_kernel, with_faces=faces is not None, emit_u=emit_u, emit_sides=emit_sides)
    return pl.pallas_call(
        kernel,
        grid=(ncomp,),
        in_specs=in_specs,
        out_specs=out_specs,
        out_shape=out_shape,
        scratch_shapes=[pltpu.VMEM((nn // 2, 2 * n), f32), pltpu.VMEM((nn // 4, 4 * n), f32)],
        interpret=interpret,
    )(*args)


def orient(face_field, code_table, extent):
    square = face_field.reshape(face_field.shape[:-1] + (extent, extent))
    flip_rows = (code_table % 2 == 1)[..., None, None, None]
    flip_cols = (code_table // 2 == 1)[..., None, None, None]
    square = jnp.where(flip_rows, jnp.flip(square, -2), square)
    square = jnp.where(flip_cols, jnp.flip(square, -1), square)
    return square.reshape(face_field.shape)


def face_data(solution, moduli):
    extent = solution.shape[-2]
    cube_view = solution.reshape(solution.shape[:-1] + (extent, extent))
    flat_shape = solution.shape[:-2] + (extent * extent,)

    def pack_side(planes):
        normal_slope = 11.0 / 6.0 * planes[0] - 3.0 * planes[1] + 1.5 * planes[2] - planes[3] / 3.0
        return (planes[0], moduli[..., None] * normal_slope)

    x_high = pack_side([solution[..., extent - 1 - plane_depth, :] for plane_depth in range(4)])
    x_low = pack_side([solution[..., plane_depth, :] for plane_depth in range(4)])
    y_high = pack_side(
        [
            cube_view[..., extent - 1 - plane_depth, :].reshape(flat_shape)
            for plane_depth in range(4)
        ]
    )
    y_low = pack_side(
        [cube_view[..., plane_depth, :].reshape(flat_shape) for plane_depth in range(4)]
    )
    return (x_high, x_low, y_high, y_low)


def place_faces(source_field, moduli, x_low, x_high, y_low, y_high):
    extent = source_field.shape[-2]
    added = jnp.zeros_like(source_field)
    added = added.at[..., 0, :].add(x_low)
    added = added.at[..., extent - 1, :].add(x_high)
    cube_view = added.reshape(added.shape[:-1] + (extent, extent))
    low_square = y_low.reshape(y_low.shape[:-1] + (extent, extent))
    high_square = y_high.reshape(y_high.shape[:-1] + (extent, extent))
    cube_view = cube_view.at[..., 0, :].add(low_square)
    cube_view = cube_view.at[..., extent - 1, :].add(high_square)
    added = cube_view.reshape(source_field.shape)
    return source_field + inject_scale * moduli[..., None, None] * added


def trace_update(current, side_a, side_b, moduli_a, moduli_b, omega_step, tangent):
    extent = tangent.shape[0]
    weight_a = moduli_a[..., None]
    weight_b = moduli_b[..., None]
    residue = (
        weight_a * side_a[0] + weight_b * side_b[0] + traction_mix * (side_a[1] + side_b[1])
    ) / (weight_a + weight_b) - current
    rows_view = residue.reshape(residue.shape[:-1] + (residue.shape[-1] // extent, extent))
    smoothed = rows_view + penalty_mix * jnp.einsum(
        "...z,zk->...k", rows_view, tangent, precision=highest
    )
    return current + omega_step * smoothed.reshape(residue.shape)


def flat_update(current, sum_a, sum_b, moduli_a, moduli_b, omega_step, tangent):
    extent = tangent.shape[0]
    residue = (sum_a + sum_b) / (moduli_a + moduli_b)[..., None] - current
    rows_view = residue.reshape(residue.shape[:-1] + (residue.shape[-1] // extent, extent))
    smoothed = rows_view + penalty_mix * jnp.einsum("...z,zk->...k", rows_view, tangent, precision=highest)
    return current + omega_step * smoothed.reshape(residue.shape)


def square_update(current, sum_a, sum_b, moduli_a, moduli_b, omega_step, tangent):
    residue = (sum_a + sum_b) / (moduli_a + moduli_b)[..., None, None] - current
    smoothed = residue + penalty_mix * jnp.einsum("...z,zk->...k", residue, tangent, precision=highest)
    return current + omega_step * smoothed


def shards(forcing, modulus, orient_codes):
    extent = forcing.shape[3]
    blocks = forcing.shape[1]
    flat = extent * extent
    source_field = forcing[0]
    moduli = modulus[0]
    codes_here = orient_codes[0]
    code_values = codes_here.astype(jnp.float32)
    tangent = tangent_matrix(extent)
    omegas = step_weights(ITERS)
    slab_count = lax.axis_size("blk")
    slab_index = lax.axis_index("blk")
    has_up = (slab_index < slab_count - 1).astype(jnp.float32)
    has_down = (slab_index > 0).astype(jnp.float32)
    lam_x_up = jnp.zeros((blocks, 3, flat), jnp.float32)
    lam_x_down = lam_x_up
    lam_y_next = jnp.zeros((blocks, 3, extent, extent), jnp.float32)
    lam_y_prev = lam_y_next
    faces = [None] * blocks
    for sweep in range(ITERS + 1):
        last = sweep == ITERS
        outs = [
            kernel_sweep(source_field[b], moduli[b], code_values[b:b + 1], faces[b], emit_u=last, emit_sides=not last)
            for b in range(blocks)
        ]
        if last:
            return jnp.stack([o[0] for o in outs], 0)[None]
        xh, xl, yh, yl = (jnp.stack([o[k] for o in outs], 0) for k in range(4))
        upper = shifted(xl, "blk", -1)
        lower = shifted(xh, "blk", 1)
        nxt = jnp.concatenate([yl[1:], shifted_2(yl[:1], "face", -1)], 0)
        prv = jnp.concatenate([shifted_2(yh[-1:], "face", 1), yh[:-1]], 0)
        if sweep == 0:
            moduli_up = upper[:, :, 1, 0]
            moduli_down = lower[:, :, 1, 0]
            codes_down = lower[:, 0, 2, 0].astype(jnp.int32)
            moduli_next = nxt[:, :, 1, 0, 0]
            moduli_prev = prv[:, :, 1, 0, 0]
        lam_x_up = (
            flat_update(
                lam_x_up, xh[:, :, 0], orient(upper[:, :, 0], codes_here, extent),
                moduli, moduli_up, omegas[sweep], tangent,
            )
            * has_up
        )
        lam_x_down = (
            flat_update(
                lam_x_down, lower[:, :, 0], orient(xl[:, :, 0], codes_down, extent),
                moduli_down, moduli, omegas[sweep], tangent,
            )
            * has_down
        )
        lam_y_next = square_update(
            lam_y_next, yh[:, :, 0], nxt[:, :, 0], moduli, moduli_next, omegas[sweep], tangent
        )
        lam_y_prev = square_update(
            lam_y_prev, prv[:, :, 0], yl[:, :, 0], moduli_prev, moduli, omegas[sweep], tangent
        )
        x_low = orient(lam_x_down, codes_down, extent)
        yadd = jnp.concatenate([lam_y_prev, lam_y_next], -1)
        faces = [(x_low[b], lam_x_up[b], yadd[b]) for b in range(blocks)]


def solution(mesh):
    placed = (P("blk", "face", None, None, None), P("blk", "face", None), P("blk", "face"))
    return jax.shard_map(
        shards,
        mesh=mesh,
        in_specs=placed,
        out_specs=P("blk", "face", None, None, None),
        check_vma=False,
    )
```

```python
import functools
import math

import jax
import jax.numpy as jnp
from jax import lax
from jax.sharding import PartitionSpec as P
from jax.experimental import pallas as pl
from jax.experimental.pallas import tpu as pltpu
import numpy as np
import ml_dtypes

ITERS = 2


mass_shift = 0.02
inject_scale = 2.0
traction_mix = 0.5
penalty_mix = 0.25
lower_edge = 0.3
upper_edge = 1.5
highest = lax.Precision.HIGHEST


def shifted(shard, axis, by):
    length = lax.axis_size(axis)
    pairs = [(i, i + by) for i in range(length) if 0 <= i + by < length]
    return lax.ppermute(shard, axis, pairs)


def shifted_2(shard, axis, by):
    length = lax.axis_size(axis)
    return lax.ppermute(shard, axis, [(i, (i + by) % length) for i in range(length)])


def tables(extent):
    node_index = jnp.arange(extent, dtype=jnp.float32) + 1.0
    basis = math.sqrt(2.0 / (extent + 1)) * jnp.sin(
        math.pi * node_index[:, None] * node_index[None, :] / (extent + 1)
    )
    eigenvalues = 2.0 - 2.0 * jnp.cos(math.pi * node_index / (extent + 1))
    return (basis, eigenvalues)


def tangent_matrix(extent):
    node_index = jnp.arange(extent, dtype=jnp.int32)
    distance = jnp.abs(node_index[:, None] - node_index[None, :])
    end_rows = ((node_index == 0) | (node_index == extent - 1)).astype(jnp.float32)
    adjacent = (distance == 1).astype(jnp.float32)
    diagonal_part = (distance == 0).astype(jnp.float32) * (2.0 - end_rows[:, None])
    return adjacent - diagonal_part


def step_weights(step_count):
    midpoint = 0.5 * (upper_edge + lower_edge)
    radius = 0.5 * (upper_edge - lower_edge)
    return [
        1.0 / (midpoint + radius * math.cos(math.pi * (2 * turn_index + 1) / (2 * step_count)))
        for turn_index in range(step_count)
    ]


def divisor(moduli, eigenvalues):
    extent = eigenvalues.shape[0]
    summed = eigenvalues[:, None, None] + eigenvalues[None, :, None] + eigenvalues[None, None, :]
    scaled = moduli[..., None, None, None] * summed + mass_shift
    return scaled.reshape(moduli.shape + (extent, extent * extent))


def body_transform(field_data, basis, paired_basis):
    extent = basis.shape[0]
    full_shape = field_data.shape
    pair_width = paired_basis.shape[0]
    sectioned = jnp.einsum("ix,bcxm->bcim", basis, field_data, precision=highest)
    sectioned = sectioned.reshape(full_shape[:-1] + (full_shape[-1] // pair_width, pair_width))
    sectioned = jnp.einsum("bcxpz,kz->bcxpk", sectioned, paired_basis, precision=highest)
    sectioned = sectioned.reshape(full_shape[:-1] + (extent, extent))
    sectioned = jnp.einsum("jy,bcxyz->bcxjz", basis, sectioned, precision=highest)
    return sectioned.reshape(full_shape)


def body_solve(right_side, scale_table, basis, paired_basis):
    return body_transform(
        body_transform(right_side, basis, paired_basis) / scale_table, basis, paired_basis
    )


f32 = jnp.float32


def np_tables(n):
    g = np.float32
    idx = np.arange(n, dtype=g) + g(1.0)
    arg = (g(math.pi) * idx[:, None]) * idx[None, :] / g(n + 1)
    q = g(math.sqrt(2.0 / (n + 1))) * np.sin(arg)
    e = g(2.0) - g(2.0) * np.cos(g(math.pi) * idx / g(n + 1))
    return q.astype(g), e.astype(g)


def consts(n):
    q, e = np_tables(n)
    h = n // 2
    p4 = np.kron(np.eye(4, dtype=np.float32), q.T)
    w = np.zeros((2, 4, h, 2, 4, h), np.float32)
    qq = q.reshape(h, 2, h, 2)
    for xl in range(4):
        w[:, xl, :, :, xl, :] = np.transpose(qq, (3, 2, 1, 0))
    wy = w.reshape(8 * h, 8 * h)
    ng = n // 4
    lane_h = np.arange(8 * h) // (4 * h)
    lane_xl = (np.arange(8 * h) // h) % 4
    lane_c = np.arange(8 * h) % h
    exy = (e[4 * np.arange(ng)[:, None] + lane_xl[None, :]] + e[2 * lane_c + lane_h][None, :]).astype(np.float32)
    ez = np.ascontiguousarray(np.broadcast_to(e[:, None], (n, 8 * h))).astype(np.float32)
    return stack_left(q), stack_right(p4), stack_right(wy), exy, ez


BF = jnp.bfloat16

def np_split3(w):
    b = ml_dtypes.bfloat16
    w1 = w.astype(b)
    r1 = w - w1.astype(np.float32)
    w2 = r1.astype(b)
    w3 = (r1 - w2.astype(np.float32)).astype(b)
    return w1, w2, w3


def stack_right(w):
    w1, w2, w3 = np_split3(w)
    return np.concatenate([w1, w2, w1, w1], 0)


def stack_left(w):
    w1, w2, w3 = np_split3(w)
    return np.concatenate([w1, w2, w1, w1], 1)


def split3(d):
    d1 = d.astype(BF)
    r1 = d - d1.astype(f32)
    d2 = r1.astype(BF)
    d3 = (r1 - d2.astype(f32)).astype(BF)
    return d1, d2, d3


def sdot(d, w6):
    d1, d2, d3 = split3(d)
    return jnp.dot(jnp.concatenate([d1, d1, d2, d3], 1), w6, preferred_element_type=f32)


def sdot_left(w6, d):
    d1, d2, d3 = split3(d)
    return jnp.dot(w6, jnp.concatenate([d1, d1, d2, d3], 0), preferred_element_type=f32)


def solve_kernel(*refs, with_faces, emit_u, emit_sides):
    it = iter(refs)
    mod_ref, f_ref = next(it), next(it)
    if with_faces:
        xlo_ref, xhi_ref, yadd_ref = next(it), next(it), next(it)
    q_ref, p_ref, wy_ref, exy_ref, ez_ref = next(it), next(it), next(it), next(it), next(it)
    code_ref = next(it)
    o_ref = next(it) if emit_u else None
    if emit_sides:
        xh_ref, xl_ref, yh_ref, yl_ref = next(it), next(it), next(it), next(it)
    s_ref, z_ref = next(it), next(it)
    n = q_ref.shape[0]
    h = n // 2
    w2 = 2 * n
    w4 = 4 * n
    nn = f_ref.shape[-1]
    nch = nn // w2
    npair = nn // w4
    comp = pl.program_id(0)
    m = mod_ref[comp]
    q = q_ref[...]
    r = f_ref[0]
    if with_faces:
        rows = lax.broadcasted_iota(jnp.int32, (n, nn), 0)
        added = jnp.where(rows == 0, xlo_ref[0], 0.0) + jnp.where(rows == n - 1, xhi_ref[0], 0.0)
        lane = lax.broadcasted_iota(jnp.int32, (n, w2), 1)
        yadd = yadd_ref[0]
        first = added[:, :w2] + jnp.where(lane < n, yadd, 0.0)
        last = added[:, nn - w2:] + jnp.where(lane >= n, yadd, 0.0)
        added = jnp.concatenate([first, added[:, w2:nn - w2], last], 1)
        r = r + (2.0 * m) * added
    a = sdot_left(q, r)
    for cp in range(npair):
        z_ref[cp * n:(cp + 1) * n, :] = a[:, cp * w4:(cp + 1) * w4]
    zo = sdot(z_ref[...], p_ref[...])
    for cp in range(npair):
        for cb in range(2):
            s_ref[(2 * cp + cb) * n:(2 * cp + cb + 1) * n, :] = zo[cp * n:(cp + 1) * n, cb * w2:(cb + 1) * w2]
    wy = wy_ref[...]
    ez = ez_ref[...]
    XG = 4
    GPI = 8

    def body(it_, carry):
        lhs = []
        for gi in range(GPI):
            g = it_ * GPI + gi
            blk = jnp.concatenate([s_ref[pl.ds(g * XG + xl, h, stride=n), :] for xl in range(XG)], 0)
            tb = blk.T
            lhs.append(jnp.concatenate([tb[:n], tb[n:]], 1))
        v = sdot(jnp.concatenate(lhs, 0), wy)
        div = jnp.concatenate([m * (exy_ref[pl.ds(it_ * GPI + gi, 1), :] + ez) + 0.02 for gi in range(GPI)], 0)
        v = v / div
        v = sdot(v, wy)
        for gi in range(GPI):
            g = it_ * GPI + gi
            vg = v[gi * n:(gi + 1) * n]
            tb = jnp.concatenate([vg[:, :w2], vg[:, w2:]], 0).T
            for xl in range(XG):
                s_ref[pl.ds(g * XG + xl, h, stride=n), :] = tb[xl * h:(xl + 1) * h]
        return carry
    lax.fori_loop(0, n // (XG * GPI), body, 0)
    for cp in range(npair):
        z_ref[cp * n:(cp + 1) * n, :] = jnp.concatenate(
            [s_ref[(2 * cp) * n:(2 * cp + 1) * n, :], s_ref[(2 * cp + 1) * n:(2 * cp + 2) * n, :]], 1)
    zo = sdot(z_ref[...], p_ref[...])
    b = jnp.concatenate([zo[cp * n:(cp + 1) * n, :] for cp in range(npair)], 1)
    u = sdot_left(q, b)
    if emit_u:
        o_ref[0] = u

    def slope(p0, p1, p2, p3):
        return m * (11.0 / 6.0 * p0 - 3.0 * p1 + 1.5 * p2 - p3 / 3.0)
    if emit_sides:
        m_row = jnp.full((1, nn), m, f32)
        xh_ref[0, 0:1, :] = m * u[n - 1:n] + 0.5 * slope(u[n - 1:n], u[n - 2:n - 1], u[n - 3:n - 2], u[n - 4:n - 3])
        xh_ref[0, 1:2, :] = m_row
        xh_ref[0, 2:3, :] = jnp.full((1, nn), code_ref[0], f32)
        xl_ref[0, 0:1, :] = m * u[0:1] + 0.5 * slope(u[0:1], u[1:2], u[2:3], u[3:4])
        xl_ref[0, 1:2, :] = m_row
        m_sq = jnp.full((n, n), m, f32)
        c_hi = u[:, nn - w2:]
        c_hi2 = u[:, nn - 2 * w2:nn - w2]
        s_hi = m * c_hi + 0.5 * slope(c_hi, pltpu.roll(c_hi, n, 1), c_hi2, pltpu.roll(c_hi2, n, 1))
        yh_ref[0, 0] = pltpu.roll(s_hi, n, 1)[:, :n]
        yh_ref[0, 1] = m_sq
        c_lo = u[:, :w2]
        c_lo2 = u[:, w2:2 * w2]
        s_lo = m * c_lo + 0.5 * slope(c_lo, pltpu.roll(c_lo, n, 1), c_lo2, pltpu.roll(c_lo2, n, 1))
        yl_ref[0, 0] = s_lo[:, :n]
        yl_ref[0, 1] = m_sq


def kernel_sweep(rhs, moduli, code, faces=None, emit_u=True, emit_sides=False, interpret=False):
    ncomp, n, nn = rhs.shape
    q, p4, wy, exy, ez = consts(n)
    full = lambda shp: pl.BlockSpec(shp, lambda c: (0,) * len(shp))
    comp3 = lambda shp: pl.BlockSpec((1,) + shp, lambda c: (c,) + (0,) * len(shp))
    smem = pl.BlockSpec(memory_space=pltpu.SMEM)
    in_specs = [smem, comp3((n, nn))]
    args = [moduli, rhs]
    if faces is not None:
        xlo, xhi, yadd = faces
        in_specs += [comp3((1, nn)), comp3((1, nn)), comp3((n, 2 * n))]
        args += [xlo.reshape(ncomp, 1, nn), xhi.reshape(ncomp, 1, nn), yadd]
    in_specs += [full(q.shape), full(p4.shape), full(wy.shape), full(exy.shape), full(ez.shape), smem]
    args += [q, p4, wy, exy, ez, code]
    out_specs, out_shape = [], []
    if emit_u:
        out_specs.append(comp3((n, nn)))
        out_shape.append(jax.ShapeDtypeStruct(rhs.shape, f32))
    if emit_sides:
        out_specs += [comp3((3, nn)), comp3((2, nn)), comp3((2, n, n)), comp3((2, n, n))]
        out_shape += [jax.ShapeDtypeStruct((ncomp, 3, nn), f32), jax.ShapeDtypeStruct((ncomp, 2, nn), f32),
                      jax.ShapeDtypeStruct((ncomp, 2, n, n), f32), jax.ShapeDtypeStruct((ncomp, 2, n, n), f32)]
    kernel = functools.partial(solve_kernel, with_faces=faces is not None, emit_u=emit_u, emit_sides=emit_sides)
    return pl.pallas_call(
        kernel,
        grid=(ncomp,),
        in_specs=in_specs,
        out_specs=out_specs,
        out_shape=out_shape,
        scratch_shapes=[pltpu.VMEM((nn // 2, 2 * n), f32), pltpu.VMEM((nn // 4, 4 * n), f32)],
        interpret=interpret,
    )(*args)


def orient(face_field, code_table, extent):
    square = face_field.reshape(face_field.shape[:-1] + (extent, extent))
    flip_rows = (code_table % 2 == 1)[..., None, None, None]
    flip_cols = (code_table // 2 == 1)[..., None, None, None]
    square = jnp.where(flip_rows, jnp.flip(square, -2), square)
    square = jnp.where(flip_cols, jnp.flip(square, -1), square)
    return square.reshape(face_field.shape)


def face_data(solution, moduli):
    extent = solution.shape[-2]
    cube_view = solution.reshape(solution.shape[:-1] + (extent, extent))
    flat_shape = solution.shape[:-2] + (extent * extent,)

    def pack_side(planes):
        normal_slope = 11.0 / 6.0 * planes[0] - 3.0 * planes[1] + 1.5 * planes[2] - planes[3] / 3.0
        return (planes[0], moduli[..., None] * normal_slope)

    x_high = pack_side([solution[..., extent - 1 - plane_depth, :] for plane_depth in range(4)])
    x_low = pack_side([solution[..., plane_depth, :] for plane_depth in range(4)])
    y_high = pack_side(
        [
            cube_view[..., extent - 1 - plane_depth, :].reshape(flat_shape)
            for plane_depth in range(4)
        ]
    )
    y_low = pack_side(
        [cube_view[..., plane_depth, :].reshape(flat_shape) for plane_depth in range(4)]
    )
    return (x_high, x_low, y_high, y_low)


def place_faces(source_field, moduli, x_low, x_high, y_low, y_high):
    extent = source_field.shape[-2]
    added = jnp.zeros_like(source_field)
    added = added.at[..., 0, :].add(x_low)
    added = added.at[..., extent - 1, :].add(x_high)
    cube_view = added.reshape(added.shape[:-1] + (extent, extent))
    low_square = y_low.reshape(y_low.shape[:-1] + (extent, extent))
    high_square = y_high.reshape(y_high.shape[:-1] + (extent, extent))
    cube_view = cube_view.at[..., 0, :].add(low_square)
    cube_view = cube_view.at[..., extent - 1, :].add(high_square)
    added = cube_view.reshape(source_field.shape)
    return source_field + inject_scale * moduli[..., None, None] * added


def trace_update(current, side_a, side_b, moduli_a, moduli_b, omega_step, tangent):
    extent = tangent.shape[0]
    weight_a = moduli_a[..., None]
    weight_b = moduli_b[..., None]
    residue = (
        weight_a * side_a[0] + weight_b * side_b[0] + traction_mix * (side_a[1] + side_b[1])
    ) / (weight_a + weight_b) - current
    rows_view = residue.reshape(residue.shape[:-1] + (residue.shape[-1] // extent, extent))
    smoothed = rows_view + penalty_mix * jnp.einsum(
        "...z,zk->...k", rows_view, tangent, precision=highest
    )
    return current + omega_step * smoothed.reshape(residue.shape)


def flat_update(current, sum_a, sum_b, moduli_a, moduli_b, omega_step, tangent):
    extent = tangent.shape[0]
    residue = (sum_a + sum_b) / (moduli_a + moduli_b)[..., None] - current
    rows_view = residue.reshape(residue.shape[:-1] + (residue.shape[-1] // extent, extent))
    smoothed = rows_view + penalty_mix * jnp.einsum("...z,zk->...k", rows_view, tangent, precision=highest)
    return current + omega_step * smoothed.reshape(residue.shape)


def square_update(current, sum_a, sum_b, moduli_a, moduli_b, omega_step, tangent):
    residue = (sum_a + sum_b) / (moduli_a + moduli_b)[..., None, None] - current
    smoothed = residue + penalty_mix * jnp.einsum("...z,zk->...k", residue, tangent, precision=highest)
    return current + omega_step * smoothed


def shards(forcing, modulus, orient_codes):
    extent = forcing.shape[3]
    blocks = forcing.shape[1]
    flat = extent * extent
    source_field = forcing[0]
    moduli = modulus[0]
    codes_here = orient_codes[0]
    code_values = codes_here.astype(jnp.float32)
    tangent = tangent_matrix(extent)
    omegas = step_weights(ITERS)
    slab_count = lax.axis_size("blk")
    slab_index = lax.axis_index("blk")
    has_up = (slab_index < slab_count - 1).astype(jnp.float32)
    has_down = (slab_index > 0).astype(jnp.float32)
    lam_x_up = jnp.zeros((blocks, 3, flat), jnp.float32)
    lam_x_down = lam_x_up
    lam_y_next = jnp.zeros((blocks, 3, extent, extent), jnp.float32)
    lam_y_prev = lam_y_next
    faces = [None] * blocks
    for sweep in range(ITERS + 1):
        last = sweep == ITERS
        outs = [
            kernel_sweep(source_field[b], moduli[b], code_values[b:b + 1], faces[b], emit_u=last, emit_sides=not last)
            for b in range(blocks)
        ]
        if last:
            return jnp.stack([o[0] for o in outs], 0)[None]
        xh, xl, yh, yl = (jnp.stack([o[k] for o in outs], 0) for k in range(4))
        upper = shifted(xl, "blk", -1)
        lower = shifted(xh, "blk", 1)
        nxt = jnp.concatenate([yl[1:], shifted_2(yl[:1], "face", -1)], 0)
        prv = jnp.concatenate([shifted_2(yh[-1:], "face", 1), yh[:-1]], 0)
        if sweep == 0:
            moduli_up = upper[:, :, 1, 0]
            moduli_down = lower[:, :, 1, 0]
            codes_down = lower[:, 0, 2, 0].astype(jnp.int32)
            moduli_next = nxt[:, :, 1, 0, 0]
            moduli_prev = prv[:, :, 1, 0, 0]
        lam_x_up = (
            flat_update(
                lam_x_up, xh[:, :, 0], orient(upper[:, :, 0], codes_here, extent),
                moduli, moduli_up, omegas[sweep], tangent,
            )
            * has_up
        )
        lam_x_down = (
            flat_update(
                lam_x_down, lower[:, :, 0], orient(xl[:, :, 0], codes_down, extent),
                moduli_down, moduli, omegas[sweep], tangent,
            )
            * has_down
        )
        lam_y_next = square_update(
            lam_y_next, yh[:, :, 0], nxt[:, :, 0], moduli, moduli_next, omegas[sweep], tangent
        )
        lam_y_prev = square_update(
            lam_y_prev, prv[:, :, 0], yl[:, :, 0], moduli_prev, moduli, omegas[sweep], tangent
        )
        x_low = orient(lam_x_down, codes_down, extent)
        yadd = jnp.concatenate([lam_y_prev, lam_y_next], -1)
        faces = [(x_low[b], lam_x_up[b], yadd[b]) for b in range(blocks)]


def solution(mesh):
    placed = (P("blk", "face", None, None, None), P("blk", "face", None), P("blk", "face"))
    return jax.shard_map(
        shards,
        mesh=mesh,
        in_specs=placed,
        out_specs=P("blk", "face", None, None, None),
        check_vma=False,
    )
```

```python
import functools
import math

import jax
import jax.numpy as jnp
from jax import lax
from jax.sharding import PartitionSpec as P
from jax.experimental import pallas as pl
from jax.experimental.pallas import tpu as pltpu
import numpy as np
import ml_dtypes

ITERS = 2


mass_shift = 0.02
inject_scale = 2.0
traction_mix = 0.5
penalty_mix = 0.25
lower_edge = 0.3
upper_edge = 1.5
highest = lax.Precision.HIGHEST


def shifted(shard, axis, by):
    length = lax.axis_size(axis)
    pairs = [(i, i + by) for i in range(length) if 0 <= i + by < length]
    return lax.ppermute(shard, axis, pairs)


def shifted_2(shard, axis, by):
    length = lax.axis_size(axis)
    return lax.ppermute(shard, axis, [(i, (i + by) % length) for i in range(length)])


def tables(extent):
    node_index = jnp.arange(extent, dtype=jnp.float32) + 1.0
    basis = math.sqrt(2.0 / (extent + 1)) * jnp.sin(
        math.pi * node_index[:, None] * node_index[None, :] / (extent + 1)
    )
    eigenvalues = 2.0 - 2.0 * jnp.cos(math.pi * node_index / (extent + 1))
    return (basis, eigenvalues)


def tangent_matrix(extent):
    node_index = jnp.arange(extent, dtype=jnp.int32)
    distance = jnp.abs(node_index[:, None] - node_index[None, :])
    end_rows = ((node_index == 0) | (node_index == extent - 1)).astype(jnp.float32)
    adjacent = (distance == 1).astype(jnp.float32)
    diagonal_part = (distance == 0).astype(jnp.float32) * (2.0 - end_rows[:, None])
    return adjacent - diagonal_part


def step_weights(step_count):
    midpoint = 0.5 * (upper_edge + lower_edge)
    radius = 0.5 * (upper_edge - lower_edge)
    return [
        1.0 / (midpoint + radius * math.cos(math.pi * (2 * turn_index + 1) / (2 * step_count)))
        for turn_index in range(step_count)
    ]


def divisor(moduli, eigenvalues):
    extent = eigenvalues.shape[0]
    summed = eigenvalues[:, None, None] + eigenvalues[None, :, None] + eigenvalues[None, None, :]
    scaled = moduli[..., None, None, None] * summed + mass_shift
    return scaled.reshape(moduli.shape + (extent, extent * extent))


def body_transform(field_data, basis, paired_basis):
    extent = basis.shape[0]
    full_shape = field_data.shape
    pair_width = paired_basis.shape[0]
    sectioned = jnp.einsum("ix,bcxm->bcim", basis, field_data, precision=highest)
    sectioned = sectioned.reshape(full_shape[:-1] + (full_shape[-1] // pair_width, pair_width))
    sectioned = jnp.einsum("bcxpz,kz->bcxpk", sectioned, paired_basis, precision=highest)
    sectioned = sectioned.reshape(full_shape[:-1] + (extent, extent))
    sectioned = jnp.einsum("jy,bcxyz->bcxjz", basis, sectioned, precision=highest)
    return sectioned.reshape(full_shape)


def body_solve(right_side, scale_table, basis, paired_basis):
    return body_transform(
        body_transform(right_side, basis, paired_basis) / scale_table, basis, paired_basis
    )


f32 = jnp.float32


def np_tables(n):
    g = np.float32
    idx = np.arange(n, dtype=g) + g(1.0)
    arg = (g(math.pi) * idx[:, None]) * idx[None, :] / g(n + 1)
    q = g(math.sqrt(2.0 / (n + 1))) * np.sin(arg)
    e = g(2.0) - g(2.0) * np.cos(g(math.pi) * idx / g(n + 1))
    return q.astype(g), e.astype(g)


def consts(n):
    q, e = np_tables(n)
    h = n // 2
    p4 = np.kron(np.eye(4, dtype=np.float32), q.T)
    w = np.zeros((2, 4, h, 2, 4, h), np.float32)
    qq = q.reshape(h, 2, h, 2)
    for xl in range(4):
        w[:, xl, :, :, xl, :] = np.transpose(qq, (3, 2, 1, 0))
    wy = w.reshape(8 * h, 8 * h)
    ng = n // 4
    lane_h = np.arange(8 * h) // (4 * h)
    lane_xl = (np.arange(8 * h) // h) % 4
    lane_c = np.arange(8 * h) % h
    exy = (e[4 * np.arange(ng)[:, None] + lane_xl[None, :]] + e[2 * lane_c + lane_h][None, :]).astype(np.float32)
    ez = np.ascontiguousarray(np.broadcast_to(e[:, None], (n, 8 * h))).astype(np.float32)
    return stack_left(q), stack_right(p4), stack_right(wy), exy, ez


BF = jnp.bfloat16

def np_split3(w):
    b = ml_dtypes.bfloat16
    w1 = w.astype(b)
    r1 = w - w1.astype(np.float32)
    w2 = r1.astype(b)
    w3 = (r1 - w2.astype(np.float32)).astype(b)
    return w1, w2, w3


def stack_right(w):
    w1, w2, w3 = np_split3(w)
    return np.concatenate([w1, w2, w1, w1], 0)


def stack_left(w):
    w1, w2, w3 = np_split3(w)
    return np.concatenate([w1, w2, w1, w1], 1)


def split3(d):
    d1 = d.astype(BF)
    r1 = d - d1.astype(f32)
    d2 = r1.astype(BF)
    d3 = (r1 - d2.astype(f32)).astype(BF)
    return d1, d2, d3


def sdot(d, w6):
    d1, d2, d3 = split3(d)
    return jnp.dot(jnp.concatenate([d1, d1, d2, d3], 1), w6, preferred_element_type=f32)


def sdot_left(w6, d):
    d1, d2, d3 = split3(d)
    return jnp.dot(w6, jnp.concatenate([d1, d1, d2, d3], 0), preferred_element_type=f32)


def solve_kernel(*refs, with_faces, emit_u, emit_sides, omega):
    it = iter(refs)
    mod_ref, f_ref = next(it), next(it)
    if with_faces:
        (nbm_ref, lxu_ref, lxd_ref, ly_ref, sxh_ref, sxl_ref, sy_ref,
         rup_ref, rdn_ref, ryp_ref, ryn_ref) = (next(it) for _ in range(11))
    q_ref, p_ref, wy_ref, exy_ref, ez_ref = next(it), next(it), next(it), next(it), next(it)
    code_ref = next(it)
    o_ref = next(it) if emit_u else None
    if emit_sides:
        xh_ref, xl_ref, y_ref = next(it), next(it), next(it)
    if with_faces and emit_sides:
        nlx_ref, nld_ref, nly_ref = next(it), next(it), next(it)
    elif with_faces:
        nlx_ref = nld_ref = nly_ref = None
    s_ref, z_ref = next(it), next(it)
    n = q_ref.shape[0]
    h = n // 2
    w2 = 2 * n
    w4 = 4 * n
    nn = f_ref.shape[-1]
    nch = nn // w2
    npair = nn // w4
    comp = pl.program_id(0)
    m = mod_ref[comp]
    q = q_ref[...]
    r = f_ref[0]
    if with_faces:
        m_up = nbm_ref[0, comp]
        m_dn = nbm_ref[1, comp]
        m_prev = nbm_ref[2, comp]
        m_next = nbm_ref[3, comp]
        has_up = nbm_ref[4, comp]
        has_dn = nbm_ref[5, comp]
        lane_x = lax.broadcasted_iota(jnp.int32, (1, nn), 1) % n
        lane_y = lax.broadcasted_iota(jnp.int32, (n, w2), 1)

        def smooth(res, lanes, width):
            left = pltpu.roll(res, 1, 1)
            right = pltpu.roll(res, width - 1, 1)
            left = jnp.where(lanes % n == 0, 0.0, left)
            right = jnp.where(lanes % n == n - 1, 0.0, right)
            diag = jnp.where((lanes % n == 0) | (lanes % n == n - 1), -1.0, -2.0)
            return res + 0.25 * ((left + right) + diag * res)

        xu = lxu_ref[0]
        res = (sxh_ref[0, 0:1, :] + rup_ref[0]) / (m + m_up) - xu
        xhi_face = (xu + omega * smooth(res, lane_x, nn)) * has_up
        xd = lxd_ref[0]
        res = (rdn_ref[0] + sxl_ref[0, 0:1, :]) / (m_dn + m) - xd
        xlo_face = (xd + omega * smooth(res, lane_x, nn)) * has_dn
        ly = ly_ref[0]
        lo = lane_y < n
        recv = pltpu.roll(jnp.where(lo, ryn_ref[0, 0], ryp_ref[0, 0]), n, 1)
        res = (sy_ref[0, 0] + recv) / (m + jnp.where(lo, m_prev, m_next)) - ly
        yadd = ly + omega * smooth(res, lane_y, w2)
        if nlx_ref is not None:
            nlx_ref[0] = xhi_face
            nld_ref[0] = xlo_face
            nly_ref[0] = yadd
        rows = lax.broadcasted_iota(jnp.int32, (n, nn), 0)
        added = jnp.where(rows == 0, xlo_face, 0.0) + jnp.where(rows == n - 1, xhi_face, 0.0)
        lane = lane_y
        first = added[:, :w2] + jnp.where(lane < n, yadd, 0.0)
        last = added[:, nn - w2:] + jnp.where(lane >= n, yadd, 0.0)
        added = jnp.concatenate([first, added[:, w2:nn - w2], last], 1)
        r = r + (2.0 * m) * added
    a = sdot_left(q, r)
    for cp in range(npair):
        z_ref[cp * n:(cp + 1) * n, :] = a[:, cp * w4:(cp + 1) * w4]
    zo = sdot(z_ref[...], p_ref[...])
    for cp in range(npair):
        for cb in range(2):
            s_ref[(2 * cp + cb) * n:(2 * cp + cb + 1) * n, :] = zo[cp * n:(cp + 1) * n, cb * w2:(cb + 1) * w2]
    wy = wy_ref[...]
    ez = ez_ref[...]
    XG = 4
    GPI = 8

    def body(it_, carry):
        lhs = []
        for gi in range(GPI):
            g = it_ * GPI + gi
            blk = jnp.concatenate([s_ref[pl.ds(g * XG + xl, h, stride=n), :] for xl in range(XG)], 0)
            tb = blk.T
            lhs.append(jnp.concatenate([tb[:n], tb[n:]], 1))
        v = sdot(jnp.concatenate(lhs, 0), wy)
        div = jnp.concatenate([m * (exy_ref[pl.ds(it_ * GPI + gi, 1), :] + ez) + 0.02 for gi in range(GPI)], 0)
        v = v / div
        v = sdot(v, wy)
        for gi in range(GPI):
            g = it_ * GPI + gi
            vg = v[gi * n:(gi + 1) * n]
            tb = jnp.concatenate([vg[:, :w2], vg[:, w2:]], 0).T
            for xl in range(XG):
                s_ref[pl.ds(g * XG + xl, h, stride=n), :] = tb[xl * h:(xl + 1) * h]
        return carry
    lax.fori_loop(0, n // (XG * GPI), body, 0)
    for cp in range(npair):
        z_ref[cp * n:(cp + 1) * n, :] = jnp.concatenate(
            [s_ref[(2 * cp) * n:(2 * cp + 1) * n, :], s_ref[(2 * cp + 1) * n:(2 * cp + 2) * n, :]], 1)
    zo = sdot(z_ref[...], p_ref[...])
    b = jnp.concatenate([zo[cp * n:(cp + 1) * n, :] for cp in range(npair)], 1)
    u = sdot_left(q, b)
    if emit_u:
        o_ref[0] = u

    def slope(p0, p1, p2, p3):
        return m * (11.0 / 6.0 * p0 - 3.0 * p1 + 1.5 * p2 - p3 / 3.0)
    if emit_sides:
        m_row = jnp.full((1, nn), m, f32)
        xh_ref[0, 0:1, :] = m * u[n - 1:n] + 0.5 * slope(u[n - 1:n], u[n - 2:n - 1], u[n - 3:n - 2], u[n - 4:n - 3])
        xh_ref[0, 1:2, :] = m_row
        xh_ref[0, 2:3, :] = jnp.full((1, nn), code_ref[0], f32)
        xl_ref[0, 0:1, :] = m * u[0:1] + 0.5 * slope(u[0:1], u[1:2], u[2:3], u[3:4])
        xl_ref[0, 1:2, :] = m_row
        c_hi = u[:, nn - w2:]
        c_hi2 = u[:, nn - 2 * w2:nn - w2]
        s_hi = m * c_hi + 0.5 * slope(c_hi, pltpu.roll(c_hi, n, 1), c_hi2, pltpu.roll(c_hi2, n, 1))
        c_lo = u[:, :w2]
        c_lo2 = u[:, w2:2 * w2]
        s_lo = m * c_lo + 0.5 * slope(c_lo, pltpu.roll(c_lo, n, 1), c_lo2, pltpu.roll(c_lo2, n, 1))
        lane_s = lax.broadcasted_iota(jnp.int32, (n, w2), 1)
        y_ref[0, 0] = jnp.where(lane_s < n, s_lo, s_hi)
        y_ref[0, 1] = jnp.full((n, w2), m, f32)


def kernel_sweep(rhs, moduli, code, state=None, emit_u=True, emit_sides=False, omega=0.0):
    ncomp, n, nn = rhs.shape
    q, p4, wy, exy, ez = consts(n)
    full = lambda shp: pl.BlockSpec(shp, lambda c: (0,) * len(shp))
    comp3 = lambda shp: pl.BlockSpec((1,) + shp, lambda c: (c,) + (0,) * len(shp))
    smem = pl.BlockSpec(memory_space=pltpu.SMEM)
    in_specs = [smem, comp3((n, nn))]
    args = [moduli, rhs]
    if state is not None:
        in_specs += [smem, comp3((1, nn)), comp3((1, nn)), comp3((n, 2 * n)),
                     comp3((3, nn)), comp3((2, nn)), comp3((2, n, 2 * n)),
                     comp3((1, nn)), comp3((1, nn)), comp3((2, n, 2 * n)), comp3((2, n, 2 * n))]
        args += list(state)
    in_specs += [full(q.shape), full(p4.shape), full(wy.shape), full(exy.shape), full(ez.shape), smem]
    args += [q, p4, wy, exy, ez, code]
    out_specs, out_shape = [], []
    if emit_u:
        out_specs.append(comp3((n, nn)))
        out_shape.append(jax.ShapeDtypeStruct(rhs.shape, f32))
    if emit_sides:
        out_specs += [comp3((3, nn)), comp3((2, nn)), comp3((2, n, 2 * n))]
        out_shape += [jax.ShapeDtypeStruct((ncomp, 3, nn), f32), jax.ShapeDtypeStruct((ncomp, 2, nn), f32),
                      jax.ShapeDtypeStruct((ncomp, 2, n, 2 * n), f32)]
        if state is not None:
            out_specs += [comp3((1, nn)), comp3((1, nn)), comp3((n, 2 * n))]
            out_shape += [jax.ShapeDtypeStruct((ncomp, 1, nn), f32), jax.ShapeDtypeStruct((ncomp, 1, nn), f32),
                          jax.ShapeDtypeStruct((ncomp, n, 2 * n), f32)]
    kernel = functools.partial(solve_kernel, with_faces=state is not None, emit_u=emit_u,
                               emit_sides=emit_sides, omega=omega)
    return pl.pallas_call(
        kernel,
        grid=(ncomp,),
        in_specs=in_specs,
        out_specs=out_specs,
        out_shape=out_shape,
        scratch_shapes=[pltpu.VMEM((nn // 2, 2 * n), f32), pltpu.VMEM((nn // 4, 4 * n), f32)],
    )(*args)


def orient(face_field, code_table, extent):
    square = face_field.reshape(face_field.shape[:-1] + (extent, extent))
    flip_rows = (code_table % 2 == 1)[..., None, None, None]
    flip_cols = (code_table // 2 == 1)[..., None, None, None]
    square = jnp.where(flip_rows, jnp.flip(square, -2), square)
    square = jnp.where(flip_cols, jnp.flip(square, -1), square)
    return square.reshape(face_field.shape)


def face_data(solution, moduli):
    extent = solution.shape[-2]
    cube_view = solution.reshape(solution.shape[:-1] + (extent, extent))
    flat_shape = solution.shape[:-2] + (extent * extent,)

    def pack_side(planes):
        normal_slope = 11.0 / 6.0 * planes[0] - 3.0 * planes[1] + 1.5 * planes[2] - planes[3] / 3.0
        return (planes[0], moduli[..., None] * normal_slope)

    x_high = pack_side([solution[..., extent - 1 - plane_depth, :] for plane_depth in range(4)])
    x_low = pack_side([solution[..., plane_depth, :] for plane_depth in range(4)])
    y_high = pack_side(
        [
            cube_view[..., extent - 1 - plane_depth, :].reshape(flat_shape)
            for plane_depth in range(4)
        ]
    )
    y_low = pack_side(
        [cube_view[..., plane_depth, :].reshape(flat_shape) for plane_depth in range(4)]
    )
    return (x_high, x_low, y_high, y_low)


def place_faces(source_field, moduli, x_low, x_high, y_low, y_high):
    extent = source_field.shape[-2]
    added = jnp.zeros_like(source_field)
    added = added.at[..., 0, :].add(x_low)
    added = added.at[..., extent - 1, :].add(x_high)
    cube_view = added.reshape(added.shape[:-1] + (extent, extent))
    low_square = y_low.reshape(y_low.shape[:-1] + (extent, extent))
    high_square = y_high.reshape(y_high.shape[:-1] + (extent, extent))
    cube_view = cube_view.at[..., 0, :].add(low_square)
    cube_view = cube_view.at[..., extent - 1, :].add(high_square)
    added = cube_view.reshape(source_field.shape)
    return source_field + inject_scale * moduli[..., None, None] * added


def trace_update(current, side_a, side_b, moduli_a, moduli_b, omega_step, tangent):
    extent = tangent.shape[0]
    weight_a = moduli_a[..., None]
    weight_b = moduli_b[..., None]
    residue = (
        weight_a * side_a[0] + weight_b * side_b[0] + traction_mix * (side_a[1] + side_b[1])
    ) / (weight_a + weight_b) - current
    rows_view = residue.reshape(residue.shape[:-1] + (residue.shape[-1] // extent, extent))
    smoothed = rows_view + penalty_mix * jnp.einsum(
        "...z,zk->...k", rows_view, tangent, precision=highest
    )
    return current + omega_step * smoothed.reshape(residue.shape)


def flat_update(current, sum_a, sum_b, moduli_a, moduli_b, omega_step, tangent):
    extent = tangent.shape[0]
    residue = (sum_a + sum_b) / (moduli_a + moduli_b)[..., None] - current
    rows_view = residue.reshape(residue.shape[:-1] + (residue.shape[-1] // extent, extent))
    smoothed = rows_view + penalty_mix * jnp.einsum("...z,zk->...k", rows_view, tangent, precision=highest)
    return current + omega_step * smoothed.reshape(residue.shape)


def square_update(current, sum_a, sum_b, moduli_a, moduli_b, omega_step, tangent):
    residue = (sum_a + sum_b) / (moduli_a + moduli_b)[..., None, None] - current
    smoothed = residue + penalty_mix * jnp.einsum("...z,zk->...k", residue, tangent, precision=highest)
    return current + omega_step * smoothed


def shards(forcing, modulus, orient_codes):
    extent = forcing.shape[3]
    blocks = forcing.shape[1]
    flat = extent * extent
    source_field = forcing[0]
    moduli = modulus[0]
    codes_here = orient_codes[0]
    code_values = codes_here.astype(jnp.float32)
    omegas = step_weights(ITERS)
    slab_count = lax.axis_size("blk")
    slab_index = lax.axis_index("blk")
    has_up = jnp.broadcast_to((slab_index < slab_count - 1).astype(jnp.float32), (blocks, 3))
    has_down = jnp.broadcast_to((slab_index > 0).astype(jnp.float32), (blocks, 3))
    lam_x_up = jnp.zeros((blocks, 3, 1, flat), jnp.float32)
    lam_x_down = lam_x_up
    lam_y = jnp.zeros((blocks, 3, extent, 2 * extent), jnp.float32)
    state = [None] * blocks
    for sweep in range(ITERS + 1):
        last = sweep == ITERS
        omega = omegas[sweep - 1] if sweep > 0 else 0.0
        outs = [
            kernel_sweep(source_field[b], moduli[b], code_values[b:b + 1], state[b], emit_u=last,
                         emit_sides=not last, omega=omega)
            for b in range(blocks)
        ]
        if last:
            return jnp.stack([o[0] for o in outs], 0)[None]
        xh, xl, ys = (jnp.stack([o[k] for o in outs], 0) for k in range(3))
        if sweep > 0:
            lam_x_up, lam_x_down, lam_y = (jnp.stack([o[k] for o in outs], 0) for k in range(3, 6))
        upper = shifted(xl, "blk", -1)
        lower = shifted(xh, "blk", 1)
        nxt = jnp.concatenate([ys[1:], shifted_2(ys[:1], "face", -1)], 0)
        prv = jnp.concatenate([shifted_2(ys[-1:], "face", 1), ys[:-1]], 0)
        if sweep == 0:
            codes_down = lower[:, 0, 2, 0].astype(jnp.int32)
            neighbour_moduli = jnp.stack(
                [upper[:, :, 1, 0], lower[:, :, 1, 0], prv[:, :, 1, 0, 0], nxt[:, :, 1, 0, 0], has_up, has_down], 1
            )
        up_sum = orient(upper[:, :, 0], codes_here, extent)[:, :, None]
        down_sum = orient(lower[:, :, 0], codes_down, extent)[:, :, None]
        state = [
            (neighbour_moduli[b], lam_x_up[b], lam_x_down[b], lam_y[b], xh[b], xl[b], ys[b],
             up_sum[b], down_sum[b], prv[b], nxt[b])
            for b in range(blocks)
        ]


def solution(mesh):
    placed = (P("blk", "face", None, None, None), P("blk", "face", None), P("blk", "face"))
    return jax.shard_map(
        shards,
        mesh=mesh,
        in_specs=placed,
        out_specs=P("blk", "face", None, None, None),
        check_vma=False,
    )
```

```python
import functools
import math

import jax
import jax.numpy as jnp
from jax import lax
from jax.sharding import PartitionSpec as P
from jax.experimental import pallas as pl
from jax.experimental.pallas import tpu as pltpu
import numpy as np
import ml_dtypes

ITERS = 2


mass_shift = 0.02
inject_scale = 2.0
traction_mix = 0.5
penalty_mix = 0.25
lower_edge = 0.3
upper_edge = 1.5
highest = lax.Precision.HIGHEST


def shifted(shard, axis, by):
    length = lax.axis_size(axis)
    pairs = [(i, i + by) for i in range(length) if 0 <= i + by < length]
    return lax.ppermute(shard, axis, pairs)


def shifted_2(shard, axis, by):
    length = lax.axis_size(axis)
    return lax.ppermute(shard, axis, [(i, (i + by) % length) for i in range(length)])


def tables(extent):
    node_index = jnp.arange(extent, dtype=jnp.float32) + 1.0
    basis = math.sqrt(2.0 / (extent + 1)) * jnp.sin(
        math.pi * node_index[:, None] * node_index[None, :] / (extent + 1)
    )
    eigenvalues = 2.0 - 2.0 * jnp.cos(math.pi * node_index / (extent + 1))
    return (basis, eigenvalues)


def tangent_matrix(extent):
    node_index = jnp.arange(extent, dtype=jnp.int32)
    distance = jnp.abs(node_index[:, None] - node_index[None, :])
    end_rows = ((node_index == 0) | (node_index == extent - 1)).astype(jnp.float32)
    adjacent = (distance == 1).astype(jnp.float32)
    diagonal_part = (distance == 0).astype(jnp.float32) * (2.0 - end_rows[:, None])
    return adjacent - diagonal_part


def step_weights(step_count):
    midpoint = 0.5 * (upper_edge + lower_edge)
    radius = 0.5 * (upper_edge - lower_edge)
    return [
        1.0 / (midpoint + radius * math.cos(math.pi * (2 * turn_index + 1) / (2 * step_count)))
        for turn_index in range(step_count)
    ]


def divisor(moduli, eigenvalues):
    extent = eigenvalues.shape[0]
    summed = eigenvalues[:, None, None] + eigenvalues[None, :, None] + eigenvalues[None, None, :]
    scaled = moduli[..., None, None, None] * summed + mass_shift
    return scaled.reshape(moduli.shape + (extent, extent * extent))


def body_transform(field_data, basis, paired_basis):
    extent = basis.shape[0]
    full_shape = field_data.shape
    pair_width = paired_basis.shape[0]
    sectioned = jnp.einsum("ix,bcxm->bcim", basis, field_data, precision=highest)
    sectioned = sectioned.reshape(full_shape[:-1] + (full_shape[-1] // pair_width, pair_width))
    sectioned = jnp.einsum("bcxpz,kz->bcxpk", sectioned, paired_basis, precision=highest)
    sectioned = sectioned.reshape(full_shape[:-1] + (extent, extent))
    sectioned = jnp.einsum("jy,bcxyz->bcxjz", basis, sectioned, precision=highest)
    return sectioned.reshape(full_shape)


def body_solve(right_side, scale_table, basis, paired_basis):
    return body_transform(
        body_transform(right_side, basis, paired_basis) / scale_table, basis, paired_basis
    )


f32 = jnp.float32


def np_tables(n):
    g = np.float32
    idx = np.arange(n, dtype=g) + g(1.0)
    arg = (g(math.pi) * idx[:, None]) * idx[None, :] / g(n + 1)
    q = g(math.sqrt(2.0 / (n + 1))) * np.sin(arg)
    e = g(2.0) - g(2.0) * np.cos(g(math.pi) * idx / g(n + 1))
    return q.astype(g), e.astype(g)


def consts(n):
    q, e = np_tables(n)
    h = n // 2
    p4 = np.kron(np.eye(4, dtype=np.float32), q.T)
    w = np.zeros((2, 4, h, 2, 4, h), np.float32)
    qq = q.reshape(h, 2, h, 2)
    for xl in range(4):
        w[:, xl, :, :, xl, :] = np.transpose(qq, (3, 2, 1, 0))
    wy = w.reshape(8 * h, 8 * h)
    ng = n // 4
    lane_h = np.arange(8 * h) // (4 * h)
    lane_xl = (np.arange(8 * h) // h) % 4
    lane_c = np.arange(8 * h) % h
    exy = (e[4 * np.arange(ng)[:, None] + lane_xl[None, :]] + e[2 * lane_c + lane_h][None, :]).astype(np.float32)
    ez = np.ascontiguousarray(np.broadcast_to(e[:, None], (n, 8 * h))).astype(np.float32)
    return stack_left(q), stack_right(p4), stack_right(wy), exy, ez


BF = jnp.bfloat16

def np_split3(w):
    b = ml_dtypes.bfloat16
    w1 = w.astype(b)
    r1 = w - w1.astype(np.float32)
    w2 = r1.astype(b)
    w3 = (r1 - w2.astype(np.float32)).astype(b)
    return w1, w2, w3


def stack_right(w):
    w1, w2, w3 = np_split3(w)
    return np.concatenate([w1, w2, w1, w1], 0)


def stack_left(w):
    w1, w2, w3 = np_split3(w)
    return np.concatenate([w1, w2, w1, w1], 1)


def split3(d):
    d1 = d.astype(BF)
    r1 = d - d1.astype(f32)
    d2 = r1.astype(BF)
    d3 = (r1 - d2.astype(f32)).astype(BF)
    return d1, d2, d3


def sdot(d, w6):
    d1, d2, d3 = split3(d)
    return jnp.dot(jnp.concatenate([d1, d1, d2, d3], 1), w6, preferred_element_type=f32)


def sdot_left(w6, d):
    d1, d2, d3 = split3(d)
    return jnp.dot(w6, jnp.concatenate([d1, d1, d2, d3], 0), preferred_element_type=f32)


def solve_kernel(*refs, with_faces, emit_u, emit_sides, omega, zero_lam):
    it = iter(refs)
    mod_ref, f_ref = next(it), next(it)
    if with_faces:
        nbm_ref = next(it)
        lxu_ref, lxd_ref, ly_ref = (None, None, None) if zero_lam else (next(it), next(it), next(it))
        sxh_ref, sxl_ref, sy_ref, rup_ref, rdn_ref, ryp_ref, ryn_ref = (next(it) for _ in range(7))
    q_ref, p_ref, wy_ref, exy_ref, ez_ref = next(it), next(it), next(it), next(it), next(it)
    code_ref = next(it)
    o_ref = next(it) if emit_u else None
    if emit_sides:
        xh_ref, xl_ref, y_ref = next(it), next(it), next(it)
    if with_faces and emit_sides:
        nlx_ref, nld_ref, nly_ref = next(it), next(it), next(it)
    elif with_faces:
        nlx_ref = nld_ref = nly_ref = None
    s_ref, z_ref = next(it), next(it)
    n = q_ref.shape[0]
    h = n // 2
    w2 = 2 * n
    w4 = 4 * n
    nn = f_ref.shape[-1]
    nch = nn // w2
    npair = nn // w4
    comp = pl.program_id(0)
    m = mod_ref[comp]
    q = q_ref[...]
    r = f_ref[0]
    if with_faces:
        m_up = nbm_ref[0, comp]
        m_dn = nbm_ref[1, comp]
        m_prev = nbm_ref[2, comp]
        m_next = nbm_ref[3, comp]
        has_up = nbm_ref[4, comp]
        has_dn = nbm_ref[5, comp]
        lane_x = lax.broadcasted_iota(jnp.int32, (1, nn), 1) % n
        lane_y = lax.broadcasted_iota(jnp.int32, (n, w2), 1)

        def smooth(res, lanes, width):
            left = pltpu.roll(res, 1, 1)
            right = pltpu.roll(res, width - 1, 1)
            left = jnp.where(lanes % n == 0, 0.0, left)
            right = jnp.where(lanes % n == n - 1, 0.0, right)
            diag = jnp.where((lanes % n == 0) | (lanes % n == n - 1), -1.0, -2.0)
            return res + 0.25 * ((left + right) + diag * res)

        xu = 0.0 if zero_lam else lxu_ref[0]
        res = (sxh_ref[0, 0:1, :] + rup_ref[0]) / (m + m_up) - xu
        xhi_face = (xu + omega * smooth(res, lane_x, nn)) * has_up
        xd = 0.0 if zero_lam else lxd_ref[0]
        res = (rdn_ref[0] + sxl_ref[0, 0:1, :]) / (m_dn + m) - xd
        xlo_face = (xd + omega * smooth(res, lane_x, nn)) * has_dn
        ly = 0.0 if zero_lam else ly_ref[0]
        lo = lane_y < n
        recv = pltpu.roll(jnp.where(lo, ryn_ref[0, 0], ryp_ref[0, 0]), n, 1)
        res = (sy_ref[0, 0] + recv) / (m + jnp.where(lo, m_prev, m_next)) - ly
        yadd = ly + omega * smooth(res, lane_y, w2)
        if nlx_ref is not None:
            nlx_ref[0] = xhi_face
            nld_ref[0] = xlo_face
            nly_ref[0] = yadd
        rows = lax.broadcasted_iota(jnp.int32, (n, nn), 0)
        added = jnp.where(rows == 0, xlo_face, 0.0) + jnp.where(rows == n - 1, xhi_face, 0.0)
        lane = lane_y
        first = added[:, :w2] + jnp.where(lane < n, yadd, 0.0)
        last = added[:, nn - w2:] + jnp.where(lane >= n, yadd, 0.0)
        added = jnp.concatenate([first, added[:, w2:nn - w2], last], 1)
        r = r + (2.0 * m) * added
    a = sdot_left(q, r)
    for cp in range(npair):
        z_ref[cp * n:(cp + 1) * n, :] = a[:, cp * w4:(cp + 1) * w4]
    zo = sdot(z_ref[...], p_ref[...])
    for cp in range(npair):
        for cb in range(2):
            s_ref[(2 * cp + cb) * n:(2 * cp + cb + 1) * n, :] = zo[cp * n:(cp + 1) * n, cb * w2:(cb + 1) * w2]
    wy = wy_ref[...]
    ez = ez_ref[...]
    XG = 4
    GPI = 8

    def body(it_, carry):
        lhs = []
        for gi in range(GPI):
            g = it_ * GPI + gi
            blk = jnp.concatenate([s_ref[pl.ds(g * XG + xl, h, stride=n), :] for xl in range(XG)], 0)
            tb = blk.T
            lhs.append(jnp.concatenate([tb[:n], tb[n:]], 1))
        v = sdot(jnp.concatenate(lhs, 0), wy)
        div = jnp.concatenate([m * (exy_ref[pl.ds(it_ * GPI + gi, 1), :] + ez) + 0.02 for gi in range(GPI)], 0)
        v = v / div
        v = sdot(v, wy)
        for gi in range(GPI):
            g = it_ * GPI + gi
            vg = v[gi * n:(gi + 1) * n]
            tb = jnp.concatenate([vg[:, :w2], vg[:, w2:]], 0).T
            for xl in range(XG):
                s_ref[pl.ds(g * XG + xl, h, stride=n), :] = tb[xl * h:(xl + 1) * h]
        return carry
    lax.fori_loop(0, n // (XG * GPI), body, 0)
    for cp in range(npair):
        z_ref[cp * n:(cp + 1) * n, :] = jnp.concatenate(
            [s_ref[(2 * cp) * n:(2 * cp + 1) * n, :], s_ref[(2 * cp + 1) * n:(2 * cp + 2) * n, :]], 1)
    zo = sdot(z_ref[...], p_ref[...])
    b = jnp.concatenate([zo[cp * n:(cp + 1) * n, :] for cp in range(npair)], 1)
    u = sdot_left(q, b)
    if emit_u:
        o_ref[0] = u

    def slope(p0, p1, p2, p3):
        return m * (11.0 / 6.0 * p0 - 3.0 * p1 + 1.5 * p2 - p3 / 3.0)
    if emit_sides:
        m_row = jnp.full((1, nn), m, f32)
        xh_ref[0, 0:1, :] = m * u[n - 1:n] + 0.5 * slope(u[n - 1:n], u[n - 2:n - 1], u[n - 3:n - 2], u[n - 4:n - 3])
        xh_ref[0, 1:2, :] = m_row
        xh_ref[0, 2:3, :] = jnp.full((1, nn), code_ref[0], f32)
        xl_ref[0, 0:1, :] = m * u[0:1] + 0.5 * slope(u[0:1], u[1:2], u[2:3], u[3:4])
        xl_ref[0, 1:2, :] = m_row
        c_hi = u[:, nn - w2:]
        c_hi2 = u[:, nn - 2 * w2:nn - w2]
        s_hi = m * c_hi + 0.5 * slope(c_hi, pltpu.roll(c_hi, n, 1), c_hi2, pltpu.roll(c_hi2, n, 1))
        c_lo = u[:, :w2]
        c_lo2 = u[:, w2:2 * w2]
        s_lo = m * c_lo + 0.5 * slope(c_lo, pltpu.roll(c_lo, n, 1), c_lo2, pltpu.roll(c_lo2, n, 1))
        lane_s = lax.broadcasted_iota(jnp.int32, (n, w2), 1)
        y_ref[0, 0] = jnp.where(lane_s < n, s_lo, s_hi)
        y_ref[0, 1] = jnp.full((n, w2), m, f32)


def kernel_sweep(rhs, moduli, code, state=None, emit_u=True, emit_sides=False, omega=0.0):
    ncomp, n, nn = rhs.shape
    q, p4, wy, exy, ez = consts(n)
    full = lambda shp: pl.BlockSpec(shp, lambda c: (0,) * len(shp))
    comp3 = lambda shp: pl.BlockSpec((1,) + shp, lambda c: (c,) + (0,) * len(shp))
    smem = pl.BlockSpec(memory_space=pltpu.SMEM)
    in_specs = [smem, comp3((n, nn))]
    args = [moduli, rhs]
    zero_lam = state is not None and state[1] is None
    if state is not None:
        if zero_lam:
            state = state[:1] + state[4:]
            in_specs += [smem]
        else:
            in_specs += [smem, comp3((1, nn)), comp3((1, nn)), comp3((n, 2 * n))]
        in_specs += [comp3((3, nn)), comp3((2, nn)), comp3((2, n, 2 * n)),
                     comp3((1, nn)), comp3((1, nn)), comp3((2, n, 2 * n)), comp3((2, n, 2 * n))]
        args += list(state)
    in_specs += [full(q.shape), full(p4.shape), full(wy.shape), full(exy.shape), full(ez.shape), smem]
    args += [q, p4, wy, exy, ez, code]
    out_specs, out_shape = [], []
    if emit_u:
        out_specs.append(comp3((n, nn)))
        out_shape.append(jax.ShapeDtypeStruct(rhs.shape, f32))
    if emit_sides:
        out_specs += [comp3((3, nn)), comp3((2, nn)), comp3((2, n, 2 * n))]
        out_shape += [jax.ShapeDtypeStruct((ncomp, 3, nn), f32), jax.ShapeDtypeStruct((ncomp, 2, nn), f32),
                      jax.ShapeDtypeStruct((ncomp, 2, n, 2 * n), f32)]
        if state is not None:
            out_specs += [comp3((1, nn)), comp3((1, nn)), comp3((n, 2 * n))]
            out_shape += [jax.ShapeDtypeStruct((ncomp, 1, nn), f32), jax.ShapeDtypeStruct((ncomp, 1, nn), f32),
                          jax.ShapeDtypeStruct((ncomp, n, 2 * n), f32)]
    kernel = functools.partial(solve_kernel, with_faces=state is not None, emit_u=emit_u,
                               emit_sides=emit_sides, omega=omega, zero_lam=zero_lam)
    return pl.pallas_call(
        kernel,
        grid=(ncomp,),
        in_specs=in_specs,
        out_specs=out_specs,
        out_shape=out_shape,
        scratch_shapes=[pltpu.VMEM((nn // 2, 2 * n), f32), pltpu.VMEM((nn // 4, 4 * n), f32)],
    )(*args)


def orient(face_field, code_table, extent):
    square = face_field.reshape(face_field.shape[:-1] + (extent, extent))
    flip_rows = (code_table % 2 == 1)[..., None, None, None]
    flip_cols = (code_table // 2 == 1)[..., None, None, None]
    square = jnp.where(flip_rows, jnp.flip(square, -2), square)
    square = jnp.where(flip_cols, jnp.flip(square, -1), square)
    return square.reshape(face_field.shape)


def face_data(solution, moduli):
    extent = solution.shape[-2]
    cube_view = solution.reshape(solution.shape[:-1] + (extent, extent))
    flat_shape = solution.shape[:-2] + (extent * extent,)

    def pack_side(planes):
        normal_slope = 11.0 / 6.0 * planes[0] - 3.0 * planes[1] + 1.5 * planes[2] - planes[3] / 3.0
        return (planes[0], moduli[..., None] * normal_slope)

    x_high = pack_side([solution[..., extent - 1 - plane_depth, :] for plane_depth in range(4)])
    x_low = pack_side([solution[..., plane_depth, :] for plane_depth in range(4)])
    y_high = pack_side(
        [
            cube_view[..., extent - 1 - plane_depth, :].reshape(flat_shape)
            for plane_depth in range(4)
        ]
    )
    y_low = pack_side(
        [cube_view[..., plane_depth, :].reshape(flat_shape) for plane_depth in range(4)]
    )
    return (x_high, x_low, y_high, y_low)


def place_faces(source_field, moduli, x_low, x_high, y_low, y_high):
    extent = source_field.shape[-2]
    added = jnp.zeros_like(source_field)
    added = added.at[..., 0, :].add(x_low)
    added = added.at[..., extent - 1, :].add(x_high)
    cube_view = added.reshape(added.shape[:-1] + (extent, extent))
    low_square = y_low.reshape(y_low.shape[:-1] + (extent, extent))
    high_square = y_high.reshape(y_high.shape[:-1] + (extent, extent))
    cube_view = cube_view.at[..., 0, :].add(low_square)
    cube_view = cube_view.at[..., extent - 1, :].add(high_square)
    added = cube_view.reshape(source_field.shape)
    return source_field + inject_scale * moduli[..., None, None] * added


def trace_update(current, side_a, side_b, moduli_a, moduli_b, omega_step, tangent):
    extent = tangent.shape[0]
    weight_a = moduli_a[..., None]
    weight_b = moduli_b[..., None]
    residue = (
        weight_a * side_a[0] + weight_b * side_b[0] + traction_mix * (side_a[1] + side_b[1])
    ) / (weight_a + weight_b) - current
    rows_view = residue.reshape(residue.shape[:-1] + (residue.shape[-1] // extent, extent))
    smoothed = rows_view + penalty_mix * jnp.einsum(
        "...z,zk->...k", rows_view, tangent, precision=highest
    )
    return current + omega_step * smoothed.reshape(residue.shape)


def flat_update(current, sum_a, sum_b, moduli_a, moduli_b, omega_step, tangent):
    extent = tangent.shape[0]
    residue = (sum_a + sum_b) / (moduli_a + moduli_b)[..., None] - current
    rows_view = residue.reshape(residue.shape[:-1] + (residue.shape[-1] // extent, extent))
    smoothed = rows_view + penalty_mix * jnp.einsum("...z,zk->...k", rows_view, tangent, precision=highest)
    return current + omega_step * smoothed.reshape(residue.shape)


def square_update(current, sum_a, sum_b, moduli_a, moduli_b, omega_step, tangent):
    residue = (sum_a + sum_b) / (moduli_a + moduli_b)[..., None, None] - current
    smoothed = residue + penalty_mix * jnp.einsum("...z,zk->...k", residue, tangent, precision=highest)
    return current + omega_step * smoothed


def shards(forcing, modulus, orient_codes):
    extent = forcing.shape[3]
    blocks = forcing.shape[1]
    flat = extent * extent
    source_field = forcing[0]
    moduli = modulus[0]
    codes_here = orient_codes[0]
    code_values = codes_here.astype(jnp.float32)
    omegas = step_weights(ITERS)
    slab_count = lax.axis_size("blk")
    slab_index = lax.axis_index("blk")
    has_up = jnp.broadcast_to((slab_index < slab_count - 1).astype(jnp.float32), (blocks, 3))
    has_down = jnp.broadcast_to((slab_index > 0).astype(jnp.float32), (blocks, 3))
    lam_x_up = lam_x_down = lam_y = [None] * blocks
    state = [None] * blocks
    for sweep in range(ITERS + 1):
        last = sweep == ITERS
        omega = omegas[sweep - 1] if sweep > 0 else 0.0
        outs = [
            kernel_sweep(source_field[b], moduli[b], code_values[b:b + 1], state[b], emit_u=last,
                         emit_sides=not last, omega=omega)
            for b in range(blocks)
        ]
        if last:
            return jnp.stack([o[0] for o in outs], 0)[None]
        xh, xl, ys = (jnp.stack([o[k] for o in outs], 0) for k in range(3))
        if sweep > 0:
            lam_x_up, lam_x_down, lam_y = (jnp.stack([o[k] for o in outs], 0) for k in range(3, 6))
        upper = shifted(xl, "blk", -1)
        lower = shifted(xh, "blk", 1)
        nxt = jnp.concatenate([ys[1:], shifted_2(ys[:1], "face", -1)], 0)
        prv = jnp.concatenate([shifted_2(ys[-1:], "face", 1), ys[:-1]], 0)
        if sweep == 0:
            codes_down = lower[:, 0, 2, 0].astype(jnp.int32)
            neighbour_moduli = jnp.stack(
                [upper[:, :, 1, 0], lower[:, :, 1, 0], prv[:, :, 1, 0, 0], nxt[:, :, 1, 0, 0], has_up, has_down], 1
            )
        up_sum = orient(upper[:, :, 0], codes_here, extent)[:, :, None]
        down_sum = orient(lower[:, :, 0], codes_down, extent)[:, :, None]
        state = [
            (neighbour_moduli[b], lam_x_up[b], lam_x_down[b], lam_y[b], xh[b], xl[b], ys[b],
             up_sum[b], down_sum[b], prv[b], nxt[b])
            for b in range(blocks)
        ]


def solution(mesh):
    placed = (P("blk", "face", None, None, None), P("blk", "face", None), P("blk", "face"))
    return jax.shard_map(
        shards,
        mesh=mesh,
        in_specs=placed,
        out_specs=P("blk", "face", None, None, None),
        check_vma=False,
    )
```

```python
import functools
import math

import jax
import jax.numpy as jnp
from jax import lax
from jax.sharding import PartitionSpec as P
from jax.experimental import pallas as pl
from jax.experimental.pallas import tpu as pltpu
import numpy as np
import ml_dtypes

ITERS = 2


mass_shift = 0.02
inject_scale = 2.0
traction_mix = 0.5
penalty_mix = 0.25
lower_edge = 0.3
upper_edge = 1.5
highest = lax.Precision.HIGHEST


def shifted(shard, axis, by):
    length = lax.axis_size(axis)
    pairs = [(i, i + by) for i in range(length) if 0 <= i + by < length]
    return lax.ppermute(shard, axis, pairs)


def shifted_2(shard, axis, by):
    length = lax.axis_size(axis)
    return lax.ppermute(shard, axis, [(i, (i + by) % length) for i in range(length)])


def tables(extent):
    node_index = jnp.arange(extent, dtype=jnp.float32) + 1.0
    basis = math.sqrt(2.0 / (extent + 1)) * jnp.sin(
        math.pi * node_index[:, None] * node_index[None, :] / (extent + 1)
    )
    eigenvalues = 2.0 - 2.0 * jnp.cos(math.pi * node_index / (extent + 1))
    return (basis, eigenvalues)


def tangent_matrix(extent):
    node_index = jnp.arange(extent, dtype=jnp.int32)
    distance = jnp.abs(node_index[:, None] - node_index[None, :])
    end_rows = ((node_index == 0) | (node_index == extent - 1)).astype(jnp.float32)
    adjacent = (distance == 1).astype(jnp.float32)
    diagonal_part = (distance == 0).astype(jnp.float32) * (2.0 - end_rows[:, None])
    return adjacent - diagonal_part


def step_weights(step_count):
    midpoint = 0.5 * (upper_edge + lower_edge)
    radius = 0.5 * (upper_edge - lower_edge)
    return [
        1.0 / (midpoint + radius * math.cos(math.pi * (2 * turn_index + 1) / (2 * step_count)))
        for turn_index in range(step_count)
    ]


def divisor(moduli, eigenvalues):
    extent = eigenvalues.shape[0]
    summed = eigenvalues[:, None, None] + eigenvalues[None, :, None] + eigenvalues[None, None, :]
    scaled = moduli[..., None, None, None] * summed + mass_shift
    return scaled.reshape(moduli.shape + (extent, extent * extent))


def body_transform(field_data, basis, paired_basis):
    extent = basis.shape[0]
    full_shape = field_data.shape
    pair_width = paired_basis.shape[0]
    sectioned = jnp.einsum("ix,bcxm->bcim", basis, field_data, precision=highest)
    sectioned = sectioned.reshape(full_shape[:-1] + (full_shape[-1] // pair_width, pair_width))
    sectioned = jnp.einsum("bcxpz,kz->bcxpk", sectioned, paired_basis, precision=highest)
    sectioned = sectioned.reshape(full_shape[:-1] + (extent, extent))
    sectioned = jnp.einsum("jy,bcxyz->bcxjz", basis, sectioned, precision=highest)
    return sectioned.reshape(full_shape)


def body_solve(right_side, scale_table, basis, paired_basis):
    return body_transform(
        body_transform(right_side, basis, paired_basis) / scale_table, basis, paired_basis
    )


f32 = jnp.float32


def np_tables(n):
    g = np.float32
    idx = np.arange(n, dtype=g) + g(1.0)
    arg = (g(math.pi) * idx[:, None]) * idx[None, :] / g(n + 1)
    q = g(math.sqrt(2.0 / (n + 1))) * np.sin(arg)
    e = g(2.0) - g(2.0) * np.cos(g(math.pi) * idx / g(n + 1))
    return q.astype(g), e.astype(g)


def consts(n):
    q, e = np_tables(n)
    h = n // 2
    p4 = np.kron(np.eye(4, dtype=np.float32), q.T)
    w = np.zeros((2, 4, h, 2, 4, h), np.float32)
    qq = q.reshape(h, 2, h, 2)
    for xl in range(4):
        w[:, xl, :, :, xl, :] = np.transpose(qq, (3, 2, 1, 0))
    wy = w.reshape(8 * h, 8 * h)
    ng = n // 4
    lane_h = np.arange(8 * h) // (4 * h)
    lane_xl = (np.arange(8 * h) // h) % 4
    lane_c = np.arange(8 * h) % h
    exy = (e[4 * np.arange(ng)[:, None] + lane_xl[None, :]] + e[2 * lane_c + lane_h][None, :]).astype(np.float32)
    ez = np.ascontiguousarray(np.broadcast_to(e[:, None], (n, 8 * h))).astype(np.float32)
    return stack_left(q), stack_right(p4), stack_right(wy), exy, ez


BF = jnp.bfloat16

def np_split3(w):
    b = ml_dtypes.bfloat16
    w1 = w.astype(b)
    r1 = w - w1.astype(np.float32)
    w2 = r1.astype(b)
    w3 = (r1 - w2.astype(np.float32)).astype(b)
    return w1, w2, w3


def stack_right(w):
    w1, w2, w3 = np_split3(w)
    return np.concatenate([w1, w2, w1, w1], 0)


def stack_left(w):
    w1, w2, w3 = np_split3(w)
    return np.concatenate([w1, w2, w1, w1], 1)


def split3(d):
    d1 = d.astype(BF)
    r1 = d - d1.astype(f32)
    d2 = r1.astype(BF)
    d3 = (r1 - d2.astype(f32)).astype(BF)
    return d1, d2, d3


def sdot(d, w6):
    d1, d2, d3 = split3(d)
    return jnp.dot(jnp.concatenate([d1, d1, d2, d3], 1), w6, preferred_element_type=f32)


def sdot_left(w6, d):
    d1, d2, d3 = split3(d)
    return jnp.dot(w6, jnp.concatenate([d1, d1, d2, d3], 0), preferred_element_type=f32)


def solve_kernel(*refs, with_faces, emit_u, emit_sides, omega, zero_lam, meta):
    it = iter(refs)
    mod_ref, f_ref = next(it), next(it)
    if with_faces:
        nbm_ref = next(it)
        lxu_ref, lxd_ref, ly_ref = (None, None, None) if zero_lam else (next(it), next(it), next(it))
        sxh_ref, sxl_ref, sy_ref, rup_ref, rdn_ref, ryp_ref, ryn_ref = (next(it) for _ in range(7))
    q_ref, p_ref, wy_ref, exy_ref, ez_ref = next(it), next(it), next(it), next(it), next(it)
    code_ref = next(it)
    o_ref = next(it) if emit_u else None
    if emit_sides:
        xh_ref, xl_ref, y_ref = next(it), next(it), next(it)
    if with_faces and emit_sides:
        nlx_ref, nld_ref, nly_ref = next(it), next(it), next(it)
    elif with_faces:
        nlx_ref = nld_ref = nly_ref = None
    s_ref, z_ref = next(it), next(it)
    n = q_ref.shape[0]
    h = n // 2
    w2 = 2 * n
    w4 = 4 * n
    nn = f_ref.shape[-1]
    nch = nn // w2
    npair = nn // w4
    comp = pl.program_id(0)
    m = mod_ref[comp]
    q = q_ref[...]
    r = f_ref[0]
    if with_faces:
        m_up = nbm_ref[0, comp]
        m_dn = nbm_ref[1, comp]
        m_prev = nbm_ref[2, comp]
        m_next = nbm_ref[3, comp]
        has_up = nbm_ref[4, comp]
        has_dn = nbm_ref[5, comp]
        lane_x = lax.broadcasted_iota(jnp.int32, (1, nn), 1) % n
        lane_y = lax.broadcasted_iota(jnp.int32, (n, w2), 1)

        def smooth(res, lanes, width):
            left = pltpu.roll(res, 1, 1)
            right = pltpu.roll(res, width - 1, 1)
            left = jnp.where(lanes % n == 0, 0.0, left)
            right = jnp.where(lanes % n == n - 1, 0.0, right)
            diag = jnp.where((lanes % n == 0) | (lanes % n == n - 1), -1.0, -2.0)
            return res + 0.25 * ((left + right) + diag * res)

        xu = 0.0 if zero_lam else lxu_ref[0]
        res = (sxh_ref[0, 0:1, :] + rup_ref[0]) / (m + m_up) - xu
        xhi_face = (xu + omega * smooth(res, lane_x, nn)) * has_up
        xd = 0.0 if zero_lam else lxd_ref[0]
        res = (rdn_ref[0] + sxl_ref[0, 0:1, :]) / (m_dn + m) - xd
        xlo_face = (xd + omega * smooth(res, lane_x, nn)) * has_dn
        ly = 0.0 if zero_lam else ly_ref[0]
        lo = lane_y < n
        recv = pltpu.roll(jnp.where(lo, ryn_ref[0, 0], ryp_ref[0, 0]), n, 1)
        res = (sy_ref[0, 0] + recv) / (m + jnp.where(lo, m_prev, m_next)) - ly
        yadd = ly + omega * smooth(res, lane_y, w2)
        if nlx_ref is not None:
            nlx_ref[0] = xhi_face
            nld_ref[0] = xlo_face
            nly_ref[0] = yadd
        rows = lax.broadcasted_iota(jnp.int32, (n, nn), 0)
        added = jnp.where(rows == 0, xlo_face, 0.0) + jnp.where(rows == n - 1, xhi_face, 0.0)
        lane = lane_y
        first = added[:, :w2] + jnp.where(lane < n, yadd, 0.0)
        last = added[:, nn - w2:] + jnp.where(lane >= n, yadd, 0.0)
        added = jnp.concatenate([first, added[:, w2:nn - w2], last], 1)
        r = r + (2.0 * m) * added
    a = sdot_left(q, r)
    for cp in range(npair):
        z_ref[cp * n:(cp + 1) * n, :] = a[:, cp * w4:(cp + 1) * w4]
    zo = sdot(z_ref[...], p_ref[...])
    for cp in range(npair):
        for cb in range(2):
            s_ref[(2 * cp + cb) * n:(2 * cp + cb + 1) * n, :] = zo[cp * n:(cp + 1) * n, cb * w2:(cb + 1) * w2]
    wy = wy_ref[...]
    ez = ez_ref[...]
    XG = 4
    GPI = 8

    def body(it_, carry):
        lhs = []
        for gi in range(GPI):
            g = it_ * GPI + gi
            blk = jnp.concatenate([s_ref[pl.ds(g * XG + xl, h, stride=n), :] for xl in range(XG)], 0)
            tb = blk.T
            lhs.append(jnp.concatenate([tb[:n], tb[n:]], 1))
        v = sdot(jnp.concatenate(lhs, 0), wy)
        div = jnp.concatenate([m * (exy_ref[pl.ds(it_ * GPI + gi, 1), :] + ez) + 0.02 for gi in range(GPI)], 0)
        v = v / div
        v = sdot(v, wy)
        for gi in range(GPI):
            g = it_ * GPI + gi
            vg = v[gi * n:(gi + 1) * n]
            tb = jnp.concatenate([vg[:, :w2], vg[:, w2:]], 0).T
            for xl in range(XG):
                s_ref[pl.ds(g * XG + xl, h, stride=n), :] = tb[xl * h:(xl + 1) * h]
        return carry
    lax.fori_loop(0, n // (XG * GPI), body, 0)
    for cp in range(npair):
        z_ref[cp * n:(cp + 1) * n, :] = jnp.concatenate(
            [s_ref[(2 * cp) * n:(2 * cp + 1) * n, :], s_ref[(2 * cp + 1) * n:(2 * cp + 2) * n, :]], 1)
    zo = sdot(z_ref[...], p_ref[...])
    b = jnp.concatenate([zo[cp * n:(cp + 1) * n, :] for cp in range(npair)], 1)
    u = sdot_left(q, b)
    if emit_u:
        o_ref[0] = u

    def slope(p0, p1, p2, p3):
        return m * (11.0 / 6.0 * p0 - 3.0 * p1 + 1.5 * p2 - p3 / 3.0)
    if emit_sides:
        m_row = jnp.full((1, nn), m, f32)
        xh_ref[0, 0:1, :] = m * u[n - 1:n] + 0.5 * slope(u[n - 1:n], u[n - 2:n - 1], u[n - 3:n - 2], u[n - 4:n - 3])
        if meta:
            xh_ref[0, 1:2, :] = m_row
            xh_ref[0, 2:3, :] = jnp.full((1, nn), code_ref[0], f32)
        xl_ref[0, 0:1, :] = m * u[0:1] + 0.5 * slope(u[0:1], u[1:2], u[2:3], u[3:4])
        if meta:
            xl_ref[0, 1:2, :] = m_row
        c_hi = u[:, nn - w2:]
        c_hi2 = u[:, nn - 2 * w2:nn - w2]
        s_hi = m * c_hi + 0.5 * slope(c_hi, pltpu.roll(c_hi, n, 1), c_hi2, pltpu.roll(c_hi2, n, 1))
        c_lo = u[:, :w2]
        c_lo2 = u[:, w2:2 * w2]
        s_lo = m * c_lo + 0.5 * slope(c_lo, pltpu.roll(c_lo, n, 1), c_lo2, pltpu.roll(c_lo2, n, 1))
        lane_s = lax.broadcasted_iota(jnp.int32, (n, w2), 1)
        y_ref[0, 0] = jnp.where(lane_s < n, s_lo, s_hi)
        if meta:
            y_ref[0, 1] = jnp.full((n, w2), m, f32)


def kernel_sweep(rhs, moduli, code, state=None, emit_u=True, emit_sides=False, omega=0.0, meta=False):
    ncomp, n, nn = rhs.shape
    q, p4, wy, exy, ez = consts(n)
    full = lambda shp: pl.BlockSpec(shp, lambda c: (0,) * len(shp))
    comp3 = lambda shp: pl.BlockSpec((1,) + shp, lambda c: (c,) + (0,) * len(shp))
    smem = pl.BlockSpec(memory_space=pltpu.SMEM)
    in_specs = [smem, comp3((n, nn))]
    args = [moduli, rhs]
    zero_lam = state is not None and state[1] is None
    if state is not None:
        if zero_lam:
            state = state[:1] + state[4:]
            in_specs += [smem]
        else:
            in_specs += [smem, comp3((1, nn)), comp3((1, nn)), comp3((n, 2 * n))]
        in_specs += [comp3(x.shape[1:]) for x in state[-7:]]
        args += list(state)
    in_specs += [full(q.shape), full(p4.shape), full(wy.shape), full(exy.shape), full(ez.shape), smem]
    args += [q, p4, wy, exy, ez, code]
    out_specs, out_shape = [], []
    if emit_u:
        out_specs.append(comp3((n, nn)))
        out_shape.append(jax.ShapeDtypeStruct(rhs.shape, f32))
    if emit_sides:
        rx_h, rx_l, r_y = (3, 2, 2) if meta else (1, 1, 1)
        out_specs += [comp3((rx_h, nn)), comp3((rx_l, nn)), comp3((r_y, n, 2 * n))]
        out_shape += [jax.ShapeDtypeStruct((ncomp, rx_h, nn), f32), jax.ShapeDtypeStruct((ncomp, rx_l, nn), f32),
                      jax.ShapeDtypeStruct((ncomp, r_y, n, 2 * n), f32)]
        if state is not None:
            out_specs += [comp3((1, nn)), comp3((1, nn)), comp3((n, 2 * n))]
            out_shape += [jax.ShapeDtypeStruct((ncomp, 1, nn), f32), jax.ShapeDtypeStruct((ncomp, 1, nn), f32),
                          jax.ShapeDtypeStruct((ncomp, n, 2 * n), f32)]
    kernel = functools.partial(solve_kernel, with_faces=state is not None, emit_u=emit_u,
                               emit_sides=emit_sides, omega=omega, zero_lam=zero_lam, meta=meta)
    return pl.pallas_call(
        kernel,
        grid=(ncomp,),
        in_specs=in_specs,
        out_specs=out_specs,
        out_shape=out_shape,
        scratch_shapes=[pltpu.VMEM((nn // 2, 2 * n), f32), pltpu.VMEM((nn // 4, 4 * n), f32)],
    )(*args)


def orient(face_field, code_table, extent):
    square = face_field.reshape(face_field.shape[:-1] + (extent, extent))
    flip_rows = (code_table % 2 == 1)[..., None, None, None]
    flip_cols = (code_table // 2 == 1)[..., None, None, None]
    square = jnp.where(flip_rows, jnp.flip(square, -2), square)
    square = jnp.where(flip_cols, jnp.flip(square, -1), square)
    return square.reshape(face_field.shape)


def face_data(solution, moduli):
    extent = solution.shape[-2]
    cube_view = solution.reshape(solution.shape[:-1] + (extent, extent))
    flat_shape = solution.shape[:-2] + (extent * extent,)

    def pack_side(planes):
        normal_slope = 11.0 / 6.0 * planes[0] - 3.0 * planes[1] + 1.5 * planes[2] - planes[3] / 3.0
        return (planes[0], moduli[..., None] * normal_slope)

    x_high = pack_side([solution[..., extent - 1 - plane_depth, :] for plane_depth in range(4)])
    x_low = pack_side([solution[..., plane_depth, :] for plane_depth in range(4)])
    y_high = pack_side(
        [
            cube_view[..., extent - 1 - plane_depth, :].reshape(flat_shape)
            for plane_depth in range(4)
        ]
    )
    y_low = pack_side(
        [cube_view[..., plane_depth, :].reshape(flat_shape) for plane_depth in range(4)]
    )
    return (x_high, x_low, y_high, y_low)


def place_faces(source_field, moduli, x_low, x_high, y_low, y_high):
    extent = source_field.shape[-2]
    added = jnp.zeros_like(source_field)
    added = added.at[..., 0, :].add(x_low)
    added = added.at[..., extent - 1, :].add(x_high)
    cube_view = added.reshape(added.shape[:-1] + (extent, extent))
    low_square = y_low.reshape(y_low.shape[:-1] + (extent, extent))
    high_square = y_high.reshape(y_high.shape[:-1] + (extent, extent))
    cube_view = cube_view.at[..., 0, :].add(low_square)
    cube_view = cube_view.at[..., extent - 1, :].add(high_square)
    added = cube_view.reshape(source_field.shape)
    return source_field + inject_scale * moduli[..., None, None] * added


def trace_update(current, side_a, side_b, moduli_a, moduli_b, omega_step, tangent):
    extent = tangent.shape[0]
    weight_a = moduli_a[..., None]
    weight_b = moduli_b[..., None]
    residue = (
        weight_a * side_a[0] + weight_b * side_b[0] + traction_mix * (side_a[1] + side_b[1])
    ) / (weight_a + weight_b) - current
    rows_view = residue.reshape(residue.shape[:-1] + (residue.shape[-1] // extent, extent))
    smoothed = rows_view + penalty_mix * jnp.einsum(
        "...z,zk->...k", rows_view, tangent, precision=highest
    )
    return current + omega_step * smoothed.reshape(residue.shape)


def flat_update(current, sum_a, sum_b, moduli_a, moduli_b, omega_step, tangent):
    extent = tangent.shape[0]
    residue = (sum_a + sum_b) / (moduli_a + moduli_b)[..., None] - current
    rows_view = residue.reshape(residue.shape[:-1] + (residue.shape[-1] // extent, extent))
    smoothed = rows_view + penalty_mix * jnp.einsum("...z,zk->...k", rows_view, tangent, precision=highest)
    return current + omega_step * smoothed.reshape(residue.shape)


def square_update(current, sum_a, sum_b, moduli_a, moduli_b, omega_step, tangent):
    residue = (sum_a + sum_b) / (moduli_a + moduli_b)[..., None, None] - current
    smoothed = residue + penalty_mix * jnp.einsum("...z,zk->...k", residue, tangent, precision=highest)
    return current + omega_step * smoothed


def shards(forcing, modulus, orient_codes):
    extent = forcing.shape[3]
    blocks = forcing.shape[1]
    flat = extent * extent
    source_field = forcing[0]
    moduli = modulus[0]
    codes_here = orient_codes[0]
    code_values = codes_here.astype(jnp.float32)
    omegas = step_weights(ITERS)
    slab_count = lax.axis_size("blk")
    slab_index = lax.axis_index("blk")
    has_up = jnp.broadcast_to((slab_index < slab_count - 1).astype(jnp.float32), (blocks, 3))
    has_down = jnp.broadcast_to((slab_index > 0).astype(jnp.float32), (blocks, 3))
    lam_x_up = lam_x_down = lam_y = [None] * blocks
    state = [None] * blocks
    for sweep in range(ITERS + 1):
        last = sweep == ITERS
        omega = omegas[sweep - 1] if sweep > 0 else 0.0
        outs = [
            kernel_sweep(source_field[b], moduli[b], code_values[b:b + 1], state[b], emit_u=last,
                         emit_sides=not last, omega=omega, meta=sweep == 0)
            for b in range(blocks)
        ]
        if last:
            return jnp.stack([o[0] for o in outs], 0)[None]
        xh, xl, ys = (jnp.stack([o[k] for o in outs], 0) for k in range(3))
        if sweep > 0:
            lam_x_up, lam_x_down, lam_y = (jnp.stack([o[k] for o in outs], 0) for k in range(3, 6))
        upper = shifted(xl, "blk", -1)
        lower = shifted(xh, "blk", 1)
        nxt = jnp.concatenate([ys[1:], shifted_2(ys[:1], "face", -1)], 0)
        prv = jnp.concatenate([shifted_2(ys[-1:], "face", 1), ys[:-1]], 0)
        if sweep == 0:
            codes_down = lower[:, 0, 2, 0].astype(jnp.int32)
            neighbour_moduli = jnp.stack(
                [upper[:, :, 1, 0], lower[:, :, 1, 0], prv[:, :, 1, 0, 0], nxt[:, :, 1, 0, 0], has_up, has_down], 1
            )
        up_sum = orient(upper[:, :, 0], codes_here, extent)[:, :, None]
        down_sum = orient(lower[:, :, 0], codes_down, extent)[:, :, None]
        state = [
            (neighbour_moduli[b], lam_x_up[b], lam_x_down[b], lam_y[b], xh[b], xl[b], ys[b],
             up_sum[b], down_sum[b], prv[b], nxt[b])
            for b in range(blocks)
        ]


def solution(mesh):
    placed = (P("blk", "face", None, None, None), P("blk", "face", None), P("blk", "face"))
    return jax.shard_map(
        shards,
        mesh=mesh,
        in_specs=placed,
        out_specs=P("blk", "face", None, None, None),
        check_vma=False,
    )
```

```python
import functools
import math

import jax
import jax.numpy as jnp
from jax import lax
from jax.sharding import PartitionSpec as P
from jax.experimental import pallas as pl
from jax.experimental.pallas import tpu as pltpu
import numpy as np
import ml_dtypes

ITERS = 2


mass_shift = 0.02
inject_scale = 2.0
traction_mix = 0.5
penalty_mix = 0.25
lower_edge = 0.3
upper_edge = 1.5
highest = lax.Precision.HIGHEST


def shifted(shard, axis, by):
    length = lax.axis_size(axis)
    pairs = [(i, i + by) for i in range(length) if 0 <= i + by < length]
    return lax.ppermute(shard, axis, pairs)


def shifted_2(shard, axis, by):
    length = lax.axis_size(axis)
    return lax.ppermute(shard, axis, [(i, (i + by) % length) for i in range(length)])


def tables(extent):
    node_index = jnp.arange(extent, dtype=jnp.float32) + 1.0
    basis = math.sqrt(2.0 / (extent + 1)) * jnp.sin(
        math.pi * node_index[:, None] * node_index[None, :] / (extent + 1)
    )
    eigenvalues = 2.0 - 2.0 * jnp.cos(math.pi * node_index / (extent + 1))
    return (basis, eigenvalues)


def tangent_matrix(extent):
    node_index = jnp.arange(extent, dtype=jnp.int32)
    distance = jnp.abs(node_index[:, None] - node_index[None, :])
    end_rows = ((node_index == 0) | (node_index == extent - 1)).astype(jnp.float32)
    adjacent = (distance == 1).astype(jnp.float32)
    diagonal_part = (distance == 0).astype(jnp.float32) * (2.0 - end_rows[:, None])
    return adjacent - diagonal_part


def step_weights(step_count):
    midpoint = 0.5 * (upper_edge + lower_edge)
    radius = 0.5 * (upper_edge - lower_edge)
    return [
        1.0 / (midpoint + radius * math.cos(math.pi * (2 * turn_index + 1) / (2 * step_count)))
        for turn_index in range(step_count)
    ]


def divisor(moduli, eigenvalues):
    extent = eigenvalues.shape[0]
    summed = eigenvalues[:, None, None] + eigenvalues[None, :, None] + eigenvalues[None, None, :]
    scaled = moduli[..., None, None, None] * summed + mass_shift
    return scaled.reshape(moduli.shape + (extent, extent * extent))


def body_transform(field_data, basis, paired_basis):
    extent = basis.shape[0]
    full_shape = field_data.shape
    pair_width = paired_basis.shape[0]
    sectioned = jnp.einsum("ix,bcxm->bcim", basis, field_data, precision=highest)
    sectioned = sectioned.reshape(full_shape[:-1] + (full_shape[-1] // pair_width, pair_width))
    sectioned = jnp.einsum("bcxpz,kz->bcxpk", sectioned, paired_basis, precision=highest)
    sectioned = sectioned.reshape(full_shape[:-1] + (extent, extent))
    sectioned = jnp.einsum("jy,bcxyz->bcxjz", basis, sectioned, precision=highest)
    return sectioned.reshape(full_shape)


def body_solve(right_side, scale_table, basis, paired_basis):
    return body_transform(
        body_transform(right_side, basis, paired_basis) / scale_table, basis, paired_basis
    )


f32 = jnp.float32


def np_tables(n):
    g = np.float32
    idx = np.arange(n, dtype=g) + g(1.0)
    arg = (g(math.pi) * idx[:, None]) * idx[None, :] / g(n + 1)
    q = g(math.sqrt(2.0 / (n + 1))) * np.sin(arg)
    e = g(2.0) - g(2.0) * np.cos(g(math.pi) * idx / g(n + 1))
    return q.astype(g), e.astype(g)


def consts(n):
    q, e = np_tables(n)
    h = n // 2
    p4 = np.kron(np.eye(4, dtype=np.float32), q.T)
    w = np.zeros((2, 4, h, 2, 4, h), np.float32)
    qq = q.reshape(h, 2, h, 2)
    for xl in range(4):
        w[:, xl, :, :, xl, :] = np.transpose(qq, (3, 2, 1, 0))
    wy = w.reshape(8 * h, 8 * h)
    ng = n // 4
    lane_h = np.arange(8 * h) // (4 * h)
    lane_xl = (np.arange(8 * h) // h) % 4
    lane_c = np.arange(8 * h) % h
    exy = (e[4 * np.arange(ng)[:, None] + lane_xl[None, :]] + e[2 * lane_c + lane_h][None, :]).astype(np.float32)
    ez = np.ascontiguousarray(np.broadcast_to(e[:, None], (n, 8 * h))).astype(np.float32)
    return stack_left(q), stack_right(p4), stack_right(wy), exy, ez


BF = jnp.bfloat16

def np_split3(w):
    b = ml_dtypes.bfloat16
    w1 = w.astype(b)
    r1 = w - w1.astype(np.float32)
    w2 = r1.astype(b)
    w3 = (r1 - w2.astype(np.float32)).astype(b)
    return w1, w2, w3


def stack_right(w):
    w1, w2, w3 = np_split3(w)
    return np.concatenate([w1, w2, w1, w1], 0)


def stack_left(w):
    w1, w2, w3 = np_split3(w)
    return np.concatenate([w1, w2, w1, w1], 1)


def split3(d):
    d1 = d.astype(BF)
    r1 = d - d1.astype(f32)
    d2 = r1.astype(BF)
    d3 = (r1 - d2.astype(f32)).astype(BF)
    return d1, d2, d3


def sdot(d, w6):
    d1, d2, d3 = split3(d)
    return jnp.dot(jnp.concatenate([d1, d1, d2, d3], 1), w6, preferred_element_type=f32)


def sdot_left(w6, d):
    d1, d2, d3 = split3(d)
    return jnp.dot(w6, jnp.concatenate([d1, d1, d2, d3], 0), preferred_element_type=f32)


def solve_kernel(*refs, with_faces, emit_u, emit_sides, omega, zero_lam, meta):
    it = iter(refs)
    mod_ref, f_ref = next(it), next(it)
    if with_faces:
        nbm_ref = next(it)
        lxu_ref, lxd_ref, ly_ref = (None, None, None) if zero_lam else (next(it), next(it), next(it))
        sxh_ref, sxl_ref, sy_ref, rup_ref, rdn_ref, ryp_ref, ryn_ref = (next(it) for _ in range(7))
    q_ref, p_ref, wy_ref, exy_ref, ez_ref = next(it), next(it), next(it), next(it), next(it)
    code_ref = next(it)
    o_ref = next(it) if emit_u else None
    if emit_sides:
        xh_ref, xl_ref, y_ref = next(it), next(it), next(it)
    if with_faces and emit_sides:
        nlx_ref, nld_ref, nly_ref = next(it), next(it), next(it)
    elif with_faces:
        nlx_ref = nld_ref = nly_ref = None
    s_ref, z_ref = next(it), next(it)
    n = q_ref.shape[0]
    h = n // 2
    w2 = 2 * n
    w4 = 4 * n
    nn = f_ref.shape[-1]
    nch = nn // w2
    npair = nn // w4
    comp = pl.program_id(0)
    m = mod_ref[comp]
    q = q_ref[...]
    r = f_ref[0]
    if with_faces:
        m_up = nbm_ref[0, comp]
        m_dn = nbm_ref[1, comp]
        m_prev = nbm_ref[2, comp]
        m_next = nbm_ref[3, comp]
        has_up = nbm_ref[4, comp]
        has_dn = nbm_ref[5, comp]
        lane_x = lax.broadcasted_iota(jnp.int32, (1, nn), 1) % n
        lane_y = lax.broadcasted_iota(jnp.int32, (n, w2), 1)

        def smooth(res, lanes, width):
            left = pltpu.roll(res, 1, 1)
            right = pltpu.roll(res, width - 1, 1)
            left = jnp.where(lanes % n == 0, 0.0, left)
            right = jnp.where(lanes % n == n - 1, 0.0, right)
            diag = jnp.where((lanes % n == 0) | (lanes % n == n - 1), -1.0, -2.0)
            return res + 0.25 * ((left + right) + diag * res)

        xu = 0.0 if zero_lam else lxu_ref[0]
        res = (sxh_ref[0, 0:1, 0:nn] + rup_ref[0]) / (m + m_up) - xu
        xhi_face = (xu + omega * smooth(res, lane_x, nn)) * has_up
        xd = 0.0 if zero_lam else lxd_ref[0]
        res = (rdn_ref[0] + sxl_ref[0, 0:1, 0:nn]) / (m_dn + m) - xd
        xlo_face = (xd + omega * smooth(res, lane_x, nn)) * has_dn
        ly = 0.0 if zero_lam else ly_ref[0]
        lo = lane_y < n
        recv = pltpu.roll(jnp.where(lo, ryn_ref[0, 0, 0:n], ryp_ref[0, 0, 0:n]), n, 1)
        res = (sy_ref[0, 0, 0:n] + recv) / (m + jnp.where(lo, m_prev, m_next)) - ly
        yadd = ly + omega * smooth(res, lane_y, w2)
        if nlx_ref is not None:
            nlx_ref[0] = xhi_face
            nld_ref[0] = xlo_face
            nly_ref[0] = yadd
        rows = lax.broadcasted_iota(jnp.int32, (n, nn), 0)
        added = jnp.where(rows == 0, xlo_face, 0.0) + jnp.where(rows == n - 1, xhi_face, 0.0)
        lane = lane_y
        first = added[:, :w2] + jnp.where(lane < n, yadd, 0.0)
        last = added[:, nn - w2:] + jnp.where(lane >= n, yadd, 0.0)
        added = jnp.concatenate([first, added[:, w2:nn - w2], last], 1)
        r = r + (2.0 * m) * added
    a = sdot_left(q, r)
    for cp in range(npair):
        z_ref[cp * n:(cp + 1) * n, :] = a[:, cp * w4:(cp + 1) * w4]
    zo = sdot(z_ref[...], p_ref[...])
    for cp in range(npair):
        for cb in range(2):
            s_ref[(2 * cp + cb) * n:(2 * cp + cb + 1) * n, :] = zo[cp * n:(cp + 1) * n, cb * w2:(cb + 1) * w2]
    wy = wy_ref[...]
    ez = ez_ref[...]
    XG = 4
    GPI = 8

    def body(it_, carry):
        lhs = []
        for gi in range(GPI):
            g = it_ * GPI + gi
            blk = jnp.concatenate([s_ref[pl.ds(g * XG + xl, h, stride=n), :] for xl in range(XG)], 0)
            tb = blk.T
            lhs.append(jnp.concatenate([tb[:n], tb[n:]], 1))
        v = sdot(jnp.concatenate(lhs, 0), wy)
        div = jnp.concatenate([m * (exy_ref[pl.ds(it_ * GPI + gi, 1), :] + ez) + 0.02 for gi in range(GPI)], 0)
        v = v / div
        v = sdot(v, wy)
        for gi in range(GPI):
            g = it_ * GPI + gi
            vg = v[gi * n:(gi + 1) * n]
            tb = jnp.concatenate([vg[:, :w2], vg[:, w2:]], 0).T
            for xl in range(XG):
                s_ref[pl.ds(g * XG + xl, h, stride=n), :] = tb[xl * h:(xl + 1) * h]
        return carry
    lax.fori_loop(0, n // (XG * GPI), body, 0)
    for cp in range(npair):
        z_ref[cp * n:(cp + 1) * n, :] = jnp.concatenate(
            [s_ref[(2 * cp) * n:(2 * cp + 1) * n, :], s_ref[(2 * cp + 1) * n:(2 * cp + 2) * n, :]], 1)
    zo = sdot(z_ref[...], p_ref[...])
    b = jnp.concatenate([zo[cp * n:(cp + 1) * n, :] for cp in range(npair)], 1)
    u = sdot_left(q, b)
    if emit_u:
        o_ref[0] = u

    def slope(p0, p1, p2, p3):
        return m * (11.0 / 6.0 * p0 - 3.0 * p1 + 1.5 * p2 - p3 / 3.0)
    if emit_sides:
        m_row = jnp.full((1, nn), m, f32)
        xh_ref[0, 0:1, 0:nn] = m * u[n - 1:n] + 0.5 * slope(u[n - 1:n], u[n - 2:n - 1], u[n - 3:n - 2], u[n - 4:n - 3])
        lane_t = lax.broadcasted_iota(jnp.int32, (1, w2), 1)
        if meta:
            xh_ref[0, 0:1, nn:nn + w2] = jnp.where(lane_t < n, m, code_ref[0])
        xl_ref[0, 0:1, 0:nn] = m * u[0:1] + 0.5 * slope(u[0:1], u[1:2], u[2:3], u[3:4])
        if meta:
            xl_ref[0, 0:1, nn:nn + w2] = jnp.full((1, w2), m, f32)
        c_hi = u[:, nn - w2:]
        c_hi2 = u[:, nn - 2 * w2:nn - w2]
        s_hi = m * c_hi + 0.5 * slope(c_hi, pltpu.roll(c_hi, n, 1), c_hi2, pltpu.roll(c_hi2, n, 1))
        c_lo = u[:, :w2]
        c_lo2 = u[:, w2:2 * w2]
        s_lo = m * c_lo + 0.5 * slope(c_lo, pltpu.roll(c_lo, n, 1), c_lo2, pltpu.roll(c_lo2, n, 1))
        lane_s = lax.broadcasted_iota(jnp.int32, (n, w2), 1)
        y_ref[0, 0, 0:n] = jnp.where(lane_s < n, s_lo, s_hi)
        if meta:
            y_ref[0, 0, n:n + 8] = jnp.full((8, w2), m, f32)


def kernel_sweep(rhs, moduli, code, state=None, emit_u=True, emit_sides=False, omega=0.0, meta=False):
    ncomp, n, nn = rhs.shape
    q, p4, wy, exy, ez = consts(n)
    full = lambda shp: pl.BlockSpec(shp, lambda c: (0,) * len(shp))
    comp3 = lambda shp: pl.BlockSpec((1,) + shp, lambda c: (c,) + (0,) * len(shp))
    smem = pl.BlockSpec(memory_space=pltpu.SMEM)
    in_specs = [smem, comp3((n, nn))]
    args = [moduli, rhs]
    zero_lam = state is not None and state[1] is None
    if state is not None:
        if zero_lam:
            state = state[:1] + state[4:]
            in_specs += [smem]
        else:
            in_specs += [smem, comp3((1, nn)), comp3((1, nn)), comp3((n, 2 * n))]
        in_specs += [comp3(x.shape[1:]) for x in state[-7:]]
        args += list(state)
    in_specs += [full(q.shape), full(p4.shape), full(wy.shape), full(exy.shape), full(ez.shape), smem]
    args += [q, p4, wy, exy, ez, code]
    out_specs, out_shape = [], []
    if emit_u:
        out_specs.append(comp3((n, nn)))
        out_shape.append(jax.ShapeDtypeStruct(rhs.shape, f32))
    if emit_sides:
        wx, ry = (nn + 2 * n, n + 8) if meta else (nn, n)
        out_specs += [comp3((1, wx)), comp3((1, wx)), comp3((1, ry, 2 * n))]
        out_shape += [jax.ShapeDtypeStruct((ncomp, 1, wx), f32), jax.ShapeDtypeStruct((ncomp, 1, wx), f32),
                      jax.ShapeDtypeStruct((ncomp, 1, ry, 2 * n), f32)]
        if state is not None:
            out_specs += [comp3((1, nn)), comp3((1, nn)), comp3((n, 2 * n))]
            out_shape += [jax.ShapeDtypeStruct((ncomp, 1, nn), f32), jax.ShapeDtypeStruct((ncomp, 1, nn), f32),
                          jax.ShapeDtypeStruct((ncomp, n, 2 * n), f32)]
    kernel = functools.partial(solve_kernel, with_faces=state is not None, emit_u=emit_u,
                               emit_sides=emit_sides, omega=omega, zero_lam=zero_lam, meta=meta)
    return pl.pallas_call(
        kernel,
        grid=(ncomp,),
        in_specs=in_specs,
        out_specs=out_specs,
        out_shape=out_shape,
        scratch_shapes=[pltpu.VMEM((nn // 2, 2 * n), f32), pltpu.VMEM((nn // 4, 4 * n), f32)],
    )(*args)


def orient(face_field, code_table, extent):
    square = face_field.reshape(face_field.shape[:-1] + (extent, extent))
    flip_rows = (code_table % 2 == 1)[..., None, None, None]
    flip_cols = (code_table // 2 == 1)[..., None, None, None]
    square = jnp.where(flip_rows, jnp.flip(square, -2), square)
    square = jnp.where(flip_cols, jnp.flip(square, -1), square)
    return square.reshape(face_field.shape)


def face_data(solution, moduli):
    extent = solution.shape[-2]
    cube_view = solution.reshape(solution.shape[:-1] + (extent, extent))
    flat_shape = solution.shape[:-2] + (extent * extent,)

    def pack_side(planes):
        normal_slope = 11.0 / 6.0 * planes[0] - 3.0 * planes[1] + 1.5 * planes[2] - planes[3] / 3.0
        return (planes[0], moduli[..., None] * normal_slope)

    x_high = pack_side([solution[..., extent - 1 - plane_depth, :] for plane_depth in range(4)])
    x_low = pack_side([solution[..., plane_depth, :] for plane_depth in range(4)])
    y_high = pack_side(
        [
            cube_view[..., extent - 1 - plane_depth, :].reshape(flat_shape)
            for plane_depth in range(4)
        ]
    )
    y_low = pack_side(
        [cube_view[..., plane_depth, :].reshape(flat_shape) for plane_depth in range(4)]
    )
    return (x_high, x_low, y_high, y_low)


def place_faces(source_field, moduli, x_low, x_high, y_low, y_high):
    extent = source_field.shape[-2]
    added = jnp.zeros_like(source_field)
    added = added.at[..., 0, :].add(x_low)
    added = added.at[..., extent - 1, :].add(x_high)
    cube_view = added.reshape(added.shape[:-1] + (extent, extent))
    low_square = y_low.reshape(y_low.shape[:-1] + (extent, extent))
    high_square = y_high.reshape(y_high.shape[:-1] + (extent, extent))
    cube_view = cube_view.at[..., 0, :].add(low_square)
    cube_view = cube_view.at[..., extent - 1, :].add(high_square)
    added = cube_view.reshape(source_field.shape)
    return source_field + inject_scale * moduli[..., None, None] * added


def trace_update(current, side_a, side_b, moduli_a, moduli_b, omega_step, tangent):
    extent = tangent.shape[0]
    weight_a = moduli_a[..., None]
    weight_b = moduli_b[..., None]
    residue = (
        weight_a * side_a[0] + weight_b * side_b[0] + traction_mix * (side_a[1] + side_b[1])
    ) / (weight_a + weight_b) - current
    rows_view = residue.reshape(residue.shape[:-1] + (residue.shape[-1] // extent, extent))
    smoothed = rows_view + penalty_mix * jnp.einsum(
        "...z,zk->...k", rows_view, tangent, precision=highest
    )
    return current + omega_step * smoothed.reshape(residue.shape)


def flat_update(current, sum_a, sum_b, moduli_a, moduli_b, omega_step, tangent):
    extent = tangent.shape[0]
    residue = (sum_a + sum_b) / (moduli_a + moduli_b)[..., None] - current
    rows_view = residue.reshape(residue.shape[:-1] + (residue.shape[-1] // extent, extent))
    smoothed = rows_view + penalty_mix * jnp.einsum("...z,zk->...k", rows_view, tangent, precision=highest)
    return current + omega_step * smoothed.reshape(residue.shape)


def square_update(current, sum_a, sum_b, moduli_a, moduli_b, omega_step, tangent):
    residue = (sum_a + sum_b) / (moduli_a + moduli_b)[..., None, None] - current
    smoothed = residue + penalty_mix * jnp.einsum("...z,zk->...k", residue, tangent, precision=highest)
    return current + omega_step * smoothed


def shards(forcing, modulus, orient_codes):
    extent = forcing.shape[3]
    blocks = forcing.shape[1]
    flat = extent * extent
    source_field = forcing[0]
    moduli = modulus[0]
    codes_here = orient_codes[0]
    code_values = codes_here.astype(jnp.float32)
    omegas = step_weights(ITERS)
    slab_count = lax.axis_size("blk")
    slab_index = lax.axis_index("blk")
    has_up = jnp.broadcast_to((slab_index < slab_count - 1).astype(jnp.float32), (blocks, 3))
    has_down = jnp.broadcast_to((slab_index > 0).astype(jnp.float32), (blocks, 3))
    lam_x_up = lam_x_down = lam_y = [None] * blocks
    state = [None] * blocks
    for sweep in range(ITERS + 1):
        last = sweep == ITERS
        omega = omegas[sweep - 1] if sweep > 0 else 0.0
        outs = [
            kernel_sweep(source_field[b], moduli[b], code_values[b:b + 1], state[b], emit_u=last,
                         emit_sides=not last, omega=omega, meta=sweep == 0)
            for b in range(blocks)
        ]
        if last:
            return jnp.stack([o[0] for o in outs], 0)[None]
        xh, xl, ys = (jnp.stack([o[k] for o in outs], 0) for k in range(3))
        if sweep > 0:
            lam_x_up, lam_x_down, lam_y = (jnp.stack([o[k] for o in outs], 0) for k in range(3, 6))
        upper = shifted(xl, "blk", -1)
        lower = shifted(xh, "blk", 1)
        nxt = jnp.concatenate([ys[1:], shifted_2(ys[:1], "face", -1)], 0)
        prv = jnp.concatenate([shifted_2(ys[-1:], "face", 1), ys[:-1]], 0)
        if sweep == 0:
            codes_down = lower[:, 0, 0, flat + extent].astype(jnp.int32)
            neighbour_moduli = jnp.stack(
                [upper[:, :, 0, flat], lower[:, :, 0, flat], prv[:, :, 0, extent, 0], nxt[:, :, 0, extent, 0],
                 has_up, has_down], 1
            )
        up_sum = orient(upper[:, :, 0, :flat], codes_here, extent)[:, :, None]
        down_sum = orient(lower[:, :, 0, :flat], codes_down, extent)[:, :, None]
        state = [
            (neighbour_moduli[b], lam_x_up[b], lam_x_down[b], lam_y[b], xh[b], xl[b], ys[b],
             up_sum[b], down_sum[b], prv[b], nxt[b])
            for b in range(blocks)
        ]


def solution(mesh):
    placed = (P("blk", "face", None, None, None), P("blk", "face", None), P("blk", "face"))
    return jax.shard_map(
        shards,
        mesh=mesh,
        in_specs=placed,
        out_specs=P("blk", "face", None, None, None),
        check_vma=False,
    )
```

```python
import functools
import math

import jax
import jax.numpy as jnp
from jax import lax
from jax.sharding import PartitionSpec as P
from jax.experimental import pallas as pl
from jax.experimental.pallas import tpu as pltpu
import numpy as np
import ml_dtypes

ITERS = 2


mass_shift = 0.02
inject_scale = 2.0
traction_mix = 0.5
penalty_mix = 0.25
lower_edge = 0.3
upper_edge = 1.5
highest = lax.Precision.HIGHEST


def shifted(shard, axis, by):
    length = lax.axis_size(axis)
    pairs = [(i, i + by) for i in range(length) if 0 <= i + by < length]
    return lax.ppermute(shard, axis, pairs)


def shifted_2(shard, axis, by):
    length = lax.axis_size(axis)
    return lax.ppermute(shard, axis, [(i, (i + by) % length) for i in range(length)])


def tables(extent):
    node_index = jnp.arange(extent, dtype=jnp.float32) + 1.0
    basis = math.sqrt(2.0 / (extent + 1)) * jnp.sin(
        math.pi * node_index[:, None] * node_index[None, :] / (extent + 1)
    )
    eigenvalues = 2.0 - 2.0 * jnp.cos(math.pi * node_index / (extent + 1))
    return (basis, eigenvalues)


def tangent_matrix(extent):
    node_index = jnp.arange(extent, dtype=jnp.int32)
    distance = jnp.abs(node_index[:, None] - node_index[None, :])
    end_rows = ((node_index == 0) | (node_index == extent - 1)).astype(jnp.float32)
    adjacent = (distance == 1).astype(jnp.float32)
    diagonal_part = (distance == 0).astype(jnp.float32) * (2.0 - end_rows[:, None])
    return adjacent - diagonal_part


def step_weights(step_count):
    midpoint = 0.5 * (upper_edge + lower_edge)
    radius = 0.5 * (upper_edge - lower_edge)
    return [
        1.0 / (midpoint + radius * math.cos(math.pi * (2 * turn_index + 1) / (2 * step_count)))
        for turn_index in range(step_count)
    ]


def divisor(moduli, eigenvalues):
    extent = eigenvalues.shape[0]
    summed = eigenvalues[:, None, None] + eigenvalues[None, :, None] + eigenvalues[None, None, :]
    scaled = moduli[..., None, None, None] * summed + mass_shift
    return scaled.reshape(moduli.shape + (extent, extent * extent))


def body_transform(field_data, basis, paired_basis):
    extent = basis.shape[0]
    full_shape = field_data.shape
    pair_width = paired_basis.shape[0]
    sectioned = jnp.einsum("ix,bcxm->bcim", basis, field_data, precision=highest)
    sectioned = sectioned.reshape(full_shape[:-1] + (full_shape[-1] // pair_width, pair_width))
    sectioned = jnp.einsum("bcxpz,kz->bcxpk", sectioned, paired_basis, precision=highest)
    sectioned = sectioned.reshape(full_shape[:-1] + (extent, extent))
    sectioned = jnp.einsum("jy,bcxyz->bcxjz", basis, sectioned, precision=highest)
    return sectioned.reshape(full_shape)


def body_solve(right_side, scale_table, basis, paired_basis):
    return body_transform(
        body_transform(right_side, basis, paired_basis) / scale_table, basis, paired_basis
    )


f32 = jnp.float32


def np_tables(n):
    g = np.float32
    idx = np.arange(n, dtype=g) + g(1.0)
    arg = (g(math.pi) * idx[:, None]) * idx[None, :] / g(n + 1)
    q = g(math.sqrt(2.0 / (n + 1))) * np.sin(arg)
    e = g(2.0) - g(2.0) * np.cos(g(math.pi) * idx / g(n + 1))
    return q.astype(g), e.astype(g)


def consts(n):
    q, e = np_tables(n)
    h = n // 2
    p4 = np.kron(np.eye(4, dtype=np.float32), q.T)
    w = np.zeros((2, 4, h, 2, 4, h), np.float32)
    qq = q.reshape(h, 2, h, 2)
    for xl in range(4):
        w[:, xl, :, :, xl, :] = np.transpose(qq, (3, 2, 1, 0))
    wy = w.reshape(8 * h, 8 * h)
    ng = n // 4
    lane_h = np.arange(8 * h) // (4 * h)
    lane_xl = (np.arange(8 * h) // h) % 4
    lane_c = np.arange(8 * h) % h
    exy = (e[4 * np.arange(ng)[:, None] + lane_xl[None, :]] + e[2 * lane_c + lane_h][None, :]).astype(np.float32)
    ez = np.ascontiguousarray(np.broadcast_to(e[:, None], (n, 8 * h))).astype(np.float32)
    return stack_left(q), stack_right(p4), stack_right(wy), exy, ez


BF = jnp.bfloat16

def np_split3(w):
    b = ml_dtypes.bfloat16
    w1 = w.astype(b)
    r1 = w - w1.astype(np.float32)
    w2 = r1.astype(b)
    w3 = (r1 - w2.astype(np.float32)).astype(b)
    return w1, w2, w3


def stack_right(w):
    w1, w2, w3 = np_split3(w)
    return np.concatenate([w1, w2, w1, w1], 0)


def stack_left(w):
    w1, w2, w3 = np_split3(w)
    return np.concatenate([w1, w2, w1, w1], 1)


def split3(d):
    d1 = d.astype(BF)
    r1 = d - d1.astype(f32)
    d2 = r1.astype(BF)
    d3 = (r1 - d2.astype(f32)).astype(BF)
    return d1, d2, d3


def sdot(d, w6):
    d1, d2, d3 = split3(d)
    return jnp.dot(jnp.concatenate([d1, d1, d2, d3], 1), w6, preferred_element_type=f32)


def sdot_left(w6, d):
    d1, d2, d3 = split3(d)
    return jnp.dot(w6, jnp.concatenate([d1, d1, d2, d3], 0), preferred_element_type=f32)


def solve_kernel(*refs, with_faces, emit_u, emit_sides, omega, zero_lam, meta):
    it = iter(refs)
    mod_ref, f_ref = next(it), next(it)
    if with_faces:
        nbm_ref = next(it)
        lxu_ref, lxd_ref, ly_ref = (None, None, None) if zero_lam else (next(it), next(it), next(it))
        sxh_ref, sxl_ref, sylo_ref, syhi_ref, rup_ref, rdn_ref, ryp_ref, ryn_ref = (next(it) for _ in range(8))
    q_ref, p_ref, wy_ref, exy_ref, ez_ref = next(it), next(it), next(it), next(it), next(it)
    code_ref = next(it)
    o_ref = next(it) if emit_u else None
    if emit_sides:
        xh_ref, xl_ref, ylo_ref, yhi_ref = next(it), next(it), next(it), next(it)
    if with_faces and emit_sides:
        nlx_ref, nld_ref, nly_ref = next(it), next(it), next(it)
    elif with_faces:
        nlx_ref = nld_ref = nly_ref = None
    s_ref, z_ref = next(it), next(it)
    n = q_ref.shape[0]
    h = n // 2
    w2 = 2 * n
    w4 = 4 * n
    nn = f_ref.shape[-1]
    nch = nn // w2
    npair = nn // w4
    comp = pl.program_id(0)
    m = mod_ref[comp]
    q = q_ref[...]
    r = f_ref[0]
    if with_faces:
        m_up = nbm_ref[0, comp]
        m_dn = nbm_ref[1, comp]
        m_prev = nbm_ref[2, comp]
        m_next = nbm_ref[3, comp]
        has_up = nbm_ref[4, comp]
        has_dn = nbm_ref[5, comp]
        lane_x = lax.broadcasted_iota(jnp.int32, (1, nn), 1) % n
        lane_y = lax.broadcasted_iota(jnp.int32, (n, w2), 1)

        def smooth(res, lanes, width):
            left = pltpu.roll(res, 1, 1)
            right = pltpu.roll(res, width - 1, 1)
            left = jnp.where(lanes % n == 0, 0.0, left)
            right = jnp.where(lanes % n == n - 1, 0.0, right)
            diag = jnp.where((lanes % n == 0) | (lanes % n == n - 1), -1.0, -2.0)
            return res + 0.25 * ((left + right) + diag * res)

        xu = 0.0 if zero_lam else lxu_ref[0]
        res = (sxh_ref[0, 0:1, 0:nn] + rup_ref[0]) / (m + m_up) - xu
        xhi_face = (xu + omega * smooth(res, lane_x, nn)) * has_up
        xd = 0.0 if zero_lam else lxd_ref[0]
        res = (rdn_ref[0] + sxl_ref[0, 0:1, 0:nn]) / (m_dn + m) - xd
        xlo_face = (xd + omega * smooth(res, lane_x, nn)) * has_dn
        ly = 0.0 if zero_lam else ly_ref[0]
        lo = lane_y < n
        recv = jnp.concatenate([ryp_ref[0, 0, 0:n], ryn_ref[0, 0, 0:n]], 1)
        own = jnp.concatenate([sylo_ref[0, 0, 0:n], syhi_ref[0, 0, 0:n]], 1)
        res = (own + recv) / (m + jnp.where(lo, m_prev, m_next)) - ly
        yadd = ly + omega * smooth(res, lane_y, w2)
        if nlx_ref is not None:
            nlx_ref[0] = xhi_face
            nld_ref[0] = xlo_face
            nly_ref[0] = yadd
        rows = lax.broadcasted_iota(jnp.int32, (n, nn), 0)
        added = jnp.where(rows == 0, xlo_face, 0.0) + jnp.where(rows == n - 1, xhi_face, 0.0)
        lane = lane_y
        first = added[:, :w2] + jnp.where(lane < n, yadd, 0.0)
        last = added[:, nn - w2:] + jnp.where(lane >= n, yadd, 0.0)
        added = jnp.concatenate([first, added[:, w2:nn - w2], last], 1)
        r = r + (2.0 * m) * added
    a = sdot_left(q, r)
    for cp in range(npair):
        z_ref[cp * n:(cp + 1) * n, :] = a[:, cp * w4:(cp + 1) * w4]
    zo = sdot(z_ref[...], p_ref[...])
    for cp in range(npair):
        for cb in range(2):
            s_ref[(2 * cp + cb) * n:(2 * cp + cb + 1) * n, :] = zo[cp * n:(cp + 1) * n, cb * w2:(cb + 1) * w2]
    wy = wy_ref[...]
    ez = ez_ref[...]
    XG = 4
    GPI = 8

    def body(it_, carry):
        lhs = []
        for gi in range(GPI):
            g = it_ * GPI + gi
            blk = jnp.concatenate([s_ref[pl.ds(g * XG + xl, h, stride=n), :] for xl in range(XG)], 0)
            tb = blk.T
            lhs.append(jnp.concatenate([tb[:n], tb[n:]], 1))
        v = sdot(jnp.concatenate(lhs, 0), wy)
        div = jnp.concatenate([m * (exy_ref[pl.ds(it_ * GPI + gi, 1), :] + ez) + 0.02 for gi in range(GPI)], 0)
        v = v / div
        v = sdot(v, wy)
        for gi in range(GPI):
            g = it_ * GPI + gi
            vg = v[gi * n:(gi + 1) * n]
            tb = jnp.concatenate([vg[:, :w2], vg[:, w2:]], 0).T
            for xl in range(XG):
                s_ref[pl.ds(g * XG + xl, h, stride=n), :] = tb[xl * h:(xl + 1) * h]
        return carry
    lax.fori_loop(0, n // (XG * GPI), body, 0)
    for cp in range(npair):
        z_ref[cp * n:(cp + 1) * n, :] = jnp.concatenate(
            [s_ref[(2 * cp) * n:(2 * cp + 1) * n, :], s_ref[(2 * cp + 1) * n:(2 * cp + 2) * n, :]], 1)
    zo = sdot(z_ref[...], p_ref[...])
    b = jnp.concatenate([zo[cp * n:(cp + 1) * n, :] for cp in range(npair)], 1)
    u = sdot_left(q, b)
    if emit_u:
        o_ref[0] = u

    def slope(p0, p1, p2, p3):
        return m * (11.0 / 6.0 * p0 - 3.0 * p1 + 1.5 * p2 - p3 / 3.0)
    if emit_sides:
        m_row = jnp.full((1, nn), m, f32)
        xh_ref[0, 0:1, 0:nn] = m * u[n - 1:n] + 0.5 * slope(u[n - 1:n], u[n - 2:n - 1], u[n - 3:n - 2], u[n - 4:n - 3])
        lane_t = lax.broadcasted_iota(jnp.int32, (1, w2), 1)
        if meta:
            xh_ref[0, 0:1, nn:nn + w2] = jnp.where(lane_t < n, m, code_ref[0])
        xl_ref[0, 0:1, 0:nn] = m * u[0:1] + 0.5 * slope(u[0:1], u[1:2], u[2:3], u[3:4])
        if meta:
            xl_ref[0, 0:1, nn:nn + w2] = jnp.full((1, w2), m, f32)
        c_hi = u[:, nn - w2:]
        c_hi2 = u[:, nn - 2 * w2:nn - w2]
        s_hi = m * c_hi + 0.5 * slope(c_hi, pltpu.roll(c_hi, n, 1), c_hi2, pltpu.roll(c_hi2, n, 1))
        c_lo = u[:, :w2]
        c_lo2 = u[:, w2:2 * w2]
        s_lo = m * c_lo + 0.5 * slope(c_lo, pltpu.roll(c_lo, n, 1), c_lo2, pltpu.roll(c_lo2, n, 1))
        lane_s = lax.broadcasted_iota(jnp.int32, (n, w2), 1)
        ylo_ref[0, 0, 0:n] = s_lo[:, :n]
        yhi_ref[0, 0, 0:n] = pltpu.roll(s_hi, n, 1)[:, :n]
        if meta:
            ylo_ref[0, 0, n:n + 8] = jnp.full((8, n), m, f32)
            yhi_ref[0, 0, n:n + 8] = jnp.full((8, n), m, f32)


def kernel_sweep(rhs, moduli, code, state=None, emit_u=True, emit_sides=False, omega=0.0, meta=False):
    ncomp, n, nn = rhs.shape
    q, p4, wy, exy, ez = consts(n)
    full = lambda shp: pl.BlockSpec(shp, lambda c: (0,) * len(shp))
    comp3 = lambda shp: pl.BlockSpec((1,) + shp, lambda c: (c,) + (0,) * len(shp))
    smem = pl.BlockSpec(memory_space=pltpu.SMEM)
    in_specs = [smem, comp3((n, nn))]
    args = [moduli, rhs]
    zero_lam = state is not None and state[1] is None
    if state is not None:
        if zero_lam:
            state = state[:1] + state[4:]
            in_specs += [smem]
        else:
            in_specs += [smem, comp3((1, nn)), comp3((1, nn)), comp3((n, 2 * n))]
        in_specs += [comp3(x.shape[1:]) for x in state[-8:]]
        args += list(state)
    in_specs += [full(q.shape), full(p4.shape), full(wy.shape), full(exy.shape), full(ez.shape), smem]
    args += [q, p4, wy, exy, ez, code]
    out_specs, out_shape = [], []
    if emit_u:
        out_specs.append(comp3((n, nn)))
        out_shape.append(jax.ShapeDtypeStruct(rhs.shape, f32))
    if emit_sides:
        wx, ry = (nn + 2 * n, n + 8) if meta else (nn, n)
        out_specs += [comp3((1, wx)), comp3((1, wx)), comp3((1, ry, n)), comp3((1, ry, n))]
        out_shape += [jax.ShapeDtypeStruct((ncomp, 1, wx), f32), jax.ShapeDtypeStruct((ncomp, 1, wx), f32),
                      jax.ShapeDtypeStruct((ncomp, 1, ry, n), f32), jax.ShapeDtypeStruct((ncomp, 1, ry, n), f32)]
        if state is not None:
            out_specs += [comp3((1, nn)), comp3((1, nn)), comp3((n, 2 * n))]
            out_shape += [jax.ShapeDtypeStruct((ncomp, 1, nn), f32), jax.ShapeDtypeStruct((ncomp, 1, nn), f32),
                          jax.ShapeDtypeStruct((ncomp, n, 2 * n), f32)]
    kernel = functools.partial(solve_kernel, with_faces=state is not None, emit_u=emit_u,
                               emit_sides=emit_sides, omega=omega, zero_lam=zero_lam, meta=meta)
    return pl.pallas_call(
        kernel,
        grid=(ncomp,),
        in_specs=in_specs,
        out_specs=out_specs,
        out_shape=out_shape,
        scratch_shapes=[pltpu.VMEM((nn // 2, 2 * n), f32), pltpu.VMEM((nn // 4, 4 * n), f32)],
    )(*args)


def orient(face_field, code_table, extent):
    square = face_field.reshape(face_field.shape[:-1] + (extent, extent))
    flip_rows = (code_table % 2 == 1)[..., None, None, None]
    flip_cols = (code_table // 2 == 1)[..., None, None, None]
    square = jnp.where(flip_rows, jnp.flip(square, -2), square)
    square = jnp.where(flip_cols, jnp.flip(square, -1), square)
    return square.reshape(face_field.shape)


def face_data(solution, moduli):
    extent = solution.shape[-2]
    cube_view = solution.reshape(solution.shape[:-1] + (extent, extent))
    flat_shape = solution.shape[:-2] + (extent * extent,)

    def pack_side(planes):
        normal_slope = 11.0 / 6.0 * planes[0] - 3.0 * planes[1] + 1.5 * planes[2] - planes[3] / 3.0
        return (planes[0], moduli[..., None] * normal_slope)

    x_high = pack_side([solution[..., extent - 1 - plane_depth, :] for plane_depth in range(4)])
    x_low = pack_side([solution[..., plane_depth, :] for plane_depth in range(4)])
    y_high = pack_side(
        [
            cube_view[..., extent - 1 - plane_depth, :].reshape(flat_shape)
            for plane_depth in range(4)
        ]
    )
    y_low = pack_side(
        [cube_view[..., plane_depth, :].reshape(flat_shape) for plane_depth in range(4)]
    )
    return (x_high, x_low, y_high, y_low)


def place_faces(source_field, moduli, x_low, x_high, y_low, y_high):
    extent = source_field.shape[-2]
    added = jnp.zeros_like(source_field)
    added = added.at[..., 0, :].add(x_low)
    added = added.at[..., extent - 1, :].add(x_high)
    cube_view = added.reshape(added.shape[:-1] + (extent, extent))
    low_square = y_low.reshape(y_low.shape[:-1] + (extent, extent))
    high_square = y_high.reshape(y_high.shape[:-1] + (extent, extent))
    cube_view = cube_view.at[..., 0, :].add(low_square)
    cube_view = cube_view.at[..., extent - 1, :].add(high_square)
    added = cube_view.reshape(source_field.shape)
    return source_field + inject_scale * moduli[..., None, None] * added


def trace_update(current, side_a, side_b, moduli_a, moduli_b, omega_step, tangent):
    extent = tangent.shape[0]
    weight_a = moduli_a[..., None]
    weight_b = moduli_b[..., None]
    residue = (
        weight_a * side_a[0] + weight_b * side_b[0] + traction_mix * (side_a[1] + side_b[1])
    ) / (weight_a + weight_b) - current
    rows_view = residue.reshape(residue.shape[:-1] + (residue.shape[-1] // extent, extent))
    smoothed = rows_view + penalty_mix * jnp.einsum(
        "...z,zk->...k", rows_view, tangent, precision=highest
    )
    return current + omega_step * smoothed.reshape(residue.shape)


def flat_update(current, sum_a, sum_b, moduli_a, moduli_b, omega_step, tangent):
    extent = tangent.shape[0]
    residue = (sum_a + sum_b) / (moduli_a + moduli_b)[..., None] - current
    rows_view = residue.reshape(residue.shape[:-1] + (residue.shape[-1] // extent, extent))
    smoothed = rows_view + penalty_mix * jnp.einsum("...z,zk->...k", rows_view, tangent, precision=highest)
    return current + omega_step * smoothed.reshape(residue.shape)


def square_update(current, sum_a, sum_b, moduli_a, moduli_b, omega_step, tangent):
    residue = (sum_a + sum_b) / (moduli_a + moduli_b)[..., None, None] - current
    smoothed = residue + penalty_mix * jnp.einsum("...z,zk->...k", residue, tangent, precision=highest)
    return current + omega_step * smoothed


def shards(forcing, modulus, orient_codes):
    extent = forcing.shape[3]
    blocks = forcing.shape[1]
    flat = extent * extent
    source_field = forcing[0]
    moduli = modulus[0]
    codes_here = orient_codes[0]
    code_values = codes_here.astype(jnp.float32)
    omegas = step_weights(ITERS)
    slab_count = lax.axis_size("blk")
    slab_index = lax.axis_index("blk")
    has_up = jnp.broadcast_to((slab_index < slab_count - 1).astype(jnp.float32), (blocks, 3))
    has_down = jnp.broadcast_to((slab_index > 0).astype(jnp.float32), (blocks, 3))
    lam_x_up = lam_x_down = lam_y = [None] * blocks
    state = [None] * blocks
    for sweep in range(ITERS + 1):
        last = sweep == ITERS
        omega = omegas[sweep - 1] if sweep > 0 else 0.0
        outs = [
            kernel_sweep(source_field[b], moduli[b], code_values[b:b + 1], state[b], emit_u=last,
                         emit_sides=not last, omega=omega, meta=sweep == 0)
            for b in range(blocks)
        ]
        if last:
            return jnp.stack([o[0] for o in outs], 0)[None]
        xh, xl, ylo, yhi = (jnp.stack([o[k] for o in outs], 0) for k in range(4))
        if sweep > 0:
            lam_x_up, lam_x_down, lam_y = (jnp.stack([o[k] for o in outs], 0) for k in range(4, 7))
        upper = shifted(xl, "blk", -1)
        lower = shifted(xh, "blk", 1)
        nxt = jnp.concatenate([ylo[1:], shifted_2(ylo[:1], "face", -1)], 0)
        prv = jnp.concatenate([shifted_2(yhi[-1:], "face", 1), yhi[:-1]], 0)
        if sweep == 0:
            codes_down = lower[:, 0, 0, flat + extent].astype(jnp.int32)
            neighbour_moduli = jnp.stack(
                [upper[:, :, 0, flat], lower[:, :, 0, flat], prv[:, :, 0, extent, 0], nxt[:, :, 0, extent, 0],
                 has_up, has_down], 1
            )
        up_sum = orient(upper[:, :, 0, :flat], codes_here, extent)[:, :, None]
        down_sum = orient(lower[:, :, 0, :flat], codes_down, extent)[:, :, None]
        state = [
            (neighbour_moduli[b], lam_x_up[b], lam_x_down[b], lam_y[b], xh[b], xl[b], ylo[b], yhi[b],
             up_sum[b], down_sum[b], prv[b], nxt[b])
            for b in range(blocks)
        ]


def solution(mesh):
    placed = (P("blk", "face", None, None, None), P("blk", "face", None), P("blk", "face"))
    return jax.shard_map(
        shards,
        mesh=mesh,
        in_specs=placed,
        out_specs=P("blk", "face", None, None, None),
        check_vma=False,
    )
```

```python
import functools
import math

import jax
import jax.numpy as jnp
from jax import lax
from jax.sharding import PartitionSpec as P
from jax.experimental import pallas as pl
from jax.experimental.pallas import tpu as pltpu
import numpy as np
import ml_dtypes

ITERS = 2


mass_shift = 0.02
inject_scale = 2.0
traction_mix = 0.5
penalty_mix = 0.25
lower_edge = 0.3
upper_edge = 1.5
highest = lax.Precision.HIGHEST


def shifted(shard, axis, by):
    length = lax.axis_size(axis)
    pairs = [(i, i + by) for i in range(length) if 0 <= i + by < length]
    return lax.ppermute(shard, axis, pairs)


def shifted_2(shard, axis, by):
    length = lax.axis_size(axis)
    return lax.ppermute(shard, axis, [(i, (i + by) % length) for i in range(length)])


def tables(extent):
    node_index = jnp.arange(extent, dtype=jnp.float32) + 1.0
    basis = math.sqrt(2.0 / (extent + 1)) * jnp.sin(
        math.pi * node_index[:, None] * node_index[None, :] / (extent + 1)
    )
    eigenvalues = 2.0 - 2.0 * jnp.cos(math.pi * node_index / (extent + 1))
    return (basis, eigenvalues)


def tangent_matrix(extent):
    node_index = jnp.arange(extent, dtype=jnp.int32)
    distance = jnp.abs(node_index[:, None] - node_index[None, :])
    end_rows = ((node_index == 0) | (node_index == extent - 1)).astype(jnp.float32)
    adjacent = (distance == 1).astype(jnp.float32)
    diagonal_part = (distance == 0).astype(jnp.float32) * (2.0 - end_rows[:, None])
    return adjacent - diagonal_part


def step_weights(step_count):
    midpoint = 0.5 * (upper_edge + lower_edge)
    radius = 0.5 * (upper_edge - lower_edge)
    return [
        1.0 / (midpoint + radius * math.cos(math.pi * (2 * turn_index + 1) / (2 * step_count)))
        for turn_index in range(step_count)
    ]


def divisor(moduli, eigenvalues):
    extent = eigenvalues.shape[0]
    summed = eigenvalues[:, None, None] + eigenvalues[None, :, None] + eigenvalues[None, None, :]
    scaled = moduli[..., None, None, None] * summed + mass_shift
    return scaled.reshape(moduli.shape + (extent, extent * extent))


def body_transform(field_data, basis, paired_basis):
    extent = basis.shape[0]
    full_shape = field_data.shape
    pair_width = paired_basis.shape[0]
    sectioned = jnp.einsum("ix,bcxm->bcim", basis, field_data, precision=highest)
    sectioned = sectioned.reshape(full_shape[:-1] + (full_shape[-1] // pair_width, pair_width))
    sectioned = jnp.einsum("bcxpz,kz->bcxpk", sectioned, paired_basis, precision=highest)
    sectioned = sectioned.reshape(full_shape[:-1] + (extent, extent))
    sectioned = jnp.einsum("jy,bcxyz->bcxjz", basis, sectioned, precision=highest)
    return sectioned.reshape(full_shape)


def body_solve(right_side, scale_table, basis, paired_basis):
    return body_transform(
        body_transform(right_side, basis, paired_basis) / scale_table, basis, paired_basis
    )


f32 = jnp.float32


def np_tables(n):
    g = np.float32
    idx = np.arange(n, dtype=g) + g(1.0)
    arg = (g(math.pi) * idx[:, None]) * idx[None, :] / g(n + 1)
    q = g(math.sqrt(2.0 / (n + 1))) * np.sin(arg)
    e = g(2.0) - g(2.0) * np.cos(g(math.pi) * idx / g(n + 1))
    return q.astype(g), e.astype(g)


def consts(n):
    q, e = np_tables(n)
    h = n // 2
    p4 = np.kron(np.eye(4, dtype=np.float32), q.T)
    w = np.zeros((2, 4, h, 2, 4, h), np.float32)
    qq = q.reshape(h, 2, h, 2)
    for xl in range(4):
        w[:, xl, :, :, xl, :] = np.transpose(qq, (3, 2, 1, 0))
    wy = w.reshape(8 * h, 8 * h)
    ng = n // 4
    lane_h = np.arange(8 * h) // (4 * h)
    lane_xl = (np.arange(8 * h) // h) % 4
    lane_c = np.arange(8 * h) % h
    exy = (e[4 * np.arange(ng)[:, None] + lane_xl[None, :]] + e[2 * lane_c + lane_h][None, :]).astype(np.float32)
    ez = np.ascontiguousarray(np.broadcast_to(e[:, None], (n, 8 * h))).astype(np.float32)
    return stack_left(q), stack_right(p4), stack_right(wy), exy, ez


BF = jnp.bfloat16

def np_split3(w):
    b = ml_dtypes.bfloat16
    w1 = w.astype(b)
    r1 = w - w1.astype(np.float32)
    w2 = r1.astype(b)
    w3 = (r1 - w2.astype(np.float32)).astype(b)
    return w1, w2, w3


def stack_right(w):
    w1, w2, w3 = np_split3(w)
    return np.concatenate([w1, w2, w1, w1], 0)


def stack_left(w):
    w1, w2, w3 = np_split3(w)
    return np.concatenate([w1, w2, w1, w1], 1)


def split3(d):
    d1 = d.astype(BF)
    r1 = d - d1.astype(f32)
    d2 = r1.astype(BF)
    d3 = (r1 - d2.astype(f32)).astype(BF)
    return d1, d2, d3


def sdot(d, w6):
    d1, d2, d3 = split3(d)
    return jnp.dot(jnp.concatenate([d1, d1, d2, d3], 1), w6, preferred_element_type=f32)


def sdot_left(w6, d):
    d1, d2, d3 = split3(d)
    return jnp.dot(w6, jnp.concatenate([d1, d1, d2, d3], 0), preferred_element_type=f32)


def solve_kernel(*refs, with_faces, emit_u, emit_sides, omega, zero_lam, meta):
    it = iter(refs)
    mod_ref, f_ref = next(it), next(it)
    if with_faces:
        nbm_ref = next(it)
        lxu_ref, lxd_ref, ly_ref = (None, None, None) if zero_lam else (next(it), next(it), next(it))
        sxh_ref, sxl_ref, sylo_ref, syhi_ref, rup_ref, rdn_ref, ryp_ref, ryn_ref = (next(it) for _ in range(8))
    q_ref, p_ref, wy_ref, exy_ref, ez_ref = next(it), next(it), next(it), next(it), next(it)
    code_ref = next(it)
    o_ref = next(it) if emit_u else None
    if emit_sides:
        xh_ref, xl_ref, ylo_ref, yhi_ref = next(it), next(it), next(it), next(it)
    if with_faces and emit_sides:
        nlx_ref, nld_ref, nly_ref = next(it), next(it), next(it)
    elif with_faces:
        nlx_ref = nld_ref = nly_ref = None
    s_ref, z_ref = next(it), next(it)
    n = q_ref.shape[0]
    h = n // 2
    w2 = 2 * n
    w4 = 4 * n
    nn = f_ref.shape[-1]
    nch = nn // w2
    npair = nn // w4
    comp = pl.program_id(0)
    m = mod_ref[comp]
    q = q_ref[...]
    r = f_ref[0]
    if with_faces:
        m_up = nbm_ref[0, comp]
        m_dn = nbm_ref[1, comp]
        m_prev = nbm_ref[2, comp]
        m_next = nbm_ref[3, comp]
        has_up = nbm_ref[4, comp]
        has_dn = nbm_ref[5, comp]
        lane_x = lax.broadcasted_iota(jnp.int32, (1, nn), 1) % n
        lane_y = lax.broadcasted_iota(jnp.int32, (n, w2), 1)

        def smooth(res, lanes, width):
            left = pltpu.roll(res, 1, 1)
            right = pltpu.roll(res, width - 1, 1)
            left = jnp.where(lanes % n == 0, 0.0, left)
            right = jnp.where(lanes % n == n - 1, 0.0, right)
            diag = jnp.where((lanes % n == 0) | (lanes % n == n - 1), -1.0, -2.0)
            return res + 0.25 * ((left + right) + diag * res)

        xu = 0.0 if zero_lam else lxu_ref[0]
        res = (sxh_ref[0, 0:1, 0:nn] + rup_ref[0]) / (m + m_up) - xu
        xhi_face = (xu + omega * smooth(res, lane_x, nn)) * has_up
        xd = 0.0 if zero_lam else lxd_ref[0]
        res = (rdn_ref[0] + sxl_ref[0, 0:1, 0:nn]) / (m_dn + m) - xd
        xlo_face = (xd + omega * smooth(res, lane_x, nn)) * has_dn
        ly = 0.0 if zero_lam else ly_ref[0]
        lo = lane_y < n
        recv = jnp.concatenate([ryp_ref[0, 0:n], ryn_ref[0, 0:n]], 1)
        own = jnp.concatenate([sylo_ref[0, 0:n], syhi_ref[0, 0:n]], 1)
        res = (own + recv) / (m + jnp.where(lo, m_prev, m_next)) - ly
        yadd = ly + omega * smooth(res, lane_y, w2)
        if nlx_ref is not None:
            nlx_ref[0] = xhi_face
            nld_ref[0] = xlo_face
            nly_ref[0] = yadd
        rows = lax.broadcasted_iota(jnp.int32, (n, nn), 0)
        added = jnp.where(rows == 0, xlo_face, 0.0) + jnp.where(rows == n - 1, xhi_face, 0.0)
        lane = lane_y
        first = added[:, :w2] + jnp.where(lane < n, yadd, 0.0)
        last = added[:, nn - w2:] + jnp.where(lane >= n, yadd, 0.0)
        added = jnp.concatenate([first, added[:, w2:nn - w2], last], 1)
        r = r + (2.0 * m) * added
    a = sdot_left(q, r)
    for cp in range(npair):
        z_ref[cp * n:(cp + 1) * n, :] = a[:, cp * w4:(cp + 1) * w4]
    zo = sdot(z_ref[...], p_ref[...])
    for cp in range(npair):
        for cb in range(2):
            s_ref[(2 * cp + cb) * n:(2 * cp + cb + 1) * n, :] = zo[cp * n:(cp + 1) * n, cb * w2:(cb + 1) * w2]
    wy = wy_ref[...]
    ez = ez_ref[...]
    XG = 4
    GPI = 8

    def body(it_, carry):
        lhs = []
        for gi in range(GPI):
            g = it_ * GPI + gi
            blk = jnp.concatenate([s_ref[pl.ds(g * XG + xl, h, stride=n), :] for xl in range(XG)], 0)
            tb = blk.T
            lhs.append(jnp.concatenate([tb[:n], tb[n:]], 1))
        v = sdot(jnp.concatenate(lhs, 0), wy)
        div = jnp.concatenate([m * (exy_ref[pl.ds(it_ * GPI + gi, 1), :] + ez) + 0.02 for gi in range(GPI)], 0)
        v = v / div
        v = sdot(v, wy)
        for gi in range(GPI):
            g = it_ * GPI + gi
            vg = v[gi * n:(gi + 1) * n]
            tb = jnp.concatenate([vg[:, :w2], vg[:, w2:]], 0).T
            for xl in range(XG):
                s_ref[pl.ds(g * XG + xl, h, stride=n), :] = tb[xl * h:(xl + 1) * h]
        return carry
    lax.fori_loop(0, n // (XG * GPI), body, 0)
    for cp in range(npair):
        z_ref[cp * n:(cp + 1) * n, :] = jnp.concatenate(
            [s_ref[(2 * cp) * n:(2 * cp + 1) * n, :], s_ref[(2 * cp + 1) * n:(2 * cp + 2) * n, :]], 1)
    zo = sdot(z_ref[...], p_ref[...])
    b = jnp.concatenate([zo[cp * n:(cp + 1) * n, :] for cp in range(npair)], 1)
    u = sdot_left(q, b)
    if emit_u:
        o_ref[0] = u

    def slope(p0, p1, p2, p3):
        return m * (11.0 / 6.0 * p0 - 3.0 * p1 + 1.5 * p2 - p3 / 3.0)
    if emit_sides:
        m_row = jnp.full((1, nn), m, f32)
        xh_ref[0, 0:1, 0:nn] = m * u[n - 1:n] + 0.5 * slope(u[n - 1:n], u[n - 2:n - 1], u[n - 3:n - 2], u[n - 4:n - 3])
        lane_t = lax.broadcasted_iota(jnp.int32, (1, w2), 1)
        if meta:
            xh_ref[0, 0:1, nn:nn + w2] = jnp.where(lane_t < n, m, code_ref[0])
        xl_ref[0, 0:1, 0:nn] = m * u[0:1] + 0.5 * slope(u[0:1], u[1:2], u[2:3], u[3:4])
        if meta:
            xl_ref[0, 0:1, nn:nn + w2] = jnp.full((1, w2), m, f32)
        c_hi = u[:, nn - w2:]
        c_hi2 = u[:, nn - 2 * w2:nn - w2]
        s_hi = m * c_hi + 0.5 * slope(c_hi, pltpu.roll(c_hi, n, 1), c_hi2, pltpu.roll(c_hi2, n, 1))
        c_lo = u[:, :w2]
        c_lo2 = u[:, w2:2 * w2]
        s_lo = m * c_lo + 0.5 * slope(c_lo, pltpu.roll(c_lo, n, 1), c_lo2, pltpu.roll(c_lo2, n, 1))
        lane_s = lax.broadcasted_iota(jnp.int32, (n, w2), 1)
        ylo_ref[0, 0:n] = s_lo[:, :n]
        yhi_ref[0, 0:n] = pltpu.roll(s_hi, n, 1)[:, :n]
        if meta:
            ylo_ref[0, n:n + 8] = jnp.full((8, n), m, f32)
            yhi_ref[0, n:n + 8] = jnp.full((8, n), m, f32)


def kernel_sweep(rhs, moduli, code, state=None, emit_u=True, emit_sides=False, omega=0.0, meta=False):
    ncomp, n, nn = rhs.shape
    q, p4, wy, exy, ez = consts(n)
    full = lambda shp: pl.BlockSpec(shp, lambda c: (0,) * len(shp))
    comp3 = lambda shp: pl.BlockSpec((1,) + shp, lambda c: (c,) + (0,) * len(shp))
    smem = pl.BlockSpec(memory_space=pltpu.SMEM)
    in_specs = [smem, comp3((n, nn))]
    args = [moduli, rhs]
    zero_lam = state is not None and state[1] is None
    if state is not None:
        if zero_lam:
            state = state[:1] + state[4:]
            in_specs += [smem]
        else:
            in_specs += [smem, comp3((1, nn)), comp3((1, nn)), comp3((n, 2 * n))]
        in_specs += [comp3(x.shape[1:]) for x in state[-8:]]
        args += list(state)
    in_specs += [full(q.shape), full(p4.shape), full(wy.shape), full(exy.shape), full(ez.shape), smem]
    args += [q, p4, wy, exy, ez, code]
    out_specs, out_shape = [], []
    if emit_u:
        out_specs.append(comp3((n, nn)))
        out_shape.append(jax.ShapeDtypeStruct(rhs.shape, f32))
    if emit_sides:
        wx, ry = (nn + 2 * n, n + 8) if meta else (nn, n)
        out_specs += [comp3((1, wx)), comp3((1, wx)), comp3((ry, n)), comp3((ry, n))]
        out_shape += [jax.ShapeDtypeStruct((ncomp, 1, wx), f32), jax.ShapeDtypeStruct((ncomp, 1, wx), f32),
                      jax.ShapeDtypeStruct((ncomp, ry, n), f32), jax.ShapeDtypeStruct((ncomp, ry, n), f32)]
        if state is not None:
            out_specs += [comp3((1, nn)), comp3((1, nn)), comp3((n, 2 * n))]
            out_shape += [jax.ShapeDtypeStruct((ncomp, 1, nn), f32), jax.ShapeDtypeStruct((ncomp, 1, nn), f32),
                          jax.ShapeDtypeStruct((ncomp, n, 2 * n), f32)]
    kernel = functools.partial(solve_kernel, with_faces=state is not None, emit_u=emit_u,
                               emit_sides=emit_sides, omega=omega, zero_lam=zero_lam, meta=meta)
    return pl.pallas_call(
        kernel,
        grid=(ncomp,),
        in_specs=in_specs,
        out_specs=out_specs,
        out_shape=out_shape,
        scratch_shapes=[pltpu.VMEM((nn // 2, 2 * n), f32), pltpu.VMEM((nn // 4, 4 * n), f32)],
    )(*args)


def orient(face_field, code_table, extent):
    square = face_field.reshape(face_field.shape[:-1] + (extent, extent))
    flip_rows = (code_table % 2 == 1)[..., None, None, None]
    flip_cols = (code_table // 2 == 1)[..., None, None, None]
    square = jnp.where(flip_rows, jnp.flip(square, -2), square)
    square = jnp.where(flip_cols, jnp.flip(square, -1), square)
    return square.reshape(face_field.shape)


def face_data(solution, moduli):
    extent = solution.shape[-2]
    cube_view = solution.reshape(solution.shape[:-1] + (extent, extent))
    flat_shape = solution.shape[:-2] + (extent * extent,)

    def pack_side(planes):
        normal_slope = 11.0 / 6.0 * planes[0] - 3.0 * planes[1] + 1.5 * planes[2] - planes[3] / 3.0
        return (planes[0], moduli[..., None] * normal_slope)

    x_high = pack_side([solution[..., extent - 1 - plane_depth, :] for plane_depth in range(4)])
    x_low = pack_side([solution[..., plane_depth, :] for plane_depth in range(4)])
    y_high = pack_side(
        [
            cube_view[..., extent - 1 - plane_depth, :].reshape(flat_shape)
            for plane_depth in range(4)
        ]
    )
    y_low = pack_side(
        [cube_view[..., plane_depth, :].reshape(flat_shape) for plane_depth in range(4)]
    )
    return (x_high, x_low, y_high, y_low)


def place_faces(source_field, moduli, x_low, x_high, y_low, y_high):
    extent = source_field.shape[-2]
    added = jnp.zeros_like(source_field)
    added = added.at[..., 0, :].add(x_low)
    added = added.at[..., extent - 1, :].add(x_high)
    cube_view = added.reshape(added.shape[:-1] + (extent, extent))
    low_square = y_low.reshape(y_low.shape[:-1] + (extent, extent))
    high_square = y_high.reshape(y_high.shape[:-1] + (extent, extent))
    cube_view = cube_view.at[..., 0, :].add(low_square)
    cube_view = cube_view.at[..., extent - 1, :].add(high_square)
    added = cube_view.reshape(source_field.shape)
    return source_field + inject_scale * moduli[..., None, None] * added


def trace_update(current, side_a, side_b, moduli_a, moduli_b, omega_step, tangent):
    extent = tangent.shape[0]
    weight_a = moduli_a[..., None]
    weight_b = moduli_b[..., None]
    residue = (
        weight_a * side_a[0] + weight_b * side_b[0] + traction_mix * (side_a[1] + side_b[1])
    ) / (weight_a + weight_b) - current
    rows_view = residue.reshape(residue.shape[:-1] + (residue.shape[-1] // extent, extent))
    smoothed = rows_view + penalty_mix * jnp.einsum(
        "...z,zk->...k", rows_view, tangent, precision=highest
    )
    return current + omega_step * smoothed.reshape(residue.shape)


def flat_update(current, sum_a, sum_b, moduli_a, moduli_b, omega_step, tangent):
    extent = tangent.shape[0]
    residue = (sum_a + sum_b) / (moduli_a + moduli_b)[..., None] - current
    rows_view = residue.reshape(residue.shape[:-1] + (residue.shape[-1] // extent, extent))
    smoothed = rows_view + penalty_mix * jnp.einsum("...z,zk->...k", rows_view, tangent, precision=highest)
    return current + omega_step * smoothed.reshape(residue.shape)


def square_update(current, sum_a, sum_b, moduli_a, moduli_b, omega_step, tangent):
    residue = (sum_a + sum_b) / (moduli_a + moduli_b)[..., None, None] - current
    smoothed = residue + penalty_mix * jnp.einsum("...z,zk->...k", residue, tangent, precision=highest)
    return current + omega_step * smoothed


def shards(forcing, modulus, orient_codes):
    extent = forcing.shape[3]
    blocks = forcing.shape[1]
    flat = extent * extent
    source_field = forcing[0]
    moduli = modulus[0]
    codes_here = orient_codes[0]
    code_values = codes_here.astype(jnp.float32)
    omegas = step_weights(ITERS)
    slab_count = lax.axis_size("blk")
    slab_index = lax.axis_index("blk")
    has_up = jnp.broadcast_to((slab_index < slab_count - 1).astype(jnp.float32), (blocks, 3))
    has_down = jnp.broadcast_to((slab_index > 0).astype(jnp.float32), (blocks, 3))
    lam_x_up = lam_x_down = lam_y = [None] * blocks
    state = [None] * blocks
    for sweep in range(ITERS + 1):
        last = sweep == ITERS
        omega = omegas[sweep - 1] if sweep > 0 else 0.0
        outs = [
            kernel_sweep(source_field[b], moduli[b], code_values[b:b + 1], state[b], emit_u=last,
                         emit_sides=not last, omega=omega, meta=sweep == 0)
            for b in range(blocks)
        ]
        if last:
            return jnp.stack([o[0] for o in outs], 0)[None]
        xh, xl, ylo, yhi = (jnp.stack([o[k] for o in outs], 0) for k in range(4))
        if sweep > 0:
            lam_x_up, lam_x_down, lam_y = (jnp.stack([o[k] for o in outs], 0) for k in range(4, 7))
        upper = shifted(xl, "blk", -1)
        lower = shifted(xh, "blk", 1)
        nxt = jnp.concatenate([ylo[1:], shifted_2(ylo[:1], "face", -1)], 0)
        prv = jnp.concatenate([shifted_2(yhi[-1:], "face", 1), yhi[:-1]], 0)
        if sweep == 0:
            codes_down = lower[:, 0, 0, flat + extent].astype(jnp.int32)
            neighbour_moduli = jnp.stack(
                [upper[:, :, 0, flat], lower[:, :, 0, flat], prv[:, :, extent, 0], nxt[:, :, extent, 0],
                 has_up, has_down], 1
            )
        up_sum = orient(upper[:, :, 0, :flat], codes_here, extent)[:, :, None]
        down_sum = orient(lower[:, :, 0, :flat], codes_down, extent)[:, :, None]
        state = [
            (neighbour_moduli[b], lam_x_up[b], lam_x_down[b], lam_y[b], xh[b], xl[b], ylo[b], yhi[b],
             up_sum[b], down_sum[b], prv[b], nxt[b])
            for b in range(blocks)
        ]


def solution(mesh):
    placed = (P("blk", "face", None, None, None), P("blk", "face", None), P("blk", "face"))
    return jax.shard_map(
        shards,
        mesh=mesh,
        in_specs=placed,
        out_specs=P("blk", "face", None, None, None),
        check_vma=False,
    )
```

```python
import functools
import math

import jax
import jax.numpy as jnp
from jax import lax
from jax.sharding import PartitionSpec as P
from jax.experimental import pallas as pl
from jax.experimental.pallas import tpu as pltpu
import numpy as np
import ml_dtypes

ITERS = 2


mass_shift = 0.02
inject_scale = 2.0
traction_mix = 0.5
penalty_mix = 0.25
lower_edge = 0.3
upper_edge = 1.5
highest = lax.Precision.HIGHEST


def shifted(shard, axis, by):
    length = lax.axis_size(axis)
    pairs = [(i, i + by) for i in range(length) if 0 <= i + by < length]
    return lax.ppermute(shard, axis, pairs)


def shifted_2(shard, axis, by):
    length = lax.axis_size(axis)
    return lax.ppermute(shard, axis, [(i, (i + by) % length) for i in range(length)])


def tables(extent):
    node_index = jnp.arange(extent, dtype=jnp.float32) + 1.0
    basis = math.sqrt(2.0 / (extent + 1)) * jnp.sin(
        math.pi * node_index[:, None] * node_index[None, :] / (extent + 1)
    )
    eigenvalues = 2.0 - 2.0 * jnp.cos(math.pi * node_index / (extent + 1))
    return (basis, eigenvalues)


def tangent_matrix(extent):
    node_index = jnp.arange(extent, dtype=jnp.int32)
    distance = jnp.abs(node_index[:, None] - node_index[None, :])
    end_rows = ((node_index == 0) | (node_index == extent - 1)).astype(jnp.float32)
    adjacent = (distance == 1).astype(jnp.float32)
    diagonal_part = (distance == 0).astype(jnp.float32) * (2.0 - end_rows[:, None])
    return adjacent - diagonal_part


def step_weights(step_count):
    midpoint = 0.5 * (upper_edge + lower_edge)
    radius = 0.5 * (upper_edge - lower_edge)
    return [
        1.0 / (midpoint + radius * math.cos(math.pi * (2 * turn_index + 1) / (2 * step_count)))
        for turn_index in range(step_count)
    ]


def divisor(moduli, eigenvalues):
    extent = eigenvalues.shape[0]
    summed = eigenvalues[:, None, None] + eigenvalues[None, :, None] + eigenvalues[None, None, :]
    scaled = moduli[..., None, None, None] * summed + mass_shift
    return scaled.reshape(moduli.shape + (extent, extent * extent))


def body_transform(field_data, basis, paired_basis):
    extent = basis.shape[0]
    full_shape = field_data.shape
    pair_width = paired_basis.shape[0]
    sectioned = jnp.einsum("ix,bcxm->bcim", basis, field_data, precision=highest)
    sectioned = sectioned.reshape(full_shape[:-1] + (full_shape[-1] // pair_width, pair_width))
    sectioned = jnp.einsum("bcxpz,kz->bcxpk", sectioned, paired_basis, precision=highest)
    sectioned = sectioned.reshape(full_shape[:-1] + (extent, extent))
    sectioned = jnp.einsum("jy,bcxyz->bcxjz", basis, sectioned, precision=highest)
    return sectioned.reshape(full_shape)


def body_solve(right_side, scale_table, basis, paired_basis):
    return body_transform(
        body_transform(right_side, basis, paired_basis) / scale_table, basis, paired_basis
    )


f32 = jnp.float32


def np_tables(n):
    g = np.float32
    idx = np.arange(n, dtype=g) + g(1.0)
    arg = (g(math.pi) * idx[:, None]) * idx[None, :] / g(n + 1)
    q = g(math.sqrt(2.0 / (n + 1))) * np.sin(arg)
    e = g(2.0) - g(2.0) * np.cos(g(math.pi) * idx / g(n + 1))
    return q.astype(g), e.astype(g)


def consts(n):
    q, e = np_tables(n)
    h = n // 2
    p4 = np.kron(np.eye(4, dtype=np.float32), q.T)
    w = np.zeros((2, 4, h, 2, 4, h), np.float32)
    qq = q.reshape(h, 2, h, 2)
    for xl in range(4):
        w[:, xl, :, :, xl, :] = np.transpose(qq, (3, 2, 1, 0))
    wy = w.reshape(8 * h, 8 * h)
    ng = n // 4
    lane_h = np.arange(8 * h) // (4 * h)
    lane_xl = (np.arange(8 * h) // h) % 4
    lane_c = np.arange(8 * h) % h
    exy = (e[4 * np.arange(ng)[:, None] + lane_xl[None, :]] + e[2 * lane_c + lane_h][None, :]).astype(np.float32)
    ez = np.ascontiguousarray(np.broadcast_to(e[:, None], (n, 8 * h))).astype(np.float32)
    return stack_left(q), stack_right(p4), stack_right(wy), exy, ez


BF = jnp.bfloat16

def np_split3(w):
    b = ml_dtypes.bfloat16
    w1 = w.astype(b)
    r1 = w - w1.astype(np.float32)
    w2 = r1.astype(b)
    w3 = (r1 - w2.astype(np.float32)).astype(b)
    return w1, w2, w3


def stack_right(w):
    w1, w2, w3 = np_split3(w)
    return np.concatenate([w1, w2, w1, w1], 0)


def stack_left(w):
    w1, w2, w3 = np_split3(w)
    return np.concatenate([w1, w2, w1, w1], 1)


def split3(d):
    d1 = d.astype(BF)
    r1 = d - d1.astype(f32)
    d2 = r1.astype(BF)
    d3 = (r1 - d2.astype(f32)).astype(BF)
    return d1, d2, d3


def sdot(d, w6):
    d1, d2, d3 = split3(d)
    return jnp.dot(jnp.concatenate([d1, d1, d2, d3], 1), w6, preferred_element_type=f32)


def sdot_left(w6, d):
    d1, d2, d3 = split3(d)
    return jnp.dot(w6, jnp.concatenate([d1, d1, d2, d3], 0), preferred_element_type=f32)


def solve_kernel(*refs, with_faces, emit_u, emit_sides, omega, zero_lam, meta):
    it = iter(refs)
    mod_ref, f_ref = next(it), next(it)
    if with_faces:
        nbm_ref = next(it)
        lxu_ref, lxd_ref, ly_ref = (None, None, None) if zero_lam else (next(it), next(it), next(it))
        sxh_ref, sxl_ref, sylo_ref, syhi_ref, rup_ref, rdn_ref, ryp_ref, ryn_ref = (next(it) for _ in range(8))
    q_ref, p_ref, wy_ref, exy_ref, ez_ref = next(it), next(it), next(it), next(it), next(it)
    code_ref = next(it)
    o_ref = next(it) if emit_u else None
    if emit_sides:
        xh_ref, xl_ref, ylo_ref, yhi_ref = next(it), next(it), next(it), next(it)
    if with_faces and emit_sides:
        nlx_ref, nld_ref, nly_ref = next(it), next(it), next(it)
    elif with_faces:
        nlx_ref = nld_ref = nly_ref = None
    s_ref, z_ref = next(it), next(it)
    n = q_ref.shape[0]
    h = n // 2
    w2 = 2 * n
    w4 = 4 * n
    nn = f_ref.shape[-1]
    nch = nn // w2
    npair = nn // w4
    comp = pl.program_id(0)
    m = mod_ref[comp]
    q = q_ref[...]
    r = f_ref[0]
    if with_faces:
        m_up = nbm_ref[0, comp]
        m_dn = nbm_ref[1, comp]
        m_prev = nbm_ref[2, comp]
        m_next = nbm_ref[3, comp]
        has_up = nbm_ref[4, comp]
        has_dn = nbm_ref[5, comp]
        lane_x = lax.broadcasted_iota(jnp.int32, (1, nn), 1) % n
        lane_y = lax.broadcasted_iota(jnp.int32, (n, w2), 1)

        def smooth(res, lanes, width):
            left = pltpu.roll(res, 1, 1)
            right = pltpu.roll(res, width - 1, 1)
            left = jnp.where(lanes % n == 0, 0.0, left)
            right = jnp.where(lanes % n == n - 1, 0.0, right)
            diag = jnp.where((lanes % n == 0) | (lanes % n == n - 1), -1.0, -2.0)
            return res + 0.25 * ((left + right) + diag * res)

        xu = 0.0 if zero_lam else lxu_ref[0]
        res = (sxh_ref[0, 0:1, 0:nn] + rup_ref[0]) / (m + m_up) - xu
        xhi_face = (xu + omega * smooth(res, lane_x, nn)) * has_up
        xd = 0.0 if zero_lam else lxd_ref[0]
        res = (rdn_ref[0] + sxl_ref[0, 0:1, 0:nn]) / (m_dn + m) - xd
        xlo_face = (xd + omega * smooth(res, lane_x, nn)) * has_dn
        ly = 0.0 if zero_lam else ly_ref[0]
        lo = lane_y < n
        recv = jnp.concatenate([ryp_ref[0, 0, 0:n], ryn_ref[0, 0, 0:n]], 1)
        own = jnp.concatenate([sylo_ref[0, 0, 0:n], syhi_ref[0, 0, 0:n]], 1)
        res = (own + recv) / (m + jnp.where(lo, m_prev, m_next)) - ly
        yadd = ly + omega * smooth(res, lane_y, w2)
        if nlx_ref is not None:
            nlx_ref[0] = xhi_face
            nld_ref[0] = xlo_face
            nly_ref[0] = yadd
        rows = lax.broadcasted_iota(jnp.int32, (n, nn), 0)
        added = jnp.where(rows == 0, xlo_face, 0.0) + jnp.where(rows == n - 1, xhi_face, 0.0)
        lane = lane_y
        first = added[:, :w2] + jnp.where(lane < n, yadd, 0.0)
        last = added[:, nn - w2:] + jnp.where(lane >= n, yadd, 0.0)
        added = jnp.concatenate([first, added[:, w2:nn - w2], last], 1)
        r = r + (2.0 * m) * added
    a = sdot_left(q, r)
    for cp in range(npair):
        z_ref[cp * n:(cp + 1) * n, :] = a[:, cp * w4:(cp + 1) * w4]
    zo = sdot(z_ref[...], p_ref[...])
    for cp in range(npair):
        for cb in range(2):
            s_ref[(2 * cp + cb) * n:(2 * cp + cb + 1) * n, :] = zo[cp * n:(cp + 1) * n, cb * w2:(cb + 1) * w2]
    wy = wy_ref[...]
    ez = ez_ref[...]
    XG = 4
    GPI = 8

    def body(it_, carry):
        lhs = []
        for gi in range(GPI):
            g = it_ * GPI + gi
            blk = jnp.concatenate([s_ref[pl.ds(g * XG + xl, h, stride=n), :] for xl in range(XG)], 0)
            tb = blk.T
            lhs.append(jnp.concatenate([tb[:n], tb[n:]], 1))
        v = sdot(jnp.concatenate(lhs, 0), wy)
        div = jnp.concatenate([m * (exy_ref[pl.ds(it_ * GPI + gi, 1), :] + ez) + 0.02 for gi in range(GPI)], 0)
        v = v / div
        v = sdot(v, wy)
        for gi in range(GPI):
            g = it_ * GPI + gi
            vg = v[gi * n:(gi + 1) * n]
            tb = jnp.concatenate([vg[:, :w2], vg[:, w2:]], 0).T
            for xl in range(XG):
                s_ref[pl.ds(g * XG + xl, h, stride=n), :] = tb[xl * h:(xl + 1) * h]
        return carry
    lax.fori_loop(0, n // (XG * GPI), body, 0)
    for cp in range(npair):
        z_ref[cp * n:(cp + 1) * n, :] = jnp.concatenate(
            [s_ref[(2 * cp) * n:(2 * cp + 1) * n, :], s_ref[(2 * cp + 1) * n:(2 * cp + 2) * n, :]], 1)
    zo = sdot(z_ref[...], p_ref[...])
    b = jnp.concatenate([zo[cp * n:(cp + 1) * n, :] for cp in range(npair)], 1)
    u = sdot_left(q, b)
    if emit_u:
        o_ref[0] = u

    def slope(p0, p1, p2, p3):
        return m * (11.0 / 6.0 * p0 - 3.0 * p1 + 1.5 * p2 - p3 / 3.0)
    if emit_sides:
        m_row = jnp.full((1, nn), m, f32)
        xh_ref[0, 0:1, 0:nn] = m * u[n - 1:n] + 0.5 * slope(u[n - 1:n], u[n - 2:n - 1], u[n - 3:n - 2], u[n - 4:n - 3])
        lane_t = lax.broadcasted_iota(jnp.int32, (1, w2), 1)
        if meta:
            xh_ref[0, 0:1, nn:nn + w2] = jnp.where(lane_t < n, m, code_ref[0])
        xl_ref[0, 0:1, 0:nn] = m * u[0:1] + 0.5 * slope(u[0:1], u[1:2], u[2:3], u[3:4])
        if meta:
            xl_ref[0, 0:1, nn:nn + w2] = jnp.full((1, w2), m, f32)
        c_hi = u[:, nn - w2:]
        c_hi2 = u[:, nn - 2 * w2:nn - w2]
        s_hi = m * c_hi + 0.5 * slope(c_hi, pltpu.roll(c_hi, n, 1), c_hi2, pltpu.roll(c_hi2, n, 1))
        c_lo = u[:, :w2]
        c_lo2 = u[:, w2:2 * w2]
        s_lo = m * c_lo + 0.5 * slope(c_lo, pltpu.roll(c_lo, n, 1), c_lo2, pltpu.roll(c_lo2, n, 1))
        lane_s = lax.broadcasted_iota(jnp.int32, (n, w2), 1)
        ylo_ref[0, 0, 0:n] = s_lo[:, :n]
        yhi_ref[0, 0, 0:n] = pltpu.roll(s_hi, n, 1)[:, :n]
        if meta:
            ylo_ref[0, 0, n:n + 8] = jnp.full((8, n), m, f32)
            yhi_ref[0, 0, n:n + 8] = jnp.full((8, n), m, f32)


def kernel_sweep(rhs, moduli, code, state=None, emit_u=True, emit_sides=False, omega=0.0, meta=False):
    ncomp, n, nn = rhs.shape
    q, p4, wy, exy, ez = consts(n)
    full = lambda shp: pl.BlockSpec(shp, lambda c: (0,) * len(shp))
    comp3 = lambda shp: pl.BlockSpec((1,) + shp, lambda c: (c,) + (0,) * len(shp))
    smem = pl.BlockSpec(memory_space=pltpu.SMEM)
    in_specs = [smem, comp3((n, nn))]
    args = [moduli, rhs]
    zero_lam = state is not None and state[1] is None
    if state is not None:
        if zero_lam:
            state = state[:1] + state[4:]
            in_specs += [smem]
        else:
            in_specs += [smem, comp3((1, nn)), comp3((1, nn)), comp3((n, 2 * n))]
        in_specs += [comp3(x.shape[1:]) for x in state[-8:]]
        args += list(state)
    in_specs += [full(q.shape), full(p4.shape), full(wy.shape), full(exy.shape), full(ez.shape), smem]
    args += [q, p4, wy, exy, ez, code]
    out_specs, out_shape = [], []
    if emit_u:
        out_specs.append(comp3((n, nn)))
        out_shape.append(jax.ShapeDtypeStruct(rhs.shape, f32))
    if emit_sides:
        wx, ry = (nn + 2 * n, n + 8) if meta else (nn, n)
        out_specs += [comp3((1, wx)), comp3((1, wx)), comp3((1, ry, n)), comp3((1, ry, n))]
        out_shape += [jax.ShapeDtypeStruct((ncomp, 1, wx), f32), jax.ShapeDtypeStruct((ncomp, 1, wx), f32),
                      jax.ShapeDtypeStruct((ncomp, 1, ry, n), f32), jax.ShapeDtypeStruct((ncomp, 1, ry, n), f32)]
        if state is not None:
            out_specs += [comp3((1, nn)), comp3((1, nn)), comp3((n, 2 * n))]
            out_shape += [jax.ShapeDtypeStruct((ncomp, 1, nn), f32), jax.ShapeDtypeStruct((ncomp, 1, nn), f32),
                          jax.ShapeDtypeStruct((ncomp, n, 2 * n), f32)]
    kernel = functools.partial(solve_kernel, with_faces=state is not None, emit_u=emit_u,
                               emit_sides=emit_sides, omega=omega, zero_lam=zero_lam, meta=meta)
    return pl.pallas_call(
        kernel,
        grid=(ncomp,),
        in_specs=in_specs,
        out_specs=out_specs,
        out_shape=out_shape,
        scratch_shapes=[pltpu.VMEM((nn // 2, 2 * n), f32), pltpu.VMEM((nn // 4, 4 * n), f32)],
    )(*args)


def orient(face_field, code_table, extent):
    square = face_field.reshape(face_field.shape[:-1] + (extent, extent))
    flip_rows = (code_table % 2 == 1)[..., None, None, None]
    flip_cols = (code_table // 2 == 1)[..., None, None, None]
    square = jnp.where(flip_rows, jnp.flip(square, -2), square)
    square = jnp.where(flip_cols, jnp.flip(square, -1), square)
    return square.reshape(face_field.shape)


def face_data(solution, moduli):
    extent = solution.shape[-2]
    cube_view = solution.reshape(solution.shape[:-1] + (extent, extent))
    flat_shape = solution.shape[:-2] + (extent * extent,)

    def pack_side(planes):
        normal_slope = 11.0 / 6.0 * planes[0] - 3.0 * planes[1] + 1.5 * planes[2] - planes[3] / 3.0
        return (planes[0], moduli[..., None] * normal_slope)

    x_high = pack_side([solution[..., extent - 1 - plane_depth, :] for plane_depth in range(4)])
    x_low = pack_side([solution[..., plane_depth, :] for plane_depth in range(4)])
    y_high = pack_side(
        [
            cube_view[..., extent - 1 - plane_depth, :].reshape(flat_shape)
            for plane_depth in range(4)
        ]
    )
    y_low = pack_side(
        [cube_view[..., plane_depth, :].reshape(flat_shape) for plane_depth in range(4)]
    )
    return (x_high, x_low, y_high, y_low)


def place_faces(source_field, moduli, x_low, x_high, y_low, y_high):
    extent = source_field.shape[-2]
    added = jnp.zeros_like(source_field)
    added = added.at[..., 0, :].add(x_low)
    added = added.at[..., extent - 1, :].add(x_high)
    cube_view = added.reshape(added.shape[:-1] + (extent, extent))
    low_square = y_low.reshape(y_low.shape[:-1] + (extent, extent))
    high_square = y_high.reshape(y_high.shape[:-1] + (extent, extent))
    cube_view = cube_view.at[..., 0, :].add(low_square)
    cube_view = cube_view.at[..., extent - 1, :].add(high_square)
    added = cube_view.reshape(source_field.shape)
    return source_field + inject_scale * moduli[..., None, None] * added


def trace_update(current, side_a, side_b, moduli_a, moduli_b, omega_step, tangent):
    extent = tangent.shape[0]
    weight_a = moduli_a[..., None]
    weight_b = moduli_b[..., None]
    residue = (
        weight_a * side_a[0] + weight_b * side_b[0] + traction_mix * (side_a[1] + side_b[1])
    ) / (weight_a + weight_b) - current
    rows_view = residue.reshape(residue.shape[:-1] + (residue.shape[-1] // extent, extent))
    smoothed = rows_view + penalty_mix * jnp.einsum(
        "...z,zk->...k", rows_view, tangent, precision=highest
    )
    return current + omega_step * smoothed.reshape(residue.shape)


def flat_update(current, sum_a, sum_b, moduli_a, moduli_b, omega_step, tangent):
    extent = tangent.shape[0]
    residue = (sum_a + sum_b) / (moduli_a + moduli_b)[..., None] - current
    rows_view = residue.reshape(residue.shape[:-1] + (residue.shape[-1] // extent, extent))
    smoothed = rows_view + penalty_mix * jnp.einsum("...z,zk->...k", rows_view, tangent, precision=highest)
    return current + omega_step * smoothed.reshape(residue.shape)


def square_update(current, sum_a, sum_b, moduli_a, moduli_b, omega_step, tangent):
    residue = (sum_a + sum_b) / (moduli_a + moduli_b)[..., None, None] - current
    smoothed = residue + penalty_mix * jnp.einsum("...z,zk->...k", residue, tangent, precision=highest)
    return current + omega_step * smoothed


def shards(forcing, modulus, orient_codes):
    extent = forcing.shape[3]
    blocks = forcing.shape[1]
    flat = extent * extent
    source_field = forcing[0]
    moduli = modulus[0]
    codes_here = orient_codes[0]
    code_values = codes_here.astype(jnp.float32)
    omegas = step_weights(ITERS)
    slab_count = lax.axis_size("blk")
    slab_index = lax.axis_index("blk")
    has_up = jnp.broadcast_to((slab_index < slab_count - 1).astype(jnp.float32), (blocks, 3))
    has_down = jnp.broadcast_to((slab_index > 0).astype(jnp.float32), (blocks, 3))
    lam_x_up = lam_x_down = lam_y = [None] * blocks
    state = [None] * blocks
    for sweep in range(ITERS + 1):
        last = sweep == ITERS
        omega = omegas[sweep - 1] if sweep > 0 else 0.0
        outs = [
            kernel_sweep(source_field[b], moduli[b], code_values[b:b + 1], state[b], emit_u=last,
                         emit_sides=not last, omega=omega, meta=sweep == 0)
            for b in range(blocks)
        ]
        if last:
            return jnp.stack([o[0] for o in outs], 0)[None]
        xh, xl, ylo, yhi = (jnp.stack([o[k] for o in outs], 0) for k in range(4))
        if sweep > 0:
            lam_x_up, lam_x_down, lam_y = (jnp.stack([o[k] for o in outs], 0) for k in range(4, 7))
        high_sum = orient(xh[:, :, 0, :flat], codes_here, extent)[:, :, None]
        if sweep == 0:
            high_sum = jnp.concatenate([high_sum, xh[:, :, :, flat:]], -1)
        upper = shifted(xl, "blk", -1)
        lower = shifted(high_sum, "blk", 1)
        nxt = jnp.concatenate([ylo[1:], shifted_2(ylo[:1], "face", -1)], 0)
        prv = jnp.concatenate([shifted_2(yhi[-1:], "face", 1), yhi[:-1]], 0)
        if sweep == 0:
            codes_down = lower[:, 0, 0, flat + extent].astype(jnp.int32)
            neighbour_moduli = jnp.stack(
                [upper[:, :, 0, flat], lower[:, :, 0, flat], prv[:, :, 0, extent, 0], nxt[:, :, 0, extent, 0],
                 has_up, has_down], 1
            )
        up_sum = orient(upper[:, :, 0, :flat], codes_here, extent)[:, :, None]
        down_sum = lower[:, :, :, :flat]
        state = [
            (neighbour_moduli[b], lam_x_up[b], lam_x_down[b], lam_y[b], xh[b], xl[b], ylo[b], yhi[b],
             up_sum[b], down_sum[b], prv[b], nxt[b])
            for b in range(blocks)
        ]


def solution(mesh):
    placed = (P("blk", "face", None, None, None), P("blk", "face", None), P("blk", "face"))
    return jax.shard_map(
        shards,
        mesh=mesh,
        in_specs=placed,
        out_specs=P("blk", "face", None, None, None),
        check_vma=False,
    )
```

```python
import functools
import math

import jax
import jax.numpy as jnp
from jax import lax
from jax.sharding import PartitionSpec as P
from jax.experimental import pallas as pl
from jax.experimental.pallas import tpu as pltpu
import numpy as np
import ml_dtypes

ITERS = 2


mass_shift = 0.02
inject_scale = 2.0
traction_mix = 0.5
penalty_mix = 0.25
lower_edge = 0.3
upper_edge = 1.5
highest = lax.Precision.HIGHEST


def shifted(shard, axis, by):
    length = lax.axis_size(axis)
    pairs = [(i, i + by) for i in range(length) if 0 <= i + by < length]
    return lax.ppermute(shard, axis, pairs)


def shifted_2(shard, axis, by):
    length = lax.axis_size(axis)
    return lax.ppermute(shard, axis, [(i, (i + by) % length) for i in range(length)])


def tables(extent):
    node_index = jnp.arange(extent, dtype=jnp.float32) + 1.0
    basis = math.sqrt(2.0 / (extent + 1)) * jnp.sin(
        math.pi * node_index[:, None] * node_index[None, :] / (extent + 1)
    )
    eigenvalues = 2.0 - 2.0 * jnp.cos(math.pi * node_index / (extent + 1))
    return (basis, eigenvalues)


def tangent_matrix(extent):
    node_index = jnp.arange(extent, dtype=jnp.int32)
    distance = jnp.abs(node_index[:, None] - node_index[None, :])
    end_rows = ((node_index == 0) | (node_index == extent - 1)).astype(jnp.float32)
    adjacent = (distance == 1).astype(jnp.float32)
    diagonal_part = (distance == 0).astype(jnp.float32) * (2.0 - end_rows[:, None])
    return adjacent - diagonal_part


def step_weights(step_count):
    midpoint = 0.5 * (upper_edge + lower_edge)
    radius = 0.5 * (upper_edge - lower_edge)
    return [
        1.0 / (midpoint + radius * math.cos(math.pi * (2 * turn_index + 1) / (2 * step_count)))
        for turn_index in range(step_count)
    ]


def divisor(moduli, eigenvalues):
    extent = eigenvalues.shape[0]
    summed = eigenvalues[:, None, None] + eigenvalues[None, :, None] + eigenvalues[None, None, :]
    scaled = moduli[..., None, None, None] * summed + mass_shift
    return scaled.reshape(moduli.shape + (extent, extent * extent))


def body_transform(field_data, basis, paired_basis):
    extent = basis.shape[0]
    full_shape = field_data.shape
    pair_width = paired_basis.shape[0]
    sectioned = jnp.einsum("ix,bcxm->bcim", basis, field_data, precision=highest)
    sectioned = sectioned.reshape(full_shape[:-1] + (full_shape[-1] // pair_width, pair_width))
    sectioned = jnp.einsum("bcxpz,kz->bcxpk", sectioned, paired_basis, precision=highest)
    sectioned = sectioned.reshape(full_shape[:-1] + (extent, extent))
    sectioned = jnp.einsum("jy,bcxyz->bcxjz", basis, sectioned, precision=highest)
    return sectioned.reshape(full_shape)


def body_solve(right_side, scale_table, basis, paired_basis):
    return body_transform(
        body_transform(right_side, basis, paired_basis) / scale_table, basis, paired_basis
    )


f32 = jnp.float32


def np_tables(n):
    g = np.float32
    idx = np.arange(n, dtype=g) + g(1.0)
    arg = (g(math.pi) * idx[:, None]) * idx[None, :] / g(n + 1)
    q = g(math.sqrt(2.0 / (n + 1))) * np.sin(arg)
    e = g(2.0) - g(2.0) * np.cos(g(math.pi) * idx / g(n + 1))
    return q.astype(g), e.astype(g)


def consts(n):
    q, e = np_tables(n)
    h = n // 2
    p4 = np.kron(np.eye(4, dtype=np.float32), q.T)
    w = np.zeros((2, 4, h, 2, 4, h), np.float32)
    qq = q.reshape(h, 2, h, 2)
    for xl in range(4):
        w[:, xl, :, :, xl, :] = np.transpose(qq, (3, 2, 1, 0))
    wy = w.reshape(8 * h, 8 * h)
    ng = n // 4
    lane_h = np.arange(8 * h) // (4 * h)
    lane_xl = (np.arange(8 * h) // h) % 4
    lane_c = np.arange(8 * h) % h
    exy = (e[4 * np.arange(ng)[:, None] + lane_xl[None, :]] + e[2 * lane_c + lane_h][None, :]).astype(np.float32)
    ez = np.ascontiguousarray(np.broadcast_to(e[:, None], (n, 8 * h))).astype(np.float32)
    return stack_left(q), stack_right(p4), stack_right(wy), exy, ez


BF = jnp.bfloat16

def np_split3(w):
    b = ml_dtypes.bfloat16
    w1 = w.astype(b)
    r1 = w - w1.astype(np.float32)
    w2 = r1.astype(b)
    w3 = (r1 - w2.astype(np.float32)).astype(b)
    return w1, w2, w3


def stack_right(w):
    w1, w2, w3 = np_split3(w)
    return np.concatenate([w1, w2, w1, w1], 0)


def stack_left(w):
    w1, w2, w3 = np_split3(w)
    return np.concatenate([w1, w2, w1, w1], 1)


def split3(d):
    d1 = d.astype(BF)
    r1 = d - d1.astype(f32)
    d2 = r1.astype(BF)
    d3 = (r1 - d2.astype(f32)).astype(BF)
    return d1, d2, d3


def sdot(d, w6):
    d1, d2, d3 = split3(d)
    return jnp.dot(jnp.concatenate([d1, d1, d2, d3], 1), w6, preferred_element_type=f32)


def sdot_left(w6, d):
    d1, d2, d3 = split3(d)
    return jnp.dot(w6, jnp.concatenate([d1, d1, d2, d3], 0), preferred_element_type=f32)


def solve_kernel(*refs, with_faces, emit_u, emit_sides, omega, zero_lam, meta):
    it = iter(refs)
    mod_ref, f_ref = next(it), next(it)
    if with_faces:
        nbm_ref = next(it)
        lxu_ref, lxd_ref, ly_ref = (None, None, None) if zero_lam else (next(it), next(it), next(it))
        sxh_ref, sxl_ref, sylo_ref, syhi_ref, rup_ref, rdn_ref, ryp_ref, ryn_ref = (next(it) for _ in range(8))
    q_ref, p_ref, wy_ref, exy_ref, ez_ref = next(it), next(it), next(it), next(it), next(it)
    code_ref = next(it)
    o_ref = next(it) if emit_u else None
    if emit_sides:
        xh_ref, xl_ref, ylo_ref, yhi_ref = next(it), next(it), next(it), next(it)
    if with_faces and emit_sides:
        nlx_ref, nld_ref, nly_ref = next(it), next(it), next(it)
    elif with_faces:
        nlx_ref = nld_ref = nly_ref = None
    s_ref, z_ref = next(it), next(it)
    n = q_ref.shape[0]
    h = n // 2
    w2 = 2 * n
    w4 = 4 * n
    nn = f_ref.shape[-1]
    nch = nn // w2
    npair = nn // w4
    comp = pl.program_id(0)
    m = mod_ref[comp]
    q = q_ref[...]
    r = f_ref[0]
    if with_faces:
        m_up = nbm_ref[0, comp]
        m_dn = nbm_ref[1, comp]
        m_prev = nbm_ref[2, comp]
        m_next = nbm_ref[3, comp]
        has_up = nbm_ref[4, comp]
        has_dn = nbm_ref[5, comp]
        lane_x = lax.broadcasted_iota(jnp.int32, (1, nn), 1) % n
        lane_y = lax.broadcasted_iota(jnp.int32, (n, w2), 1)

        def smooth(res, lanes, width):
            left = pltpu.roll(res, 1, 1)
            right = pltpu.roll(res, width - 1, 1)
            left = jnp.where(lanes % n == 0, 0.0, left)
            right = jnp.where(lanes % n == n - 1, 0.0, right)
            diag = jnp.where((lanes % n == 0) | (lanes % n == n - 1), -1.0, -2.0)
            return res + 0.25 * ((left + right) + diag * res)

        xu = 0.0 if zero_lam else lxu_ref[0]
        res = (sxh_ref[0, 0:1, 0:nn] + rup_ref[0]) / (m + m_up) - xu
        xhi_face = (xu + omega * smooth(res, lane_x, nn)) * has_up
        xd = 0.0 if zero_lam else lxd_ref[0]
        res = (rdn_ref[0] + sxl_ref[0, 0:1, 0:nn]) / (m_dn + m) - xd
        xlo_face = (xd + omega * smooth(res, lane_x, nn)) * has_dn
        ly = 0.0 if zero_lam else ly_ref[0]
        lo = lane_y < n
        recv = jnp.concatenate([ryp_ref[0, 0, 0:n], ryn_ref[0, 0, 0:n]], 1)
        own = jnp.concatenate([sylo_ref[0, 0, 0:n], syhi_ref[0, 0, 0:n]], 1)
        res = (own + recv) / (m + jnp.where(lo, m_prev, m_next)) - ly
        yadd = ly + omega * smooth(res, lane_y, w2)
        if nlx_ref is not None:
            nlx_ref[0] = xhi_face
            nld_ref[0] = xlo_face
            nly_ref[0] = yadd
        rows = lax.broadcasted_iota(jnp.int32, (n, nn), 0)
        added = jnp.where(rows == 0, xlo_face, 0.0) + jnp.where(rows == n - 1, xhi_face, 0.0)
        lane = lane_y
        first = added[:, :w2] + jnp.where(lane < n, yadd, 0.0)
        last = added[:, nn - w2:] + jnp.where(lane >= n, yadd, 0.0)
        added = jnp.concatenate([first, added[:, w2:nn - w2], last], 1)
        r = r + (2.0 * m) * added
    a = sdot_left(q, r)
    for cp in range(npair):
        z_ref[cp * n:(cp + 1) * n, :] = a[:, cp * w4:(cp + 1) * w4]
    zo = sdot(z_ref[...], p_ref[...])
    for cp in range(npair):
        for cb in range(2):
            s_ref[(2 * cp + cb) * n:(2 * cp + cb + 1) * n, :] = zo[cp * n:(cp + 1) * n, cb * w2:(cb + 1) * w2]
    wy = wy_ref[...]
    ez = ez_ref[...]
    XG = 4
    GPI = 8

    def body(it_, carry):
        lhs = []
        for gi in range(GPI):
            g = it_ * GPI + gi
            blk = jnp.concatenate([s_ref[pl.ds(g * XG + xl, h, stride=n), :] for xl in range(XG)], 0)
            tb = blk.T
            lhs.append(jnp.concatenate([tb[:n], tb[n:]], 1))
        v = sdot(jnp.concatenate(lhs, 0), wy)
        div = jnp.concatenate([m * (exy_ref[pl.ds(it_ * GPI + gi, 1), :] + ez) + 0.02 for gi in range(GPI)], 0)
        v = v / div
        v = sdot(v, wy)
        for gi in range(GPI):
            g = it_ * GPI + gi
            vg = v[gi * n:(gi + 1) * n]
            tb = jnp.concatenate([vg[:, :w2], vg[:, w2:]], 0).T
            for xl in range(XG):
                s_ref[pl.ds(g * XG + xl, h, stride=n), :] = tb[xl * h:(xl + 1) * h]
        return carry
    lax.fori_loop(0, n // (XG * GPI), body, 0)
    for cp in range(npair):
        z_ref[cp * n:(cp + 1) * n, :] = jnp.concatenate(
            [s_ref[(2 * cp) * n:(2 * cp + 1) * n, :], s_ref[(2 * cp + 1) * n:(2 * cp + 2) * n, :]], 1)
    zo = sdot(z_ref[...], p_ref[...])
    b = jnp.concatenate([zo[cp * n:(cp + 1) * n, :] for cp in range(npair)], 1)
    u = sdot_left(q, b)
    if emit_u:
        o_ref[0] = u

    def slope(p0, p1, p2, p3):
        return m * (11.0 / 6.0 * p0 - 3.0 * p1 + 1.5 * p2 - p3 / 3.0)
    if emit_sides:
        m_row = jnp.full((1, nn), m, f32)
        xh_ref[0, 0:1, 0:nn] = m * u[n - 1:n] + 0.5 * slope(u[n - 1:n], u[n - 2:n - 1], u[n - 3:n - 2], u[n - 4:n - 3])
        lane_t = lax.broadcasted_iota(jnp.int32, (1, w2), 1)
        if meta:
            xh_ref[0, 0:1, nn:nn + w2] = jnp.where(lane_t < n, m, code_ref[0])
        xl_ref[0, 0:1, 0:nn] = m * u[0:1] + 0.5 * slope(u[0:1], u[1:2], u[2:3], u[3:4])
        if meta:
            xl_ref[0, 0:1, nn:nn + w2] = jnp.full((1, w2), m, f32)
        c_hi = u[:, nn - w2:]
        c_hi2 = u[:, nn - 2 * w2:nn - w2]
        s_hi = m * c_hi + 0.5 * slope(c_hi, pltpu.roll(c_hi, n, 1), c_hi2, pltpu.roll(c_hi2, n, 1))
        c_lo = u[:, :w2]
        c_lo2 = u[:, w2:2 * w2]
        s_lo = m * c_lo + 0.5 * slope(c_lo, pltpu.roll(c_lo, n, 1), c_lo2, pltpu.roll(c_lo2, n, 1))
        lane_s = lax.broadcasted_iota(jnp.int32, (n, w2), 1)
        ylo_ref[0, 0, 0:n] = s_lo[:, :n]
        yhi_ref[0, 0, 0:n] = pltpu.roll(s_hi, n, 1)[:, :n]
        if meta:
            ylo_ref[0, 0, n:n + 8] = jnp.full((8, n), m, f32)
            yhi_ref[0, 0, n:n + 8] = jnp.full((8, n), m, f32)


def kernel_sweep(rhs, moduli, code, state=None, emit_u=True, emit_sides=False, omega=0.0, meta=False):
    ncomp, n, nn = rhs.shape
    q, p4, wy, exy, ez = consts(n)
    full = lambda shp: pl.BlockSpec(shp, lambda c: (0,) * len(shp))
    comp3 = lambda shp: pl.BlockSpec((1,) + shp, lambda c: (c,) + (0,) * len(shp))
    smem = pl.BlockSpec(memory_space=pltpu.SMEM)
    in_specs = [smem, comp3((n, nn))]
    args = [moduli, rhs]
    zero_lam = state is not None and state[1] is None
    if state is not None:
        if zero_lam:
            state = state[:1] + state[4:]
            in_specs += [smem]
        else:
            in_specs += [smem, comp3((1, nn)), comp3((1, nn)), comp3((n, 2 * n))]
        in_specs += [comp3(x.shape[1:]) for x in state[-8:]]
        args += list(state)
    in_specs += [full(q.shape), full(p4.shape), full(wy.shape), full(exy.shape), full(ez.shape), smem]
    args += [q, p4, wy, exy, ez, code]
    out_specs, out_shape = [], []
    if emit_u:
        out_specs.append(comp3((n, nn)))
        out_shape.append(jax.ShapeDtypeStruct(rhs.shape, f32))
    if emit_sides:
        wx, ry = (nn + 2 * n, n + 8) if meta else (nn, n)
        out_specs += [comp3((1, wx)), comp3((1, wx)), comp3((1, ry, n)), comp3((1, ry, n))]
        out_shape += [jax.ShapeDtypeStruct((ncomp, 1, wx), f32), jax.ShapeDtypeStruct((ncomp, 1, wx), f32),
                      jax.ShapeDtypeStruct((ncomp, 1, ry, n), f32), jax.ShapeDtypeStruct((ncomp, 1, ry, n), f32)]
        if state is not None:
            out_specs += [comp3((1, nn)), comp3((1, nn)), comp3((n, 2 * n))]
            out_shape += [jax.ShapeDtypeStruct((ncomp, 1, nn), f32), jax.ShapeDtypeStruct((ncomp, 1, nn), f32),
                          jax.ShapeDtypeStruct((ncomp, n, 2 * n), f32)]
    kernel = functools.partial(solve_kernel, with_faces=state is not None, emit_u=emit_u,
                               emit_sides=emit_sides, omega=omega, zero_lam=zero_lam, meta=meta)
    return pl.pallas_call(
        kernel,
        grid=(ncomp,),
        in_specs=in_specs,
        out_specs=out_specs,
        out_shape=out_shape,
        scratch_shapes=[pltpu.VMEM((nn // 2, 2 * n), f32), pltpu.VMEM((nn // 4, 4 * n), f32)],
    )(*args)


def orient(face_field, code_table, extent):
    square = face_field.reshape(face_field.shape[:-1] + (extent, extent))
    flip_rows = (code_table % 2 == 1)[..., None, None, None]
    flip_cols = (code_table // 2 == 1)[..., None, None, None]
    square = jnp.where(flip_rows, jnp.flip(square, -2), square)
    square = jnp.where(flip_cols, jnp.flip(square, -1), square)
    return square.reshape(face_field.shape)


def face_data(solution, moduli):
    extent = solution.shape[-2]
    cube_view = solution.reshape(solution.shape[:-1] + (extent, extent))
    flat_shape = solution.shape[:-2] + (extent * extent,)

    def pack_side(planes):
        normal_slope = 11.0 / 6.0 * planes[0] - 3.0 * planes[1] + 1.5 * planes[2] - planes[3] / 3.0
        return (planes[0], moduli[..., None] * normal_slope)

    x_high = pack_side([solution[..., extent - 1 - plane_depth, :] for plane_depth in range(4)])
    x_low = pack_side([solution[..., plane_depth, :] for plane_depth in range(4)])
    y_high = pack_side(
        [
            cube_view[..., extent - 1 - plane_depth, :].reshape(flat_shape)
            for plane_depth in range(4)
        ]
    )
    y_low = pack_side(
        [cube_view[..., plane_depth, :].reshape(flat_shape) for plane_depth in range(4)]
    )
    return (x_high, x_low, y_high, y_low)


def place_faces(source_field, moduli, x_low, x_high, y_low, y_high):
    extent = source_field.shape[-2]
    added = jnp.zeros_like(source_field)
    added = added.at[..., 0, :].add(x_low)
    added = added.at[..., extent - 1, :].add(x_high)
    cube_view = added.reshape(added.shape[:-1] + (extent, extent))
    low_square = y_low.reshape(y_low.shape[:-1] + (extent, extent))
    high_square = y_high.reshape(y_high.shape[:-1] + (extent, extent))
    cube_view = cube_view.at[..., 0, :].add(low_square)
    cube_view = cube_view.at[..., extent - 1, :].add(high_square)
    added = cube_view.reshape(source_field.shape)
    return source_field + inject_scale * moduli[..., None, None] * added


def trace_update(current, side_a, side_b, moduli_a, moduli_b, omega_step, tangent):
    extent = tangent.shape[0]
    weight_a = moduli_a[..., None]
    weight_b = moduli_b[..., None]
    residue = (
        weight_a * side_a[0] + weight_b * side_b[0] + traction_mix * (side_a[1] + side_b[1])
    ) / (weight_a + weight_b) - current
    rows_view = residue.reshape(residue.shape[:-1] + (residue.shape[-1] // extent, extent))
    smoothed = rows_view + penalty_mix * jnp.einsum(
        "...z,zk->...k", rows_view, tangent, precision=highest
    )
    return current + omega_step * smoothed.reshape(residue.shape)


def flat_update(current, sum_a, sum_b, moduli_a, moduli_b, omega_step, tangent):
    extent = tangent.shape[0]
    residue = (sum_a + sum_b) / (moduli_a + moduli_b)[..., None] - current
    rows_view = residue.reshape(residue.shape[:-1] + (residue.shape[-1] // extent, extent))
    smoothed = rows_view + penalty_mix * jnp.einsum("...z,zk->...k", rows_view, tangent, precision=highest)
    return current + omega_step * smoothed.reshape(residue.shape)


def square_update(current, sum_a, sum_b, moduli_a, moduli_b, omega_step, tangent):
    residue = (sum_a + sum_b) / (moduli_a + moduli_b)[..., None, None] - current
    smoothed = residue + penalty_mix * jnp.einsum("...z,zk->...k", residue, tangent, precision=highest)
    return current + omega_step * smoothed


def shards(forcing, modulus, orient_codes):
    extent = forcing.shape[3]
    blocks = forcing.shape[1]
    flat = extent * extent
    source_field = forcing[0]
    moduli = modulus[0]
    codes_here = orient_codes[0]
    code_values = codes_here.astype(jnp.float32)
    omegas = step_weights(ITERS)
    slab_count = lax.axis_size("blk")
    slab_index = lax.axis_index("blk")
    has_up = jnp.broadcast_to((slab_index < slab_count - 1).astype(jnp.float32), (blocks, 3))
    has_down = jnp.broadcast_to((slab_index > 0).astype(jnp.float32), (blocks, 3))
    lam_x_up = lam_x_down = lam_y = [None] * blocks
    state = [None] * blocks
    for sweep in range(ITERS + 1):
        last = sweep == ITERS
        omega = omegas[sweep - 1] if sweep > 0 else 0.0
        outs = [
            kernel_sweep(source_field[b], moduli[b], code_values[b:b + 1], state[b], emit_u=last,
                         emit_sides=not last, omega=omega, meta=sweep == 0)
            for b in range(blocks)
        ]
        if last:
            return jnp.stack([o[0] for o in outs], 0)[None]
        xh, xl, ylo, yhi = (jnp.stack([o[k] for o in outs], 0) for k in range(4))
        if sweep > 0:
            lam_x_up, lam_x_down, lam_y = (jnp.stack([o[k] for o in outs], 0) for k in range(4, 7))
        upper = shifted(xl, "blk", -1)
        lower = shifted(xh, "blk", 1)
        nxt = jnp.concatenate([ylo[1:], shifted_2(ylo[:1], "face", -1)], 0)
        prv = jnp.concatenate([shifted_2(yhi[-1:], "face", 1), yhi[:-1]], 0)
        if sweep == 0:
            codes_down = lower[:, 0, 0, flat + extent].astype(jnp.int32)
            neighbour_moduli = jnp.stack(
                [upper[:, :, 0, flat], lower[:, :, 0, flat], prv[:, :, 0, extent, 0], nxt[:, :, 0, extent, 0],
                 has_up, has_down], 1
            )
        both = orient(
            jnp.stack([upper[:, :, 0, :flat], lower[:, :, 0, :flat]], 0),
            jnp.stack([codes_here, codes_down], 0),
            extent,
        )
        up_sum = both[0][:, :, None]
        down_sum = both[1][:, :, None]
        state = [
            (neighbour_moduli[b], lam_x_up[b], lam_x_down[b], lam_y[b], xh[b], xl[b], ylo[b], yhi[b],
             up_sum[b], down_sum[b], prv[b], nxt[b])
            for b in range(blocks)
        ]


def solution(mesh):
    placed = (P("blk", "face", None, None, None), P("blk", "face", None), P("blk", "face"))
    return jax.shard_map(
        shards,
        mesh=mesh,
        in_specs=placed,
        out_specs=P("blk", "face", None, None, None),
        check_vma=False,
    )
```

```python
import functools
import math

import jax
import jax.numpy as jnp
from jax import lax
from jax.sharding import PartitionSpec as P
from jax.experimental import pallas as pl
from jax.experimental.pallas import tpu as pltpu
import numpy as np
import ml_dtypes

ITERS = 2


mass_shift = 0.02
inject_scale = 2.0
traction_mix = 0.5
penalty_mix = 0.25
lower_edge = 0.3
upper_edge = 1.5
highest = lax.Precision.HIGHEST


def shifted(shard, axis, by):
    length = lax.axis_size(axis)
    pairs = [(i, i + by) for i in range(length) if 0 <= i + by < length]
    return lax.ppermute(shard, axis, pairs)


def shifted_2(shard, axis, by):
    length = lax.axis_size(axis)
    return lax.ppermute(shard, axis, [(i, (i + by) % length) for i in range(length)])


def tables(extent):
    node_index = jnp.arange(extent, dtype=jnp.float32) + 1.0
    basis = math.sqrt(2.0 / (extent + 1)) * jnp.sin(
        math.pi * node_index[:, None] * node_index[None, :] / (extent + 1)
    )
    eigenvalues = 2.0 - 2.0 * jnp.cos(math.pi * node_index / (extent + 1))
    return (basis, eigenvalues)


def tangent_matrix(extent):
    node_index = jnp.arange(extent, dtype=jnp.int32)
    distance = jnp.abs(node_index[:, None] - node_index[None, :])
    end_rows = ((node_index == 0) | (node_index == extent - 1)).astype(jnp.float32)
    adjacent = (distance == 1).astype(jnp.float32)
    diagonal_part = (distance == 0).astype(jnp.float32) * (2.0 - end_rows[:, None])
    return adjacent - diagonal_part


def step_weights(step_count):
    midpoint = 0.5 * (upper_edge + lower_edge)
    radius = 0.5 * (upper_edge - lower_edge)
    return [
        1.0 / (midpoint + radius * math.cos(math.pi * (2 * turn_index + 1) / (2 * step_count)))
        for turn_index in range(step_count)
    ]


def divisor(moduli, eigenvalues):
    extent = eigenvalues.shape[0]
    summed = eigenvalues[:, None, None] + eigenvalues[None, :, None] + eigenvalues[None, None, :]
    scaled = moduli[..., None, None, None] * summed + mass_shift
    return scaled.reshape(moduli.shape + (extent, extent * extent))


def body_transform(field_data, basis, paired_basis):
    extent = basis.shape[0]
    full_shape = field_data.shape
    pair_width = paired_basis.shape[0]
    sectioned = jnp.einsum("ix,bcxm->bcim", basis, field_data, precision=highest)
    sectioned = sectioned.reshape(full_shape[:-1] + (full_shape[-1] // pair_width, pair_width))
    sectioned = jnp.einsum("bcxpz,kz->bcxpk", sectioned, paired_basis, precision=highest)
    sectioned = sectioned.reshape(full_shape[:-1] + (extent, extent))
    sectioned = jnp.einsum("jy,bcxyz->bcxjz", basis, sectioned, precision=highest)
    return sectioned.reshape(full_shape)


def body_solve(right_side, scale_table, basis, paired_basis):
    return body_transform(
        body_transform(right_side, basis, paired_basis) / scale_table, basis, paired_basis
    )


f32 = jnp.float32


def np_tables(n):
    g = np.float32
    idx = np.arange(n, dtype=g) + g(1.0)
    arg = (g(math.pi) * idx[:, None]) * idx[None, :] / g(n + 1)
    q = g(math.sqrt(2.0 / (n + 1))) * np.sin(arg)
    e = g(2.0) - g(2.0) * np.cos(g(math.pi) * idx / g(n + 1))
    return q.astype(g), e.astype(g)


def consts(n):
    q, e = np_tables(n)
    h = n // 2
    p4 = np.kron(np.eye(4, dtype=np.float32), q.T)
    w = np.zeros((2, 4, h, 2, 4, h), np.float32)
    qq = q.reshape(h, 2, h, 2)
    for xl in range(4):
        w[:, xl, :, :, xl, :] = np.transpose(qq, (3, 2, 1, 0))
    wy = w.reshape(8 * h, 8 * h)
    ng = n // 4
    lane_h = np.arange(8 * h) // (4 * h)
    lane_xl = (np.arange(8 * h) // h) % 4
    lane_c = np.arange(8 * h) % h
    exy = (e[4 * np.arange(ng)[:, None] + lane_xl[None, :]] + e[2 * lane_c + lane_h][None, :]).astype(np.float32)
    ez = np.ascontiguousarray(np.broadcast_to(e[:, None], (n, 8 * h))).astype(np.float32)
    return stack_left(q), stack_right(p4), stack_right(wy), exy, ez


BF = jnp.bfloat16

def np_split3(w):
    b = ml_dtypes.bfloat16
    w1 = w.astype(b)
    r1 = w - w1.astype(np.float32)
    w2 = r1.astype(b)
    w3 = (r1 - w2.astype(np.float32)).astype(b)
    return w1, w2, w3


def stack_right(w):
    w1, w2, w3 = np_split3(w)
    return np.concatenate([w1, w2, w1, w1], 0)


def stack_left(w):
    w1, w2, w3 = np_split3(w)
    return np.concatenate([w1, w2, w1, w1], 1)


def split3(d):
    d1 = d.astype(BF)
    r1 = d - d1.astype(f32)
    d2 = r1.astype(BF)
    d3 = (r1 - d2.astype(f32)).astype(BF)
    return d1, d2, d3


def sdot(d, w6):
    d1, d2, d3 = split3(d)
    return jnp.dot(jnp.concatenate([d1, d1, d2, d3], 1), w6, preferred_element_type=f32)


def sdot_left(w6, d):
    d1, d2, d3 = split3(d)
    return jnp.dot(w6, jnp.concatenate([d1, d1, d2, d3], 0), preferred_element_type=f32)


def solve_kernel(*refs, with_faces, emit_u, emit_sides, omega, zero_lam, meta):
    it = iter(refs)
    mod_ref, f_ref = next(it), next(it)
    if with_faces:
        nbm_ref = next(it)
        lxu_ref, lxd_ref, ly_ref = (None, None, None) if zero_lam else (next(it), next(it), next(it))
        sxh_ref, sxl_ref, sylo_ref, syhi_ref, rup_ref, rdn_ref, ryp_ref, ryn_ref = (next(it) for _ in range(8))
    q_ref, p_ref, wy_ref, exy_ref, ez_ref = next(it), next(it), next(it), next(it), next(it)
    code_ref = next(it)
    o_ref = next(it) if emit_u else None
    if emit_sides:
        xh_ref, xl_ref, ylo_ref, yhi_ref = next(it), next(it), next(it), next(it)
    if with_faces and emit_sides:
        nlx_ref, nld_ref, nly_ref = next(it), next(it), next(it)
    elif with_faces:
        nlx_ref = nld_ref = nly_ref = None
    s_ref, z_ref = next(it), next(it)
    n = q_ref.shape[0]
    h = n // 2
    w2 = 2 * n
    w4 = 4 * n
    nn = f_ref.shape[-1]
    nch = nn // w2
    npair = nn // w4
    comp = pl.program_id(0)
    m = mod_ref[comp]
    q = q_ref[...]
    r = f_ref[0]
    if with_faces:
        m_up = nbm_ref[0, comp]
        m_dn = nbm_ref[1, comp]
        m_prev = nbm_ref[2, comp]
        m_next = nbm_ref[3, comp]
        has_up = nbm_ref[4, comp]
        has_dn = nbm_ref[5, comp]
        lane_x = lax.broadcasted_iota(jnp.int32, (1, nn), 1) % n
        lane_y = lax.broadcasted_iota(jnp.int32, (n, w2), 1)

        def smooth(res, lanes, width):
            left = pltpu.roll(res, 1, 1)
            right = pltpu.roll(res, width - 1, 1)
            left = jnp.where(lanes % n == 0, 0.0, left)
            right = jnp.where(lanes % n == n - 1, 0.0, right)
            diag = jnp.where((lanes % n == 0) | (lanes % n == n - 1), -1.0, -2.0)
            return res + 0.25 * ((left + right) + diag * res)

        xu = 0.0 if zero_lam else lxu_ref[0]
        res = (sxh_ref[0, 0:1, 0:nn] + rup_ref[0]) / (m + m_up) - xu
        xhi_face = (xu + omega * smooth(res, lane_x, nn)) * has_up
        xd = 0.0 if zero_lam else lxd_ref[0]
        res = (rdn_ref[0] + sxl_ref[0, 0:1, 0:nn]) / (m_dn + m) - xd
        xlo_face = (xd + omega * smooth(res, lane_x, nn)) * has_dn
        ly = 0.0 if zero_lam else ly_ref[0]
        lo = lane_y < n
        recv = jnp.concatenate([ryp_ref[0, 0, 0:n], ryn_ref[0, 0, 0:n]], 1)
        own = jnp.concatenate([sylo_ref[0, 0, 0:n], syhi_ref[0, 0, 0:n]], 1)
        res = (own + recv) / (m + jnp.where(lo, m_prev, m_next)) - ly
        yadd = ly + omega * smooth(res, lane_y, w2)
        if nlx_ref is not None:
            nlx_ref[0] = xhi_face
            nld_ref[0] = xlo_face
            nly_ref[0] = yadd
        rows = lax.broadcasted_iota(jnp.int32, (n, nn), 0)
        added = jnp.where(rows == 0, xlo_face, 0.0) + jnp.where(rows == n - 1, xhi_face, 0.0)
        lane = lane_y
        first = added[:, :w2] + jnp.where(lane < n, yadd, 0.0)
        last = added[:, nn - w2:] + jnp.where(lane >= n, yadd, 0.0)
        added = jnp.concatenate([first, added[:, w2:nn - w2], last], 1)
        r = r + (2.0 * m) * added
    a = sdot_left(q, r)
    for cp in range(npair):
        z_ref[cp * n:(cp + 1) * n, :] = a[:, cp * w4:(cp + 1) * w4]
    zo = sdot(z_ref[...], p_ref[...])
    for cp in range(npair):
        for cb in range(2):
            s_ref[(2 * cp + cb) * n:(2 * cp + cb + 1) * n, :] = zo[cp * n:(cp + 1) * n, cb * w2:(cb + 1) * w2]
    wy = wy_ref[...]
    ez = ez_ref[...]
    XG = 4
    GPI = 8

    def body(it_, carry):
        lhs = []
        for gi in range(GPI):
            g = it_ * GPI + gi
            blk = jnp.concatenate([s_ref[pl.ds(g * XG + xl, h, stride=n), :] for xl in range(XG)], 0)
            tb = blk.T
            lhs.append(jnp.concatenate([tb[:n], tb[n:]], 1))
        v = sdot(jnp.concatenate(lhs, 0), wy)
        div = jnp.concatenate([m * (exy_ref[pl.ds(it_ * GPI + gi, 1), :] + ez) + 0.02 for gi in range(GPI)], 0)
        v = v / div
        v = sdot(v, wy)
        for gi in range(GPI):
            g = it_ * GPI + gi
            vg = v[gi * n:(gi + 1) * n]
            tb = jnp.concatenate([vg[:, :w2], vg[:, w2:]], 0).T
            for xl in range(XG):
                s_ref[pl.ds(g * XG + xl, h, stride=n), :] = tb[xl * h:(xl + 1) * h]
        return carry
    lax.fori_loop(0, n // (XG * GPI), body, 0, unroll=True)
    for cp in range(npair):
        z_ref[cp * n:(cp + 1) * n, :] = jnp.concatenate(
            [s_ref[(2 * cp) * n:(2 * cp + 1) * n, :], s_ref[(2 * cp + 1) * n:(2 * cp + 2) * n, :]], 1)
    zo = sdot(z_ref[...], p_ref[...])
    b = jnp.concatenate([zo[cp * n:(cp + 1) * n, :] for cp in range(npair)], 1)
    u = sdot_left(q, b)
    if emit_u:
        o_ref[0] = u

    def slope(p0, p1, p2, p3):
        return m * (11.0 / 6.0 * p0 - 3.0 * p1 + 1.5 * p2 - p3 / 3.0)
    if emit_sides:
        m_row = jnp.full((1, nn), m, f32)
        xh_ref[0, 0:1, 0:nn] = m * u[n - 1:n] + 0.5 * slope(u[n - 1:n], u[n - 2:n - 1], u[n - 3:n - 2], u[n - 4:n - 3])
        lane_t = lax.broadcasted_iota(jnp.int32, (1, w2), 1)
        if meta:
            xh_ref[0, 0:1, nn:nn + w2] = jnp.where(lane_t < n, m, code_ref[0])
        xl_ref[0, 0:1, 0:nn] = m * u[0:1] + 0.5 * slope(u[0:1], u[1:2], u[2:3], u[3:4])
        if meta:
            xl_ref[0, 0:1, nn:nn + w2] = jnp.full((1, w2), m, f32)
        c_hi = u[:, nn - w2:]
        c_hi2 = u[:, nn - 2 * w2:nn - w2]
        s_hi = m * c_hi + 0.5 * slope(c_hi, pltpu.roll(c_hi, n, 1), c_hi2, pltpu.roll(c_hi2, n, 1))
        c_lo = u[:, :w2]
        c_lo2 = u[:, w2:2 * w2]
        s_lo = m * c_lo + 0.5 * slope(c_lo, pltpu.roll(c_lo, n, 1), c_lo2, pltpu.roll(c_lo2, n, 1))
        lane_s = lax.broadcasted_iota(jnp.int32, (n, w2), 1)
        ylo_ref[0, 0, 0:n] = s_lo[:, :n]
        yhi_ref[0, 0, 0:n] = pltpu.roll(s_hi, n, 1)[:, :n]
        if meta:
            ylo_ref[0, 0, n:n + 8] = jnp.full((8, n), m, f32)
            yhi_ref[0, 0, n:n + 8] = jnp.full((8, n), m, f32)


def kernel_sweep(rhs, moduli, code, state=None, emit_u=True, emit_sides=False, omega=0.0, meta=False):
    ncomp, n, nn = rhs.shape
    q, p4, wy, exy, ez = consts(n)
    full = lambda shp: pl.BlockSpec(shp, lambda c: (0,) * len(shp))
    comp3 = lambda shp: pl.BlockSpec((1,) + shp, lambda c: (c,) + (0,) * len(shp))
    smem = pl.BlockSpec(memory_space=pltpu.SMEM)
    in_specs = [smem, comp3((n, nn))]
    args = [moduli, rhs]
    zero_lam = state is not None and state[1] is None
    if state is not None:
        if zero_lam:
            state = state[:1] + state[4:]
            in_specs += [smem]
        else:
            in_specs += [smem, comp3((1, nn)), comp3((1, nn)), comp3((n, 2 * n))]
        in_specs += [comp3(x.shape[1:]) for x in state[-8:]]
        args += list(state)
    in_specs += [full(q.shape), full(p4.shape), full(wy.shape), full(exy.shape), full(ez.shape), smem]
    args += [q, p4, wy, exy, ez, code]
    out_specs, out_shape = [], []
    if emit_u:
        out_specs.append(comp3((n, nn)))
        out_shape.append(jax.ShapeDtypeStruct(rhs.shape, f32))
    if emit_sides:
        wx, ry = (nn + 2 * n, n + 8) if meta else (nn, n)
        out_specs += [comp3((1, wx)), comp3((1, wx)), comp3((1, ry, n)), comp3((1, ry, n))]
        out_shape += [jax.ShapeDtypeStruct((ncomp, 1, wx), f32), jax.ShapeDtypeStruct((ncomp, 1, wx), f32),
                      jax.ShapeDtypeStruct((ncomp, 1, ry, n), f32), jax.ShapeDtypeStruct((ncomp, 1, ry, n), f32)]
        if state is not None:
            out_specs += [comp3((1, nn)), comp3((1, nn)), comp3((n, 2 * n))]
            out_shape += [jax.ShapeDtypeStruct((ncomp, 1, nn), f32), jax.ShapeDtypeStruct((ncomp, 1, nn), f32),
                          jax.ShapeDtypeStruct((ncomp, n, 2 * n), f32)]
    kernel = functools.partial(solve_kernel, with_faces=state is not None, emit_u=emit_u,
                               emit_sides=emit_sides, omega=omega, zero_lam=zero_lam, meta=meta)
    return pl.pallas_call(
        kernel,
        grid=(ncomp,),
        in_specs=in_specs,
        out_specs=out_specs,
        out_shape=out_shape,
        scratch_shapes=[pltpu.VMEM((nn // 2, 2 * n), f32), pltpu.VMEM((nn // 4, 4 * n), f32)],
    )(*args)


def orient(face_field, code_table, extent):
    square = face_field.reshape(face_field.shape[:-1] + (extent, extent))
    flip_rows = (code_table % 2 == 1)[..., None, None, None]
    flip_cols = (code_table // 2 == 1)[..., None, None, None]
    square = jnp.where(flip_rows, jnp.flip(square, -2), square)
    square = jnp.where(flip_cols, jnp.flip(square, -1), square)
    return square.reshape(face_field.shape)


def face_data(solution, moduli):
    extent = solution.shape[-2]
    cube_view = solution.reshape(solution.shape[:-1] + (extent, extent))
    flat_shape = solution.shape[:-2] + (extent * extent,)

    def pack_side(planes):
        normal_slope = 11.0 / 6.0 * planes[0] - 3.0 * planes[1] + 1.5 * planes[2] - planes[3] / 3.0
        return (planes[0], moduli[..., None] * normal_slope)

    x_high = pack_side([solution[..., extent - 1 - plane_depth, :] for plane_depth in range(4)])
    x_low = pack_side([solution[..., plane_depth, :] for plane_depth in range(4)])
    y_high = pack_side(
        [
            cube_view[..., extent - 1 - plane_depth, :].reshape(flat_shape)
            for plane_depth in range(4)
        ]
    )
    y_low = pack_side(
        [cube_view[..., plane_depth, :].reshape(flat_shape) for plane_depth in range(4)]
    )
    return (x_high, x_low, y_high, y_low)


def place_faces(source_field, moduli, x_low, x_high, y_low, y_high):
    extent = source_field.shape[-2]
    added = jnp.zeros_like(source_field)
    added = added.at[..., 0, :].add(x_low)
    added = added.at[..., extent - 1, :].add(x_high)
    cube_view = added.reshape(added.shape[:-1] + (extent, extent))
    low_square = y_low.reshape(y_low.shape[:-1] + (extent, extent))
    high_square = y_high.reshape(y_high.shape[:-1] + (extent, extent))
    cube_view = cube_view.at[..., 0, :].add(low_square)
    cube_view = cube_view.at[..., extent - 1, :].add(high_square)
    added = cube_view.reshape(source_field.shape)
    return source_field + inject_scale * moduli[..., None, None] * added


def trace_update(current, side_a, side_b, moduli_a, moduli_b, omega_step, tangent):
    extent = tangent.shape[0]
    weight_a = moduli_a[..., None]
    weight_b = moduli_b[..., None]
    residue = (
        weight_a * side_a[0] + weight_b * side_b[0] + traction_mix * (side_a[1] + side_b[1])
    ) / (weight_a + weight_b) - current
    rows_view = residue.reshape(residue.shape[:-1] + (residue.shape[-1] // extent, extent))
    smoothed = rows_view + penalty_mix * jnp.einsum(
        "...z,zk->...k", rows_view, tangent, precision=highest
    )
    return current + omega_step * smoothed.reshape(residue.shape)


def flat_update(current, sum_a, sum_b, moduli_a, moduli_b, omega_step, tangent):
    extent = tangent.shape[0]
    residue = (sum_a + sum_b) / (moduli_a + moduli_b)[..., None] - current
    rows_view = residue.reshape(residue.shape[:-1] + (residue.shape[-1] // extent, extent))
    smoothed = rows_view + penalty_mix * jnp.einsum("...z,zk->...k", rows_view, tangent, precision=highest)
    return current + omega_step * smoothed.reshape(residue.shape)


def square_update(current, sum_a, sum_b, moduli_a, moduli_b, omega_step, tangent):
    residue = (sum_a + sum_b) / (moduli_a + moduli_b)[..., None, None] - current
    smoothed = residue + penalty_mix * jnp.einsum("...z,zk->...k", residue, tangent, precision=highest)
    return current + omega_step * smoothed


def shards(forcing, modulus, orient_codes):
    extent = forcing.shape[3]
    blocks = forcing.shape[1]
    flat = extent * extent
    source_field = forcing[0]
    moduli = modulus[0]
    codes_here = orient_codes[0]
    code_values = codes_here.astype(jnp.float32)
    omegas = step_weights(ITERS)
    slab_count = lax.axis_size("blk")
    slab_index = lax.axis_index("blk")
    has_up = jnp.broadcast_to((slab_index < slab_count - 1).astype(jnp.float32), (blocks, 3))
    has_down = jnp.broadcast_to((slab_index > 0).astype(jnp.float32), (blocks, 3))
    lam_x_up = lam_x_down = lam_y = [None] * blocks
    state = [None] * blocks
    for sweep in range(ITERS + 1):
        last = sweep == ITERS
        omega = omegas[sweep - 1] if sweep > 0 else 0.0
        outs = [
            kernel_sweep(source_field[b], moduli[b], code_values[b:b + 1], state[b], emit_u=last,
                         emit_sides=not last, omega=omega, meta=sweep == 0)
            for b in range(blocks)
        ]
        if last:
            return jnp.stack([o[0] for o in outs], 0)[None]
        xh, xl, ylo, yhi = (jnp.stack([o[k] for o in outs], 0) for k in range(4))
        if sweep > 0:
            lam_x_up, lam_x_down, lam_y = (jnp.stack([o[k] for o in outs], 0) for k in range(4, 7))
        upper = shifted(xl, "blk", -1)
        lower = shifted(xh, "blk", 1)
        nxt = jnp.concatenate([ylo[1:], shifted_2(ylo[:1], "face", -1)], 0)
        prv = jnp.concatenate([shifted_2(yhi[-1:], "face", 1), yhi[:-1]], 0)
        if sweep == 0:
            codes_down = lower[:, 0, 0, flat + extent].astype(jnp.int32)
            neighbour_moduli = jnp.stack(
                [upper[:, :, 0, flat], lower[:, :, 0, flat], prv[:, :, 0, extent, 0], nxt[:, :, 0, extent, 0],
                 has_up, has_down], 1
            )
        up_sum = orient(upper[:, :, 0, :flat], codes_here, extent)[:, :, None]
        down_sum = orient(lower[:, :, 0, :flat], codes_down, extent)[:, :, None]
        state = [
            (neighbour_moduli[b], lam_x_up[b], lam_x_down[b], lam_y[b], xh[b], xl[b], ylo[b], yhi[b],
             up_sum[b], down_sum[b], prv[b], nxt[b])
            for b in range(blocks)
        ]


def solution(mesh):
    placed = (P("blk", "face", None, None, None), P("blk", "face", None), P("blk", "face"))
    return jax.shard_map(
        shards,
        mesh=mesh,
        in_specs=placed,
        out_specs=P("blk", "face", None, None, None),
        check_vma=False,
    )
```

```python
import functools
import math

import jax
import jax.numpy as jnp
from jax import lax
from jax.sharding import PartitionSpec as P
from jax.experimental import pallas as pl
from jax.experimental.pallas import tpu as pltpu
import numpy as np
import ml_dtypes

ITERS = 2


mass_shift = 0.02
inject_scale = 2.0
traction_mix = 0.5
penalty_mix = 0.25
lower_edge = 0.3
upper_edge = 1.5
highest = lax.Precision.HIGHEST


def shifted(shard, axis, by):
    length = lax.axis_size(axis)
    pairs = [(i, i + by) for i in range(length) if 0 <= i + by < length]
    return lax.ppermute(shard, axis, pairs)


def shifted_2(shard, axis, by):
    length = lax.axis_size(axis)
    return lax.ppermute(shard, axis, [(i, (i + by) % length) for i in range(length)])


def tables(extent):
    node_index = jnp.arange(extent, dtype=jnp.float32) + 1.0
    basis = math.sqrt(2.0 / (extent + 1)) * jnp.sin(
        math.pi * node_index[:, None] * node_index[None, :] / (extent + 1)
    )
    eigenvalues = 2.0 - 2.0 * jnp.cos(math.pi * node_index / (extent + 1))
    return (basis, eigenvalues)


def tangent_matrix(extent):
    node_index = jnp.arange(extent, dtype=jnp.int32)
    distance = jnp.abs(node_index[:, None] - node_index[None, :])
    end_rows = ((node_index == 0) | (node_index == extent - 1)).astype(jnp.float32)
    adjacent = (distance == 1).astype(jnp.float32)
    diagonal_part = (distance == 0).astype(jnp.float32) * (2.0 - end_rows[:, None])
    return adjacent - diagonal_part


def step_weights(step_count):
    midpoint = 0.5 * (upper_edge + lower_edge)
    radius = 0.5 * (upper_edge - lower_edge)
    return [
        1.0 / (midpoint + radius * math.cos(math.pi * (2 * turn_index + 1) / (2 * step_count)))
        for turn_index in range(step_count)
    ]


def divisor(moduli, eigenvalues):
    extent = eigenvalues.shape[0]
    summed = eigenvalues[:, None, None] + eigenvalues[None, :, None] + eigenvalues[None, None, :]
    scaled = moduli[..., None, None, None] * summed + mass_shift
    return scaled.reshape(moduli.shape + (extent, extent * extent))


def body_transform(field_data, basis, paired_basis):
    extent = basis.shape[0]
    full_shape = field_data.shape
    pair_width = paired_basis.shape[0]
    sectioned = jnp.einsum("ix,bcxm->bcim", basis, field_data, precision=highest)
    sectioned = sectioned.reshape(full_shape[:-1] + (full_shape[-1] // pair_width, pair_width))
    sectioned = jnp.einsum("bcxpz,kz->bcxpk", sectioned, paired_basis, precision=highest)
    sectioned = sectioned.reshape(full_shape[:-1] + (extent, extent))
    sectioned = jnp.einsum("jy,bcxyz->bcxjz", basis, sectioned, precision=highest)
    return sectioned.reshape(full_shape)


def body_solve(right_side, scale_table, basis, paired_basis):
    return body_transform(
        body_transform(right_side, basis, paired_basis) / scale_table, basis, paired_basis
    )


f32 = jnp.float32


def np_tables(n):
    g = np.float32
    idx = np.arange(n, dtype=g) + g(1.0)
    arg = (g(math.pi) * idx[:, None]) * idx[None, :] / g(n + 1)
    q = g(math.sqrt(2.0 / (n + 1))) * np.sin(arg)
    e = g(2.0) - g(2.0) * np.cos(g(math.pi) * idx / g(n + 1))
    return q.astype(g), e.astype(g)


def consts(n):
    q, e = np_tables(n)
    h = n // 2
    p4 = np.kron(np.eye(4, dtype=np.float32), q.T)
    w = np.zeros((2, 4, h, 2, 4, h), np.float32)
    qq = q.reshape(h, 2, h, 2)
    for xl in range(4):
        w[:, xl, :, :, xl, :] = np.transpose(qq, (3, 2, 1, 0))
    wy = w.reshape(8 * h, 8 * h)
    ng = n // 4
    lane_h = np.arange(8 * h) // (4 * h)
    lane_xl = (np.arange(8 * h) // h) % 4
    lane_c = np.arange(8 * h) % h
    exy = (e[4 * np.arange(ng)[:, None] + lane_xl[None, :]] + e[2 * lane_c + lane_h][None, :]).astype(np.float32)
    ez = np.ascontiguousarray(np.broadcast_to(e[:, None], (n, 8 * h))).astype(np.float32)
    return stack_left(q), stack_right(p4), stack_right(wy), exy, ez


BF = jnp.bfloat16

def np_split3(w):
    b = ml_dtypes.bfloat16
    w1 = w.astype(b)
    r1 = w - w1.astype(np.float32)
    w2 = r1.astype(b)
    w3 = (r1 - w2.astype(np.float32)).astype(b)
    return w1, w2, w3


def stack_right(w):
    w1, w2, w3 = np_split3(w)
    return np.concatenate([w1, w2, w1, w1], 0)


def stack_left(w):
    w1, w2, w3 = np_split3(w)
    return np.concatenate([w1, w2, w1, w1], 1)


def split3(d):
    d1 = d.astype(BF)
    r1 = d - d1.astype(f32)
    d2 = r1.astype(BF)
    d3 = (r1 - d2.astype(f32)).astype(BF)
    return d1, d2, d3


def sdot(d, w6):
    d1, d2, d3 = split3(d)
    return jnp.dot(jnp.concatenate([d1, d1, d2, d3], 1), w6, preferred_element_type=f32)


def sdot_left(w6, d):
    d1, d2, d3 = split3(d)
    return jnp.dot(w6, jnp.concatenate([d1, d1, d2, d3], 0), preferred_element_type=f32)


def solve_kernel(*refs, with_faces, emit_u, emit_sides, omega, zero_lam, meta):
    it = iter(refs)
    mod_ref, f_ref = next(it), next(it)
    if with_faces:
        nbm_ref = next(it)
        lxu_ref, lxd_ref, ly_ref = (None, None, None) if zero_lam else (next(it), next(it), next(it))
        sxh_ref, sxl_ref, sylo_ref, syhi_ref, rup_ref, rdn_ref, ryp_ref, ryn_ref = (next(it) for _ in range(8))
    q_ref, p_ref, wy_ref, exy_ref, ez_ref = next(it), next(it), next(it), next(it), next(it)
    code_ref = next(it)
    o_ref = next(it) if emit_u else None
    if emit_sides:
        xh_ref, xl_ref, ylo_ref, yhi_ref = next(it), next(it), next(it), next(it)
    if with_faces and emit_sides:
        nlx_ref, nld_ref, nly_ref = next(it), next(it), next(it)
    elif with_faces:
        nlx_ref = nld_ref = nly_ref = None
    s_ref, z_ref = next(it), next(it)
    n = q_ref.shape[0]
    h = n // 2
    w2 = 2 * n
    w4 = 4 * n
    nn = f_ref.shape[-1]
    nch = nn // w2
    npair = nn // w4
    comp = pl.program_id(0)
    m = mod_ref[comp]
    q = q_ref[...]
    r = f_ref[0]
    if with_faces:
        m_up = nbm_ref[0, comp]
        m_dn = nbm_ref[1, comp]
        m_prev = nbm_ref[2, comp]
        m_next = nbm_ref[3, comp]
        has_up = nbm_ref[4, comp]
        has_dn = nbm_ref[5, comp]
        lane_x = lax.broadcasted_iota(jnp.int32, (1, nn), 1) % n
        lane_y = lax.broadcasted_iota(jnp.int32, (n, w2), 1)

        def smooth(res, lanes, width):
            left = pltpu.roll(res, 1, 1)
            right = pltpu.roll(res, width - 1, 1)
            left = jnp.where(lanes % n == 0, 0.0, left)
            right = jnp.where(lanes % n == n - 1, 0.0, right)
            diag = jnp.where((lanes % n == 0) | (lanes % n == n - 1), -1.0, -2.0)
            return res + 0.25 * ((left + right) + diag * res)

        xu = 0.0 if zero_lam else lxu_ref[0]
        res = (sxh_ref[0, 0:1, 0:nn] + rup_ref[0]) / (m + m_up) - xu
        xhi_face = (xu + omega * smooth(res, lane_x, nn)) * has_up
        xd = 0.0 if zero_lam else lxd_ref[0]
        res = (rdn_ref[0] + sxl_ref[0, 0:1, 0:nn]) / (m_dn + m) - xd
        xlo_face = (xd + omega * smooth(res, lane_x, nn)) * has_dn
        ly = 0.0 if zero_lam else ly_ref[0]
        lo = lane_y < n
        recv = jnp.concatenate([ryp_ref[0, 0, 0:n], ryn_ref[0, 0, 0:n]], 1)
        own = jnp.concatenate([sylo_ref[0, 0, 0:n], syhi_ref[0, 0, 0:n]], 1)
        res = (own + recv) / (m + jnp.where(lo, m_prev, m_next)) - ly
        yadd = ly + omega * smooth(res, lane_y, w2)
        if nlx_ref is not None:
            nlx_ref[0] = xhi_face
            nld_ref[0] = xlo_face
            nly_ref[0] = yadd
        rows = lax.broadcasted_iota(jnp.int32, (n, nn), 0)
        added = jnp.where(rows == 0, xlo_face, 0.0) + jnp.where(rows == n - 1, xhi_face, 0.0)
        lane = lane_y
        first = added[:, :w2] + jnp.where(lane < n, yadd, 0.0)
        last = added[:, nn - w2:] + jnp.where(lane >= n, yadd, 0.0)
        added = jnp.concatenate([first, added[:, w2:nn - w2], last], 1)
        r = r + (2.0 * m) * added
    a = sdot_left(q, r)
    for cp in range(npair):
        z_ref[cp * n:(cp + 1) * n, :] = a[:, cp * w4:(cp + 1) * w4]
    zo = sdot(z_ref[...], p_ref[...])
    for cp in range(npair):
        for cb in range(2):
            s_ref[(2 * cp + cb) * n:(2 * cp + cb + 1) * n, :] = zo[cp * n:(cp + 1) * n, cb * w2:(cb + 1) * w2]
    wy = wy_ref[...]
    ez = ez_ref[...]
    XG = 4
    GPI = 4

    def body(it_, carry):
        lhs = []
        for gi in range(GPI):
            g = it_ * GPI + gi
            blk = jnp.concatenate([s_ref[pl.ds(g * XG + xl, h, stride=n), :] for xl in range(XG)], 0)
            tb = blk.T
            lhs.append(jnp.concatenate([tb[:n], tb[n:]], 1))
        v = sdot(jnp.concatenate(lhs, 0), wy)
        div = jnp.concatenate([m * (exy_ref[pl.ds(it_ * GPI + gi, 1), :] + ez) + 0.02 for gi in range(GPI)], 0)
        v = v / div
        v = sdot(v, wy)
        for gi in range(GPI):
            g = it_ * GPI + gi
            vg = v[gi * n:(gi + 1) * n]
            tb = jnp.concatenate([vg[:, :w2], vg[:, w2:]], 0).T
            for xl in range(XG):
                s_ref[pl.ds(g * XG + xl, h, stride=n), :] = tb[xl * h:(xl + 1) * h]
        return carry
    lax.fori_loop(0, n // (XG * GPI), body, 0, unroll=True)
    for cp in range(npair):
        z_ref[cp * n:(cp + 1) * n, :] = jnp.concatenate(
            [s_ref[(2 * cp) * n:(2 * cp + 1) * n, :], s_ref[(2 * cp + 1) * n:(2 * cp + 2) * n, :]], 1)
    zo = sdot(z_ref[...], p_ref[...])
    b = jnp.concatenate([zo[cp * n:(cp + 1) * n, :] for cp in range(npair)], 1)
    u = sdot_left(q, b)
    if emit_u:
        o_ref[0] = u

    def slope(p0, p1, p2, p3):
        return m * (11.0 / 6.0 * p0 - 3.0 * p1 + 1.5 * p2 - p3 / 3.0)
    if emit_sides:
        m_row = jnp.full((1, nn), m, f32)
        xh_ref[0, 0:1, 0:nn] = m * u[n - 1:n] + 0.5 * slope(u[n - 1:n], u[n - 2:n - 1], u[n - 3:n - 2], u[n - 4:n - 3])
        lane_t = lax.broadcasted_iota(jnp.int32, (1, w2), 1)
        if meta:
            xh_ref[0, 0:1, nn:nn + w2] = jnp.where(lane_t < n, m, code_ref[0])
        xl_ref[0, 0:1, 0:nn] = m * u[0:1] + 0.5 * slope(u[0:1], u[1:2], u[2:3], u[3:4])
        if meta:
            xl_ref[0, 0:1, nn:nn + w2] = jnp.full((1, w2), m, f32)
        c_hi = u[:, nn - w2:]
        c_hi2 = u[:, nn - 2 * w2:nn - w2]
        s_hi = m * c_hi + 0.5 * slope(c_hi, pltpu.roll(c_hi, n, 1), c_hi2, pltpu.roll(c_hi2, n, 1))
        c_lo = u[:, :w2]
        c_lo2 = u[:, w2:2 * w2]
        s_lo = m * c_lo + 0.5 * slope(c_lo, pltpu.roll(c_lo, n, 1), c_lo2, pltpu.roll(c_lo2, n, 1))
        lane_s = lax.broadcasted_iota(jnp.int32, (n, w2), 1)
        ylo_ref[0, 0, 0:n] = s_lo[:, :n]
        yhi_ref[0, 0, 0:n] = pltpu.roll(s_hi, n, 1)[:, :n]
        if meta:
            ylo_ref[0, 0, n:n + 8] = jnp.full((8, n), m, f32)
            yhi_ref[0, 0, n:n + 8] = jnp.full((8, n), m, f32)


def kernel_sweep(rhs, moduli, code, state=None, emit_u=True, emit_sides=False, omega=0.0, meta=False):
    ncomp, n, nn = rhs.shape
    q, p4, wy, exy, ez = consts(n)
    full = lambda shp: pl.BlockSpec(shp, lambda c: (0,) * len(shp))
    comp3 = lambda shp: pl.BlockSpec((1,) + shp, lambda c: (c,) + (0,) * len(shp))
    smem = pl.BlockSpec(memory_space=pltpu.SMEM)
    in_specs = [smem, comp3((n, nn))]
    args = [moduli, rhs]
    zero_lam = state is not None and state[1] is None
    if state is not None:
        if zero_lam:
            state = state[:1] + state[4:]
            in_specs += [smem]
        else:
            in_specs += [smem, comp3((1, nn)), comp3((1, nn)), comp3((n, 2 * n))]
        in_specs += [comp3(x.shape[1:]) for x in state[-8:]]
        args += list(state)
    in_specs += [full(q.shape), full(p4.shape), full(wy.shape), full(exy.shape), full(ez.shape), smem]
    args += [q, p4, wy, exy, ez, code]
    out_specs, out_shape = [], []
    if emit_u:
        out_specs.append(comp3((n, nn)))
        out_shape.append(jax.ShapeDtypeStruct(rhs.shape, f32))
    if emit_sides:
        wx, ry = (nn + 2 * n, n + 8) if meta else (nn, n)
        out_specs += [comp3((1, wx)), comp3((1, wx)), comp3((1, ry, n)), comp3((1, ry, n))]
        out_shape += [jax.ShapeDtypeStruct((ncomp, 1, wx), f32), jax.ShapeDtypeStruct((ncomp, 1, wx), f32),
                      jax.ShapeDtypeStruct((ncomp, 1, ry, n), f32), jax.ShapeDtypeStruct((ncomp, 1, ry, n), f32)]
        if state is not None:
            out_specs += [comp3((1, nn)), comp3((1, nn)), comp3((n, 2 * n))]
            out_shape += [jax.ShapeDtypeStruct((ncomp, 1, nn), f32), jax.ShapeDtypeStruct((ncomp, 1, nn), f32),
                          jax.ShapeDtypeStruct((ncomp, n, 2 * n), f32)]
    kernel = functools.partial(solve_kernel, with_faces=state is not None, emit_u=emit_u,
                               emit_sides=emit_sides, omega=omega, zero_lam=zero_lam, meta=meta)
    return pl.pallas_call(
        kernel,
        grid=(ncomp,),
        in_specs=in_specs,
        out_specs=out_specs,
        out_shape=out_shape,
        scratch_shapes=[pltpu.VMEM((nn // 2, 2 * n), f32), pltpu.VMEM((nn // 4, 4 * n), f32)],
    )(*args)


def orient(face_field, code_table, extent):
    square = face_field.reshape(face_field.shape[:-1] + (extent, extent))
    flip_rows = (code_table % 2 == 1)[..., None, None, None]
    flip_cols = (code_table // 2 == 1)[..., None, None, None]
    square = jnp.where(flip_rows, jnp.flip(square, -2), square)
    square = jnp.where(flip_cols, jnp.flip(square, -1), square)
    return square.reshape(face_field.shape)


def face_data(solution, moduli):
    extent = solution.shape[-2]
    cube_view = solution.reshape(solution.shape[:-1] + (extent, extent))
    flat_shape = solution.shape[:-2] + (extent * extent,)

    def pack_side(planes):
        normal_slope = 11.0 / 6.0 * planes[0] - 3.0 * planes[1] + 1.5 * planes[2] - planes[3] / 3.0
        return (planes[0], moduli[..., None] * normal_slope)

    x_high = pack_side([solution[..., extent - 1 - plane_depth, :] for plane_depth in range(4)])
    x_low = pack_side([solution[..., plane_depth, :] for plane_depth in range(4)])
    y_high = pack_side(
        [
            cube_view[..., extent - 1 - plane_depth, :].reshape(flat_shape)
            for plane_depth in range(4)
        ]
    )
    y_low = pack_side(
        [cube_view[..., plane_depth, :].reshape(flat_shape) for plane_depth in range(4)]
    )
    return (x_high, x_low, y_high, y_low)


def place_faces(source_field, moduli, x_low, x_high, y_low, y_high):
    extent = source_field.shape[-2]
    added = jnp.zeros_like(source_field)
    added = added.at[..., 0, :].add(x_low)
    added = added.at[..., extent - 1, :].add(x_high)
    cube_view = added.reshape(added.shape[:-1] + (extent, extent))
    low_square = y_low.reshape(y_low.shape[:-1] + (extent, extent))
    high_square = y_high.reshape(y_high.shape[:-1] + (extent, extent))
    cube_view = cube_view.at[..., 0, :].add(low_square)
    cube_view = cube_view.at[..., extent - 1, :].add(high_square)
    added = cube_view.reshape(source_field.shape)
    return source_field + inject_scale * moduli[..., None, None] * added


def trace_update(current, side_a, side_b, moduli_a, moduli_b, omega_step, tangent):
    extent = tangent.shape[0]
    weight_a = moduli_a[..., None]
    weight_b = moduli_b[..., None]
    residue = (
        weight_a * side_a[0] + weight_b * side_b[0] + traction_mix * (side_a[1] + side_b[1])
    ) / (weight_a + weight_b) - current
    rows_view = residue.reshape(residue.shape[:-1] + (residue.shape[-1] // extent, extent))
    smoothed = rows_view + penalty_mix * jnp.einsum(
        "...z,zk->...k", rows_view, tangent, precision=highest
    )
    return current + omega_step * smoothed.reshape(residue.shape)


def flat_update(current, sum_a, sum_b, moduli_a, moduli_b, omega_step, tangent):
    extent = tangent.shape[0]
    residue = (sum_a + sum_b) / (moduli_a + moduli_b)[..., None] - current
    rows_view = residue.reshape(residue.shape[:-1] + (residue.shape[-1] // extent, extent))
    smoothed = rows_view + penalty_mix * jnp.einsum("...z,zk->...k", rows_view, tangent, precision=highest)
    return current + omega_step * smoothed.reshape(residue.shape)


def square_update(current, sum_a, sum_b, moduli_a, moduli_b, omega_step, tangent):
    residue = (sum_a + sum_b) / (moduli_a + moduli_b)[..., None, None] - current
    smoothed = residue + penalty_mix * jnp.einsum("...z,zk->...k", residue, tangent, precision=highest)
    return current + omega_step * smoothed


def shards(forcing, modulus, orient_codes):
    extent = forcing.shape[3]
    blocks = forcing.shape[1]
    flat = extent * extent
    source_field = forcing[0]
    moduli = modulus[0]
    codes_here = orient_codes[0]
    code_values = codes_here.astype(jnp.float32)
    omegas = step_weights(ITERS)
    slab_count = lax.axis_size("blk")
    slab_index = lax.axis_index("blk")
    has_up = jnp.broadcast_to((slab_index < slab_count - 1).astype(jnp.float32), (blocks, 3))
    has_down = jnp.broadcast_to((slab_index > 0).astype(jnp.float32), (blocks, 3))
    lam_x_up = lam_x_down = lam_y = [None] * blocks
    state = [None] * blocks
    for sweep in range(ITERS + 1):
        last = sweep == ITERS
        omega = omegas[sweep - 1] if sweep > 0 else 0.0
        outs = [
            kernel_sweep(source_field[b], moduli[b], code_values[b:b + 1], state[b], emit_u=last,
                         emit_sides=not last, omega=omega, meta=sweep == 0)
            for b in range(blocks)
        ]
        if last:
            return jnp.stack([o[0] for o in outs], 0)[None]
        xh, xl, ylo, yhi = (jnp.stack([o[k] for o in outs], 0) for k in range(4))
        if sweep > 0:
            lam_x_up, lam_x_down, lam_y = (jnp.stack([o[k] for o in outs], 0) for k in range(4, 7))
        upper = shifted(xl, "blk", -1)
        lower = shifted(xh, "blk", 1)
        nxt = jnp.concatenate([ylo[1:], shifted_2(ylo[:1], "face", -1)], 0)
        prv = jnp.concatenate([shifted_2(yhi[-1:], "face", 1), yhi[:-1]], 0)
        if sweep == 0:
            codes_down = lower[:, 0, 0, flat + extent].astype(jnp.int32)
            neighbour_moduli = jnp.stack(
                [upper[:, :, 0, flat], lower[:, :, 0, flat], prv[:, :, 0, extent, 0], nxt[:, :, 0, extent, 0],
                 has_up, has_down], 1
            )
        up_sum = orient(upper[:, :, 0, :flat], codes_here, extent)[:, :, None]
        down_sum = orient(lower[:, :, 0, :flat], codes_down, extent)[:, :, None]
        state = [
            (neighbour_moduli[b], lam_x_up[b], lam_x_down[b], lam_y[b], xh[b], xl[b], ylo[b], yhi[b],
             up_sum[b], down_sum[b], prv[b], nxt[b])
            for b in range(blocks)
        ]


def solution(mesh):
    placed = (P("blk", "face", None, None, None), P("blk", "face", None), P("blk", "face"))
    return jax.shard_map(
        shards,
        mesh=mesh,
        in_specs=placed,
        out_specs=P("blk", "face", None, None, None),
        check_vma=False,
    )
```

```python
import functools
import math

import jax
import jax.numpy as jnp
from jax import lax
from jax.sharding import PartitionSpec as P
from jax.experimental import pallas as pl
from jax.experimental.pallas import tpu as pltpu
import numpy as np
import ml_dtypes

ITERS = 2


mass_shift = 0.02
inject_scale = 2.0
traction_mix = 0.5
penalty_mix = 0.25
lower_edge = 0.3
upper_edge = 1.5
highest = lax.Precision.HIGHEST


def shifted(shard, axis, by):
    length = lax.axis_size(axis)
    pairs = [(i, i + by) for i in range(length) if 0 <= i + by < length]
    return lax.ppermute(shard, axis, pairs)


def shifted_2(shard, axis, by):
    length = lax.axis_size(axis)
    return lax.ppermute(shard, axis, [(i, (i + by) % length) for i in range(length)])


def tables(extent):
    node_index = jnp.arange(extent, dtype=jnp.float32) + 1.0
    basis = math.sqrt(2.0 / (extent + 1)) * jnp.sin(
        math.pi * node_index[:, None] * node_index[None, :] / (extent + 1)
    )
    eigenvalues = 2.0 - 2.0 * jnp.cos(math.pi * node_index / (extent + 1))
    return (basis, eigenvalues)


def tangent_matrix(extent):
    node_index = jnp.arange(extent, dtype=jnp.int32)
    distance = jnp.abs(node_index[:, None] - node_index[None, :])
    end_rows = ((node_index == 0) | (node_index == extent - 1)).astype(jnp.float32)
    adjacent = (distance == 1).astype(jnp.float32)
    diagonal_part = (distance == 0).astype(jnp.float32) * (2.0 - end_rows[:, None])
    return adjacent - diagonal_part


def step_weights(step_count):
    midpoint = 0.5 * (upper_edge + lower_edge)
    radius = 0.5 * (upper_edge - lower_edge)
    return [
        1.0 / (midpoint + radius * math.cos(math.pi * (2 * turn_index + 1) / (2 * step_count)))
        for turn_index in range(step_count)
    ]


def divisor(moduli, eigenvalues):
    extent = eigenvalues.shape[0]
    summed = eigenvalues[:, None, None] + eigenvalues[None, :, None] + eigenvalues[None, None, :]
    scaled = moduli[..., None, None, None] * summed + mass_shift
    return scaled.reshape(moduli.shape + (extent, extent * extent))


def body_transform(field_data, basis, paired_basis):
    extent = basis.shape[0]
    full_shape = field_data.shape
    pair_width = paired_basis.shape[0]
    sectioned = jnp.einsum("ix,bcxm->bcim", basis, field_data, precision=highest)
    sectioned = sectioned.reshape(full_shape[:-1] + (full_shape[-1] // pair_width, pair_width))
    sectioned = jnp.einsum("bcxpz,kz->bcxpk", sectioned, paired_basis, precision=highest)
    sectioned = sectioned.reshape(full_shape[:-1] + (extent, extent))
    sectioned = jnp.einsum("jy,bcxyz->bcxjz", basis, sectioned, precision=highest)
    return sectioned.reshape(full_shape)


def body_solve(right_side, scale_table, basis, paired_basis):
    return body_transform(
        body_transform(right_side, basis, paired_basis) / scale_table, basis, paired_basis
    )


f32 = jnp.float32


def np_tables(n):
    g = np.float32
    idx = np.arange(n, dtype=g) + g(1.0)
    arg = (g(math.pi) * idx[:, None]) * idx[None, :] / g(n + 1)
    q = g(math.sqrt(2.0 / (n + 1))) * np.sin(arg)
    e = g(2.0) - g(2.0) * np.cos(g(math.pi) * idx / g(n + 1))
    return q.astype(g), e.astype(g)


def consts(n):
    q, e = np_tables(n)
    h = n // 2
    p4 = np.kron(np.eye(4, dtype=np.float32), q.T)
    w = np.zeros((2, 4, h, 2, 4, h), np.float32)
    qq = q.reshape(h, 2, h, 2)
    for xl in range(4):
        w[:, xl, :, :, xl, :] = np.transpose(qq, (3, 2, 1, 0))
    wy = w.reshape(8 * h, 8 * h)
    ng = n // 4
    lane_h = np.arange(8 * h) // (4 * h)
    lane_xl = (np.arange(8 * h) // h) % 4
    lane_c = np.arange(8 * h) % h
    exy = (e[4 * np.arange(ng)[:, None] + lane_xl[None, :]] + e[2 * lane_c + lane_h][None, :]).astype(np.float32)
    ez = np.ascontiguousarray(np.broadcast_to(e[:, None], (n, 8 * h))).astype(np.float32)
    return stack_left(q), stack_right(p4), stack_right(wy), exy, ez


BF = jnp.bfloat16

def np_split3(w):
    b = ml_dtypes.bfloat16
    w1 = w.astype(b)
    r1 = w - w1.astype(np.float32)
    w2 = r1.astype(b)
    w3 = (r1 - w2.astype(np.float32)).astype(b)
    return w1, w2, w3


def stack_right(w):
    w1, w2, w3 = np_split3(w)
    return np.concatenate([w1, w2, w1, w1], 0)


def stack_left(w):
    w1, w2, w3 = np_split3(w)
    return np.concatenate([w1, w2, w1, w1], 1)


def split3(d):
    d1 = d.astype(BF)
    r1 = d - d1.astype(f32)
    d2 = r1.astype(BF)
    d3 = (r1 - d2.astype(f32)).astype(BF)
    return d1, d2, d3


def sdot(d, w6):
    d1, d2, d3 = split3(d)
    return jnp.dot(jnp.concatenate([d1, d1, d2, d3], 1), w6, preferred_element_type=f32)


def sdot_left(w6, d):
    d1, d2, d3 = split3(d)
    return jnp.dot(w6, jnp.concatenate([d1, d1, d2, d3], 0), preferred_element_type=f32)


def solve_kernel(*refs, with_faces, emit_u, emit_sides, omega, zero_lam, meta):
    it = iter(refs)
    mod_ref, f_ref = next(it), next(it)
    if with_faces:
        nbm_ref = next(it)
        lxu_ref, lxd_ref, ly_ref = (None, None, None) if zero_lam else (next(it), next(it), next(it))
        sxh_ref, sxl_ref, sylo_ref, syhi_ref, rup_ref, rdn_ref, ryp_ref, ryn_ref = (next(it) for _ in range(8))
    q_ref, p_ref, wy_ref, exy_ref, ez_ref = next(it), next(it), next(it), next(it), next(it)
    code_ref = next(it)
    o_ref = next(it) if emit_u else None
    if emit_sides:
        xh_ref, xl_ref, ylo_ref, yhi_ref = next(it), next(it), next(it), next(it)
    if with_faces and emit_sides:
        nlx_ref, nld_ref, nly_ref = next(it), next(it), next(it)
    elif with_faces:
        nlx_ref = nld_ref = nly_ref = None
    s_ref, z_ref = next(it), next(it)
    n = q_ref.shape[0]
    h = n // 2
    w2 = 2 * n
    w4 = 4 * n
    nn = f_ref.shape[-1]
    nch = nn // w2
    npair = nn // w4
    comp = pl.program_id(0)
    m = mod_ref[comp]
    q = q_ref[...]
    r = f_ref[0]
    if with_faces:
        m_up = nbm_ref[0, comp]
        m_dn = nbm_ref[1, comp]
        m_prev = nbm_ref[2, comp]
        m_next = nbm_ref[3, comp]
        has_up = nbm_ref[4, comp]
        has_dn = nbm_ref[5, comp]
        lane_x = lax.broadcasted_iota(jnp.int32, (1, nn), 1) % n
        lane_y = lax.broadcasted_iota(jnp.int32, (n, w2), 1)

        def smooth(res, lanes, width):
            left = pltpu.roll(res, 1, 1)
            right = pltpu.roll(res, width - 1, 1)
            left = jnp.where(lanes % n == 0, 0.0, left)
            right = jnp.where(lanes % n == n - 1, 0.0, right)
            diag = jnp.where((lanes % n == 0) | (lanes % n == n - 1), -1.0, -2.0)
            return res + 0.25 * ((left + right) + diag * res)

        xu = 0.0 if zero_lam else lxu_ref[0]
        res = (sxh_ref[0, 0:1, 0:nn] + rup_ref[0]) / (m + m_up) - xu
        xhi_face = (xu + omega * smooth(res, lane_x, nn)) * has_up
        xd = 0.0 if zero_lam else lxd_ref[0]
        res = (rdn_ref[0] + sxl_ref[0, 0:1, 0:nn]) / (m_dn + m) - xd
        xlo_face = (xd + omega * smooth(res, lane_x, nn)) * has_dn
        ly = 0.0 if zero_lam else ly_ref[0]
        lo = lane_y < n
        recv = jnp.concatenate([ryp_ref[0, 0, 0:n], ryn_ref[0, 0, 0:n]], 1)
        own = jnp.concatenate([sylo_ref[0, 0, 0:n], syhi_ref[0, 0, 0:n]], 1)
        res = (own + recv) / (m + jnp.where(lo, m_prev, m_next)) - ly
        yadd = ly + omega * smooth(res, lane_y, w2)
        if nlx_ref is not None:
            nlx_ref[0] = xhi_face
            nld_ref[0] = xlo_face
            nly_ref[0] = yadd
        rows = lax.broadcasted_iota(jnp.int32, (n, nn), 0)
        added = jnp.where(rows == 0, xlo_face, 0.0) + jnp.where(rows == n - 1, xhi_face, 0.0)
        lane = lane_y
        first = added[:, :w2] + jnp.where(lane < n, yadd, 0.0)
        last = added[:, nn - w2:] + jnp.where(lane >= n, yadd, 0.0)
        added = jnp.concatenate([first, added[:, w2:nn - w2], last], 1)
        r = r + (2.0 * m) * added
    a = sdot_left(q, r)
    for cp in range(npair):
        z_ref[cp * n:(cp + 1) * n, :] = a[:, cp * w4:(cp + 1) * w4]
    zo = sdot(z_ref[...], p_ref[...])
    for cp in range(npair):
        for cb in range(2):
            s_ref[(2 * cp + cb) * n:(2 * cp + cb + 1) * n, :] = zo[cp * n:(cp + 1) * n, cb * w2:(cb + 1) * w2]
    wy = wy_ref[...]
    ez = ez_ref[...]
    XG = 4
    GPI = 16

    def body(it_, carry):
        lhs = []
        for gi in range(GPI):
            g = it_ * GPI + gi
            blk = jnp.concatenate([s_ref[pl.ds(g * XG + xl, h, stride=n), :] for xl in range(XG)], 0)
            tb = blk.T
            lhs.append(jnp.concatenate([tb[:n], tb[n:]], 1))
        v = sdot(jnp.concatenate(lhs, 0), wy)
        div = jnp.concatenate([m * (exy_ref[pl.ds(it_ * GPI + gi, 1), :] + ez) + 0.02 for gi in range(GPI)], 0)
        v = v / div
        v = sdot(v, wy)
        for gi in range(GPI):
            g = it_ * GPI + gi
            vg = v[gi * n:(gi + 1) * n]
            tb = jnp.concatenate([vg[:, :w2], vg[:, w2:]], 0).T
            for xl in range(XG):
                s_ref[pl.ds(g * XG + xl, h, stride=n), :] = tb[xl * h:(xl + 1) * h]
        return carry
    lax.fori_loop(0, n // (XG * GPI), body, 0, unroll=True)
    for cp in range(npair):
        z_ref[cp * n:(cp + 1) * n, :] = jnp.concatenate(
            [s_ref[(2 * cp) * n:(2 * cp + 1) * n, :], s_ref[(2 * cp + 1) * n:(2 * cp + 2) * n, :]], 1)
    zo = sdot(z_ref[...], p_ref[...])
    b = jnp.concatenate([zo[cp * n:(cp + 1) * n, :] for cp in range(npair)], 1)
    u = sdot_left(q, b)
    if emit_u:
        o_ref[0] = u

    def slope(p0, p1, p2, p3):
        return m * (11.0 / 6.0 * p0 - 3.0 * p1 + 1.5 * p2 - p3 / 3.0)
    if emit_sides:
        m_row = jnp.full((1, nn), m, f32)
        xh_ref[0, 0:1, 0:nn] = m * u[n - 1:n] + 0.5 * slope(u[n - 1:n], u[n - 2:n - 1], u[n - 3:n - 2], u[n - 4:n - 3])
        lane_t = lax.broadcasted_iota(jnp.int32, (1, w2), 1)
        if meta:
            xh_ref[0, 0:1, nn:nn + w2] = jnp.where(lane_t < n, m, code_ref[0])
        xl_ref[0, 0:1, 0:nn] = m * u[0:1] + 0.5 * slope(u[0:1], u[1:2], u[2:3], u[3:4])
        if meta:
            xl_ref[0, 0:1, nn:nn + w2] = jnp.full((1, w2), m, f32)
        c_hi = u[:, nn - w2:]
        c_hi2 = u[:, nn - 2 * w2:nn - w2]
        s_hi = m * c_hi + 0.5 * slope(c_hi, pltpu.roll(c_hi, n, 1), c_hi2, pltpu.roll(c_hi2, n, 1))
        c_lo = u[:, :w2]
        c_lo2 = u[:, w2:2 * w2]
        s_lo = m * c_lo + 0.5 * slope(c_lo, pltpu.roll(c_lo, n, 1), c_lo2, pltpu.roll(c_lo2, n, 1))
        lane_s = lax.broadcasted_iota(jnp.int32, (n, w2), 1)
        ylo_ref[0, 0, 0:n] = s_lo[:, :n]
        yhi_ref[0, 0, 0:n] = pltpu.roll(s_hi, n, 1)[:, :n]
        if meta:
            ylo_ref[0, 0, n:n + 8] = jnp.full((8, n), m, f32)
            yhi_ref[0, 0, n:n + 8] = jnp.full((8, n), m, f32)


def kernel_sweep(rhs, moduli, code, state=None, emit_u=True, emit_sides=False, omega=0.0, meta=False):
    ncomp, n, nn = rhs.shape
    q, p4, wy, exy, ez = consts(n)
    full = lambda shp: pl.BlockSpec(shp, lambda c: (0,) * len(shp))
    comp3 = lambda shp: pl.BlockSpec((1,) + shp, lambda c: (c,) + (0,) * len(shp))
    smem = pl.BlockSpec(memory_space=pltpu.SMEM)
    in_specs = [smem, comp3((n, nn))]
    args = [moduli, rhs]
    zero_lam = state is not None and state[1] is None
    if state is not None:
        if zero_lam:
            state = state[:1] + state[4:]
            in_specs += [smem]
        else:
            in_specs += [smem, comp3((1, nn)), comp3((1, nn)), comp3((n, 2 * n))]
        in_specs += [comp3(x.shape[1:]) for x in state[-8:]]
        args += list(state)
    in_specs += [full(q.shape), full(p4.shape), full(wy.shape), full(exy.shape), full(ez.shape), smem]
    args += [q, p4, wy, exy, ez, code]
    out_specs, out_shape = [], []
    if emit_u:
        out_specs.append(comp3((n, nn)))
        out_shape.append(jax.ShapeDtypeStruct(rhs.shape, f32))
    if emit_sides:
        wx, ry = (nn + 2 * n, n + 8) if meta else (nn, n)
        out_specs += [comp3((1, wx)), comp3((1, wx)), comp3((1, ry, n)), comp3((1, ry, n))]
        out_shape += [jax.ShapeDtypeStruct((ncomp, 1, wx), f32), jax.ShapeDtypeStruct((ncomp, 1, wx), f32),
                      jax.ShapeDtypeStruct((ncomp, 1, ry, n), f32), jax.ShapeDtypeStruct((ncomp, 1, ry, n), f32)]
        if state is not None:
            out_specs += [comp3((1, nn)), comp3((1, nn)), comp3((n, 2 * n))]
            out_shape += [jax.ShapeDtypeStruct((ncomp, 1, nn), f32), jax.ShapeDtypeStruct((ncomp, 1, nn), f32),
                          jax.ShapeDtypeStruct((ncomp, n, 2 * n), f32)]
    kernel = functools.partial(solve_kernel, with_faces=state is not None, emit_u=emit_u,
                               emit_sides=emit_sides, omega=omega, zero_lam=zero_lam, meta=meta)
    return pl.pallas_call(
        kernel,
        grid=(ncomp,),
        in_specs=in_specs,
        out_specs=out_specs,
        out_shape=out_shape,
        scratch_shapes=[pltpu.VMEM((nn // 2, 2 * n), f32), pltpu.VMEM((nn // 4, 4 * n), f32)],
    )(*args)


def orient(face_field, code_table, extent):
    square = face_field.reshape(face_field.shape[:-1] + (extent, extent))
    flip_rows = (code_table % 2 == 1)[..., None, None, None]
    flip_cols = (code_table // 2 == 1)[..., None, None, None]
    square = jnp.where(flip_rows, jnp.flip(square, -2), square)
    square = jnp.where(flip_cols, jnp.flip(square, -1), square)
    return square.reshape(face_field.shape)


def face_data(solution, moduli):
    extent = solution.shape[-2]
    cube_view = solution.reshape(solution.shape[:-1] + (extent, extent))
    flat_shape = solution.shape[:-2] + (extent * extent,)

    def pack_side(planes):
        normal_slope = 11.0 / 6.0 * planes[0] - 3.0 * planes[1] + 1.5 * planes[2] - planes[3] / 3.0
        return (planes[0], moduli[..., None] * normal_slope)

    x_high = pack_side([solution[..., extent - 1 - plane_depth, :] for plane_depth in range(4)])
    x_low = pack_side([solution[..., plane_depth, :] for plane_depth in range(4)])
    y_high = pack_side(
        [
            cube_view[..., extent - 1 - plane_depth, :].reshape(flat_shape)
            for plane_depth in range(4)
        ]
    )
    y_low = pack_side(
        [cube_view[..., plane_depth, :].reshape(flat_shape) for plane_depth in range(4)]
    )
    return (x_high, x_low, y_high, y_low)


def place_faces(source_field, moduli, x_low, x_high, y_low, y_high):
    extent = source_field.shape[-2]
    added = jnp.zeros_like(source_field)
    added = added.at[..., 0, :].add(x_low)
    added = added.at[..., extent - 1, :].add(x_high)
    cube_view = added.reshape(added.shape[:-1] + (extent, extent))
    low_square = y_low.reshape(y_low.shape[:-1] + (extent, extent))
    high_square = y_high.reshape(y_high.shape[:-1] + (extent, extent))
    cube_view = cube_view.at[..., 0, :].add(low_square)
    cube_view = cube_view.at[..., extent - 1, :].add(high_square)
    added = cube_view.reshape(source_field.shape)
    return source_field + inject_scale * moduli[..., None, None] * added


def trace_update(current, side_a, side_b, moduli_a, moduli_b, omega_step, tangent):
    extent = tangent.shape[0]
    weight_a = moduli_a[..., None]
    weight_b = moduli_b[..., None]
    residue = (
        weight_a * side_a[0] + weight_b * side_b[0] + traction_mix * (side_a[1] + side_b[1])
    ) / (weight_a + weight_b) - current
    rows_view = residue.reshape(residue.shape[:-1] + (residue.shape[-1] // extent, extent))
    smoothed = rows_view + penalty_mix * jnp.einsum(
        "...z,zk->...k", rows_view, tangent, precision=highest
    )
    return current + omega_step * smoothed.reshape(residue.shape)


def flat_update(current, sum_a, sum_b, moduli_a, moduli_b, omega_step, tangent):
    extent = tangent.shape[0]
    residue = (sum_a + sum_b) / (moduli_a + moduli_b)[..., None] - current
    rows_view = residue.reshape(residue.shape[:-1] + (residue.shape[-1] // extent, extent))
    smoothed = rows_view + penalty_mix * jnp.einsum("...z,zk->...k", rows_view, tangent, precision=highest)
    return current + omega_step * smoothed.reshape(residue.shape)


def square_update(current, sum_a, sum_b, moduli_a, moduli_b, omega_step, tangent):
    residue = (sum_a + sum_b) / (moduli_a + moduli_b)[..., None, None] - current
    smoothed = residue + penalty_mix * jnp.einsum("...z,zk->...k", residue, tangent, precision=highest)
    return current + omega_step * smoothed


def shards(forcing, modulus, orient_codes):
    extent = forcing.shape[3]
    blocks = forcing.shape[1]
    flat = extent * extent
    source_field = forcing[0]
    moduli = modulus[0]
    codes_here = orient_codes[0]
    code_values = codes_here.astype(jnp.float32)
    omegas = step_weights(ITERS)
    slab_count = lax.axis_size("blk")
    slab_index = lax.axis_index("blk")
    has_up = jnp.broadcast_to((slab_index < slab_count - 1).astype(jnp.float32), (blocks, 3))
    has_down = jnp.broadcast_to((slab_index > 0).astype(jnp.float32), (blocks, 3))
    lam_x_up = lam_x_down = lam_y = [None] * blocks
    state = [None] * blocks
    for sweep in range(ITERS + 1):
        last = sweep == ITERS
        omega = omegas[sweep - 1] if sweep > 0 else 0.0
        outs = [
            kernel_sweep(source_field[b], moduli[b], code_values[b:b + 1], state[b], emit_u=last,
                         emit_sides=not last, omega=omega, meta=sweep == 0)
            for b in range(blocks)
        ]
        if last:
            return jnp.stack([o[0] for o in outs], 0)[None]
        xh, xl, ylo, yhi = (jnp.stack([o[k] for o in outs], 0) for k in range(4))
        if sweep > 0:
            lam_x_up, lam_x_down, lam_y = (jnp.stack([o[k] for o in outs], 0) for k in range(4, 7))
        upper = shifted(xl, "blk", -1)
        lower = shifted(xh, "blk", 1)
        nxt = jnp.concatenate([ylo[1:], shifted_2(ylo[:1], "face", -1)], 0)
        prv = jnp.concatenate([shifted_2(yhi[-1:], "face", 1), yhi[:-1]], 0)
        if sweep == 0:
            codes_down = lower[:, 0, 0, flat + extent].astype(jnp.int32)
            neighbour_moduli = jnp.stack(
                [upper[:, :, 0, flat], lower[:, :, 0, flat], prv[:, :, 0, extent, 0], nxt[:, :, 0, extent, 0],
                 has_up, has_down], 1
            )
        up_sum = orient(upper[:, :, 0, :flat], codes_here, extent)[:, :, None]
        down_sum = orient(lower[:, :, 0, :flat], codes_down, extent)[:, :, None]
        state = [
            (neighbour_moduli[b], lam_x_up[b], lam_x_down[b], lam_y[b], xh[b], xl[b], ylo[b], yhi[b],
             up_sum[b], down_sum[b], prv[b], nxt[b])
            for b in range(blocks)
        ]


def solution(mesh):
    placed = (P("blk", "face", None, None, None), P("blk", "face", None), P("blk", "face"))
    return jax.shard_map(
        shards,
        mesh=mesh,
        in_specs=placed,
        out_specs=P("blk", "face", None, None, None),
        check_vma=False,
    )
```
